32 devices in a mesh: shard: 2 (over core), context: 4 (over z), tensor: 4 (over y, x).
Axes of the slice: x: 2, y: 2, z: 4, core: 2. Of those that a mesh axis runs over, the one named last changes fastest.
Arguments:
- inputs: bfloat16 [2, 2048, 2048], P('shard', 'context'), may hold values from -6 to 6
- segments: int32 [2, 2048], P('shard', 'context'), may hold values from 0 to 2, as said below
- positions: int32 [2, 2048], P('shard', 'context'), may hold values from 0 to 2047, as said below
- w_q: bfloat16 [2048, 2048], P(('shard', 'context'), 'tensor'), may hold values from -0.125 to 0.125
- w_k: bfloat16 [2048, 2048], P(('shard', 'context'), 'tensor'), may hold values from -0.125 to 0.125
- w_v: bfloat16 [2048, 2048], P(('shard', 'context'), 'tensor'), may hold values from -0.125 to 0.125
- w_o: bfloat16 [2048, 2048], P(('shard', 'context'), 'tensor'), may hold values from -0.75 to 0.75
- w_gate: bfloat16 [2048, 8192], P(('shard', 'context'), 'tensor'), may hold values from -0.125 to 0.125
- w_up: bfloat16 [2048, 8192], P(('shard', 'context'), 'tensor'), may hold values from -0.125 to 0.125
- w_down: bfloat16 [2048, 8192], P(('shard', 'context'), 'tensor'), may hold values from -0.0625 to 0.0625
- g_attn: bfloat16 [2048], P(('shard', 'context')), may hold values from 0.5 to 1.5
- g_mlp: bfloat16 [2048], P(('shard', 'context')), may hold values from 0.5 to 1.5
- d_out: bfloat16 [2, 2048, 2048], P('shard', 'context'), may hold values from -6 to 6
Outputs:
- out: bfloat16 [2, 2048, 2048], P('shard', 'context')
- d_x: bfloat16 [2, 2048, 2048], P('shard', 'context')
- d_w_q: float32 [2048, 2048], P(('shard', 'context'), 'tensor')
- d_w_k: float32 [2048, 2048], P(('shard', 'context'), 'tensor')
- d_w_v: float32 [2048, 2048], P(('shard', 'context'), 'tensor')
- d_w_o: float32 [2048, 2048], P(('shard', 'context'), 'tensor')
- d_w_gate: float32 [2048, 8192], P(('shard', 'context'), 'tensor')
- d_w_up: float32 [2048, 8192], P(('shard', 'context'), 'tensor')
- d_w_down: float32 [2048, 8192], P(('shard', 'context'), 'tensor')
- d_g_attn: float32 [2048], P(('shard', 'context'))
- d_g_mlp: float32 [2048], P(('shard', 'context'))
The draws below stay inside these ranges and needn't reach their ends.
Inputs may be any that keep to these rules, and one draw needn't show every extreme that they name: In each sequence the positions are a permutation of 0 to 2047, laid out by halves of 512 tokens: with p a permutation of the context indices, device c holds either halves 2 * p(c) and 2 * p(c) + 1 in order, or halves p(c) and 7 - p(c). `segments`: segment numbers never fall as the position grows; the first position of a sequence is in segment 0, and every sequence holds exactly 3 documents.
All inputs are finite; a program needn't handle non-finite values.
Results may differ from the reference program's by a relative error of at most 0.024.
Values may be sent and summed in bfloat16 or wider, within the bound.
No kernel may reach another device: no remote copies, remote signals or barrier semaphores. Data moves between devices by JAX's collectives and lax.ppermute only.
A program may use at most 192 MiB of HBM per device.

```python
import math
import jax
import jax.numpy as jnp
from jax import lax

D = 2048
H = 32
HD = 64
FF = 8192
GROUP = 512
LEN = 2048
SEQS = 2


def packed_layout(key):
    first_key = jax.random.fold_in(key, 11)
    second_key = jax.random.fold_in(key, 12)
    third_key = jax.random.fold_in(key, 13)
    mode = jax.random.randint(first_key, (SEQS, 1), 0, 2)
    devices = LEN // GROUP
    pieces = 2 * devices
    half = GROUP // 2
    slot = jnp.arange(pieces, dtype=jnp.int32)
    device = slot // 2
    perm_keys = jax.random.split(third_key, SEQS)
    owner = jax.vmap(lambda item: jax.random.permutation(item, devices))(perm_keys).astype(jnp.int32)
    paired = owner[:, device]
    ordered = 2 * paired + (slot % 2)[None, :]
    mirrored = jnp.where((slot % 2 == 0)[None, :], paired, pieces - 1 - paired)
    piece = jnp.where(mode == 1, mirrored, ordered)
    global_pos = (piece[:, :, None] * half + jnp.arange(half, dtype=jnp.int32)[None, None, :]).reshape(SEQS, LEN).astype(jnp.int32)
    starts_count = LEN // (2 * GROUP)
    seq_keys = jax.random.split(second_key, SEQS)
    orders = jax.vmap(lambda item: jax.random.permutation(item, LEN - 1))(seq_keys)
    inner_starts = orders < starts_count
    starts = jnp.concatenate([jnp.zeros((SEQS, 1), dtype=bool), inner_starts], axis=1)
    seg_global = jnp.cumsum(starts.astype(jnp.int32), axis=1).astype(jnp.int32)
    segment = jnp.take_along_axis(seg_global, global_pos, axis=1)
    return (segment, global_pos)


def draw_segments(key, part):
    return packed_layout(key)[0]


def draw_positions(key, part):
    return packed_layout(key)[1]


def steps_of(key, dims, cuts, smallest, high):
    level, own = 1.0, jax.random.fold_in(key, 6)
    for axis_at, parts in cuts:
        draws = jnp.exp(jax.random.uniform(jax.random.fold_in(own, axis_at), (parts,), jnp.float32, smallest / len(cuts), high / len(cuts)))
        level = level * jnp.repeat(draws, dims[axis_at] // parts).reshape([-1 if axis == axis_at else 1 for axis in range(len(dims))])
    return level


def normal_values(stream_key, shape, spread, limit, cuts=(), kind=jnp.bfloat16):
    level = steps_of(stream_key, shape, cuts, -0.22, 0.18) if cuts else 1.0
    values = jax.random.normal(stream_key, shape, jnp.float32) * spread * level
    return jnp.minimum(jnp.maximum(values, -limit), limit).astype(kind)


def setup_inputs(seed: int = 0) -> dict:
    key_list = jax.random.split(jax.random.key(seed), 14)
    inputs = normal_values(key_list[0], (SEQS, LEN, D), 1.0, 6.0, ((0, 2), (1, 4)))
    segments = draw_segments(jax.random.fold_in(key_list[13], 71), 0)
    positions = draw_positions(jax.random.fold_in(key_list[13], 71), 0)
    w_q = normal_values(key_list[3], (D, D), D ** -0.5, 0.125, ((0, 8), (1, 4)))
    w_k = normal_values(key_list[4], (D, D), D ** -0.5, 0.125, ((0, 8), (1, 4)))
    w_v = normal_values(key_list[5], (D, D), D ** -0.5, 0.125, ((0, 8), (1, 4)))
    w_o = normal_values(key_list[6], (D, D), (D // 32) ** -0.5, 0.75, ((0, 8), (1, 4)))
    w_gate = normal_values(key_list[7], (D, FF), D ** -0.5, 0.125, ((0, 8), (1, 4)))
    w_up = normal_values(key_list[8], (D, FF), D ** -0.5, 0.125, ((0, 8), (1, 4)))
    w_down = normal_values(key_list[9], (D, FF), FF ** -0.5, 0.0625, ((0, 8), (1, 4)))
    g_attn = jnp.clip(1.0 + 0.1 * jax.random.normal(key_list[10], (D,), jnp.float32), 0.5, 1.5).astype(jnp.bfloat16)
    g_mlp = jnp.clip(1.0 + 0.1 * jax.random.normal(key_list[11], (D,), jnp.float32), 0.5, 1.5).astype(jnp.bfloat16)
    d_out = normal_values(key_list[12], (SEQS, LEN, D), 1.0, 6.0, ((0, 2), (1, 4)))
    return {"inputs": inputs, "segments": segments, "positions": positions, "w_q": w_q, "w_k": w_k, "w_v": w_v, "w_o": w_o, "w_gate": w_gate, "w_up": w_up, "w_down": w_down, "g_attn": g_attn, "g_mlp": g_mlp, "d_out": d_out}


EPS = 1e-05
THETA = 130000.0
NEG = -1e+30

def rounded(value):
    return lax.optimization_barrier(value.astype(jnp.bfloat16))

def rope_tables(position):
    index = jnp.arange(HD // 2, dtype=jnp.float32)
    inverse = jnp.power(jnp.float32(THETA), -2.0 * index / HD)
    angle = position.astype(jnp.float32)[:, None] * inverse[None, :]
    return (jnp.cos(angle), jnp.sin(angle))

def rotate(tensor, cosine, sine):
    half = tensor.shape[-1] // 2
    first = tensor[..., :half]
    second = tensor[..., half:]
    cosine = cosine[:, None, :]
    sine = sine[:, None, :]
    return jnp.concatenate([first * cosine - second * sine, second * cosine + first * sine], axis=-1)

def rotate_back(grad, cosine, sine):
    half = grad.shape[-1] // 2
    first = grad[..., :half]
    second = grad[..., half:]
    cosine = cosine[:, None, :]
    sine = sine[:, None, :]
    return jnp.concatenate([first * cosine + second * sine, second * cosine - first * sine], axis=-1)

def normalize(value):
    inv_rms = lax.rsqrt(lax.optimization_barrier(jnp.mean(value * value, axis=-1, keepdims=True)) + EPS)
    return (value * inv_rms, inv_rms)

def norm_back(grad, normed, inv_rms, gain):
    scaled = grad * gain.astype(jnp.float32)
    return inv_rms * (scaled - normed * lax.optimization_barrier(jnp.mean(scaled * normed, axis=-1, keepdims=True)))

def masked_scores(query_block, key_f, seg_block, pos_block, segment, position):
    scale = 1.0 / math.sqrt(HD)
    scores = jnp.einsum('qhd,khd->hqk', query_block.astype(jnp.float32), key_f) * scale
    allowed = (seg_block[:, None] == segment[None, :]) & (position[None, :] <= pos_block[:, None])
    return (jnp.where(allowed[None], scores, NEG), allowed)

def attend(query, keys, values, segment, position):
    block = GROUP // 2
    count = LEN // block
    key_f = keys.astype(jnp.float32)
    value_f = values.astype(jnp.float32)

    def one_block(items):
        query_block, seg_block, pos_block = items
        scores, allowed = masked_scores(query_block, key_f, seg_block, pos_block, segment, position)
        peak = lax.optimization_barrier(jnp.max(scores, axis=-1))
        weights = jnp.where(allowed[None], jnp.exp(scores - peak[..., None]), 0.0)
        total = lax.optimization_barrier(jnp.sum(weights, axis=-1))
        mixed = jnp.einsum('hqk,khd->qhd', rounded(weights).astype(jnp.float32), value_f)
        mixed = mixed / total.T[:, :, None]
        return (mixed.astype(jnp.bfloat16), peak + jnp.log(total))
    outputs, log_totals = lax.map(one_block, (query.reshape(count, block, H, HD), segment.reshape(count, block), position.reshape(count, block)))
    return (outputs.reshape(LEN, H, HD), log_totals)

def attend_back(query, keys, values, segment, position, outputs, grad_out, log_totals):
    block = GROUP // 2
    count = LEN // block
    scale = 1.0 / math.sqrt(HD)
    key_f = keys.astype(jnp.float32)
    value_f = values.astype(jnp.float32)

    def one_step(carry, items):
        grad_key, grad_value = carry
        query_block, out_block, grad_block, seg_block, pos_block, log_block = items
        scores, allowed = masked_scores(query_block, key_f, seg_block, pos_block, segment, position)
        probs = jnp.where(allowed[None], jnp.exp(scores - log_block[..., None]), 0.0)
        grad_f = grad_block.astype(jnp.float32)
        grad_value = grad_value + jnp.einsum('hqk,qhd->khd', rounded(probs).astype(jnp.float32), grad_f)
        grad_probs = jnp.einsum('qhd,khd->hqk', grad_f, value_f)
        inner = lax.optimization_barrier(jnp.sum(grad_f * out_block.astype(jnp.float32), axis=-1)).T
        grad_scores = rounded(probs * (grad_probs - inner[..., None]) * scale).astype(jnp.float32)
        grad_query = jnp.einsum('hqk,khd->qhd', grad_scores, key_f)
        grad_key = grad_key + jnp.einsum('hqk,qhd->khd', grad_scores, query_block.astype(jnp.float32))
        return ((grad_key, grad_value), grad_query)
    zeros = jnp.zeros((LEN, H, HD), jnp.float32)
    items = (query.reshape(count, block, H, HD), outputs.reshape(count, block, H, HD), grad_out.reshape(count, block, H, HD), segment.reshape(count, block), position.reshape(count, block), log_totals)
    (grad_key, grad_value), grad_query = lax.scan(one_step, (zeros, zeros), items)
    return (grad_query.reshape(LEN, H, HD), grad_key, grad_value)

def reference(inputs, segments, positions, w_q, w_k, w_v, w_o, w_gate, w_up, w_down, g_attn, g_mlp, d_out):
    f32 = jnp.float32
    bf16 = jnp.bfloat16
    grad_wq = jnp.zeros((D, D), f32)
    grad_wk = jnp.zeros((D, D), f32)
    grad_wv = jnp.zeros((D, D), f32)
    grad_wo = jnp.zeros((D, D), f32)
    grad_wgate = jnp.zeros((D, FF), f32)
    grad_wup = jnp.zeros((D, FF), f32)
    grad_wdown = jnp.zeros((D, FF), f32)
    grad_gattn = jnp.zeros((D,), f32)
    grad_gmlp = jnp.zeros((D,), f32)
    out_list = []
    dx_list = []
    for sequence in range(SEQS):
        tokens = inputs[sequence]
        segment = segments[sequence]
        position = positions[sequence]
        resid1 = tokens.astype(f32)
        norm1, inv1 = normalize(resid1)
        h1 = (norm1 * g_attn.astype(f32)).astype(bf16)
        cosine, sine = rope_tables(position)
        query = rotate(jnp.dot(h1, w_q, preferred_element_type=f32).reshape(LEN, H, HD), cosine, sine).astype(bf16)
        keys = rotate(jnp.dot(h1, w_k, preferred_element_type=f32).reshape(LEN, H, HD), cosine, sine).astype(bf16)
        values = jnp.dot(h1, w_v, preferred_element_type=f32).astype(bf16).reshape(LEN, H, HD)
        attended, log_totals = attend(query, keys, values, segment, position)
        attended_flat = attended.reshape(LEN, D)
        resid2 = resid1 + jnp.dot(attended_flat, w_o.T, preferred_element_type=f32)
        norm2, inv2 = normalize(resid2)
        h2 = (norm2 * g_mlp.astype(f32)).astype(bf16)
        gate = jnp.dot(h2, w_gate, preferred_element_type=f32)
        up = jnp.dot(h2, w_up, preferred_element_type=f32)
        active = jax.nn.silu(gate)
        hidden = (active * up).astype(bf16)
        out_list.append((resid2 + jnp.dot(hidden, w_down.T, preferred_element_type=f32)).astype(bf16))
        grad_y = d_out[sequence]
        grad_hidden = jnp.dot(grad_y, w_down, preferred_element_type=f32)
        sigma = jax.nn.sigmoid(gate)
        grad_gate = (grad_hidden * up * sigma * (1.0 + gate * (1.0 - sigma))).astype(bf16)
        grad_up = (grad_hidden * active).astype(bf16)
        grad_h2 = jnp.dot(grad_gate, w_gate.T, preferred_element_type=f32) + jnp.dot(grad_up, w_up.T, preferred_element_type=f32)
        grad_gmlp = grad_gmlp + lax.optimization_barrier(jnp.sum(grad_h2 * norm2, axis=0))
        grad_resid = grad_y.astype(f32) + norm_back(grad_h2, norm2, inv2, g_mlp)
        grad_resid_b = grad_resid.astype(bf16)
        grad_attended = jnp.dot(grad_resid_b, w_o, preferred_element_type=f32).astype(bf16).reshape(LEN, H, HD)
        grad_query, grad_keys, grad_values = attend_back(query, keys, values, segment, position, attended, grad_attended, log_totals)
        grad_qin = rotate_back(grad_query, cosine, sine).astype(bf16).reshape(LEN, D)
        grad_kin = rotate_back(grad_keys, cosine, sine).astype(bf16).reshape(LEN, D)
        grad_vin = grad_values.astype(bf16).reshape(LEN, D)
        grad_h1 = jnp.dot(grad_qin, w_q.T, preferred_element_type=f32) + jnp.dot(grad_kin, w_k.T, preferred_element_type=f32) + jnp.dot(grad_vin, w_v.T, preferred_element_type=f32)
        grad_gattn = grad_gattn + lax.optimization_barrier(jnp.sum(grad_h1 * norm1, axis=0))
        dx_list.append((grad_resid + norm_back(grad_h1, norm1, inv1, g_attn)).astype(bf16))
        grad_wq = grad_wq + jnp.dot(h1.T, grad_qin, preferred_element_type=f32)
        grad_wk = grad_wk + jnp.dot(h1.T, grad_kin, preferred_element_type=f32)
        grad_wv = grad_wv + jnp.dot(h1.T, grad_vin, preferred_element_type=f32)
        grad_wo = grad_wo + jnp.dot(grad_resid_b.T, attended_flat, preferred_element_type=f32)
        grad_wgate = grad_wgate + jnp.dot(h2.T, grad_gate, preferred_element_type=f32)
        grad_wup = grad_wup + jnp.dot(h2.T, grad_up, preferred_element_type=f32)
        grad_wdown = grad_wdown + jnp.dot(grad_y.T, hidden, preferred_element_type=f32)
    return (jnp.stack(out_list), jnp.stack(dx_list), grad_wq, grad_wk, grad_wv, grad_wo, grad_wgate, grad_wup, grad_wdown, grad_gattn, grad_gmlp)
```

```python
import math

import jax
import jax.numpy as jnp
from jax import lax
from jax.sharding import PartitionSpec as P

HD = 64


EPS = 1e-05
THETA = 130000.0
NEG = -1e30
ROWS = ("shard", "context")


def passed_along(value, axis, steps):
    count = lax.axis_size(axis)
    pairs = [(source, (source + steps) % count) for source in range(count)]
    return lax.ppermute(value, axis, pairs)


def rope_tables(position):
    index = jnp.arange(HD // 2, dtype=jnp.float32)
    inverse = jnp.power(jnp.float32(THETA), -2.0 * index / HD)
    angle = position.astype(jnp.float32)[:, None] * inverse[None, :]
    return (jnp.cos(angle), jnp.sin(angle))


def rotate(tensor, cosine, sine):
    half = tensor.shape[-1] // 2
    first = tensor[..., :half]
    second = tensor[..., half:]
    cosine = cosine[:, None, :]
    sine = sine[:, None, :]
    return jnp.concatenate(
        [first * cosine - second * sine, second * cosine + first * sine], axis=-1
    )


def rotate_back(grad, cosine, sine):
    half = grad.shape[-1] // 2
    first = grad[..., :half]
    second = grad[..., half:]
    cosine = cosine[:, None, :]
    sine = sine[:, None, :]
    return jnp.concatenate(
        [first * cosine + second * sine, second * cosine - first * sine], axis=-1
    )


def normalize(value):
    inv_rms = lax.rsqrt(jnp.mean(value * value, axis=-1, keepdims=True) + EPS)
    return (value * inv_rms, inv_rms)


def norm_back(grad, normed, inv_rms, gain):
    scaled = grad * gain.astype(jnp.float32)
    return inv_rms * (scaled - normed * jnp.mean(scaled * normed, axis=-1, keepdims=True))


def contract_last(left, right):
    return lax.dot_general(
        left, right, (((1,), (1,)), ((), ())), preferred_element_type=jnp.float32
    )


def contract_first(left, right):
    return lax.dot_general(
        left, right, (((0,), (0,)), ((), ())), preferred_element_type=jnp.float32
    )


def half_of(value, bit):
    size = value.shape[0] // 2
    return lax.dynamic_slice_in_dim(value, bit * size, size, axis=0)


def joined(mine, other, bit):
    low = jnp.where(bit == 0, mine, other)
    high = jnp.where(bit == 0, other, mine)
    return jnp.concatenate([low, high], axis=0)


def tensor_total(partial_sum):
    count = lax.axis_size("tensor")
    rows = partial_sum.shape[0]
    if count != 4 or rows % 8:
        return lax.psum(partial_sum.astype(jnp.bfloat16), "tensor").astype(jnp.float32)
    f32 = jnp.float32
    bf16 = jnp.bfloat16
    index = lax.axis_index("tensor")
    x_bit = index % 2
    y_bit = index // 2
    x_pairs = [(i, i ^ 1) for i in range(4)]
    y_pairs = [(i, i ^ 2) for i in range(4)]

    def swap(value, pairs):
        return lax.ppermute(value.astype(bf16), "tensor", pairs).astype(f32)

    first = partial_sum[: rows // 2]
    second = partial_sum[rows // 2 :]
    first = half_of(first, x_bit) + swap(half_of(first, 1 - x_bit), x_pairs)
    second = half_of(second, y_bit) + swap(half_of(second, 1 - y_bit), y_pairs)
    first = half_of(first, y_bit) + swap(half_of(first, 1 - y_bit), y_pairs)
    second = half_of(second, x_bit) + swap(half_of(second, 1 - x_bit), x_pairs)
    first = first.astype(bf16)
    second = second.astype(bf16)
    first = joined(first, lax.ppermute(first, "tensor", y_pairs), y_bit)
    second = joined(second, lax.ppermute(second, "tensor", x_pairs), x_bit)
    first = joined(first, lax.ppermute(first, "tensor", x_pairs), x_bit)
    second = joined(second, lax.ppermute(second, "tensor", y_pairs), y_bit)
    return jnp.concatenate([first, second], axis=0).astype(f32)


def rows_total(grad):
    staged = lax.psum_scatter(grad.astype(jnp.bfloat16), "shard", scatter_dimension=0, tiled=True)
    return lax.psum_scatter(staged, "context", scatter_dimension=0, tiled=True).astype(jnp.float32)


def pass_grads(grad_key, grad_value):
    return (
        passed_along(grad_key.astype(jnp.bfloat16), "context", 1).astype(grad_key.dtype),
        passed_along(grad_value.astype(jnp.bfloat16), "context", 1).astype(grad_value.dtype),
    )


def key_scores(query_heads, query_seg, query_pos, piece):
    key_flat, value_flat, key_seg, key_pos = piece
    heads = query_heads.shape[1]
    key_heads = key_flat.reshape(key_flat.shape[0], heads, HD)
    value_heads = value_flat.reshape(value_flat.shape[0], heads, HD)
    scores = jnp.einsum(
        "qhd,khd->hqk", query_heads, key_heads, preferred_element_type=jnp.float32
    ) * (1.0 / math.sqrt(HD))
    allowed = (query_seg[:, None] == key_seg[None, :]) & (key_pos[None, :] <= query_pos[:, None])
    return (jnp.where(allowed[None], scores, NEG), allowed, key_heads, value_heads)


def forward_fold(stats, piece, query_heads, query_seg, query_pos):
    peak, total, accum = stats
    scores, allowed, key_heads, value_heads = key_scores(query_heads, query_seg, query_pos, piece)
    new_peak = jnp.maximum(peak, jnp.max(scores, axis=-1))
    weights = jnp.where(allowed[None], jnp.exp(scores - new_peak[..., None]), 0.0)
    factor = jnp.exp(peak - new_peak)
    total = total * factor + jnp.sum(weights, axis=-1)
    accum = accum * factor[..., None] + jnp.einsum(
        "hqk,khd->hqd",
        weights.astype(jnp.bfloat16),
        value_heads,
        preferred_element_type=jnp.float32,
    )
    return (new_peak, total, accum)


def backward_piece(piece, query_heads, grad_heads, log_total, inner, query_seg, query_pos):
    scores, allowed, key_heads, value_heads = key_scores(query_heads, query_seg, query_pos, piece)
    probs = jnp.where(allowed[None], jnp.exp(scores - log_total[..., None]), 0.0)
    grad_value = jnp.einsum(
        "hqk,qhd->khd", probs.astype(jnp.bfloat16), grad_heads, preferred_element_type=jnp.float32
    )
    grad_probs = jnp.einsum(
        "qhd,khd->hqk", grad_heads, value_heads, preferred_element_type=jnp.float32
    )
    grad_scores = (probs * (grad_probs - inner[..., None]) * (1.0 / math.sqrt(HD))).astype(
        jnp.bfloat16
    )
    grad_query = jnp.einsum(
        "hqk,khd->qhd", grad_scores, key_heads, preferred_element_type=jnp.float32
    )
    grad_key = jnp.einsum(
        "hqk,qhd->khd", grad_scores, query_heads, preferred_element_type=jnp.float32
    )
    key_rows = grad_key.shape[0]
    return (grad_query, grad_key.reshape(key_rows, -1), grad_value.reshape(key_rows, -1))


class RingAttention:
    def __init__(self, query, key_flat, value_flat, segment, position, cosine, sine):
        self.query = query
        self.piece = (key_flat, value_flat, segment, position)
        self.segment = segment
        self.position = position
        self.cosine = cosine
        self.sine = sine

    def forward(self):
        f32 = jnp.float32
        query, segment, position = self.query, self.segment, self.position
        rows, heads = query.shape[0], query.shape[1]
        start_stats = (
            jnp.full((heads, rows), NEG, f32),
            jnp.zeros((heads, rows), f32),
            jnp.zeros((heads, rows, HD), f32),
        )
        stats = forward_fold(start_stats, self.piece, query, segment, position)

        def cycle_turn(index, carry):
            moving, current = carry
            moving = passed_along(moving, "context", 1)
            current = forward_fold(current, moving, query, segment, position)
            return (moving, current)

        peak, total, accum = lax.fori_loop(
            0, lax.axis_size("context") - 1, cycle_turn, (self.piece, stats)
        )[1]
        self.attended = jnp.transpose(accum / total[..., None], (1, 0, 2)).astype(jnp.bfloat16)
        self.log_total = peak + jnp.log(total)
        return self.attended

    def backward(self, grad_heads):
        bf16 = jnp.bfloat16
        query, segment, position = self.query, self.segment, self.position
        rows, heads = query.shape[0], query.shape[1]
        inner = jnp.sum(grad_heads.astype(jnp.float32) * self.attended.astype(jnp.float32), axis=-1).T

        def piece_grads(piece):
            return backward_piece(piece, query, grad_heads, self.log_total, inner, segment, position)

        grad_query, grad_key, grad_value = piece_grads(self.piece)

        def grad_turn(index, carry):
            moving, acc_query, acc_key, acc_value = carry
            moving = passed_along(moving, "context", 1)
            acc_key, acc_value = pass_grads(acc_key, acc_value)
            part_query, part_key, part_value = piece_grads(moving)
            return (moving, acc_query + part_query, acc_key + part_key, acc_value + part_value)

        carried = lax.fori_loop(
            0,
            lax.axis_size("context") - 1,
            grad_turn,
            (self.piece, grad_query, grad_key, grad_value),
        )
        grad_query = carried[1]
        grad_key, grad_value = pass_grads(carried[2], carried[3])
        grad_qin = rotate_back(grad_query, self.cosine, self.sine).astype(bf16)
        grad_kin = rotate_back(grad_key.reshape(rows, heads, HD), self.cosine, self.sine).astype(bf16)
        grad_vin = grad_value.astype(bf16).reshape(rows, heads, HD)
        return grad_qin, grad_kin, grad_vin


class HeadAttention:
    BLOCK = 512

    def __init__(self, query, key_heads, value_heads, segment, position, cosine, sine):
        ways = lax.axis_size("context")
        rows, heads = query.shape[0], query.shape[1]
        self.ways = ways
        self.rows = rows
        self.heads = heads
        self.group = heads // ways
        stacked = jnp.stack([query, key_heads, value_heads], axis=1)
        stacked = stacked.reshape(rows, 3, ways, self.group, HD)
        stacked = lax.all_to_all(stacked, "context", 2, 0, tiled=True)
        stacked = stacked.reshape(rows * ways, 3, self.group, HD)
        self.query = stacked[:, 0]
        self.keys = stacked[:, 1]
        self.values = stacked[:, 2]
        tags = jnp.stack([segment, position], axis=0)[None]
        tags = jnp.broadcast_to(tags, (ways, 2, rows))
        tags = lax.all_to_all(tags, "context", 0, 0, tiled=True)
        tags = jnp.transpose(tags, (1, 0, 2)).reshape(2, rows * ways)
        self.seg_all = tags[0]
        self.pos_all = tags[1]
        self.cos_all, self.sin_all = rope_tables(self.pos_all)

    def _blocks(self):
        total = self.rows * self.ways
        block = min(self.BLOCK, total)
        return [(start, block) for start in range(0, total, block)]

    def _scores(self, start, size):
        query = lax.dynamic_slice_in_dim(self.query, start, size, axis=0)
        seg_q = lax.dynamic_slice_in_dim(self.seg_all, start, size, axis=0)
        pos_q = lax.dynamic_slice_in_dim(self.pos_all, start, size, axis=0)
        scores = jnp.einsum(
            "qhd,khd->hqk", query, self.keys, preferred_element_type=jnp.float32
        ) * (1.0 / math.sqrt(HD))
        allowed = (seg_q[:, None] == self.seg_all[None, :]) & (
            self.pos_all[None, :] <= pos_q[:, None]
        )
        return query, jnp.where(allowed[None], scores, NEG), allowed

    def forward(self):
        outs = []
        logs = []
        for start, size in self._blocks():
            _, scores, allowed = self._scores(start, size)
            peak = jnp.max(scores, axis=-1)
            weights = jnp.where(allowed[None], jnp.exp(scores - peak[..., None]), 0.0)
            total = jnp.sum(weights, axis=-1)
            mixed = jnp.einsum(
                "hqk,khd->qhd",
                weights.astype(jnp.bfloat16),
                self.values,
                preferred_element_type=jnp.float32,
            )
            outs.append((mixed / total.T[:, :, None]).astype(jnp.bfloat16))
            logs.append(peak + jnp.log(total))
        self.attended = jnp.concatenate(outs, axis=0)
        self.log_total = jnp.concatenate(logs, axis=1)
        back = self.attended.reshape(self.rows * self.ways, 1, self.group, HD)
        back = lax.all_to_all(back, "context", 0, 1, tiled=True)
        return back.reshape(self.rows, self.heads, HD)

    def backward(self, grad_heads):
        f32 = jnp.float32
        bf16 = jnp.bfloat16
        scale = 1.0 / math.sqrt(HD)
        grad = grad_heads.reshape(self.rows, self.ways, self.group, HD)
        grad = lax.all_to_all(grad, "context", 1, 0, tiled=True)
        grad = grad.reshape(self.rows * self.ways, self.group, HD)
        inner = jnp.sum(grad.astype(f32) * self.attended.astype(f32), axis=-1).T
        grad_key = jnp.zeros(self.keys.shape, f32)
        grad_value = jnp.zeros(self.values.shape, f32)
        grad_queries = []
        for start, size in self._blocks():
            query, scores, allowed = self._scores(start, size)
            log_block = lax.dynamic_slice_in_dim(self.log_total, start, size, axis=1)
            inner_block = lax.dynamic_slice_in_dim(inner, start, size, axis=1)
            grad_block = lax.dynamic_slice_in_dim(grad, start, size, axis=0)
            probs = jnp.where(allowed[None], jnp.exp(scores - log_block[..., None]), 0.0)
            grad_value = grad_value + jnp.einsum(
                "hqk,qhd->khd", probs.astype(bf16), grad_block, preferred_element_type=f32
            )
            grad_probs = jnp.einsum(
                "qhd,khd->hqk", grad_block, self.values, preferred_element_type=f32
            )
            grad_scores = (probs * (grad_probs - inner_block[..., None]) * scale).astype(bf16)
            grad_queries.append(
                jnp.einsum("hqk,khd->qhd", grad_scores, self.keys, preferred_element_type=f32)
            )
            grad_key = grad_key + jnp.einsum(
                "hqk,qhd->khd", grad_scores, query, preferred_element_type=f32
            )
        grad_query = jnp.concatenate(grad_queries, axis=0)
        grad_qin = rotate_back(grad_query, self.cos_all, self.sin_all).astype(bf16)
        grad_kin = rotate_back(grad_key, self.cos_all, self.sin_all).astype(bf16)
        grad_vin = grad_value.astype(bf16)
        stacked = jnp.stack([grad_qin, grad_kin, grad_vin], axis=1)
        stacked = stacked.reshape(self.rows * self.ways, 3, 1, self.group, HD)
        stacked = lax.all_to_all(stacked, "context", 0, 2, tiled=True)
        stacked = stacked.reshape(self.rows, 3, self.heads, HD)
        return stacked[:, 0], stacked[:, 1], stacked[:, 2]


def on_device(
    inputs, segments, positions, w_q, w_k, w_v, w_o, w_gate, w_up, w_down, g_attn, g_mlp, d_out
):
    f32 = jnp.float32
    bf16 = jnp.bfloat16
    rows = inputs.shape[1]
    width = inputs.shape[2]
    cols = w_q.shape[1]
    tokens = inputs.reshape(rows, width)
    segment = segments.reshape(rows)
    position = positions.reshape(rows)
    full_qkv = lax.all_gather(jnp.concatenate([w_q, w_k, w_v], axis=1), ROWS, axis=0, tiled=True)
    full_o = lax.all_gather(w_o, ROWS, axis=0, tiled=True)
    gains = lax.all_gather(
        jnp.concatenate([g_attn, g_mlp])[None], ROWS, axis=0, tiled=True
    )
    gain_attn = gains[:, : g_attn.shape[0]].reshape(width)
    gain_mlp = gains[:, g_attn.shape[0] :].reshape(width)
    full_gate = lax.all_gather(w_gate, ROWS, axis=0, tiled=True)
    full_up = lax.all_gather(w_up, ROWS, axis=0, tiled=True)
    full_down = lax.all_gather(w_down, ROWS, axis=0, tiled=True)
    heads = cols // HD
    cosine, sine = rope_tables(position)
    resid1 = tokens.astype(f32)
    norm1, inv1 = normalize(resid1)
    h1 = (norm1 * gain_attn.astype(f32)).astype(bf16)
    projected = jnp.dot(h1, full_qkv, preferred_element_type=f32)
    query = rotate(projected[:, :cols].reshape(rows, heads, HD), cosine, sine).astype(bf16)
    key_heads = rotate(projected[:, cols : 2 * cols].reshape(rows, heads, HD), cosine, sine).astype(
        bf16
    )
    value_heads = projected[:, 2 * cols :].astype(bf16).reshape(rows, heads, HD)
    if heads % lax.axis_size("context") == 0:
        attention = HeadAttention(query, key_heads, value_heads, segment, position, cosine, sine)
    else:
        attention = RingAttention(
            query,
            key_heads.reshape(rows, cols),
            value_heads.reshape(rows, cols),
            segment,
            position,
            cosine,
            sine,
        )
    attended = attention.forward()
    attended_flat = attended.reshape(rows, cols)
    resid2 = resid1 + tensor_total(contract_last(attended_flat, full_o))
    norm2, inv2 = normalize(resid2)
    h2_part = (norm2 * gain_mlp.astype(f32)).astype(bf16)
    gate = jnp.dot(h2_part, full_gate, preferred_element_type=f32)
    up = jnp.dot(h2_part, full_up, preferred_element_type=f32)
    active = jax.nn.silu(gate)
    hidden = (active * up).astype(bf16)
    grad_y = d_out.reshape(rows, width)
    reduced_down = rows_total(contract_first(grad_y, hidden))
    result = (resid2 + tensor_total(contract_last(hidden, full_down))).astype(bf16)
    grad_hidden = jnp.dot(grad_y, full_down, preferred_element_type=f32)
    sigma = jax.nn.sigmoid(gate)
    grad_gate = (grad_hidden * up * sigma * (1.0 + gate * (1.0 - sigma))).astype(bf16)
    grad_up = (grad_hidden * active).astype(bf16)
    reduced_gate = rows_total(contract_first(h2_part, grad_gate))
    reduced_up = rows_total(contract_first(h2_part, grad_up))
    grad_h2 = tensor_total(contract_last(grad_gate, full_gate) + contract_last(grad_up, full_up))
    grad_gmlp = jnp.sum(grad_h2 * norm2, axis=0)
    grad_resid = grad_y.astype(f32) + norm_back(grad_h2, norm2, inv2, gain_mlp)
    grad_resid_part = grad_resid.astype(bf16)
    reduced_o = rows_total(contract_first(grad_resid_part, attended_flat))
    grad_heads = (
        jnp.dot(grad_resid_part, full_o, preferred_element_type=f32)
        .astype(bf16)
        .reshape(rows, heads, HD)
    )
    grad_qin, grad_kin, grad_vin = attention.backward(grad_heads)
    grad_qkv = jnp.concatenate(
        [grad_qin.reshape(rows, cols), grad_kin.reshape(rows, cols), grad_vin.reshape(rows, cols)],
        axis=1,
    )
    grad_h1 = tensor_total(contract_last(grad_qkv, full_qkv))
    grad_gattn = jnp.sum(grad_h1 * norm1, axis=0)
    grad_x_part = (grad_resid + norm_back(grad_h1, norm1, inv1, gain_attn)).astype(bf16)
    reduced_qkv = rows_total(contract_first(h1, grad_qkv))
    reduced_gains = lax.psum_scatter(
        jnp.stack([grad_gattn, grad_gmlp], axis=1), ROWS, scatter_dimension=0, tiled=True
    )
    return (
        result.reshape(1, rows, width),
        grad_x_part.reshape(1, rows, width),
        reduced_qkv[:, :cols],
        reduced_qkv[:, cols : 2 * cols],
        reduced_qkv[:, 2 * cols :],
        reduced_o,
        reduced_gate,
        reduced_up,
        reduced_down,
        reduced_gains[:, 0],
        reduced_gains[:, 1],
    )


def solution(mesh):
    placed = (
        P("shard", "context", None),
        P("shard", "context"),
        P("shard", "context"),
        P(ROWS, "tensor"),
        P(ROWS, "tensor"),
        P(ROWS, "tensor"),
        P(ROWS, "tensor"),
        P(ROWS, "tensor"),
        P(ROWS, "tensor"),
        P(ROWS, "tensor"),
        P(ROWS),
        P(ROWS),
        P("shard", "context", None),
    )
    return jax.shard_map(
        on_device,
        mesh=mesh,
        in_specs=placed,
        out_specs=(
            P("shard", "context", None),
            P("shard", "context", None),
            P(ROWS, "tensor"),
            P(ROWS, "tensor"),
            P(ROWS, "tensor"),
            P(ROWS, "tensor"),
            P(ROWS, "tensor"),
            P(ROWS, "tensor"),
            P(ROWS, "tensor"),
            P(ROWS),
            P(ROWS),
        ),
        check_vma=False,
    )
```

```python
import math

import jax
import jax.numpy as jnp
from jax import lax
from jax.sharding import PartitionSpec as P

HD = 64


EPS = 1e-05
THETA = 130000.0
NEG = -1e30
ROWS = ("shard", "context")


def passed_along(value, axis, steps):
    count = lax.axis_size(axis)
    pairs = [(source, (source + steps) % count) for source in range(count)]
    return lax.ppermute(value, axis, pairs)


def rope_tables(position):
    index = jnp.arange(HD // 2, dtype=jnp.float32)
    inverse = jnp.power(jnp.float32(THETA), -2.0 * index / HD)
    angle = position.astype(jnp.float32)[:, None] * inverse[None, :]
    return (jnp.cos(angle), jnp.sin(angle))


def rotate(tensor, cosine, sine):
    half = tensor.shape[-1] // 2
    first = tensor[..., :half]
    second = tensor[..., half:]
    cosine = cosine[:, None, :]
    sine = sine[:, None, :]
    return jnp.concatenate(
        [first * cosine - second * sine, second * cosine + first * sine], axis=-1
    )


def rotate_back(grad, cosine, sine):
    half = grad.shape[-1] // 2
    first = grad[..., :half]
    second = grad[..., half:]
    cosine = cosine[:, None, :]
    sine = sine[:, None, :]
    return jnp.concatenate(
        [first * cosine + second * sine, second * cosine - first * sine], axis=-1
    )


def normalize(value):
    inv_rms = lax.rsqrt(jnp.mean(value * value, axis=-1, keepdims=True) + EPS)
    return (value * inv_rms, inv_rms)


def norm_back(grad, normed, inv_rms, gain):
    scaled = grad * gain.astype(jnp.float32)
    return inv_rms * (scaled - normed * jnp.mean(scaled * normed, axis=-1, keepdims=True))


def contract_last(left, right):
    return lax.dot_general(
        left, right, (((1,), (1,)), ((), ())), preferred_element_type=jnp.float32
    )


def contract_first(left, right):
    return lax.dot_general(
        left, right, (((0,), (0,)), ((), ())), preferred_element_type=jnp.float32
    )


def half_of(value, bit):
    size = value.shape[0] // 2
    return lax.dynamic_slice_in_dim(value, bit * size, size, axis=0)


def joined(mine, other, bit):
    low = jnp.where(bit == 0, mine, other)
    high = jnp.where(bit == 0, other, mine)
    return jnp.concatenate([low, high], axis=0)


def tensor_total(partial_sum):
    count = lax.axis_size("tensor")
    rows = partial_sum.shape[0]
    if count != 4 or rows % 8:
        return lax.psum(partial_sum.astype(jnp.bfloat16), "tensor").astype(jnp.float32)
    f32 = jnp.float32
    bf16 = jnp.bfloat16
    index = lax.axis_index("tensor")
    x_bit = index % 2
    y_bit = index // 2
    x_pairs = [(i, i ^ 1) for i in range(4)]
    y_pairs = [(i, i ^ 2) for i in range(4)]

    def swap(value, pairs):
        return lax.ppermute(value.astype(bf16), "tensor", pairs).astype(f32)

    first = partial_sum[: rows // 2]
    second = partial_sum[rows // 2 :]
    first = half_of(first, x_bit) + swap(half_of(first, 1 - x_bit), x_pairs)
    second = half_of(second, y_bit) + swap(half_of(second, 1 - y_bit), y_pairs)
    first = half_of(first, y_bit) + swap(half_of(first, 1 - y_bit), y_pairs)
    second = half_of(second, x_bit) + swap(half_of(second, 1 - x_bit), x_pairs)
    first = first.astype(bf16)
    second = second.astype(bf16)
    first = joined(first, lax.ppermute(first, "tensor", y_pairs), y_bit)
    second = joined(second, lax.ppermute(second, "tensor", x_pairs), x_bit)
    first = joined(first, lax.ppermute(first, "tensor", x_pairs), x_bit)
    second = joined(second, lax.ppermute(second, "tensor", y_pairs), y_bit)
    return jnp.concatenate([first, second], axis=0).astype(f32)


def chip_total(grad):
    return lax.psum_scatter(grad.astype(jnp.bfloat16), "shard", scatter_dimension=0, tiled=True)


def line_total(staged):
    return lax.psum_scatter(staged, "context", scatter_dimension=0, tiled=True).astype(jnp.float32)


def rows_total(grad):
    return line_total(chip_total(grad))


def pass_grads(grad_key, grad_value):
    return (
        passed_along(grad_key.astype(jnp.bfloat16), "context", 1).astype(grad_key.dtype),
        passed_along(grad_value.astype(jnp.bfloat16), "context", 1).astype(grad_value.dtype),
    )


def key_scores(query_heads, query_seg, query_pos, piece):
    key_flat, value_flat, key_seg, key_pos = piece
    heads = query_heads.shape[1]
    key_heads = key_flat.reshape(key_flat.shape[0], heads, HD)
    value_heads = value_flat.reshape(value_flat.shape[0], heads, HD)
    scores = jnp.einsum(
        "qhd,khd->hqk", query_heads, key_heads, preferred_element_type=jnp.float32
    ) * (1.0 / math.sqrt(HD))
    allowed = (query_seg[:, None] == key_seg[None, :]) & (key_pos[None, :] <= query_pos[:, None])
    return (jnp.where(allowed[None], scores, NEG), allowed, key_heads, value_heads)


def forward_fold(stats, piece, query_heads, query_seg, query_pos):
    peak, total, accum = stats
    scores, allowed, key_heads, value_heads = key_scores(query_heads, query_seg, query_pos, piece)
    new_peak = jnp.maximum(peak, jnp.max(scores, axis=-1))
    weights = jnp.where(allowed[None], jnp.exp(scores - new_peak[..., None]), 0.0)
    factor = jnp.exp(peak - new_peak)
    total = total * factor + jnp.sum(weights, axis=-1)
    accum = accum * factor[..., None] + jnp.einsum(
        "hqk,khd->hqd",
        weights.astype(jnp.bfloat16),
        value_heads,
        preferred_element_type=jnp.float32,
    )
    return (new_peak, total, accum)


def backward_piece(piece, query_heads, grad_heads, log_total, inner, query_seg, query_pos):
    scores, allowed, key_heads, value_heads = key_scores(query_heads, query_seg, query_pos, piece)
    probs = jnp.where(allowed[None], jnp.exp(scores - log_total[..., None]), 0.0)
    grad_value = jnp.einsum(
        "hqk,qhd->khd", probs.astype(jnp.bfloat16), grad_heads, preferred_element_type=jnp.float32
    )
    grad_probs = jnp.einsum(
        "qhd,khd->hqk", grad_heads, value_heads, preferred_element_type=jnp.float32
    )
    grad_scores = (probs * (grad_probs - inner[..., None]) * (1.0 / math.sqrt(HD))).astype(
        jnp.bfloat16
    )
    grad_query = jnp.einsum(
        "hqk,khd->qhd", grad_scores, key_heads, preferred_element_type=jnp.float32
    )
    grad_key = jnp.einsum(
        "hqk,qhd->khd", grad_scores, query_heads, preferred_element_type=jnp.float32
    )
    key_rows = grad_key.shape[0]
    return (grad_query, grad_key.reshape(key_rows, -1), grad_value.reshape(key_rows, -1))


class RingAttention:
    def __init__(self, query, key_flat, value_flat, segment, position, cosine, sine):
        self.query = query
        self.piece = (key_flat, value_flat, segment, position)
        self.segment = segment
        self.position = position
        self.cosine = cosine
        self.sine = sine

    def forward(self):
        f32 = jnp.float32
        query, segment, position = self.query, self.segment, self.position
        rows, heads = query.shape[0], query.shape[1]
        start_stats = (
            jnp.full((heads, rows), NEG, f32),
            jnp.zeros((heads, rows), f32),
            jnp.zeros((heads, rows, HD), f32),
        )
        stats = forward_fold(start_stats, self.piece, query, segment, position)

        def cycle_turn(index, carry):
            moving, current = carry
            moving = passed_along(moving, "context", 1)
            current = forward_fold(current, moving, query, segment, position)
            return (moving, current)

        peak, total, accum = lax.fori_loop(
            0, lax.axis_size("context") - 1, cycle_turn, (self.piece, stats)
        )[1]
        self.attended = jnp.transpose(accum / total[..., None], (1, 0, 2)).astype(jnp.bfloat16)
        self.log_total = peak + jnp.log(total)
        return self.attended

    def backward(self, grad_heads, early, late):
        bf16 = jnp.bfloat16
        query, segment, position = self.query, self.segment, self.position
        rows, heads = query.shape[0], query.shape[1]
        inner = jnp.sum(grad_heads.astype(jnp.float32) * self.attended.astype(jnp.float32), axis=-1).T

        def piece_grads(piece):
            return backward_piece(piece, query, grad_heads, self.log_total, inner, segment, position)

        grad_query, grad_key, grad_value = piece_grads(self.piece)

        def grad_turn(index, carry):
            moving, acc_query, acc_key, acc_value = carry
            moving = passed_along(moving, "context", 1)
            acc_key, acc_value = pass_grads(acc_key, acc_value)
            part_query, part_key, part_value = piece_grads(moving)
            return (moving, acc_query + part_query, acc_key + part_key, acc_value + part_value)

        carried = lax.fori_loop(
            0,
            lax.axis_size("context") - 1,
            grad_turn,
            (self.piece, grad_query, grad_key, grad_value),
        )
        grad_query = carried[1]
        grad_key, grad_value = pass_grads(carried[2], carried[3])
        grad_qin = rotate_back(grad_query, self.cosine, self.sine).astype(bf16)
        grad_kin = rotate_back(grad_key.reshape(rows, heads, HD), self.cosine, self.sine).astype(bf16)
        grad_vin = grad_value.astype(bf16).reshape(rows, heads, HD)
        return grad_qin, grad_kin, grad_vin, early, late


class HeadAttention:
    BLOCK = 512

    def __init__(self, query, key_heads, value_heads, segment, position, cosine, sine):
        ways = lax.axis_size("context")
        rows, heads = query.shape[0], query.shape[1]
        self.ways = ways
        self.rows = rows
        self.heads = heads
        self.group = heads // ways
        stacked = jnp.stack([query, key_heads, value_heads], axis=1)
        stacked = stacked.reshape(rows, 3, ways, self.group, HD)
        stacked = lax.all_to_all(stacked, "context", 2, 0, tiled=True)
        stacked = stacked.reshape(rows * ways, 3, self.group, HD)
        self.query = stacked[:, 0]
        self.keys = stacked[:, 1]
        self.values = stacked[:, 2]
        tags = jnp.stack([segment, position], axis=0)[None]
        tags = jnp.broadcast_to(tags, (ways, 2, rows))
        tags = lax.all_to_all(tags, "context", 0, 0, tiled=True)
        tags = jnp.transpose(tags, (1, 0, 2)).reshape(2, rows * ways)
        self.seg_all = tags[0]
        self.pos_all = tags[1]
        self.cos_all, self.sin_all = rope_tables(self.pos_all)

    def _blocks(self):
        total = self.rows * self.ways
        block = min(self.BLOCK, total)
        return [(start, block) for start in range(0, total, block)]

    def _scores(self, start, size):
        query = lax.dynamic_slice_in_dim(self.query, start, size, axis=0)
        seg_q = lax.dynamic_slice_in_dim(self.seg_all, start, size, axis=0)
        pos_q = lax.dynamic_slice_in_dim(self.pos_all, start, size, axis=0)
        scores = jnp.einsum(
            "qhd,khd->hqk", query, self.keys, preferred_element_type=jnp.float32
        ) * (1.0 / math.sqrt(HD))
        allowed = (seg_q[:, None] == self.seg_all[None, :]) & (
            self.pos_all[None, :] <= pos_q[:, None]
        )
        return query, jnp.where(allowed[None], scores, NEG), allowed

    def forward(self):
        outs = []
        logs = []
        for start, size in self._blocks():
            _, scores, allowed = self._scores(start, size)
            peak = jnp.max(scores, axis=-1)
            weights = jnp.where(allowed[None], jnp.exp(scores - peak[..., None]), 0.0)
            total = jnp.sum(weights, axis=-1)
            mixed = jnp.einsum(
                "hqk,khd->qhd",
                weights.astype(jnp.bfloat16),
                self.values,
                preferred_element_type=jnp.float32,
            )
            outs.append((mixed / total.T[:, :, None]).astype(jnp.bfloat16))
            logs.append(peak + jnp.log(total))
        self.attended = jnp.concatenate(outs, axis=0)
        self.log_total = jnp.concatenate(logs, axis=1)
        back = self.attended.reshape(self.rows * self.ways, 1, self.group, HD)
        back = lax.all_to_all(back, "context", 0, 1, tiled=True)
        return back.reshape(self.rows, self.heads, HD)

    def backward(self, grad_heads, early, late):
        f32 = jnp.float32
        bf16 = jnp.bfloat16
        scale = 1.0 / math.sqrt(HD)
        grad = grad_heads.reshape(self.rows, self.ways, self.group, HD)
        grad = lax.all_to_all(grad, "context", 1, 0, tiled=True)
        grad, early = lax.optimization_barrier((grad, early))
        grad = grad.reshape(self.rows * self.ways, self.group, HD)
        inner = jnp.sum(grad.astype(f32) * self.attended.astype(f32), axis=-1).T
        grad_key = jnp.zeros(self.keys.shape, f32)
        grad_value = jnp.zeros(self.values.shape, f32)
        grad_queries = []
        for start, size in self._blocks():
            query, scores, allowed = self._scores(start, size)
            log_block = lax.dynamic_slice_in_dim(self.log_total, start, size, axis=1)
            inner_block = lax.dynamic_slice_in_dim(inner, start, size, axis=1)
            grad_block = lax.dynamic_slice_in_dim(grad, start, size, axis=0)
            probs = jnp.where(allowed[None], jnp.exp(scores - log_block[..., None]), 0.0)
            grad_value = grad_value + jnp.einsum(
                "hqk,qhd->khd", probs.astype(bf16), grad_block, preferred_element_type=f32
            )
            grad_probs = jnp.einsum(
                "qhd,khd->hqk", grad_block, self.values, preferred_element_type=f32
            )
            grad_scores = (probs * (grad_probs - inner_block[..., None]) * scale).astype(bf16)
            grad_queries.append(
                jnp.einsum("hqk,khd->qhd", grad_scores, self.keys, preferred_element_type=f32)
            )
            grad_key = grad_key + jnp.einsum(
                "hqk,qhd->khd", grad_scores, query, preferred_element_type=f32
            )
        grad_query = jnp.concatenate(grad_queries, axis=0)
        grad_qin = rotate_back(grad_query, self.cos_all, self.sin_all).astype(bf16)
        grad_kin = rotate_back(grad_key, self.cos_all, self.sin_all).astype(bf16)
        grad_vin = grad_value.astype(bf16)
        stacked = jnp.stack([grad_qin, grad_kin, grad_vin], axis=1)
        stacked, late = lax.optimization_barrier((stacked, late))
        stacked = stacked.reshape(self.rows * self.ways, 3, 1, self.group, HD)
        stacked = lax.all_to_all(stacked, "context", 0, 2, tiled=True)
        stacked = stacked.reshape(self.rows, 3, self.heads, HD)
        return stacked[:, 0], stacked[:, 1], stacked[:, 2], early, late


def mlp_chunks(hidden_cols):
    for count in (2, 1):
        if hidden_cols % (count * 128) == 0:
            return count
    return 1


def on_device(
    inputs, segments, positions, w_q, w_k, w_v, w_o, w_gate, w_up, w_down, g_attn, g_mlp, d_out
):
    f32 = jnp.float32
    bf16 = jnp.bfloat16
    rows = inputs.shape[1]
    width = inputs.shape[2]
    cols = w_q.shape[1]
    hidden_cols = w_gate.shape[1]
    tokens = inputs.reshape(rows, width)
    segment = segments.reshape(rows)
    position = positions.reshape(rows)
    full_qkv = lax.all_gather(jnp.concatenate([w_q, w_k, w_v], axis=1), ROWS, axis=0, tiled=True)
    full_o = lax.all_gather(w_o, ROWS, axis=0, tiled=True)
    gains = lax.all_gather(
        jnp.concatenate([g_attn, g_mlp])[None], ROWS, axis=0, tiled=True
    )
    gain_attn = gains[:, : g_attn.shape[0]].reshape(width)
    gain_mlp = gains[:, g_attn.shape[0] :].reshape(width)
    count = mlp_chunks(hidden_cols)
    step = hidden_cols // count
    fetched = []
    for index in range(count):
        part = slice(index * step, (index + 1) * step)
        fetched.append(
            tuple(
                lax.all_gather(weight[:, part], ROWS, axis=0, tiled=True)
                for weight in (w_gate, w_up, w_down)
            )
        )
    heads = cols // HD
    cosine, sine = rope_tables(position)
    resid1 = tokens.astype(f32)
    norm1, inv1 = normalize(resid1)
    h1 = (norm1 * gain_attn.astype(f32)).astype(bf16)
    projected = jnp.dot(h1, full_qkv, preferred_element_type=f32)
    query = rotate(projected[:, :cols].reshape(rows, heads, HD), cosine, sine).astype(bf16)
    key_heads = rotate(projected[:, cols : 2 * cols].reshape(rows, heads, HD), cosine, sine).astype(
        bf16
    )
    value_heads = projected[:, 2 * cols :].astype(bf16).reshape(rows, heads, HD)
    if heads % lax.axis_size("context") == 0:
        attention = HeadAttention(query, key_heads, value_heads, segment, position, cosine, sine)
    else:
        attention = RingAttention(
            query,
            key_heads.reshape(rows, cols),
            value_heads.reshape(rows, cols),
            segment,
            position,
            cosine,
            sine,
        )
    attended = attention.forward()
    attended_flat = attended.reshape(rows, cols)
    resid2 = resid1 + tensor_total(contract_last(attended_flat, full_o))
    norm2, inv2 = normalize(resid2)
    h2_part = (norm2 * gain_mlp.astype(f32)).astype(bf16)
    grad_y = d_out.reshape(rows, width)
    mlp_partial = None
    h2_grad_partial = None
    staged = []
    for full_gate, full_up, full_down in fetched:
        gate = jnp.dot(h2_part, full_gate, preferred_element_type=f32)
        up = jnp.dot(h2_part, full_up, preferred_element_type=f32)
        active = jax.nn.silu(gate)
        hidden = (active * up).astype(bf16)
        out_part = contract_last(hidden, full_down)
        mlp_partial = out_part if mlp_partial is None else mlp_partial + out_part
        grad_hidden = jnp.dot(grad_y, full_down, preferred_element_type=f32)
        sigma = jax.nn.sigmoid(gate)
        grad_gate = (grad_hidden * up * sigma * (1.0 + gate * (1.0 - sigma))).astype(bf16)
        grad_up = (grad_hidden * active).astype(bf16)
        back_part = contract_last(grad_gate, full_gate) + contract_last(grad_up, full_up)
        pending = (
            contract_first(h2_part, grad_gate),
            contract_first(h2_part, grad_up),
            contract_first(grad_y, hidden),
        )
        if staged:
            back_part, staged[-1] = lax.optimization_barrier((back_part, staged[-1]))
        h2_grad_partial = back_part if h2_grad_partial is None else h2_grad_partial + back_part
        staged.append(tuple(chip_total(value) for value in pending))
    grad_h2 = tensor_total(h2_grad_partial)
    grad_h2, staged[-1] = lax.optimization_barrier((grad_h2, staged[-1]))
    reduced = [tuple(line_total(value) for value in chunk) for chunk in staged]
    result = (resid2 + tensor_total(mlp_partial)).astype(bf16)
    grad_gmlp = jnp.sum(grad_h2 * norm2, axis=0)
    grad_resid = grad_y.astype(f32) + norm_back(grad_h2, norm2, inv2, gain_mlp)
    grad_resid_part = grad_resid.astype(bf16)
    grad_heads = (
        jnp.dot(grad_resid_part, full_o, preferred_element_type=f32)
        .astype(bf16)
        .reshape(rows, heads, HD)
    )
    grad_heads, partial_o = lax.optimization_barrier(
        (grad_heads, contract_first(grad_resid_part, attended_flat))
    )
    early = (chip_total(partial_o), reduced[:-1])
    grad_qin, grad_kin, grad_vin, early, late = attention.backward(grad_heads, early, reduced[-1])
    staged_o, reduced[:-1] = early
    reduced[-1] = late
    reduced_o = line_total(staged_o)
    grad_qkv = jnp.concatenate(
        [grad_qin.reshape(rows, cols), grad_kin.reshape(rows, cols), grad_vin.reshape(rows, cols)],
        axis=1,
    )
    grad_h1 = tensor_total(contract_last(grad_qkv, full_qkv))
    grad_h1, reduced_o = lax.optimization_barrier((grad_h1, reduced_o))
    grad_gattn = jnp.sum(grad_h1 * norm1, axis=0)
    grad_x_part = (grad_resid + norm_back(grad_h1, norm1, inv1, gain_attn)).astype(bf16)
    reduced_qkv = rows_total(contract_first(h1, grad_qkv))
    reduced_gains = lax.psum_scatter(
        jnp.stack([grad_gattn, grad_gmlp], axis=1), ROWS, scatter_dimension=0, tiled=True
    )
    reduced_gate, reduced_up, reduced_down = (
        jnp.concatenate([chunk[which] for chunk in reduced], axis=1) for which in range(3)
    )
    return (
        result.reshape(1, rows, width),
        grad_x_part.reshape(1, rows, width),
        reduced_qkv[:, :cols],
        reduced_qkv[:, cols : 2 * cols],
        reduced_qkv[:, 2 * cols :],
        reduced_o,
        reduced_gate,
        reduced_up,
        reduced_down,
        reduced_gains[:, 0],
        reduced_gains[:, 1],
    )


def solution(mesh):
    placed = (
        P("shard", "context", None),
        P("shard", "context"),
        P("shard", "context"),
        P(ROWS, "tensor"),
        P(ROWS, "tensor"),
        P(ROWS, "tensor"),
        P(ROWS, "tensor"),
        P(ROWS, "tensor"),
        P(ROWS, "tensor"),
        P(ROWS, "tensor"),
        P(ROWS),
        P(ROWS),
        P("shard", "context", None),
    )
    return jax.shard_map(
        on_device,
        mesh=mesh,
        in_specs=placed,
        out_specs=(
            P("shard", "context", None),
            P("shard", "context", None),
            P(ROWS, "tensor"),
            P(ROWS, "tensor"),
            P(ROWS, "tensor"),
            P(ROWS, "tensor"),
            P(ROWS, "tensor"),
            P(ROWS, "tensor"),
            P(ROWS, "tensor"),
            P(ROWS),
            P(ROWS),
        ),
        check_vma=False,
    )
```

```python
import math

import jax
import jax.numpy as jnp
from jax import lax
from jax.sharding import PartitionSpec as P

HD = 64


EPS = 1e-05
THETA = 130000.0
NEG = -1e30
ROWS = ("shard", "context")


def passed_along(value, axis, steps):
    count = lax.axis_size(axis)
    pairs = [(source, (source + steps) % count) for source in range(count)]
    return lax.ppermute(value, axis, pairs)


def rope_tables(position):
    index = jnp.arange(HD // 2, dtype=jnp.float32)
    inverse = jnp.power(jnp.float32(THETA), -2.0 * index / HD)
    angle = position.astype(jnp.float32)[:, None] * inverse[None, :]
    return (jnp.cos(angle), jnp.sin(angle))


def rotate(tensor, cosine, sine):
    half = tensor.shape[-1] // 2
    first = tensor[..., :half]
    second = tensor[..., half:]
    cosine = cosine[:, None, :]
    sine = sine[:, None, :]
    return jnp.concatenate(
        [first * cosine - second * sine, second * cosine + first * sine], axis=-1
    )


def rotate_back(grad, cosine, sine):
    half = grad.shape[-1] // 2
    first = grad[..., :half]
    second = grad[..., half:]
    cosine = cosine[:, None, :]
    sine = sine[:, None, :]
    return jnp.concatenate(
        [first * cosine + second * sine, second * cosine - first * sine], axis=-1
    )


def normalize(value):
    inv_rms = lax.rsqrt(jnp.mean(value * value, axis=-1, keepdims=True) + EPS)
    return (value * inv_rms, inv_rms)


def norm_back(grad, normed, inv_rms, gain):
    scaled = grad * gain.astype(jnp.float32)
    return inv_rms * (scaled - normed * jnp.mean(scaled * normed, axis=-1, keepdims=True))


def contract_last(left, right):
    return lax.dot_general(
        left, right, (((1,), (1,)), ((), ())), preferred_element_type=jnp.float32
    )


def contract_first(left, right):
    return lax.dot_general(
        left, right, (((0,), (0,)), ((), ())), preferred_element_type=jnp.float32
    )


def half_of(value, bit):
    size = value.shape[0] // 2
    return lax.dynamic_slice_in_dim(value, bit * size, size, axis=0)


def joined(mine, other, bit):
    low = jnp.where(bit == 0, mine, other)
    high = jnp.where(bit == 0, other, mine)
    return jnp.concatenate([low, high], axis=0)


def tensor_total(partial_sum):
    count = lax.axis_size("tensor")
    rows = partial_sum.shape[0]
    if count != 4 or rows % 8:
        return lax.psum(partial_sum.astype(jnp.bfloat16), "tensor").astype(jnp.float32)
    f32 = jnp.float32
    bf16 = jnp.bfloat16
    index = lax.axis_index("tensor")
    x_bit = index % 2
    y_bit = index // 2
    x_pairs = [(i, i ^ 1) for i in range(4)]
    y_pairs = [(i, i ^ 2) for i in range(4)]

    def swap(value, pairs):
        return lax.ppermute(value.astype(bf16), "tensor", pairs).astype(f32)

    first = partial_sum[: rows // 2]
    second = partial_sum[rows // 2 :]
    first = half_of(first, x_bit) + swap(half_of(first, 1 - x_bit), x_pairs)
    second = half_of(second, y_bit) + swap(half_of(second, 1 - y_bit), y_pairs)
    first = half_of(first, y_bit) + swap(half_of(first, 1 - y_bit), y_pairs)
    second = half_of(second, x_bit) + swap(half_of(second, 1 - x_bit), x_pairs)
    first = first.astype(bf16)
    second = second.astype(bf16)
    first = joined(first, lax.ppermute(first, "tensor", y_pairs), y_bit)
    second = joined(second, lax.ppermute(second, "tensor", x_pairs), x_bit)
    first = joined(first, lax.ppermute(first, "tensor", x_pairs), x_bit)
    second = joined(second, lax.ppermute(second, "tensor", y_pairs), y_bit)
    return jnp.concatenate([first, second], axis=0).astype(f32)


def chip_total(grad):
    f32 = jnp.float32
    shard = lax.axis_index("shard")
    mine = half_of(grad, shard)
    other = half_of(grad, 1 - shard)
    got = lax.ppermute(other.astype(jnp.bfloat16), "shard", [(0, 1), (1, 0)])
    return mine.astype(f32) + got.astype(f32)


def line_total(staged):
    return lax.psum_scatter(
        staged.astype(jnp.bfloat16), "context", scatter_dimension=0, tiled=True
    ).astype(jnp.float32)


def line_pipeline(staged):
    f32 = jnp.float32
    bf16 = jnp.bfloat16
    ways = lax.axis_size("context")
    me = lax.axis_index("context")
    size = staged.shape[0] // ways

    def block(index):
        index = jnp.clip(index, 0, ways - 1)
        return lax.dynamic_slice_in_dim(staged, index * size, size, axis=0)

    rightward = jnp.zeros((size,) + staged.shape[1:], f32)
    leftward = jnp.zeros((size,) + staged.shape[1:], f32)
    for step in range(1, ways):
        right_pairs = [(d, d + 1) for d in range(step)]
        left_pairs = [(d, d - 1) for d in range(ways - step, ways)]
        sent_right = block(ways - step + me) + rightward
        sent_left = block(me + step - ways) + leftward
        rightward = lax.ppermute(sent_right.astype(bf16), "context", right_pairs).astype(f32)
        leftward = lax.ppermute(sent_left.astype(bf16), "context", left_pairs).astype(f32)
    return block(me) + rightward + leftward


def rows_total(grad):
    return line_total(chip_total(grad))


def pass_grads(grad_key, grad_value):
    return (
        passed_along(grad_key.astype(jnp.bfloat16), "context", 1).astype(grad_key.dtype),
        passed_along(grad_value.astype(jnp.bfloat16), "context", 1).astype(grad_value.dtype),
    )


def key_scores(query_heads, query_seg, query_pos, piece):
    key_flat, value_flat, key_seg, key_pos = piece
    heads = query_heads.shape[1]
    key_heads = key_flat.reshape(key_flat.shape[0], heads, HD)
    value_heads = value_flat.reshape(value_flat.shape[0], heads, HD)
    scores = jnp.einsum(
        "qhd,khd->hqk", query_heads, key_heads, preferred_element_type=jnp.float32
    ) * (1.0 / math.sqrt(HD))
    allowed = (query_seg[:, None] == key_seg[None, :]) & (key_pos[None, :] <= query_pos[:, None])
    return (jnp.where(allowed[None], scores, NEG), allowed, key_heads, value_heads)


def forward_fold(stats, piece, query_heads, query_seg, query_pos):
    peak, total, accum = stats
    scores, allowed, key_heads, value_heads = key_scores(query_heads, query_seg, query_pos, piece)
    new_peak = jnp.maximum(peak, jnp.max(scores, axis=-1))
    weights = jnp.where(allowed[None], jnp.exp(scores - new_peak[..., None]), 0.0)
    factor = jnp.exp(peak - new_peak)
    total = total * factor + jnp.sum(weights, axis=-1)
    accum = accum * factor[..., None] + jnp.einsum(
        "hqk,khd->hqd",
        weights.astype(jnp.bfloat16),
        value_heads,
        preferred_element_type=jnp.float32,
    )
    return (new_peak, total, accum)


def backward_piece(piece, query_heads, grad_heads, log_total, inner, query_seg, query_pos):
    scores, allowed, key_heads, value_heads = key_scores(query_heads, query_seg, query_pos, piece)
    probs = jnp.where(allowed[None], jnp.exp(scores - log_total[..., None]), 0.0)
    grad_value = jnp.einsum(
        "hqk,qhd->khd", probs.astype(jnp.bfloat16), grad_heads, preferred_element_type=jnp.float32
    )
    grad_probs = jnp.einsum(
        "qhd,khd->hqk", grad_heads, value_heads, preferred_element_type=jnp.float32
    )
    grad_scores = (probs * (grad_probs - inner[..., None]) * (1.0 / math.sqrt(HD))).astype(
        jnp.bfloat16
    )
    grad_query = jnp.einsum(
        "hqk,khd->qhd", grad_scores, key_heads, preferred_element_type=jnp.float32
    )
    grad_key = jnp.einsum(
        "hqk,qhd->khd", grad_scores, query_heads, preferred_element_type=jnp.float32
    )
    key_rows = grad_key.shape[0]
    return (grad_query, grad_key.reshape(key_rows, -1), grad_value.reshape(key_rows, -1))


class RingAttention:
    def __init__(self, query, key_flat, value_flat, segment, position, cosine, sine):
        self.query = query
        self.piece = (key_flat, value_flat, segment, position)
        self.segment = segment
        self.position = position
        self.cosine = cosine
        self.sine = sine

    def forward(self):
        f32 = jnp.float32
        query, segment, position = self.query, self.segment, self.position
        rows, heads = query.shape[0], query.shape[1]
        start_stats = (
            jnp.full((heads, rows), NEG, f32),
            jnp.zeros((heads, rows), f32),
            jnp.zeros((heads, rows, HD), f32),
        )
        stats = forward_fold(start_stats, self.piece, query, segment, position)

        def cycle_turn(index, carry):
            moving, current = carry
            moving = passed_along(moving, "context", 1)
            current = forward_fold(current, moving, query, segment, position)
            return (moving, current)

        peak, total, accum = lax.fori_loop(
            0, lax.axis_size("context") - 1, cycle_turn, (self.piece, stats)
        )[1]
        self.attended = jnp.transpose(accum / total[..., None], (1, 0, 2)).astype(jnp.bfloat16)
        self.log_total = peak + jnp.log(total)
        return self.attended

    def backward(self, grad_heads, early, late):
        bf16 = jnp.bfloat16
        query, segment, position = self.query, self.segment, self.position
        rows, heads = query.shape[0], query.shape[1]
        inner = jnp.sum(grad_heads.astype(jnp.float32) * self.attended.astype(jnp.float32), axis=-1).T

        def piece_grads(piece):
            return backward_piece(piece, query, grad_heads, self.log_total, inner, segment, position)

        grad_query, grad_key, grad_value = piece_grads(self.piece)

        def grad_turn(index, carry):
            moving, acc_query, acc_key, acc_value = carry
            moving = passed_along(moving, "context", 1)
            acc_key, acc_value = pass_grads(acc_key, acc_value)
            part_query, part_key, part_value = piece_grads(moving)
            return (moving, acc_query + part_query, acc_key + part_key, acc_value + part_value)

        carried = lax.fori_loop(
            0,
            lax.axis_size("context") - 1,
            grad_turn,
            (self.piece, grad_query, grad_key, grad_value),
        )
        grad_query = carried[1]
        grad_key, grad_value = pass_grads(carried[2], carried[3])
        grad_qin = rotate_back(grad_query, self.cosine, self.sine).astype(bf16)
        grad_kin = rotate_back(grad_key.reshape(rows, heads, HD), self.cosine, self.sine).astype(bf16)
        grad_vin = grad_value.astype(bf16).reshape(rows, heads, HD)
        return grad_qin, grad_kin, grad_vin, early, late


class HeadAttention:
    BLOCK = 512

    def __init__(self, query, key_heads, value_heads, segment, position, cosine, sine):
        ways = lax.axis_size("context")
        rows, heads = query.shape[0], query.shape[1]
        self.ways = ways
        self.rows = rows
        self.heads = heads
        self.group = heads // ways
        stacked = jnp.stack([query, key_heads, value_heads], axis=1)
        stacked = stacked.reshape(rows, 3, ways, self.group, HD)
        stacked = lax.all_to_all(stacked, "context", 2, 0, tiled=True)
        stacked = stacked.reshape(rows * ways, 3, self.group, HD)
        self.query = stacked[:, 0]
        self.keys = stacked[:, 1]
        self.values = stacked[:, 2]
        tags = jnp.stack([segment, position], axis=0)[None]
        tags = jnp.broadcast_to(tags, (ways, 2, rows))
        tags = lax.all_to_all(tags, "context", 0, 0, tiled=True)
        tags = jnp.transpose(tags, (1, 0, 2)).reshape(2, rows * ways)
        self.seg_all = tags[0]
        self.pos_all = tags[1]
        self.cos_all, self.sin_all = rope_tables(self.pos_all)

    def _blocks(self):
        total = self.rows * self.ways
        block = min(self.BLOCK, total)
        return [(start, block) for start in range(0, total, block)]

    def _scores(self, start, size):
        query = lax.dynamic_slice_in_dim(self.query, start, size, axis=0)
        seg_q = lax.dynamic_slice_in_dim(self.seg_all, start, size, axis=0)
        pos_q = lax.dynamic_slice_in_dim(self.pos_all, start, size, axis=0)
        scores = jnp.einsum(
            "qhd,khd->hqk", query, self.keys, preferred_element_type=jnp.float32
        ) * (1.0 / math.sqrt(HD))
        allowed = (seg_q[:, None] == self.seg_all[None, :]) & (
            self.pos_all[None, :] <= pos_q[:, None]
        )
        return query, jnp.where(allowed[None], scores, NEG), allowed

    def forward(self):
        outs = []
        logs = []
        for start, size in self._blocks():
            _, scores, allowed = self._scores(start, size)
            peak = jnp.max(scores, axis=-1)
            weights = jnp.where(allowed[None], jnp.exp(scores - peak[..., None]), 0.0)
            total = jnp.sum(weights, axis=-1)
            mixed = jnp.einsum(
                "hqk,khd->qhd",
                weights.astype(jnp.bfloat16),
                self.values,
                preferred_element_type=jnp.float32,
            )
            outs.append((mixed / total.T[:, :, None]).astype(jnp.bfloat16))
            logs.append(peak + jnp.log(total))
        self.attended = jnp.concatenate(outs, axis=0)
        self.log_total = jnp.concatenate(logs, axis=1)
        back = self.attended.reshape(self.rows * self.ways, 1, self.group, HD)
        back = lax.all_to_all(back, "context", 0, 1, tiled=True)
        return back.reshape(self.rows, self.heads, HD)

    def backward(self, grad_heads, early, late):
        f32 = jnp.float32
        bf16 = jnp.bfloat16
        scale = 1.0 / math.sqrt(HD)
        grad = grad_heads.reshape(self.rows, self.ways, self.group, HD)
        grad = lax.all_to_all(grad, "context", 1, 0, tiled=True)
        grad, early = lax.optimization_barrier((grad, early))
        grad = grad.reshape(self.rows * self.ways, self.group, HD)
        inner = jnp.sum(grad.astype(f32) * self.attended.astype(f32), axis=-1).T
        grad_key = jnp.zeros(self.keys.shape, f32)
        grad_value = jnp.zeros(self.values.shape, f32)
        grad_queries = []
        for start, size in self._blocks():
            query, scores, allowed = self._scores(start, size)
            log_block = lax.dynamic_slice_in_dim(self.log_total, start, size, axis=1)
            inner_block = lax.dynamic_slice_in_dim(inner, start, size, axis=1)
            grad_block = lax.dynamic_slice_in_dim(grad, start, size, axis=0)
            probs = jnp.where(allowed[None], jnp.exp(scores - log_block[..., None]), 0.0)
            grad_value = grad_value + jnp.einsum(
                "hqk,qhd->khd", probs.astype(bf16), grad_block, preferred_element_type=f32
            )
            grad_probs = jnp.einsum(
                "qhd,khd->hqk", grad_block, self.values, preferred_element_type=f32
            )
            grad_scores = (probs * (grad_probs - inner_block[..., None]) * scale).astype(bf16)
            grad_queries.append(
                jnp.einsum("hqk,khd->qhd", grad_scores, self.keys, preferred_element_type=f32)
            )
            grad_key = grad_key + jnp.einsum(
                "hqk,qhd->khd", grad_scores, query, preferred_element_type=f32
            )
        grad_query = jnp.concatenate(grad_queries, axis=0)
        grad_qin = rotate_back(grad_query, self.cos_all, self.sin_all).astype(bf16)
        grad_kin = rotate_back(grad_key, self.cos_all, self.sin_all).astype(bf16)
        grad_vin = grad_value.astype(bf16)
        stacked = jnp.stack([grad_qin, grad_kin, grad_vin], axis=1)
        stacked, late = lax.optimization_barrier((stacked, late))
        stacked = stacked.reshape(self.rows * self.ways, 3, 1, self.group, HD)
        stacked = lax.all_to_all(stacked, "context", 0, 2, tiled=True)
        stacked = stacked.reshape(self.rows, 3, self.heads, HD)
        return stacked[:, 0], stacked[:, 1], stacked[:, 2], early, late


def mlp_chunks(hidden_cols):
    for count in (2, 1):
        if hidden_cols % (count * 128) == 0:
            return count
    return 1


def on_device(
    inputs, segments, positions, w_q, w_k, w_v, w_o, w_gate, w_up, w_down, g_attn, g_mlp, d_out
):
    f32 = jnp.float32
    bf16 = jnp.bfloat16
    rows = inputs.shape[1]
    width = inputs.shape[2]
    cols = w_q.shape[1]
    hidden_cols = w_gate.shape[1]
    tokens = inputs.reshape(rows, width)
    segment = segments.reshape(rows)
    position = positions.reshape(rows)
    full_qkv = lax.all_gather(jnp.concatenate([w_q, w_k, w_v], axis=1), ROWS, axis=0, tiled=True)
    full_o = lax.all_gather(w_o, ROWS, axis=0, tiled=True)
    gains = lax.all_gather(
        jnp.concatenate([g_attn, g_mlp])[None], ROWS, axis=0, tiled=True
    )
    gain_attn = gains[:, : g_attn.shape[0]].reshape(width)
    gain_mlp = gains[:, g_attn.shape[0] :].reshape(width)
    count = mlp_chunks(hidden_cols)
    step = hidden_cols // count
    fetched = []
    for index in range(count):
        part = slice(index * step, (index + 1) * step)
        fetched.append(
            tuple(
                lax.all_gather(weight[:, part], ROWS, axis=0, tiled=True)
                for weight in (w_gate, w_up, w_down)
            )
        )
    heads = cols // HD
    cosine, sine = rope_tables(position)
    resid1 = tokens.astype(f32)
    norm1, inv1 = normalize(resid1)
    h1 = (norm1 * gain_attn.astype(f32)).astype(bf16)
    projected = jnp.dot(h1, full_qkv, preferred_element_type=f32)
    query = rotate(projected[:, :cols].reshape(rows, heads, HD), cosine, sine).astype(bf16)
    key_heads = rotate(projected[:, cols : 2 * cols].reshape(rows, heads, HD), cosine, sine).astype(
        bf16
    )
    value_heads = projected[:, 2 * cols :].astype(bf16).reshape(rows, heads, HD)
    if heads % lax.axis_size("context") == 0:
        attention = HeadAttention(query, key_heads, value_heads, segment, position, cosine, sine)
    else:
        attention = RingAttention(
            query,
            key_heads.reshape(rows, cols),
            value_heads.reshape(rows, cols),
            segment,
            position,
            cosine,
            sine,
        )
    attended = attention.forward()
    attended_flat = attended.reshape(rows, cols)
    resid2 = resid1 + tensor_total(contract_last(attended_flat, full_o))
    norm2, inv2 = normalize(resid2)
    h2_part = (norm2 * gain_mlp.astype(f32)).astype(bf16)
    grad_y = d_out.reshape(rows, width)
    mlp_partial = None
    h2_grad_partial = None
    staged = []
    for full_gate, full_up, full_down in fetched:
        gate = jnp.dot(h2_part, full_gate, preferred_element_type=f32)
        up = jnp.dot(h2_part, full_up, preferred_element_type=f32)
        active = jax.nn.silu(gate)
        hidden = (active * up).astype(bf16)
        out_part = contract_last(hidden, full_down)
        mlp_partial = out_part if mlp_partial is None else mlp_partial + out_part
        grad_hidden = jnp.dot(grad_y, full_down, preferred_element_type=f32)
        sigma = jax.nn.sigmoid(gate)
        grad_gate = (grad_hidden * up * sigma * (1.0 + gate * (1.0 - sigma))).astype(bf16)
        grad_up = (grad_hidden * active).astype(bf16)
        back_part = contract_last(grad_gate, full_gate) + contract_last(grad_up, full_up)
        pending = (
            contract_first(h2_part, grad_gate),
            contract_first(h2_part, grad_up),
            contract_first(grad_y, hidden),
        )
        if staged:
            back_part, staged[-1] = lax.optimization_barrier((back_part, staged[-1]))
        h2_grad_partial = back_part if h2_grad_partial is None else h2_grad_partial + back_part
        staged.append(tuple(chip_total(value) for value in pending))
    grad_h2 = tensor_total(h2_grad_partial)
    grad_h2, staged[-1] = lax.optimization_barrier((grad_h2, staged[-1]))
    reduced = []
    for index, chunk in enumerate(staged):
        if index == 0 and len(staged) > 1:
            widths = [value.shape[1] for value in chunk]
            joined_sum = line_pipeline(jnp.concatenate(chunk, axis=1))
            edges = [sum(widths[:i]) for i in range(len(widths) + 1)]
            reduced.append(
                tuple(joined_sum[:, edges[i] : edges[i + 1]] for i in range(len(widths)))
            )
        else:
            reduced.append(tuple(line_total(value) for value in chunk))
    result = (resid2 + tensor_total(mlp_partial)).astype(bf16)
    grad_gmlp = jnp.sum(grad_h2 * norm2, axis=0)
    grad_resid = grad_y.astype(f32) + norm_back(grad_h2, norm2, inv2, gain_mlp)
    grad_resid_part = grad_resid.astype(bf16)
    grad_heads = (
        jnp.dot(grad_resid_part, full_o, preferred_element_type=f32)
        .astype(bf16)
        .reshape(rows, heads, HD)
    )
    grad_heads, partial_o = lax.optimization_barrier(
        (grad_heads, contract_first(grad_resid_part, attended_flat))
    )
    early = (chip_total(partial_o), reduced[:-1])
    grad_qin, grad_kin, grad_vin, early, late = attention.backward(grad_heads, early, reduced[-1])
    staged_o, reduced[:-1] = early
    reduced[-1] = late
    reduced_o = line_total(staged_o)
    grad_qkv = jnp.concatenate(
        [grad_qin.reshape(rows, cols), grad_kin.reshape(rows, cols), grad_vin.reshape(rows, cols)],
        axis=1,
    )
    grad_h1 = tensor_total(contract_last(grad_qkv, full_qkv))
    grad_h1, reduced_o = lax.optimization_barrier((grad_h1, reduced_o))
    grad_gattn = jnp.sum(grad_h1 * norm1, axis=0)
    grad_x_part = (grad_resid + norm_back(grad_h1, norm1, inv1, gain_attn)).astype(bf16)
    gain_slab = jnp.pad(jnp.stack([grad_gattn, grad_gmlp], axis=1), ((0, 0), (0, 126)))
    reduced_qkv = rows_total(
        jnp.concatenate([contract_first(h1, grad_qkv), gain_slab], axis=1)
    )
    reduced_gains = reduced_qkv[:, 3 * cols :]
    reduced_gate, reduced_up, reduced_down = (
        jnp.concatenate([chunk[which] for chunk in reduced], axis=1) for which in range(3)
    )
    return (
        result.reshape(1, rows, width),
        grad_x_part.reshape(1, rows, width),
        reduced_qkv[:, :cols],
        reduced_qkv[:, cols : 2 * cols],
        reduced_qkv[:, 2 * cols : 3 * cols],
        reduced_o,
        reduced_gate,
        reduced_up,
        reduced_down,
        reduced_gains[:, 0],
        reduced_gains[:, 1],
    )


def solution(mesh):
    placed = (
        P("shard", "context", None),
        P("shard", "context"),
        P("shard", "context"),
        P(ROWS, "tensor"),
        P(ROWS, "tensor"),
        P(ROWS, "tensor"),
        P(ROWS, "tensor"),
        P(ROWS, "tensor"),
        P(ROWS, "tensor"),
        P(ROWS, "tensor"),
        P(ROWS),
        P(ROWS),
        P("shard", "context", None),
    )
    return jax.shard_map(
        on_device,
        mesh=mesh,
        in_specs=placed,
        out_specs=(
            P("shard", "context", None),
            P("shard", "context", None),
            P(ROWS, "tensor"),
            P(ROWS, "tensor"),
            P(ROWS, "tensor"),
            P(ROWS, "tensor"),
            P(ROWS, "tensor"),
            P(ROWS, "tensor"),
            P(ROWS, "tensor"),
            P(ROWS),
            P(ROWS),
        ),
        check_vma=False,
    )
```

```python
import math

import jax
import jax.numpy as jnp
from jax import lax
from jax.sharding import PartitionSpec as P

HD = 64


EPS = 1e-05
THETA = 130000.0
NEG = -1e30
ROWS = ("shard", "context")


def passed_along(value, axis, steps):
    count = lax.axis_size(axis)
    pairs = [(source, (source + steps) % count) for source in range(count)]
    return lax.ppermute(value, axis, pairs)


def rope_tables(position):
    index = jnp.arange(HD // 2, dtype=jnp.float32)
    inverse = jnp.power(jnp.float32(THETA), -2.0 * index / HD)
    angle = position.astype(jnp.float32)[:, None] * inverse[None, :]
    return (jnp.cos(angle), jnp.sin(angle))


def rotate(tensor, cosine, sine):
    half = tensor.shape[-1] // 2
    first = tensor[..., :half]
    second = tensor[..., half:]
    cosine = cosine[:, None, :]
    sine = sine[:, None, :]
    return jnp.concatenate(
        [first * cosine - second * sine, second * cosine + first * sine], axis=-1
    )


def rotate_back(grad, cosine, sine):
    half = grad.shape[-1] // 2
    first = grad[..., :half]
    second = grad[..., half:]
    cosine = cosine[:, None, :]
    sine = sine[:, None, :]
    return jnp.concatenate(
        [first * cosine + second * sine, second * cosine - first * sine], axis=-1
    )


def normalize(value):
    inv_rms = lax.rsqrt(jnp.mean(value * value, axis=-1, keepdims=True) + EPS)
    return (value * inv_rms, inv_rms)


def norm_back(grad, normed, inv_rms, gain):
    scaled = grad * gain.astype(jnp.float32)
    return inv_rms * (scaled - normed * jnp.mean(scaled * normed, axis=-1, keepdims=True))


def contract_last(left, right):
    return lax.dot_general(
        left, right, (((1,), (1,)), ((), ())), preferred_element_type=jnp.float32
    )


def contract_first(left, right):
    return lax.dot_general(
        left, right, (((0,), (0,)), ((), ())), preferred_element_type=jnp.float32
    )


def half_of(value, bit):
    size = value.shape[0] // 2
    return lax.dynamic_slice_in_dim(value, bit * size, size, axis=0)


def joined(mine, other, bit):
    low = jnp.where(bit == 0, mine, other)
    high = jnp.where(bit == 0, other, mine)
    return jnp.concatenate([low, high], axis=0)


def tensor_total(partial_sum):
    count = lax.axis_size("tensor")
    rows = partial_sum.shape[0]
    if count != 4 or rows % 8:
        return lax.psum(partial_sum.astype(jnp.bfloat16), "tensor").astype(jnp.float32)
    f32 = jnp.float32
    bf16 = jnp.bfloat16
    index = lax.axis_index("tensor")
    x_bit = index % 2
    y_bit = index // 2
    x_pairs = [(i, i ^ 1) for i in range(4)]
    y_pairs = [(i, i ^ 2) for i in range(4)]

    def swap(value, pairs):
        return lax.ppermute(value.astype(bf16), "tensor", pairs).astype(f32)

    first = partial_sum[: rows // 2]
    second = partial_sum[rows // 2 :]
    first = half_of(first, x_bit) + swap(half_of(first, 1 - x_bit), x_pairs)
    second = half_of(second, y_bit) + swap(half_of(second, 1 - y_bit), y_pairs)
    first = half_of(first, y_bit) + swap(half_of(first, 1 - y_bit), y_pairs)
    second = half_of(second, x_bit) + swap(half_of(second, 1 - x_bit), x_pairs)
    first = first.astype(bf16)
    second = second.astype(bf16)
    first = joined(first, lax.ppermute(first, "tensor", y_pairs), y_bit)
    second = joined(second, lax.ppermute(second, "tensor", x_pairs), x_bit)
    first = joined(first, lax.ppermute(first, "tensor", x_pairs), x_bit)
    second = joined(second, lax.ppermute(second, "tensor", y_pairs), y_bit)
    return jnp.concatenate([first, second], axis=0).astype(f32)


def chip_total(grad):
    f32 = jnp.float32
    shard = lax.axis_index("shard")
    mine = half_of(grad, shard)
    other = half_of(grad, 1 - shard)
    got = lax.ppermute(other.astype(jnp.bfloat16), "shard", [(0, 1), (1, 0)])
    return mine.astype(f32) + got.astype(f32)


def line_total(staged):
    return lax.psum_scatter(
        staged.astype(jnp.bfloat16), "context", scatter_dimension=0, tiled=True
    ).astype(jnp.float32)


def rows_total(grad):
    return line_total(chip_total(grad))


def pass_grads(grad_key, grad_value):
    return (
        passed_along(grad_key.astype(jnp.bfloat16), "context", 1).astype(grad_key.dtype),
        passed_along(grad_value.astype(jnp.bfloat16), "context", 1).astype(grad_value.dtype),
    )


def key_scores(query_heads, query_seg, query_pos, piece):
    key_flat, value_flat, key_seg, key_pos = piece
    heads = query_heads.shape[1]
    key_heads = key_flat.reshape(key_flat.shape[0], heads, HD)
    value_heads = value_flat.reshape(value_flat.shape[0], heads, HD)
    scores = jnp.einsum(
        "qhd,khd->hqk", query_heads, key_heads, preferred_element_type=jnp.float32
    ) * (1.0 / math.sqrt(HD))
    allowed = (query_seg[:, None] == key_seg[None, :]) & (key_pos[None, :] <= query_pos[:, None])
    return (jnp.where(allowed[None], scores, NEG), allowed, key_heads, value_heads)


def forward_fold(stats, piece, query_heads, query_seg, query_pos):
    peak, total, accum = stats
    scores, allowed, key_heads, value_heads = key_scores(query_heads, query_seg, query_pos, piece)
    new_peak = jnp.maximum(peak, jnp.max(scores, axis=-1))
    weights = jnp.where(allowed[None], jnp.exp(scores - new_peak[..., None]), 0.0)
    factor = jnp.exp(peak - new_peak)
    total = total * factor + jnp.sum(weights, axis=-1)
    accum = accum * factor[..., None] + jnp.einsum(
        "hqk,khd->hqd",
        weights.astype(jnp.bfloat16),
        value_heads,
        preferred_element_type=jnp.float32,
    )
    return (new_peak, total, accum)


def backward_piece(piece, query_heads, grad_heads, log_total, inner, query_seg, query_pos):
    scores, allowed, key_heads, value_heads = key_scores(query_heads, query_seg, query_pos, piece)
    probs = jnp.where(allowed[None], jnp.exp(scores - log_total[..., None]), 0.0)
    grad_value = jnp.einsum(
        "hqk,qhd->khd", probs.astype(jnp.bfloat16), grad_heads, preferred_element_type=jnp.float32
    )
    grad_probs = jnp.einsum(
        "qhd,khd->hqk", grad_heads, value_heads, preferred_element_type=jnp.float32
    )
    grad_scores = (probs * (grad_probs - inner[..., None]) * (1.0 / math.sqrt(HD))).astype(
        jnp.bfloat16
    )
    grad_query = jnp.einsum(
        "hqk,khd->qhd", grad_scores, key_heads, preferred_element_type=jnp.float32
    )
    grad_key = jnp.einsum(
        "hqk,qhd->khd", grad_scores, query_heads, preferred_element_type=jnp.float32
    )
    key_rows = grad_key.shape[0]
    return (grad_query, grad_key.reshape(key_rows, -1), grad_value.reshape(key_rows, -1))


class RingAttention:
    def __init__(self, query, key_flat, value_flat, segment, position, cosine, sine):
        self.query = query
        self.piece = (key_flat, value_flat, segment, position)
        self.segment = segment
        self.position = position
        self.cosine = cosine
        self.sine = sine

    def forward(self):
        f32 = jnp.float32
        query, segment, position = self.query, self.segment, self.position
        rows, heads = query.shape[0], query.shape[1]
        start_stats = (
            jnp.full((heads, rows), NEG, f32),
            jnp.zeros((heads, rows), f32),
            jnp.zeros((heads, rows, HD), f32),
        )
        stats = forward_fold(start_stats, self.piece, query, segment, position)

        def cycle_turn(index, carry):
            moving, current = carry
            moving = passed_along(moving, "context", 1)
            current = forward_fold(current, moving, query, segment, position)
            return (moving, current)

        peak, total, accum = lax.fori_loop(
            0, lax.axis_size("context") - 1, cycle_turn, (self.piece, stats)
        )[1]
        self.attended = jnp.transpose(accum / total[..., None], (1, 0, 2)).astype(jnp.bfloat16)
        self.log_total = peak + jnp.log(total)
        return self.attended

    def backward(self, grad_heads, early, late):
        bf16 = jnp.bfloat16
        query, segment, position = self.query, self.segment, self.position
        rows, heads = query.shape[0], query.shape[1]
        inner = jnp.sum(grad_heads.astype(jnp.float32) * self.attended.astype(jnp.float32), axis=-1).T

        def piece_grads(piece):
            return backward_piece(piece, query, grad_heads, self.log_total, inner, segment, position)

        grad_query, grad_key, grad_value = piece_grads(self.piece)

        def grad_turn(index, carry):
            moving, acc_query, acc_key, acc_value = carry
            moving = passed_along(moving, "context", 1)
            acc_key, acc_value = pass_grads(acc_key, acc_value)
            part_query, part_key, part_value = piece_grads(moving)
            return (moving, acc_query + part_query, acc_key + part_key, acc_value + part_value)

        carried = lax.fori_loop(
            0,
            lax.axis_size("context") - 1,
            grad_turn,
            (self.piece, grad_query, grad_key, grad_value),
        )
        grad_query = carried[1]
        grad_key, grad_value = pass_grads(carried[2], carried[3])
        grad_qin = rotate_back(grad_query, self.cosine, self.sine).astype(bf16)
        grad_kin = rotate_back(grad_key.reshape(rows, heads, HD), self.cosine, self.sine).astype(bf16)
        grad_vin = grad_value.astype(bf16).reshape(rows, heads, HD)
        return grad_qin, grad_kin, grad_vin, early, late


class HeadAttention:
    BLOCK = 512

    def __init__(self, query, key_heads, value_heads, segment, position, cosine, sine):
        ways = lax.axis_size("context")
        rows, heads = query.shape[0], query.shape[1]
        self.ways = ways
        self.rows = rows
        self.heads = heads
        self.group = heads // ways
        stacked = jnp.stack([query, key_heads, value_heads], axis=1)
        stacked = stacked.reshape(rows, 3, ways, self.group, HD)
        stacked = lax.all_to_all(stacked, "context", 2, 0, tiled=True)
        stacked = stacked.reshape(rows * ways, 3, self.group, HD)
        self.query = stacked[:, 0]
        self.keys = stacked[:, 1]
        self.values = stacked[:, 2]
        tags = jnp.stack([segment, position], axis=0)[None]
        tags = jnp.broadcast_to(tags, (ways, 2, rows))
        tags = lax.all_to_all(tags, "context", 0, 0, tiled=True)
        tags = jnp.transpose(tags, (1, 0, 2)).reshape(2, rows * ways)
        self.seg_all = tags[0]
        self.pos_all = tags[1]
        self.cos_all, self.sin_all = rope_tables(self.pos_all)

    def _blocks(self):
        total = self.rows * self.ways
        block = min(self.BLOCK, total)
        return [(start, block) for start in range(0, total, block)]

    def _scores(self, start, size):
        query = lax.dynamic_slice_in_dim(self.query, start, size, axis=0)
        seg_q = lax.dynamic_slice_in_dim(self.seg_all, start, size, axis=0)
        pos_q = lax.dynamic_slice_in_dim(self.pos_all, start, size, axis=0)
        scores = jnp.einsum(
            "qhd,khd->hqk", query, self.keys, preferred_element_type=jnp.float32
        ) * (1.0 / math.sqrt(HD))
        allowed = (seg_q[:, None] == self.seg_all[None, :]) & (
            self.pos_all[None, :] <= pos_q[:, None]
        )
        return query, jnp.where(allowed[None], scores, NEG), allowed

    def forward(self):
        outs = []
        logs = []
        for start, size in self._blocks():
            _, scores, allowed = self._scores(start, size)
            peak = jnp.max(scores, axis=-1)
            weights = jnp.where(allowed[None], jnp.exp(scores - peak[..., None]), 0.0)
            total = jnp.sum(weights, axis=-1)
            mixed = jnp.einsum(
                "hqk,khd->qhd",
                weights.astype(jnp.bfloat16),
                self.values,
                preferred_element_type=jnp.float32,
            )
            outs.append((mixed / total.T[:, :, None]).astype(jnp.bfloat16))
            logs.append(peak + jnp.log(total))
        self.attended = jnp.concatenate(outs, axis=0)
        self.log_total = jnp.concatenate(logs, axis=1)
        back = self.attended.reshape(self.rows * self.ways, 1, self.group, HD)
        back = lax.all_to_all(back, "context", 0, 1, tiled=True)
        return back.reshape(self.rows, self.heads, HD)

    def backward(self, grad_heads, early, late):
        f32 = jnp.float32
        bf16 = jnp.bfloat16
        scale = 1.0 / math.sqrt(HD)
        grad = grad_heads.reshape(self.rows, self.ways, self.group, HD)
        grad = lax.all_to_all(grad, "context", 1, 0, tiled=True)
        grad, early = lax.optimization_barrier((grad, early))
        grad = grad.reshape(self.rows * self.ways, self.group, HD)
        inner = jnp.sum(grad.astype(f32) * self.attended.astype(f32), axis=-1).T
        grad_key = jnp.zeros(self.keys.shape, f32)
        grad_value = jnp.zeros(self.values.shape, f32)
        grad_queries = []
        for start, size in self._blocks():
            query, scores, allowed = self._scores(start, size)
            log_block = lax.dynamic_slice_in_dim(self.log_total, start, size, axis=1)
            inner_block = lax.dynamic_slice_in_dim(inner, start, size, axis=1)
            grad_block = lax.dynamic_slice_in_dim(grad, start, size, axis=0)
            probs = jnp.where(allowed[None], jnp.exp(scores - log_block[..., None]), 0.0)
            grad_value = grad_value + jnp.einsum(
                "hqk,qhd->khd", probs.astype(bf16), grad_block, preferred_element_type=f32
            )
            grad_probs = jnp.einsum(
                "qhd,khd->hqk", grad_block, self.values, preferred_element_type=f32
            )
            grad_scores = (probs * (grad_probs - inner_block[..., None]) * scale).astype(bf16)
            grad_queries.append(
                jnp.einsum("hqk,khd->qhd", grad_scores, self.keys, preferred_element_type=f32)
            )
            grad_key = grad_key + jnp.einsum(
                "hqk,qhd->khd", grad_scores, query, preferred_element_type=f32
            )
        grad_query = jnp.concatenate(grad_queries, axis=0)
        grad_qin = rotate_back(grad_query, self.cos_all, self.sin_all).astype(bf16)
        grad_kin = rotate_back(grad_key, self.cos_all, self.sin_all).astype(bf16)
        grad_vin = grad_value.astype(bf16)
        stacked = jnp.stack([grad_qin, grad_kin, grad_vin], axis=1)
        stacked, late = lax.optimization_barrier((stacked, late))
        stacked = stacked.reshape(self.rows * self.ways, 3, 1, self.group, HD)
        stacked = lax.all_to_all(stacked, "context", 0, 2, tiled=True)
        stacked = stacked.reshape(self.rows, 3, self.heads, HD)
        return stacked[:, 0], stacked[:, 1], stacked[:, 2], early, late


def mlp_chunks(hidden_cols):
    for count in (2, 1):
        if hidden_cols % (count * 128) == 0:
            return count
    return 1


def on_device(
    inputs, segments, positions, w_q, w_k, w_v, w_o, w_gate, w_up, w_down, g_attn, g_mlp, d_out
):
    f32 = jnp.float32
    bf16 = jnp.bfloat16
    rows = inputs.shape[1]
    width = inputs.shape[2]
    cols = w_q.shape[1]
    hidden_cols = w_gate.shape[1]
    tokens = inputs.reshape(rows, width)
    segment = segments.reshape(rows)
    position = positions.reshape(rows)
    full_qkv = lax.all_gather(jnp.concatenate([w_q, w_k, w_v], axis=1), ROWS, axis=0, tiled=True)
    full_o = lax.all_gather(w_o, ROWS, axis=0, tiled=True)
    gains = lax.all_gather(
        jnp.concatenate([g_attn, g_mlp])[None], ROWS, axis=0, tiled=True
    )
    gain_attn = gains[:, : g_attn.shape[0]].reshape(width)
    gain_mlp = gains[:, g_attn.shape[0] :].reshape(width)
    count = mlp_chunks(hidden_cols)
    step = hidden_cols // count
    fetched = []
    for index in range(count):
        part = slice(index * step, (index + 1) * step)
        fetched.append(
            tuple(
                lax.all_gather(weight[:, part], ROWS, axis=0, tiled=True)
                for weight in (w_gate, w_up, w_down)
            )
        )
    heads = cols // HD
    cosine, sine = rope_tables(position)
    resid1 = tokens.astype(f32)
    norm1, inv1 = normalize(resid1)
    h1 = (norm1 * gain_attn.astype(f32)).astype(bf16)
    projected = jnp.dot(h1, full_qkv, preferred_element_type=f32)
    query = rotate(projected[:, :cols].reshape(rows, heads, HD), cosine, sine).astype(bf16)
    key_heads = rotate(projected[:, cols : 2 * cols].reshape(rows, heads, HD), cosine, sine).astype(
        bf16
    )
    value_heads = projected[:, 2 * cols :].astype(bf16).reshape(rows, heads, HD)
    if heads % lax.axis_size("context") == 0:
        attention = HeadAttention(query, key_heads, value_heads, segment, position, cosine, sine)
    else:
        attention = RingAttention(
            query,
            key_heads.reshape(rows, cols),
            value_heads.reshape(rows, cols),
            segment,
            position,
            cosine,
            sine,
        )
    attended = attention.forward()
    attended_flat = attended.reshape(rows, cols)
    resid2 = resid1 + tensor_total(contract_last(attended_flat, full_o))
    norm2, inv2 = normalize(resid2)
    h2_part = (norm2 * gain_mlp.astype(f32)).astype(bf16)
    grad_y = d_out.reshape(rows, width)
    mlp_partial = None
    h2_grad_partial = None
    staged = []
    for full_gate, full_up, full_down in fetched:
        gate = jnp.dot(h2_part, full_gate, preferred_element_type=f32)
        up = jnp.dot(h2_part, full_up, preferred_element_type=f32)
        active = jax.nn.silu(gate)
        hidden = (active * up).astype(bf16)
        out_part = contract_last(hidden, full_down)
        mlp_partial = out_part if mlp_partial is None else mlp_partial + out_part
        grad_hidden = jnp.dot(grad_y, full_down, preferred_element_type=f32)
        sigma = jax.nn.sigmoid(gate)
        grad_gate = (grad_hidden * up * sigma * (1.0 + gate * (1.0 - sigma))).astype(bf16)
        grad_up = (grad_hidden * active).astype(bf16)
        back_part = contract_last(grad_gate, full_gate) + contract_last(grad_up, full_up)
        pending = (
            contract_first(h2_part, grad_gate),
            contract_first(h2_part, grad_up),
            contract_first(grad_y, hidden),
        )
        if staged:
            back_part, staged[-1] = lax.optimization_barrier((back_part, staged[-1]))
        h2_grad_partial = back_part if h2_grad_partial is None else h2_grad_partial + back_part
        staged.append(tuple(chip_total(value) for value in pending))
    grad_h2 = tensor_total(h2_grad_partial)
    grad_h2, staged[-1] = lax.optimization_barrier((grad_h2, staged[-1]))
    reduced = [tuple(line_total(value) for value in chunk) for chunk in staged]
    result = (resid2 + tensor_total(mlp_partial)).astype(bf16)
    grad_gmlp = jnp.sum(grad_h2 * norm2, axis=0)
    grad_resid = grad_y.astype(f32) + norm_back(grad_h2, norm2, inv2, gain_mlp)
    grad_resid_part = grad_resid.astype(bf16)
    grad_heads = (
        jnp.dot(grad_resid_part, full_o, preferred_element_type=f32)
        .astype(bf16)
        .reshape(rows, heads, HD)
    )
    grad_heads, partial_o = lax.optimization_barrier(
        (grad_heads, contract_first(grad_resid_part, attended_flat))
    )
    early = (chip_total(partial_o), reduced[:-1])
    grad_qin, grad_kin, grad_vin, early, late = attention.backward(grad_heads, early, reduced[-1])
    staged_o, reduced[:-1] = early
    reduced[-1] = late
    reduced_o = line_total(staged_o)
    grad_qkv = jnp.concatenate(
        [grad_qin.reshape(rows, cols), grad_kin.reshape(rows, cols), grad_vin.reshape(rows, cols)],
        axis=1,
    )
    grad_h1 = tensor_total(contract_last(grad_qkv, full_qkv))
    grad_h1, reduced_o = lax.optimization_barrier((grad_h1, reduced_o))
    grad_gattn = jnp.sum(grad_h1 * norm1, axis=0)
    grad_x_part = (grad_resid + norm_back(grad_h1, norm1, inv1, gain_attn)).astype(bf16)
    gain_slab = jnp.pad(jnp.stack([grad_gattn, grad_gmlp], axis=1), ((0, 0), (0, 126)))
    reduced_qkv = rows_total(
        jnp.concatenate([contract_first(h1, grad_qkv), gain_slab], axis=1)
    )
    reduced_gains = reduced_qkv[:, 3 * cols :]
    reduced_gate, reduced_up, reduced_down = (
        jnp.concatenate([chunk[which] for chunk in reduced], axis=1) for which in range(3)
    )
    return (
        result.reshape(1, rows, width),
        grad_x_part.reshape(1, rows, width),
        reduced_qkv[:, :cols],
        reduced_qkv[:, cols : 2 * cols],
        reduced_qkv[:, 2 * cols : 3 * cols],
        reduced_o,
        reduced_gate,
        reduced_up,
        reduced_down,
        reduced_gains[:, 0],
        reduced_gains[:, 1],
    )


def solution(mesh):
    placed = (
        P("shard", "context", None),
        P("shard", "context"),
        P("shard", "context"),
        P(ROWS, "tensor"),
        P(ROWS, "tensor"),
        P(ROWS, "tensor"),
        P(ROWS, "tensor"),
        P(ROWS, "tensor"),
        P(ROWS, "tensor"),
        P(ROWS, "tensor"),
        P(ROWS),
        P(ROWS),
        P("shard", "context", None),
    )
    return jax.shard_map(
        on_device,
        mesh=mesh,
        in_specs=placed,
        out_specs=(
            P("shard", "context", None),
            P("shard", "context", None),
            P(ROWS, "tensor"),
            P(ROWS, "tensor"),
            P(ROWS, "tensor"),
            P(ROWS, "tensor"),
            P(ROWS, "tensor"),
            P(ROWS, "tensor"),
            P(ROWS, "tensor"),
            P(ROWS),
            P(ROWS),
        ),
        check_vma=False,
    )
```

```python
import math

import jax
import jax.numpy as jnp
from jax import lax
from jax.sharding import PartitionSpec as P

HD = 64


EPS = 1e-05
THETA = 130000.0
NEG = -1e30
ROWS = ("shard", "context")


def passed_along(value, axis, steps):
    count = lax.axis_size(axis)
    pairs = [(source, (source + steps) % count) for source in range(count)]
    return lax.ppermute(value, axis, pairs)


def rope_tables(position):
    index = jnp.arange(HD // 2, dtype=jnp.float32)
    inverse = jnp.power(jnp.float32(THETA), -2.0 * index / HD)
    angle = position.astype(jnp.float32)[:, None] * inverse[None, :]
    return (jnp.cos(angle), jnp.sin(angle))


def rotate(tensor, cosine, sine):
    half = tensor.shape[-1] // 2
    first = tensor[..., :half]
    second = tensor[..., half:]
    cosine = cosine[:, None, :]
    sine = sine[:, None, :]
    return jnp.concatenate(
        [first * cosine - second * sine, second * cosine + first * sine], axis=-1
    )


def rotate_back(grad, cosine, sine):
    half = grad.shape[-1] // 2
    first = grad[..., :half]
    second = grad[..., half:]
    cosine = cosine[:, None, :]
    sine = sine[:, None, :]
    return jnp.concatenate(
        [first * cosine + second * sine, second * cosine - first * sine], axis=-1
    )


def normalize(value):
    inv_rms = lax.rsqrt(jnp.mean(value * value, axis=-1, keepdims=True) + EPS)
    return (value * inv_rms, inv_rms)


def norm_back(grad, normed, inv_rms, gain):
    scaled = grad * gain.astype(jnp.float32)
    return inv_rms * (scaled - normed * jnp.mean(scaled * normed, axis=-1, keepdims=True))


def contract_last(left, right):
    return lax.dot_general(
        left, right, (((1,), (1,)), ((), ())), preferred_element_type=jnp.float32
    )


def contract_first(left, right):
    return lax.dot_general(
        left, right, (((0,), (0,)), ((), ())), preferred_element_type=jnp.float32
    )


def half_of(value, bit):
    size = value.shape[0] // 2
    return lax.dynamic_slice_in_dim(value, bit * size, size, axis=0)


def joined(mine, other, bit):
    low = jnp.where(bit == 0, mine, other)
    high = jnp.where(bit == 0, other, mine)
    return jnp.concatenate([low, high], axis=0)


def tensor_total(partial_sum):
    count = lax.axis_size("tensor")
    rows = partial_sum.shape[0]
    if count != 4 or rows % 8:
        return lax.psum(partial_sum.astype(jnp.bfloat16), "tensor").astype(jnp.float32)
    f32 = jnp.float32
    bf16 = jnp.bfloat16
    index = lax.axis_index("tensor")
    x_bit = index % 2
    y_bit = index // 2
    x_pairs = [(i, i ^ 1) for i in range(4)]
    y_pairs = [(i, i ^ 2) for i in range(4)]

    def swap(value, pairs):
        return lax.ppermute(value.astype(bf16), "tensor", pairs).astype(f32)

    first = partial_sum[: rows // 2]
    second = partial_sum[rows // 2 :]
    first = half_of(first, x_bit) + swap(half_of(first, 1 - x_bit), x_pairs)
    second = half_of(second, y_bit) + swap(half_of(second, 1 - y_bit), y_pairs)
    first = half_of(first, y_bit) + swap(half_of(first, 1 - y_bit), y_pairs)
    second = half_of(second, x_bit) + swap(half_of(second, 1 - x_bit), x_pairs)
    first = first.astype(bf16)
    second = second.astype(bf16)
    first = joined(first, lax.ppermute(first, "tensor", y_pairs), y_bit)
    second = joined(second, lax.ppermute(second, "tensor", x_pairs), x_bit)
    first = joined(first, lax.ppermute(first, "tensor", x_pairs), x_bit)
    second = joined(second, lax.ppermute(second, "tensor", y_pairs), y_bit)
    return jnp.concatenate([first, second], axis=0).astype(f32)


def chip_total(grad):
    f32 = jnp.float32
    shard = lax.axis_index("shard")
    mine = half_of(grad, shard)
    other = half_of(grad, 1 - shard)
    got = lax.ppermute(other.astype(jnp.bfloat16), "shard", [(0, 1), (1, 0)])
    return mine.astype(f32) + got.astype(f32)


def line_total(staged):
    return lax.psum_scatter(
        staged.astype(jnp.bfloat16), "context", scatter_dimension=0, tiled=True
    ).astype(jnp.float32)


def rows_total(grad):
    return line_total(chip_total(grad))


def pass_grads(grad_key, grad_value):
    return (
        passed_along(grad_key.astype(jnp.bfloat16), "context", 1).astype(grad_key.dtype),
        passed_along(grad_value.astype(jnp.bfloat16), "context", 1).astype(grad_value.dtype),
    )


def key_scores(query_heads, query_seg, query_pos, piece):
    key_flat, value_flat, key_seg, key_pos = piece
    heads = query_heads.shape[1]
    key_heads = key_flat.reshape(key_flat.shape[0], heads, HD)
    value_heads = value_flat.reshape(value_flat.shape[0], heads, HD)
    scores = jnp.einsum(
        "qhd,khd->hqk", query_heads, key_heads, preferred_element_type=jnp.float32
    ) * (1.0 / math.sqrt(HD))
    allowed = (query_seg[:, None] == key_seg[None, :]) & (key_pos[None, :] <= query_pos[:, None])
    return (jnp.where(allowed[None], scores, NEG), allowed, key_heads, value_heads)


def forward_fold(stats, piece, query_heads, query_seg, query_pos):
    peak, total, accum = stats
    scores, allowed, key_heads, value_heads = key_scores(query_heads, query_seg, query_pos, piece)
    new_peak = jnp.maximum(peak, jnp.max(scores, axis=-1))
    weights = jnp.where(allowed[None], jnp.exp(scores - new_peak[..., None]), 0.0)
    factor = jnp.exp(peak - new_peak)
    total = total * factor + jnp.sum(weights, axis=-1)
    accum = accum * factor[..., None] + jnp.einsum(
        "hqk,khd->hqd",
        weights.astype(jnp.bfloat16),
        value_heads,
        preferred_element_type=jnp.float32,
    )
    return (new_peak, total, accum)


def backward_piece(piece, query_heads, grad_heads, log_total, inner, query_seg, query_pos):
    scores, allowed, key_heads, value_heads = key_scores(query_heads, query_seg, query_pos, piece)
    probs = jnp.where(allowed[None], jnp.exp(scores - log_total[..., None]), 0.0)
    grad_value = jnp.einsum(
        "hqk,qhd->khd", probs.astype(jnp.bfloat16), grad_heads, preferred_element_type=jnp.float32
    )
    grad_probs = jnp.einsum(
        "qhd,khd->hqk", grad_heads, value_heads, preferred_element_type=jnp.float32
    )
    grad_scores = (probs * (grad_probs - inner[..., None]) * (1.0 / math.sqrt(HD))).astype(
        jnp.bfloat16
    )
    grad_query = jnp.einsum(
        "hqk,khd->qhd", grad_scores, key_heads, preferred_element_type=jnp.float32
    )
    grad_key = jnp.einsum(
        "hqk,qhd->khd", grad_scores, query_heads, preferred_element_type=jnp.float32
    )
    key_rows = grad_key.shape[0]
    return (grad_query, grad_key.reshape(key_rows, -1), grad_value.reshape(key_rows, -1))


class RingAttention:
    def __init__(self, query, key_flat, value_flat, segment, position, cosine, sine):
        self.query = query
        self.piece = (key_flat, value_flat, segment, position)
        self.segment = segment
        self.position = position
        self.cosine = cosine
        self.sine = sine

    def forward(self):
        f32 = jnp.float32
        query, segment, position = self.query, self.segment, self.position
        rows, heads = query.shape[0], query.shape[1]
        start_stats = (
            jnp.full((heads, rows), NEG, f32),
            jnp.zeros((heads, rows), f32),
            jnp.zeros((heads, rows, HD), f32),
        )
        stats = forward_fold(start_stats, self.piece, query, segment, position)

        def cycle_turn(index, carry):
            moving, current = carry
            moving = passed_along(moving, "context", 1)
            current = forward_fold(current, moving, query, segment, position)
            return (moving, current)

        peak, total, accum = lax.fori_loop(
            0, lax.axis_size("context") - 1, cycle_turn, (self.piece, stats)
        )[1]
        self.attended = jnp.transpose(accum / total[..., None], (1, 0, 2)).astype(jnp.bfloat16)
        self.log_total = peak + jnp.log(total)
        return self.attended

    def backward(self, grad_heads, early):
        bf16 = jnp.bfloat16
        query, segment, position = self.query, self.segment, self.position
        rows, heads = query.shape[0], query.shape[1]
        inner = jnp.sum(grad_heads.astype(jnp.float32) * self.attended.astype(jnp.float32), axis=-1).T

        def piece_grads(piece):
            return backward_piece(piece, query, grad_heads, self.log_total, inner, segment, position)

        grad_query, grad_key, grad_value = piece_grads(self.piece)

        def grad_turn(index, carry):
            moving, acc_query, acc_key, acc_value = carry
            moving = passed_along(moving, "context", 1)
            acc_key, acc_value = pass_grads(acc_key, acc_value)
            part_query, part_key, part_value = piece_grads(moving)
            return (moving, acc_query + part_query, acc_key + part_key, acc_value + part_value)

        carried = lax.fori_loop(
            0,
            lax.axis_size("context") - 1,
            grad_turn,
            (self.piece, grad_query, grad_key, grad_value),
        )
        grad_query = carried[1]
        grad_key, grad_value = pass_grads(carried[2], carried[3])
        grad_qin = rotate_back(grad_query, self.cosine, self.sine).astype(bf16)
        grad_kin = rotate_back(grad_key.reshape(rows, heads, HD), self.cosine, self.sine).astype(bf16)
        grad_vin = grad_value.astype(bf16).reshape(rows, heads, HD)
        return grad_qin, grad_kin, grad_vin, early


class HeadAttention:
    BLOCK = 512

    def __init__(self, query, key_heads, value_heads, segment, position, cosine, sine):
        ways = lax.axis_size("context")
        rows, heads = query.shape[0], query.shape[1]
        self.ways = ways
        self.rows = rows
        self.heads = heads
        self.group = heads // ways
        stacked = jnp.stack([query, key_heads, value_heads], axis=1)
        stacked = stacked.reshape(rows, 3, ways, self.group, HD)
        stacked = lax.all_to_all(stacked, "context", 2, 0, tiled=True)
        stacked = stacked.reshape(rows * ways, 3, self.group, HD)
        self.query = stacked[:, 0]
        self.keys = stacked[:, 1]
        self.values = stacked[:, 2]
        tags = jnp.stack([segment, position], axis=0)[None]
        tags = jnp.broadcast_to(tags, (ways, 2, rows))
        tags = lax.all_to_all(tags, "context", 0, 0, tiled=True)
        tags = jnp.transpose(tags, (1, 0, 2)).reshape(2, rows * ways)
        self.seg_all = tags[0]
        self.pos_all = tags[1]
        self.cos_all, self.sin_all = rope_tables(self.pos_all)

    def _blocks(self):
        total = self.rows * self.ways
        block = min(self.BLOCK, total)
        return [(start, block) for start in range(0, total, block)]

    def _scores(self, start, size):
        query = lax.dynamic_slice_in_dim(self.query, start, size, axis=0)
        seg_q = lax.dynamic_slice_in_dim(self.seg_all, start, size, axis=0)
        pos_q = lax.dynamic_slice_in_dim(self.pos_all, start, size, axis=0)
        scores = jnp.einsum(
            "qhd,khd->hqk", query, self.keys, preferred_element_type=jnp.float32
        ) * (1.0 / math.sqrt(HD))
        allowed = (seg_q[:, None] == self.seg_all[None, :]) & (
            self.pos_all[None, :] <= pos_q[:, None]
        )
        return query, jnp.where(allowed[None], scores, NEG), allowed

    def forward(self):
        outs = []
        logs = []
        for start, size in self._blocks():
            _, scores, allowed = self._scores(start, size)
            peak = jnp.max(scores, axis=-1)
            weights = jnp.where(allowed[None], jnp.exp(scores - peak[..., None]), 0.0)
            total = jnp.sum(weights, axis=-1)
            mixed = jnp.einsum(
                "hqk,khd->qhd",
                weights.astype(jnp.bfloat16),
                self.values,
                preferred_element_type=jnp.float32,
            )
            outs.append((mixed / total.T[:, :, None]).astype(jnp.bfloat16))
            logs.append(peak + jnp.log(total))
        self.attended = jnp.concatenate(outs, axis=0)
        self.log_total = jnp.concatenate(logs, axis=1)
        back = self.attended.reshape(self.rows * self.ways, 1, self.group, HD)
        back = lax.all_to_all(back, "context", 0, 1, tiled=True)
        return back.reshape(self.rows, self.heads, HD)

    def backward(self, grad_heads, early):
        f32 = jnp.float32
        bf16 = jnp.bfloat16
        scale = 1.0 / math.sqrt(HD)
        grad = grad_heads.reshape(self.rows, self.ways, self.group, HD)
        grad = lax.all_to_all(grad, "context", 1, 0, tiled=True)
        grad, early = lax.optimization_barrier((grad, early))
        grad = grad.reshape(self.rows * self.ways, self.group, HD)
        inner = jnp.sum(grad.astype(f32) * self.attended.astype(f32), axis=-1).T
        grad_key = jnp.zeros(self.keys.shape, f32)
        grad_value = jnp.zeros(self.values.shape, f32)
        grad_queries = []
        for start, size in self._blocks():
            query, scores, allowed = self._scores(start, size)
            log_block = lax.dynamic_slice_in_dim(self.log_total, start, size, axis=1)
            inner_block = lax.dynamic_slice_in_dim(inner, start, size, axis=1)
            grad_block = lax.dynamic_slice_in_dim(grad, start, size, axis=0)
            probs = jnp.where(allowed[None], jnp.exp(scores - log_block[..., None]), 0.0)
            grad_value = grad_value + jnp.einsum(
                "hqk,qhd->khd", probs.astype(bf16), grad_block, preferred_element_type=f32
            )
            grad_probs = jnp.einsum(
                "qhd,khd->hqk", grad_block, self.values, preferred_element_type=f32
            )
            grad_scores = (probs * (grad_probs - inner_block[..., None]) * scale).astype(bf16)
            grad_queries.append(
                jnp.einsum("hqk,khd->qhd", grad_scores, self.keys, preferred_element_type=f32)
            )
            grad_key = grad_key + jnp.einsum(
                "hqk,qhd->khd", grad_scores, query, preferred_element_type=f32
            )
        grad_query = jnp.concatenate(grad_queries, axis=0)
        grad_qin = rotate_back(grad_query, self.cos_all, self.sin_all).astype(bf16)
        grad_kin = rotate_back(grad_key, self.cos_all, self.sin_all).astype(bf16)
        grad_vin = grad_value.astype(bf16)
        returned = []
        for grad_in in (grad_qin, grad_kin, grad_vin):
            grad_in = grad_in.reshape(self.rows * self.ways, 1, self.group, HD)
            grad_in = lax.all_to_all(grad_in, "context", 0, 1, tiled=True)
            returned.append(grad_in.reshape(self.rows, self.heads, HD))
        return returned[0], returned[1], returned[2], early


def mlp_chunks(hidden_cols):
    for count in (2, 1):
        if hidden_cols % (count * 128) == 0:
            return count
    return 1


def on_device(
    inputs, segments, positions, w_q, w_k, w_v, w_o, w_gate, w_up, w_down, g_attn, g_mlp, d_out
):
    f32 = jnp.float32
    bf16 = jnp.bfloat16
    rows = inputs.shape[1]
    width = inputs.shape[2]
    cols = w_q.shape[1]
    hidden_cols = w_gate.shape[1]
    tokens = inputs.reshape(rows, width)
    segment = segments.reshape(rows)
    position = positions.reshape(rows)
    full_qkv = lax.all_gather(jnp.concatenate([w_q, w_k, w_v], axis=1), ROWS, axis=0, tiled=True)
    full_o = lax.all_gather(w_o, ROWS, axis=0, tiled=True)
    gains = lax.all_gather(
        jnp.concatenate([g_attn, g_mlp])[None], ROWS, axis=0, tiled=True
    )
    gain_attn = gains[:, : g_attn.shape[0]].reshape(width)
    gain_mlp = gains[:, g_attn.shape[0] :].reshape(width)
    count = mlp_chunks(hidden_cols)
    step = hidden_cols // count
    fetched = []
    for index in range(count):
        part = slice(index * step, (index + 1) * step)
        fetched.append(
            tuple(
                lax.all_gather(weight[:, part], ROWS, axis=0, tiled=True)
                for weight in (w_gate, w_up, w_down)
            )
        )
    heads = cols // HD
    cosine, sine = rope_tables(position)
    resid1 = tokens.astype(f32)
    norm1, inv1 = normalize(resid1)
    h1 = (norm1 * gain_attn.astype(f32)).astype(bf16)
    projected = jnp.dot(h1, full_qkv, preferred_element_type=f32)
    query = rotate(projected[:, :cols].reshape(rows, heads, HD), cosine, sine).astype(bf16)
    key_heads = rotate(projected[:, cols : 2 * cols].reshape(rows, heads, HD), cosine, sine).astype(
        bf16
    )
    value_heads = projected[:, 2 * cols :].astype(bf16).reshape(rows, heads, HD)
    if heads % lax.axis_size("context") == 0:
        attention = HeadAttention(query, key_heads, value_heads, segment, position, cosine, sine)
    else:
        attention = RingAttention(
            query,
            key_heads.reshape(rows, cols),
            value_heads.reshape(rows, cols),
            segment,
            position,
            cosine,
            sine,
        )
    attended = attention.forward()
    attended_flat = attended.reshape(rows, cols)
    resid2 = resid1 + tensor_total(contract_last(attended_flat, full_o))
    norm2, inv2 = normalize(resid2)
    h2_part = (norm2 * gain_mlp.astype(f32)).astype(bf16)
    grad_y = d_out.reshape(rows, width)
    mlp_partial = None
    h2_grad_partial = None
    staged = []
    for full_gate, full_up, full_down in fetched:
        if staged:
            full_gate, staged[-1] = lax.optimization_barrier((full_gate, staged[-1]))
        gate = jnp.dot(h2_part, full_gate, preferred_element_type=f32)
        up = jnp.dot(h2_part, full_up, preferred_element_type=f32)
        active = jax.nn.silu(gate)
        hidden = (active * up).astype(bf16)
        out_part = contract_last(hidden, full_down)
        mlp_partial = out_part if mlp_partial is None else mlp_partial + out_part
        grad_hidden = jnp.dot(grad_y, full_down, preferred_element_type=f32)
        sigma = jax.nn.sigmoid(gate)
        grad_gate = (grad_hidden * up * sigma * (1.0 + gate * (1.0 - sigma))).astype(bf16)
        grad_up = (grad_hidden * active).astype(bf16)
        back_part = contract_last(grad_gate, full_gate) + contract_last(grad_up, full_up)
        pending = (
            contract_first(h2_part, grad_gate),
            contract_first(h2_part, grad_up),
            contract_first(grad_y, hidden),
        )
        h2_grad_partial = back_part if h2_grad_partial is None else h2_grad_partial + back_part
        staged.append(tuple(chip_total(value) for value in pending))
    grad_h2 = tensor_total(h2_grad_partial)
    grad_h2, staged[-1] = lax.optimization_barrier((grad_h2, staged[-1]))
    reduced = [tuple(line_total(value) for value in chunk) for chunk in staged]
    result = (resid2 + tensor_total(mlp_partial)).astype(bf16)
    grad_gmlp = jnp.sum(grad_h2 * norm2, axis=0)
    grad_resid = grad_y.astype(f32) + norm_back(grad_h2, norm2, inv2, gain_mlp)
    grad_resid_part = grad_resid.astype(bf16)
    grad_heads = (
        jnp.dot(grad_resid_part, full_o, preferred_element_type=f32)
        .astype(bf16)
        .reshape(rows, heads, HD)
    )
    grad_heads, partial_o = lax.optimization_barrier(
        (grad_heads, contract_first(grad_resid_part, attended_flat))
    )
    early = (chip_total(partial_o), reduced[:-1])
    grad_qin, grad_kin, grad_vin, early = attention.backward(grad_heads, early)
    staged_o, reduced[:-1] = early
    reduced_o = line_total(staged_o)
    grad_qkv = jnp.concatenate(
        [grad_qin.reshape(rows, cols), grad_kin.reshape(rows, cols), grad_vin.reshape(rows, cols)],
        axis=1,
    )
    h1_grad_partial, staged_qkv = lax.optimization_barrier(
        (contract_last(grad_qkv, full_qkv), chip_total(contract_first(h1, grad_qkv)))
    )
    grad_h1 = tensor_total(h1_grad_partial)
    grad_h1, reduced_o, reduced[-1] = lax.optimization_barrier((grad_h1, reduced_o, reduced[-1]))
    grad_gattn = jnp.sum(grad_h1 * norm1, axis=0)
    grad_x_part = (grad_resid + norm_back(grad_h1, norm1, inv1, gain_attn)).astype(bf16)
    gain_slab = jnp.pad(jnp.stack([grad_gattn, grad_gmlp], axis=1), ((0, 0), (0, 126)))
    reduced_qkv = line_total(staged_qkv)
    reduced_gains = rows_total(gain_slab)
    reduced_gate, reduced_up, reduced_down = (
        jnp.concatenate([chunk[which] for chunk in reduced], axis=1) for which in range(3)
    )
    return (
        result.reshape(1, rows, width),
        grad_x_part.reshape(1, rows, width),
        reduced_qkv[:, :cols],
        reduced_qkv[:, cols : 2 * cols],
        reduced_qkv[:, 2 * cols :],
        reduced_o,
        reduced_gate,
        reduced_up,
        reduced_down,
        reduced_gains[:, 0],
        reduced_gains[:, 1],
    )


def solution(mesh):
    placed = (
        P("shard", "context", None),
        P("shard", "context"),
        P("shard", "context"),
        P(ROWS, "tensor"),
        P(ROWS, "tensor"),
        P(ROWS, "tensor"),
        P(ROWS, "tensor"),
        P(ROWS, "tensor"),
        P(ROWS, "tensor"),
        P(ROWS, "tensor"),
        P(ROWS),
        P(ROWS),
        P("shard", "context", None),
    )
    return jax.shard_map(
        on_device,
        mesh=mesh,
        in_specs=placed,
        out_specs=(
            P("shard", "context", None),
            P("shard", "context", None),
            P(ROWS, "tensor"),
            P(ROWS, "tensor"),
            P(ROWS, "tensor"),
            P(ROWS, "tensor"),
            P(ROWS, "tensor"),
            P(ROWS, "tensor"),
            P(ROWS, "tensor"),
            P(ROWS),
            P(ROWS),
        ),
        check_vma=False,
    )
```

```python
import math

import jax
import jax.numpy as jnp
from jax import lax
from jax.sharding import PartitionSpec as P

HD = 64


EPS = 1e-05
THETA = 130000.0
NEG = -1e30
ROWS = ("shard", "context")


def passed_along(value, axis, steps):
    count = lax.axis_size(axis)
    pairs = [(source, (source + steps) % count) for source in range(count)]
    return lax.ppermute(value, axis, pairs)


def rope_tables(position):
    index = jnp.arange(HD // 2, dtype=jnp.float32)
    inverse = jnp.power(jnp.float32(THETA), -2.0 * index / HD)
    angle = position.astype(jnp.float32)[:, None] * inverse[None, :]
    return (jnp.cos(angle), jnp.sin(angle))


def rotate(tensor, cosine, sine):
    half = tensor.shape[-1] // 2
    first = tensor[..., :half]
    second = tensor[..., half:]
    cosine = cosine[:, None, :]
    sine = sine[:, None, :]
    return jnp.concatenate(
        [first * cosine - second * sine, second * cosine + first * sine], axis=-1
    )


def rotate_back(grad, cosine, sine):
    half = grad.shape[-1] // 2
    first = grad[..., :half]
    second = grad[..., half:]
    cosine = cosine[:, None, :]
    sine = sine[:, None, :]
    return jnp.concatenate(
        [first * cosine + second * sine, second * cosine - first * sine], axis=-1
    )


def normalize(value):
    inv_rms = lax.rsqrt(jnp.mean(value * value, axis=-1, keepdims=True) + EPS)
    return (value * inv_rms, inv_rms)


def norm_back(grad, normed, inv_rms, gain):
    scaled = grad * gain.astype(jnp.float32)
    return inv_rms * (scaled - normed * jnp.mean(scaled * normed, axis=-1, keepdims=True))


def contract_last(left, right):
    return lax.dot_general(
        left, right, (((1,), (1,)), ((), ())), preferred_element_type=jnp.float32
    )


def contract_first(left, right):
    return lax.dot_general(
        left, right, (((0,), (0,)), ((), ())), preferred_element_type=jnp.float32
    )


def half_of(value, bit):
    size = value.shape[0] // 2
    return lax.dynamic_slice_in_dim(value, bit * size, size, axis=0)


def joined(mine, other, bit):
    low = jnp.where(bit == 0, mine, other)
    high = jnp.where(bit == 0, other, mine)
    return jnp.concatenate([low, high], axis=0)


def tensor_total(partial_sum):
    count = lax.axis_size("tensor")
    rows = partial_sum.shape[0]
    if count != 4 or rows % 8:
        return lax.psum(partial_sum.astype(jnp.bfloat16), "tensor").astype(jnp.float32)
    f32 = jnp.float32
    bf16 = jnp.bfloat16
    index = lax.axis_index("tensor")
    x_bit = index % 2
    y_bit = index // 2
    x_pairs = [(i, i ^ 1) for i in range(4)]
    y_pairs = [(i, i ^ 2) for i in range(4)]

    def swap(value, pairs):
        return lax.ppermute(value.astype(bf16), "tensor", pairs).astype(f32)

    first = partial_sum[: rows // 2]
    second = partial_sum[rows // 2 :]
    first = half_of(first, x_bit) + swap(half_of(first, 1 - x_bit), x_pairs)
    second = half_of(second, y_bit) + swap(half_of(second, 1 - y_bit), y_pairs)
    first = half_of(first, y_bit) + swap(half_of(first, 1 - y_bit), y_pairs)
    second = half_of(second, x_bit) + swap(half_of(second, 1 - x_bit), x_pairs)
    first = first.astype(bf16)
    second = second.astype(bf16)
    first = joined(first, lax.ppermute(first, "tensor", y_pairs), y_bit)
    second = joined(second, lax.ppermute(second, "tensor", x_pairs), x_bit)
    first = joined(first, lax.ppermute(first, "tensor", x_pairs), x_bit)
    second = joined(second, lax.ppermute(second, "tensor", y_pairs), y_bit)
    return jnp.concatenate([first, second], axis=0).astype(f32)


def tensor_exact_total(value):
    if lax.axis_size("tensor") != 4:
        return lax.psum(value, "tensor")
    value = value + lax.ppermute(value, "tensor", [(i, i ^ 1) for i in range(4)])
    return value + lax.ppermute(value, "tensor", [(i, i ^ 2) for i in range(4)])


def chip_total(grad):
    f32 = jnp.float32
    shard = lax.axis_index("shard")
    mine = half_of(grad, shard)
    other = half_of(grad, 1 - shard)
    got = lax.ppermute(other.astype(jnp.bfloat16), "shard", [(0, 1), (1, 0)])
    return mine.astype(f32) + got.astype(f32)


def line_total(staged):
    return lax.psum_scatter(
        staged.astype(jnp.bfloat16), "context", scatter_dimension=0, tiled=True
    ).astype(jnp.float32)


def rows_total(grad):
    return line_total(chip_total(grad))


def pass_grads(grad_key, grad_value):
    return (
        passed_along(grad_key.astype(jnp.bfloat16), "context", 1).astype(grad_key.dtype),
        passed_along(grad_value.astype(jnp.bfloat16), "context", 1).astype(grad_value.dtype),
    )


def key_scores(query_heads, query_seg, query_pos, piece):
    key_flat, value_flat, key_seg, key_pos = piece
    heads = query_heads.shape[1]
    key_heads = key_flat.reshape(key_flat.shape[0], heads, HD)
    value_heads = value_flat.reshape(value_flat.shape[0], heads, HD)
    scores = jnp.einsum(
        "qhd,khd->hqk", query_heads, key_heads, preferred_element_type=jnp.float32
    ) * (1.0 / math.sqrt(HD))
    allowed = (query_seg[:, None] == key_seg[None, :]) & (key_pos[None, :] <= query_pos[:, None])
    return (jnp.where(allowed[None], scores, NEG), allowed, key_heads, value_heads)


def forward_fold(stats, piece, query_heads, query_seg, query_pos):
    peak, total, accum = stats
    scores, allowed, key_heads, value_heads = key_scores(query_heads, query_seg, query_pos, piece)
    new_peak = jnp.maximum(peak, jnp.max(scores, axis=-1))
    weights = jnp.where(allowed[None], jnp.exp(scores - new_peak[..., None]), 0.0)
    factor = jnp.exp(peak - new_peak)
    total = total * factor + jnp.sum(weights, axis=-1)
    accum = accum * factor[..., None] + jnp.einsum(
        "hqk,khd->hqd",
        weights.astype(jnp.bfloat16),
        value_heads,
        preferred_element_type=jnp.float32,
    )
    return (new_peak, total, accum)


def backward_piece(piece, query_heads, grad_heads, log_total, inner, query_seg, query_pos):
    scores, allowed, key_heads, value_heads = key_scores(query_heads, query_seg, query_pos, piece)
    probs = jnp.where(allowed[None], jnp.exp(scores - log_total[..., None]), 0.0)
    grad_value = jnp.einsum(
        "hqk,qhd->khd", probs.astype(jnp.bfloat16), grad_heads, preferred_element_type=jnp.float32
    )
    grad_probs = jnp.einsum(
        "qhd,khd->hqk", grad_heads, value_heads, preferred_element_type=jnp.float32
    )
    grad_scores = (probs * (grad_probs - inner[..., None]) * (1.0 / math.sqrt(HD))).astype(
        jnp.bfloat16
    )
    grad_query = jnp.einsum(
        "hqk,khd->qhd", grad_scores, key_heads, preferred_element_type=jnp.float32
    )
    grad_key = jnp.einsum(
        "hqk,qhd->khd", grad_scores, query_heads, preferred_element_type=jnp.float32
    )
    key_rows = grad_key.shape[0]
    return (grad_query, grad_key.reshape(key_rows, -1), grad_value.reshape(key_rows, -1))


class RingAttention:
    def __init__(self, query, key_flat, value_flat, segment, position, cosine, sine):
        self.query = query
        self.piece = (key_flat, value_flat, segment, position)
        self.segment = segment
        self.position = position
        self.cosine = cosine
        self.sine = sine

    def forward(self):
        f32 = jnp.float32
        query, segment, position = self.query, self.segment, self.position
        rows, heads = query.shape[0], query.shape[1]
        start_stats = (
            jnp.full((heads, rows), NEG, f32),
            jnp.zeros((heads, rows), f32),
            jnp.zeros((heads, rows, HD), f32),
        )
        stats = forward_fold(start_stats, self.piece, query, segment, position)

        def cycle_turn(index, carry):
            moving, current = carry
            moving = passed_along(moving, "context", 1)
            current = forward_fold(current, moving, query, segment, position)
            return (moving, current)

        peak, total, accum = lax.fori_loop(
            0, lax.axis_size("context") - 1, cycle_turn, (self.piece, stats)
        )[1]
        self.attended = jnp.transpose(accum / total[..., None], (1, 0, 2)).astype(jnp.bfloat16)
        self.log_total = peak + jnp.log(total)
        return self.attended

    def backward(self, grad_heads, early):
        bf16 = jnp.bfloat16
        query, segment, position = self.query, self.segment, self.position
        rows, heads = query.shape[0], query.shape[1]
        inner = jnp.sum(grad_heads.astype(jnp.float32) * self.attended.astype(jnp.float32), axis=-1).T

        def piece_grads(piece):
            return backward_piece(piece, query, grad_heads, self.log_total, inner, segment, position)

        grad_query, grad_key, grad_value = piece_grads(self.piece)

        def grad_turn(index, carry):
            moving, acc_query, acc_key, acc_value = carry
            moving = passed_along(moving, "context", 1)
            acc_key, acc_value = pass_grads(acc_key, acc_value)
            part_query, part_key, part_value = piece_grads(moving)
            return (moving, acc_query + part_query, acc_key + part_key, acc_value + part_value)

        carried = lax.fori_loop(
            0,
            lax.axis_size("context") - 1,
            grad_turn,
            (self.piece, grad_query, grad_key, grad_value),
        )
        grad_query = carried[1]
        grad_key, grad_value = pass_grads(carried[2], carried[3])
        grad_qin = rotate_back(grad_query, self.cosine, self.sine).astype(bf16)
        grad_kin = rotate_back(grad_key.reshape(rows, heads, HD), self.cosine, self.sine).astype(bf16)
        grad_vin = grad_value.astype(bf16).reshape(rows, heads, HD)
        return grad_qin, grad_kin, grad_vin, early


class HeadAttention:
    BLOCK = 512

    def __init__(self, query, key_heads, value_heads, segment, position, cosine, sine):
        ways = lax.axis_size("context")
        rows, heads = query.shape[0], query.shape[1]
        self.ways = ways
        self.rows = rows
        self.heads = heads
        self.group = heads // ways
        stacked = jnp.stack([query, key_heads, value_heads], axis=1)
        stacked = stacked.reshape(rows, 3, ways, self.group, HD)
        stacked = lax.all_to_all(stacked, "context", 2, 0, tiled=True)
        stacked = stacked.reshape(rows * ways, 3, self.group, HD)
        self.query = stacked[:, 0]
        self.keys = stacked[:, 1]
        self.values = stacked[:, 2]
        tags = jnp.stack([segment, position], axis=0)[None]
        tags = jnp.broadcast_to(tags, (ways, 2, rows))
        tags = lax.all_to_all(tags, "context", 0, 0, tiled=True)
        tags = jnp.transpose(tags, (1, 0, 2)).reshape(2, rows * ways)
        self.seg_all = tags[0]
        self.pos_all = tags[1]
        self.cos_all, self.sin_all = rope_tables(self.pos_all)

    def _blocks(self):
        total = self.rows * self.ways
        block = min(self.BLOCK, total)
        return [(start, block) for start in range(0, total, block)]

    def _scores(self, start, size):
        query = lax.dynamic_slice_in_dim(self.query, start, size, axis=0)
        seg_q = lax.dynamic_slice_in_dim(self.seg_all, start, size, axis=0)
        pos_q = lax.dynamic_slice_in_dim(self.pos_all, start, size, axis=0)
        scores = jnp.einsum(
            "qhd,khd->hqk", query, self.keys, preferred_element_type=jnp.float32
        ) * (1.0 / math.sqrt(HD))
        allowed = (seg_q[:, None] == self.seg_all[None, :]) & (
            self.pos_all[None, :] <= pos_q[:, None]
        )
        return query, jnp.where(allowed[None], scores, NEG), allowed

    def forward(self):
        outs = []
        logs = []
        for start, size in self._blocks():
            _, scores, allowed = self._scores(start, size)
            peak = jnp.max(scores, axis=-1)
            weights = jnp.where(allowed[None], jnp.exp(scores - peak[..., None]), 0.0)
            total = jnp.sum(weights, axis=-1)
            mixed = jnp.einsum(
                "hqk,khd->qhd",
                weights.astype(jnp.bfloat16),
                self.values,
                preferred_element_type=jnp.float32,
            )
            outs.append((mixed / total.T[:, :, None]).astype(jnp.bfloat16))
            logs.append(peak + jnp.log(total))
        self.attended = jnp.concatenate(outs, axis=0)
        self.log_total = jnp.concatenate(logs, axis=1)
        back = self.attended.reshape(self.rows * self.ways, 1, self.group, HD)
        back = lax.all_to_all(back, "context", 0, 1, tiled=True)
        return back.reshape(self.rows, self.heads, HD)

    def backward(self, grad_heads, early):
        f32 = jnp.float32
        bf16 = jnp.bfloat16
        scale = 1.0 / math.sqrt(HD)
        grad = grad_heads.reshape(self.rows, self.ways, self.group, HD)
        grad = lax.all_to_all(grad, "context", 1, 0, tiled=True)
        grad, early = lax.optimization_barrier((grad, early))
        grad = grad.reshape(self.rows * self.ways, self.group, HD)
        inner = jnp.sum(grad.astype(f32) * self.attended.astype(f32), axis=-1).T
        grad_key = jnp.zeros(self.keys.shape, f32)
        grad_value = jnp.zeros(self.values.shape, f32)
        grad_queries = []
        for start, size in self._blocks():
            query, scores, allowed = self._scores(start, size)
            log_block = lax.dynamic_slice_in_dim(self.log_total, start, size, axis=1)
            inner_block = lax.dynamic_slice_in_dim(inner, start, size, axis=1)
            grad_block = lax.dynamic_slice_in_dim(grad, start, size, axis=0)
            probs = jnp.where(allowed[None], jnp.exp(scores - log_block[..., None]), 0.0)
            grad_value = grad_value + jnp.einsum(
                "hqk,qhd->khd", probs.astype(bf16), grad_block, preferred_element_type=f32
            )
            grad_probs = jnp.einsum(
                "qhd,khd->hqk", grad_block, self.values, preferred_element_type=f32
            )
            grad_scores = (probs * (grad_probs - inner_block[..., None]) * scale).astype(bf16)
            grad_queries.append(
                jnp.einsum("hqk,khd->qhd", grad_scores, self.keys, preferred_element_type=f32)
            )
            grad_key = grad_key + jnp.einsum(
                "hqk,qhd->khd", grad_scores, query, preferred_element_type=f32
            )
        grad_query = jnp.concatenate(grad_queries, axis=0)
        grad_qin = rotate_back(grad_query, self.cos_all, self.sin_all).astype(bf16)
        grad_kin = rotate_back(grad_key, self.cos_all, self.sin_all).astype(bf16)
        grad_vin = grad_value.astype(bf16)
        returned = []
        for grad_in in (grad_qin, grad_kin, grad_vin):
            grad_in = grad_in.reshape(self.rows * self.ways, 1, self.group, HD)
            grad_in = lax.all_to_all(grad_in, "context", 0, 1, tiled=True)
            returned.append(grad_in.reshape(self.rows, self.heads, HD))
        return returned[0], returned[1], returned[2], early


def mlp_chunks(hidden_cols):
    for count in (2, 1):
        if hidden_cols % (count * 128) == 0:
            return count
    return 1


def on_device(
    inputs, segments, positions, w_q, w_k, w_v, w_o, w_gate, w_up, w_down, g_attn, g_mlp, d_out
):
    f32 = jnp.float32
    bf16 = jnp.bfloat16
    rows = inputs.shape[1]
    width = inputs.shape[2]
    cols = w_q.shape[1]
    hidden_cols = w_gate.shape[1]
    tokens = inputs.reshape(rows, width)
    segment = segments.reshape(rows)
    position = positions.reshape(rows)
    full_qkvo = lax.all_gather(
        jnp.concatenate([w_q, w_k, w_v, w_o], axis=1), ROWS, axis=0, tiled=True
    )
    full_qkv = full_qkvo[:, : 3 * cols]
    full_o = full_qkvo[:, 3 * cols :]
    gains = lax.all_gather(
        jnp.concatenate([g_attn, g_mlp])[None], ROWS, axis=0, tiled=True
    )
    gain_attn = gains[:, : g_attn.shape[0]].reshape(width)
    gain_mlp = gains[:, g_attn.shape[0] :].reshape(width)
    count = mlp_chunks(hidden_cols)
    step = hidden_cols // count
    fetched = []
    for index in range(count):
        part = slice(index * step, (index + 1) * step)
        pair = lax.all_gather(
            jnp.concatenate([w_gate[:, part], w_up[:, part]], axis=1), ROWS, axis=0, tiled=True
        )
        fetched.append(
            (pair[:, :step], pair[:, step:], lax.all_gather(w_down[:, part], ROWS, axis=0, tiled=True))
        )
    heads = cols // HD
    cosine, sine = rope_tables(position)
    resid1 = tokens.astype(f32)
    norm1, inv1 = normalize(resid1)
    h1 = (norm1 * gain_attn.astype(f32)).astype(bf16)
    projected = jnp.dot(h1, full_qkv, preferred_element_type=f32)
    query = rotate(projected[:, :cols].reshape(rows, heads, HD), cosine, sine).astype(bf16)
    key_heads = rotate(projected[:, cols : 2 * cols].reshape(rows, heads, HD), cosine, sine).astype(
        bf16
    )
    value_heads = projected[:, 2 * cols :].astype(bf16).reshape(rows, heads, HD)
    if heads % lax.axis_size("context") == 0:
        attention = HeadAttention(query, key_heads, value_heads, segment, position, cosine, sine)
    else:
        attention = RingAttention(
            query,
            key_heads.reshape(rows, cols),
            value_heads.reshape(rows, cols),
            segment,
            position,
            cosine,
            sine,
        )
    attended = attention.forward()
    attended_flat = attended.reshape(rows, cols)
    resid2 = resid1 + tensor_total(contract_last(attended_flat, full_o))
    norm2, inv2 = normalize(resid2)
    h2_part = (norm2 * gain_mlp.astype(f32)).astype(bf16)
    grad_y = d_out.reshape(rows, width)
    mlp_partial = None
    h2_grad_partial = None
    staged = []
    for full_gate, full_up, full_down in fetched:
        if staged:
            full_gate, staged[-1] = lax.optimization_barrier((full_gate, staged[-1]))
        gate = jnp.dot(h2_part, full_gate, preferred_element_type=f32)
        up = jnp.dot(h2_part, full_up, preferred_element_type=f32)
        active = jax.nn.silu(gate)
        hidden = (active * up).astype(bf16)
        out_part = contract_last(hidden, full_down)
        mlp_partial = out_part if mlp_partial is None else mlp_partial + out_part
        grad_hidden = jnp.dot(grad_y, full_down, preferred_element_type=f32)
        sigma = jax.nn.sigmoid(gate)
        grad_gate = (grad_hidden * up * sigma * (1.0 + gate * (1.0 - sigma))).astype(bf16)
        grad_up = (grad_hidden * active).astype(bf16)
        back_part = contract_last(grad_gate, full_gate) + contract_last(grad_up, full_up)
        pending = (
            contract_first(h2_part, grad_gate),
            contract_first(h2_part, grad_up),
            contract_first(grad_y, hidden),
        )
        h2_grad_partial = back_part if h2_grad_partial is None else h2_grad_partial + back_part
        staged.append(chip_total(jnp.concatenate(pending, axis=1)))
    grad_h2 = tensor_total(h2_grad_partial)
    grad_h2, staged[-1] = lax.optimization_barrier((grad_h2, staged[-1]))
    reduced = [line_total(chunk) for chunk in staged]
    result = (resid2 + tensor_total(mlp_partial)).astype(bf16)
    grad_gmlp = jnp.sum(grad_h2 * norm2, axis=0)
    grad_resid = grad_y.astype(f32) + norm_back(grad_h2, norm2, inv2, gain_mlp)
    grad_resid_part = grad_resid.astype(bf16)
    grad_heads = (
        jnp.dot(grad_resid_part, full_o, preferred_element_type=f32)
        .astype(bf16)
        .reshape(rows, heads, HD)
    )
    grad_heads, partial_o, result = lax.optimization_barrier(
        (grad_heads, contract_first(grad_resid_part, attended_flat), result)
    )
    early = (chip_total(partial_o), reduced[:-1])
    grad_qin, grad_kin, grad_vin, early = attention.backward(grad_heads, early)
    staged_o, reduced[:-1] = early
    reduced_o = line_total(staged_o)
    grad_qkv = jnp.concatenate(
        [grad_qin.reshape(rows, cols), grad_kin.reshape(rows, cols), grad_vin.reshape(rows, cols)],
        axis=1,
    )
    h1_grad_partial = contract_last(grad_qkv, full_qkv)
    first_tensor = (lax.axis_index("tensor") == 0).astype(f32)
    gain_parts = jnp.stack(
        [jnp.sum(h1_grad_partial * norm1, axis=0), grad_gmlp * first_tensor], axis=1
    )
    gain_slab = jnp.pad(tensor_exact_total(gain_parts), ((0, 0), (0, 126)))
    h1_grad_partial, staged_qkv = lax.optimization_barrier(
        (h1_grad_partial, chip_total(jnp.concatenate([contract_first(h1, grad_qkv), gain_slab], axis=1)))
    )
    grad_h1 = tensor_total(h1_grad_partial)
    grad_h1, reduced_o, reduced[-1] = lax.optimization_barrier((grad_h1, reduced_o, reduced[-1]))
    grad_x_part = (grad_resid + norm_back(grad_h1, norm1, inv1, gain_attn)).astype(bf16)
    reduced_qkv = line_total(staged_qkv)
    reduced_gains = reduced_qkv[:, 3 * cols :]
    reduced_gate, reduced_up, reduced_down = (
        jnp.concatenate([chunk[:, which * step : (which + 1) * step] for chunk in reduced], axis=1)
        for which in range(3)
    )
    return (
        result.reshape(1, rows, width),
        grad_x_part.reshape(1, rows, width),
        reduced_qkv[:, :cols],
        reduced_qkv[:, cols : 2 * cols],
        reduced_qkv[:, 2 * cols : 3 * cols],
        reduced_o,
        reduced_gate,
        reduced_up,
        reduced_down,
        reduced_gains[:, 0],
        reduced_gains[:, 1],
    )


def solution(mesh):
    placed = (
        P("shard", "context", None),
        P("shard", "context"),
        P("shard", "context"),
        P(ROWS, "tensor"),
        P(ROWS, "tensor"),
        P(ROWS, "tensor"),
        P(ROWS, "tensor"),
        P(ROWS, "tensor"),
        P(ROWS, "tensor"),
        P(ROWS, "tensor"),
        P(ROWS),
        P(ROWS),
        P("shard", "context", None),
    )
    return jax.shard_map(
        on_device,
        mesh=mesh,
        in_specs=placed,
        out_specs=(
            P("shard", "context", None),
            P("shard", "context", None),
            P(ROWS, "tensor"),
            P(ROWS, "tensor"),
            P(ROWS, "tensor"),
            P(ROWS, "tensor"),
            P(ROWS, "tensor"),
            P(ROWS, "tensor"),
            P(ROWS, "tensor"),
            P(ROWS),
            P(ROWS),
        ),
        check_vma=False,
    )
```

```python
import math

import jax
import jax.numpy as jnp
from jax import lax
from jax.sharding import PartitionSpec as P

HD = 64


EPS = 1e-05
THETA = 130000.0
NEG = -1e30
ROWS = ("shard", "context")


def passed_along(value, axis, steps):
    count = lax.axis_size(axis)
    pairs = [(source, (source + steps) % count) for source in range(count)]
    return lax.ppermute(value, axis, pairs)


def rope_tables(position):
    index = jnp.arange(HD // 2, dtype=jnp.float32)
    inverse = jnp.power(jnp.float32(THETA), -2.0 * index / HD)
    angle = position.astype(jnp.float32)[:, None] * inverse[None, :]
    return (jnp.cos(angle), jnp.sin(angle))


def rotate(tensor, cosine, sine):
    half = tensor.shape[-1] // 2
    first = tensor[..., :half]
    second = tensor[..., half:]
    cosine = cosine[:, None, :]
    sine = sine[:, None, :]
    return jnp.concatenate(
        [first * cosine - second * sine, second * cosine + first * sine], axis=-1
    )


def rotate_back(grad, cosine, sine):
    half = grad.shape[-1] // 2
    first = grad[..., :half]
    second = grad[..., half:]
    cosine = cosine[:, None, :]
    sine = sine[:, None, :]
    return jnp.concatenate(
        [first * cosine + second * sine, second * cosine - first * sine], axis=-1
    )


def normalize(value):
    inv_rms = lax.rsqrt(jnp.mean(value * value, axis=-1, keepdims=True) + EPS)
    return (value * inv_rms, inv_rms)


def norm_back(grad, normed, inv_rms, gain):
    scaled = grad * gain.astype(jnp.float32)
    return inv_rms * (scaled - normed * jnp.mean(scaled * normed, axis=-1, keepdims=True))


def contract_last(left, right):
    return lax.dot_general(
        left, right, (((1,), (1,)), ((), ())), preferred_element_type=jnp.float32
    )


def contract_first(left, right):
    return lax.dot_general(
        left, right, (((0,), (0,)), ((), ())), preferred_element_type=jnp.float32
    )


def half_of(value, bit):
    size = value.shape[0] // 2
    return lax.dynamic_slice_in_dim(value, bit * size, size, axis=0)


def joined(mine, other, bit):
    low = jnp.where(bit == 0, mine, other)
    high = jnp.where(bit == 0, other, mine)
    return jnp.concatenate([low, high], axis=0)


def tensor_total(partial_sum):
    count = lax.axis_size("tensor")
    rows = partial_sum.shape[0]
    if count != 4 or rows % 8:
        return lax.psum(partial_sum.astype(jnp.bfloat16), "tensor").astype(jnp.float32)
    f32 = jnp.float32
    bf16 = jnp.bfloat16
    index = lax.axis_index("tensor")
    x_bit = index % 2
    y_bit = index // 2
    x_pairs = [(i, i ^ 1) for i in range(4)]
    y_pairs = [(i, i ^ 2) for i in range(4)]

    def swap(value, pairs):
        return lax.ppermute(value.astype(bf16), "tensor", pairs).astype(f32)

    first = partial_sum[: rows // 2]
    second = partial_sum[rows // 2 :]
    first = half_of(first, x_bit) + swap(half_of(first, 1 - x_bit), x_pairs)
    second = half_of(second, y_bit) + swap(half_of(second, 1 - y_bit), y_pairs)
    first = half_of(first, y_bit) + swap(half_of(first, 1 - y_bit), y_pairs)
    second = half_of(second, x_bit) + swap(half_of(second, 1 - x_bit), x_pairs)
    first = first.astype(bf16)
    second = second.astype(bf16)
    first = joined(first, lax.ppermute(first, "tensor", y_pairs), y_bit)
    second = joined(second, lax.ppermute(second, "tensor", x_pairs), x_bit)
    first = joined(first, lax.ppermute(first, "tensor", x_pairs), x_bit)
    second = joined(second, lax.ppermute(second, "tensor", y_pairs), y_bit)
    return jnp.concatenate([first, second], axis=0).astype(f32)


def tensor_exact_total(value):
    if lax.axis_size("tensor") != 4:
        return lax.psum(value, "tensor")
    value = value + lax.ppermute(value, "tensor", [(i, i ^ 1) for i in range(4)])
    return value + lax.ppermute(value, "tensor", [(i, i ^ 2) for i in range(4)])


def chip_total(grad):
    f32 = jnp.float32
    shard = lax.axis_index("shard")
    mine = half_of(grad, shard)
    other = half_of(grad, 1 - shard)
    got = lax.ppermute(other.astype(jnp.bfloat16), "shard", [(0, 1), (1, 0)])
    return mine.astype(f32) + got.astype(f32)


def line_total(staged):
    return lax.psum_scatter(
        staged.astype(jnp.bfloat16), "context", scatter_dimension=0, tiled=True
    ).astype(jnp.float32)


def rows_total(grad):
    return line_total(chip_total(grad))


def pass_grads(grad_key, grad_value):
    return (
        passed_along(grad_key.astype(jnp.bfloat16), "context", 1).astype(grad_key.dtype),
        passed_along(grad_value.astype(jnp.bfloat16), "context", 1).astype(grad_value.dtype),
    )


def key_scores(query_heads, query_seg, query_pos, piece):
    key_flat, value_flat, key_seg, key_pos = piece
    heads = query_heads.shape[1]
    key_heads = key_flat.reshape(key_flat.shape[0], heads, HD)
    value_heads = value_flat.reshape(value_flat.shape[0], heads, HD)
    scores = jnp.einsum(
        "qhd,khd->hqk", query_heads, key_heads, preferred_element_type=jnp.float32
    ) * (1.0 / math.sqrt(HD))
    allowed = (query_seg[:, None] == key_seg[None, :]) & (key_pos[None, :] <= query_pos[:, None])
    return (jnp.where(allowed[None], scores, NEG), allowed, key_heads, value_heads)


def forward_fold(stats, piece, query_heads, query_seg, query_pos):
    peak, total, accum = stats
    scores, allowed, key_heads, value_heads = key_scores(query_heads, query_seg, query_pos, piece)
    new_peak = jnp.maximum(peak, jnp.max(scores, axis=-1))
    weights = jnp.where(allowed[None], jnp.exp(scores - new_peak[..., None]), 0.0)
    factor = jnp.exp(peak - new_peak)
    total = total * factor + jnp.sum(weights, axis=-1)
    accum = accum * factor[..., None] + jnp.einsum(
        "hqk,khd->hqd",
        weights.astype(jnp.bfloat16),
        value_heads,
        preferred_element_type=jnp.float32,
    )
    return (new_peak, total, accum)


def backward_piece(piece, query_heads, grad_heads, log_total, inner, query_seg, query_pos):
    scores, allowed, key_heads, value_heads = key_scores(query_heads, query_seg, query_pos, piece)
    probs = jnp.where(allowed[None], jnp.exp(scores - log_total[..., None]), 0.0)
    grad_value = jnp.einsum(
        "hqk,qhd->khd", probs.astype(jnp.bfloat16), grad_heads, preferred_element_type=jnp.float32
    )
    grad_probs = jnp.einsum(
        "qhd,khd->hqk", grad_heads, value_heads, preferred_element_type=jnp.float32
    )
    grad_scores = (probs * (grad_probs - inner[..., None]) * (1.0 / math.sqrt(HD))).astype(
        jnp.bfloat16
    )
    grad_query = jnp.einsum(
        "hqk,khd->qhd", grad_scores, key_heads, preferred_element_type=jnp.float32
    )
    grad_key = jnp.einsum(
        "hqk,qhd->khd", grad_scores, query_heads, preferred_element_type=jnp.float32
    )
    key_rows = grad_key.shape[0]
    return (grad_query, grad_key.reshape(key_rows, -1), grad_value.reshape(key_rows, -1))


class RingAttention:
    def __init__(self, query, key_flat, value_flat, segment, position, cosine, sine):
        self.query = query
        self.piece = (key_flat, value_flat, segment, position)
        self.segment = segment
        self.position = position
        self.cosine = cosine
        self.sine = sine

    def forward(self):
        f32 = jnp.float32
        query, segment, position = self.query, self.segment, self.position
        rows, heads = query.shape[0], query.shape[1]
        start_stats = (
            jnp.full((heads, rows), NEG, f32),
            jnp.zeros((heads, rows), f32),
            jnp.zeros((heads, rows, HD), f32),
        )
        stats = forward_fold(start_stats, self.piece, query, segment, position)

        def cycle_turn(index, carry):
            moving, current = carry
            moving = passed_along(moving, "context", 1)
            current = forward_fold(current, moving, query, segment, position)
            return (moving, current)

        peak, total, accum = lax.fori_loop(
            0, lax.axis_size("context") - 1, cycle_turn, (self.piece, stats)
        )[1]
        self.attended = jnp.transpose(accum / total[..., None], (1, 0, 2)).astype(jnp.bfloat16)
        self.log_total = peak + jnp.log(total)
        return self.attended

    def backward(self, grad_heads, early):
        bf16 = jnp.bfloat16
        query, segment, position = self.query, self.segment, self.position
        rows, heads = query.shape[0], query.shape[1]
        inner = jnp.sum(grad_heads.astype(jnp.float32) * self.attended.astype(jnp.float32), axis=-1).T

        def piece_grads(piece):
            return backward_piece(piece, query, grad_heads, self.log_total, inner, segment, position)

        grad_query, grad_key, grad_value = piece_grads(self.piece)

        def grad_turn(index, carry):
            moving, acc_query, acc_key, acc_value = carry
            moving = passed_along(moving, "context", 1)
            acc_key, acc_value = pass_grads(acc_key, acc_value)
            part_query, part_key, part_value = piece_grads(moving)
            return (moving, acc_query + part_query, acc_key + part_key, acc_value + part_value)

        carried = lax.fori_loop(
            0,
            lax.axis_size("context") - 1,
            grad_turn,
            (self.piece, grad_query, grad_key, grad_value),
        )
        grad_query = carried[1]
        grad_key, grad_value = pass_grads(carried[2], carried[3])
        grad_qin = rotate_back(grad_query, self.cosine, self.sine).astype(bf16)
        grad_kin = rotate_back(grad_key.reshape(rows, heads, HD), self.cosine, self.sine).astype(bf16)
        grad_vin = grad_value.astype(bf16).reshape(rows, heads, HD)
        return grad_qin, grad_kin, grad_vin, early


class HeadAttention:
    BLOCK = 512

    def __init__(self, query, key_heads, value_heads, segment, position, cosine, sine):
        ways = lax.axis_size("context")
        rows, heads = query.shape[0], query.shape[1]
        self.ways = ways
        self.rows = rows
        self.heads = heads
        self.group = heads // ways
        stacked = jnp.stack([query, key_heads, value_heads], axis=1)
        stacked = stacked.reshape(rows, 3, ways, self.group, HD)
        stacked = lax.all_to_all(stacked, "context", 2, 0, tiled=True)
        stacked = stacked.reshape(rows * ways, 3, self.group, HD)
        self.query = stacked[:, 0]
        self.keys = stacked[:, 1]
        self.values = stacked[:, 2]
        tags = jnp.stack([segment, position], axis=0)[None]
        tags = jnp.broadcast_to(tags, (ways, 2, rows))
        tags = lax.all_to_all(tags, "context", 0, 0, tiled=True)
        tags = jnp.transpose(tags, (1, 0, 2)).reshape(2, rows * ways)
        self.seg_all = tags[0]
        self.pos_all = tags[1]
        self.cos_all, self.sin_all = rope_tables(self.pos_all)

    def _blocks(self):
        total = self.rows * self.ways
        block = min(self.BLOCK, total)
        return [(start, block) for start in range(0, total, block)]

    def _scores(self, start, size):
        query = lax.dynamic_slice_in_dim(self.query, start, size, axis=0)
        seg_q = lax.dynamic_slice_in_dim(self.seg_all, start, size, axis=0)
        pos_q = lax.dynamic_slice_in_dim(self.pos_all, start, size, axis=0)
        scores = jnp.einsum(
            "qhd,khd->hqk", query, self.keys, preferred_element_type=jnp.float32
        ) * (1.0 / math.sqrt(HD))
        allowed = (seg_q[:, None] == self.seg_all[None, :]) & (
            self.pos_all[None, :] <= pos_q[:, None]
        )
        return query, jnp.where(allowed[None], scores, NEG), allowed

    def forward(self):
        outs = []
        logs = []
        for start, size in self._blocks():
            _, scores, allowed = self._scores(start, size)
            peak = jnp.max(scores, axis=-1)
            weights = jnp.where(allowed[None], jnp.exp(scores - peak[..., None]), 0.0)
            total = jnp.sum(weights, axis=-1)
            mixed = jnp.einsum(
                "hqk,khd->qhd",
                weights.astype(jnp.bfloat16),
                self.values,
                preferred_element_type=jnp.float32,
            )
            outs.append((mixed / total.T[:, :, None]).astype(jnp.bfloat16))
            logs.append(peak + jnp.log(total))
        self.attended = jnp.concatenate(outs, axis=0)
        self.log_total = jnp.concatenate(logs, axis=1)
        back = self.attended.reshape(self.rows * self.ways, 1, self.group, HD)
        back = lax.all_to_all(back, "context", 0, 1, tiled=True)
        return back.reshape(self.rows, self.heads, HD)

    def backward(self, grad_heads, early):
        f32 = jnp.float32
        bf16 = jnp.bfloat16
        scale = 1.0 / math.sqrt(HD)
        grad = grad_heads.reshape(self.rows, self.ways, self.group, HD)
        grad = lax.all_to_all(grad, "context", 1, 0, tiled=True)
        grad, early = lax.optimization_barrier((grad, early))
        grad = grad.reshape(self.rows * self.ways, self.group, HD)
        inner = jnp.sum(grad.astype(f32) * self.attended.astype(f32), axis=-1).T
        grad_key = jnp.zeros(self.keys.shape, f32)
        grad_value = jnp.zeros(self.values.shape, f32)
        grad_queries = []
        for start, size in self._blocks():
            query, scores, allowed = self._scores(start, size)
            log_block = lax.dynamic_slice_in_dim(self.log_total, start, size, axis=1)
            inner_block = lax.dynamic_slice_in_dim(inner, start, size, axis=1)
            grad_block = lax.dynamic_slice_in_dim(grad, start, size, axis=0)
            probs = jnp.where(allowed[None], jnp.exp(scores - log_block[..., None]), 0.0)
            grad_value = grad_value + jnp.einsum(
                "hqk,qhd->khd", probs.astype(bf16), grad_block, preferred_element_type=f32
            )
            grad_probs = jnp.einsum(
                "qhd,khd->hqk", grad_block, self.values, preferred_element_type=f32
            )
            grad_scores = (probs * (grad_probs - inner_block[..., None]) * scale).astype(bf16)
            grad_queries.append(
                jnp.einsum("hqk,khd->qhd", grad_scores, self.keys, preferred_element_type=f32)
            )
            grad_key = grad_key + jnp.einsum(
                "hqk,qhd->khd", grad_scores, query, preferred_element_type=f32
            )
        grad_query = jnp.concatenate(grad_queries, axis=0)
        grad_qin = rotate_back(grad_query, self.cos_all, self.sin_all).astype(bf16)
        grad_kin = rotate_back(grad_key, self.cos_all, self.sin_all).astype(bf16)
        grad_vin = grad_value.astype(bf16)
        returned = []
        for grad_in in (grad_qin, grad_kin, grad_vin):
            grad_in = grad_in.reshape(self.rows * self.ways, 1, self.group, HD)
            grad_in = lax.all_to_all(grad_in, "context", 0, 1, tiled=True)
            returned.append(grad_in.reshape(self.rows, self.heads, HD))
        return returned[0], returned[1], returned[2], early


def mlp_chunks(hidden_cols):
    if hidden_cols % 512 == 0:
        return [hidden_cols * 3 // 4, hidden_cols // 4]
    return [hidden_cols]


def on_device(
    inputs, segments, positions, w_q, w_k, w_v, w_o, w_gate, w_up, w_down, g_attn, g_mlp, d_out
):
    f32 = jnp.float32
    bf16 = jnp.bfloat16
    rows = inputs.shape[1]
    width = inputs.shape[2]
    cols = w_q.shape[1]
    hidden_cols = w_gate.shape[1]
    tokens = inputs.reshape(rows, width)
    segment = segments.reshape(rows)
    position = positions.reshape(rows)
    full_qkvo = lax.all_gather(
        jnp.concatenate([w_q, w_k, w_v, w_o], axis=1), ROWS, axis=0, tiled=True
    )
    full_qkv = full_qkvo[:, : 3 * cols]
    full_o = full_qkvo[:, 3 * cols :]
    gains = lax.all_gather(
        jnp.concatenate([g_attn, g_mlp])[None], ROWS, axis=0, tiled=True
    )
    gain_attn = gains[:, : g_attn.shape[0]].reshape(width)
    gain_mlp = gains[:, g_attn.shape[0] :].reshape(width)
    widths = mlp_chunks(hidden_cols)
    fetched = []
    for index, step in enumerate(widths):
        begin = sum(widths[:index])
        part = slice(begin, begin + step)
        pair = lax.all_gather(
            jnp.concatenate([w_gate[:, part], w_up[:, part]], axis=1), ROWS, axis=0, tiled=True
        )
        fetched.append(
            (pair[:, :step], pair[:, step:], lax.all_gather(w_down[:, part], ROWS, axis=0, tiled=True))
        )
    heads = cols // HD
    cosine, sine = rope_tables(position)
    resid1 = tokens.astype(f32)
    norm1, inv1 = normalize(resid1)
    h1 = (norm1 * gain_attn.astype(f32)).astype(bf16)
    projected = jnp.dot(h1, full_qkv, preferred_element_type=f32)
    query = rotate(projected[:, :cols].reshape(rows, heads, HD), cosine, sine).astype(bf16)
    key_heads = rotate(projected[:, cols : 2 * cols].reshape(rows, heads, HD), cosine, sine).astype(
        bf16
    )
    value_heads = projected[:, 2 * cols :].astype(bf16).reshape(rows, heads, HD)
    if heads % lax.axis_size("context") == 0:
        attention = HeadAttention(query, key_heads, value_heads, segment, position, cosine, sine)
    else:
        attention = RingAttention(
            query,
            key_heads.reshape(rows, cols),
            value_heads.reshape(rows, cols),
            segment,
            position,
            cosine,
            sine,
        )
    attended = attention.forward()
    attended_flat = attended.reshape(rows, cols)
    resid2 = resid1 + tensor_total(contract_last(attended_flat, full_o))
    norm2, inv2 = normalize(resid2)
    h2_part = (norm2 * gain_mlp.astype(f32)).astype(bf16)
    grad_y = d_out.reshape(rows, width)
    mlp_partial = None
    h2_grad_partial = None
    staged = []
    for full_gate, full_up, full_down in fetched:
        h2_chunk = h2_part
        if staged:
            h2_chunk, staged[-1] = lax.optimization_barrier((h2_part, staged[-1]))
        gate = jnp.dot(h2_chunk, full_gate, preferred_element_type=f32)
        up = jnp.dot(h2_chunk, full_up, preferred_element_type=f32)
        active = jax.nn.silu(gate)
        hidden = (active * up).astype(bf16)
        out_part = contract_last(hidden, full_down)
        mlp_partial = out_part if mlp_partial is None else mlp_partial + out_part
        grad_hidden = jnp.dot(grad_y, full_down, preferred_element_type=f32)
        sigma = jax.nn.sigmoid(gate)
        grad_gate = (grad_hidden * up * sigma * (1.0 + gate * (1.0 - sigma))).astype(bf16)
        grad_up = (grad_hidden * active).astype(bf16)
        back_part = contract_last(grad_gate, full_gate) + contract_last(grad_up, full_up)
        pending = (
            contract_first(h2_part, grad_gate),
            contract_first(h2_part, grad_up),
            contract_first(grad_y, hidden),
        )
        h2_grad_partial = back_part if h2_grad_partial is None else h2_grad_partial + back_part
        staged.append(chip_total(jnp.concatenate(pending, axis=1)))
    grad_h2 = tensor_total(h2_grad_partial)
    grad_h2, staged[-1] = lax.optimization_barrier((grad_h2, staged[-1]))
    reduced = [line_total(chunk) for chunk in staged]
    result = (resid2 + tensor_total(mlp_partial)).astype(bf16)
    grad_gmlp = jnp.sum(grad_h2 * norm2, axis=0)
    grad_resid = grad_y.astype(f32) + norm_back(grad_h2, norm2, inv2, gain_mlp)
    grad_resid_part = grad_resid.astype(bf16)
    grad_heads = (
        jnp.dot(grad_resid_part, full_o, preferred_element_type=f32)
        .astype(bf16)
        .reshape(rows, heads, HD)
    )
    grad_heads, partial_o = lax.optimization_barrier(
        (grad_heads, contract_first(grad_resid_part, attended_flat))
    )
    early = (chip_total(partial_o), reduced[:-1])
    grad_qin, grad_kin, grad_vin, early = attention.backward(grad_heads, early)
    staged_o, reduced[:-1] = early
    reduced_o = line_total(staged_o)
    grad_qkv = jnp.concatenate(
        [grad_qin.reshape(rows, cols), grad_kin.reshape(rows, cols), grad_vin.reshape(rows, cols)],
        axis=1,
    )
    h1_grad_partial = contract_last(grad_qkv, full_qkv)
    first_tensor = (lax.axis_index("tensor") == 0).astype(f32)
    gain_parts = jnp.stack(
        [jnp.sum(h1_grad_partial * norm1, axis=0), grad_gmlp * first_tensor], axis=1
    )
    gain_slab = jnp.pad(tensor_exact_total(gain_parts), ((0, 0), (0, 126)))
    h1_grad_partial, staged_qkv = lax.optimization_barrier(
        (h1_grad_partial, chip_total(jnp.concatenate([contract_first(h1, grad_qkv), gain_slab], axis=1)))
    )
    grad_h1 = tensor_total(h1_grad_partial)
    grad_h1, reduced_o, reduced[-1], result = lax.optimization_barrier(
        (grad_h1, reduced_o, reduced[-1], result)
    )
    grad_x_part = (grad_resid + norm_back(grad_h1, norm1, inv1, gain_attn)).astype(bf16)
    reduced_qkv = line_total(staged_qkv)
    reduced_gains = reduced_qkv[:, 3 * cols :]
    reduced_gate, reduced_up, reduced_down = (
        jnp.concatenate(
            [chunk[:, which * step : (which + 1) * step] for chunk, step in zip(reduced, widths)],
            axis=1,
        )
        for which in range(3)
    )
    return (
        result.reshape(1, rows, width),
        grad_x_part.reshape(1, rows, width),
        reduced_qkv[:, :cols],
        reduced_qkv[:, cols : 2 * cols],
        reduced_qkv[:, 2 * cols : 3 * cols],
        reduced_o,
        reduced_gate,
        reduced_up,
        reduced_down,
        reduced_gains[:, 0],
        reduced_gains[:, 1],
    )


def solution(mesh):
    placed = (
        P("shard", "context", None),
        P("shard", "context"),
        P("shard", "context"),
        P(ROWS, "tensor"),
        P(ROWS, "tensor"),
        P(ROWS, "tensor"),
        P(ROWS, "tensor"),
        P(ROWS, "tensor"),
        P(ROWS, "tensor"),
        P(ROWS, "tensor"),
        P(ROWS),
        P(ROWS),
        P("shard", "context", None),
    )
    return jax.shard_map(
        on_device,
        mesh=mesh,
        in_specs=placed,
        out_specs=(
            P("shard", "context", None),
            P("shard", "context", None),
            P(ROWS, "tensor"),
            P(ROWS, "tensor"),
            P(ROWS, "tensor"),
            P(ROWS, "tensor"),
            P(ROWS, "tensor"),
            P(ROWS, "tensor"),
            P(ROWS, "tensor"),
            P(ROWS),
            P(ROWS),
        ),
        check_vma=False,
    )
```

```python
import math

import jax
import jax.numpy as jnp
from jax import lax
from jax.sharding import PartitionSpec as P

HD = 64


EPS = 1e-05
THETA = 130000.0
NEG = -1e30
ROWS = ("shard", "context")


def passed_along(value, axis, steps):
    count = lax.axis_size(axis)
    pairs = [(source, (source + steps) % count) for source in range(count)]
    return lax.ppermute(value, axis, pairs)


def rope_tables(position):
    index = jnp.arange(HD // 2, dtype=jnp.float32)
    inverse = jnp.power(jnp.float32(THETA), -2.0 * index / HD)
    angle = position.astype(jnp.float32)[:, None] * inverse[None, :]
    return (jnp.cos(angle), jnp.sin(angle))


def rotate(tensor, cosine, sine):
    half = tensor.shape[-1] // 2
    first = tensor[..., :half]
    second = tensor[..., half:]
    cosine = cosine[:, None, :]
    sine = sine[:, None, :]
    return jnp.concatenate(
        [first * cosine - second * sine, second * cosine + first * sine], axis=-1
    )


def rotate_back(grad, cosine, sine):
    half = grad.shape[-1] // 2
    first = grad[..., :half]
    second = grad[..., half:]
    cosine = cosine[:, None, :]
    sine = sine[:, None, :]
    return jnp.concatenate(
        [first * cosine + second * sine, second * cosine - first * sine], axis=-1
    )


def normalize(value):
    inv_rms = lax.rsqrt(jnp.mean(value * value, axis=-1, keepdims=True) + EPS)
    return (value * inv_rms, inv_rms)


def norm_back(grad, normed, inv_rms, gain):
    scaled = grad * gain.astype(jnp.float32)
    return inv_rms * (scaled - normed * jnp.mean(scaled * normed, axis=-1, keepdims=True))


def contract_last(left, right):
    return lax.dot_general(
        left, right, (((1,), (1,)), ((), ())), preferred_element_type=jnp.float32
    )


def contract_first(left, right):
    return lax.dot_general(
        left, right, (((0,), (0,)), ((), ())), preferred_element_type=jnp.float32
    )


def half_of(value, bit):
    size = value.shape[0] // 2
    return lax.dynamic_slice_in_dim(value, bit * size, size, axis=0)


def joined(mine, other, bit):
    low = jnp.where(bit == 0, mine, other)
    high = jnp.where(bit == 0, other, mine)
    return jnp.concatenate([low, high], axis=0)


def tensor_total(partial_sum):
    count = lax.axis_size("tensor")
    rows = partial_sum.shape[0]
    if count != 4 or rows % 8:
        return lax.psum(partial_sum.astype(jnp.bfloat16), "tensor").astype(jnp.float32)
    f32 = jnp.float32
    bf16 = jnp.bfloat16
    index = lax.axis_index("tensor")
    x_bit = index % 2
    y_bit = index // 2
    x_pairs = [(i, i ^ 1) for i in range(4)]
    y_pairs = [(i, i ^ 2) for i in range(4)]

    def swap(value, pairs):
        return lax.ppermute(value.astype(bf16), "tensor", pairs).astype(f32)

    first = partial_sum[: rows // 2]
    second = partial_sum[rows // 2 :]
    first = half_of(first, x_bit) + swap(half_of(first, 1 - x_bit), x_pairs)
    second = half_of(second, y_bit) + swap(half_of(second, 1 - y_bit), y_pairs)
    first = half_of(first, y_bit) + swap(half_of(first, 1 - y_bit), y_pairs)
    second = half_of(second, x_bit) + swap(half_of(second, 1 - x_bit), x_pairs)
    first = first.astype(bf16)
    second = second.astype(bf16)
    first = joined(first, lax.ppermute(first, "tensor", y_pairs), y_bit)
    second = joined(second, lax.ppermute(second, "tensor", x_pairs), x_bit)
    first = joined(first, lax.ppermute(first, "tensor", x_pairs), x_bit)
    second = joined(second, lax.ppermute(second, "tensor", y_pairs), y_bit)
    return jnp.concatenate([first, second], axis=0).astype(f32)


def tensor_exact_total(value):
    if lax.axis_size("tensor") != 4:
        return lax.psum(value, "tensor")
    value = value + lax.ppermute(value, "tensor", [(i, i ^ 1) for i in range(4)])
    return value + lax.ppermute(value, "tensor", [(i, i ^ 2) for i in range(4)])


def exact_total(value):
    for axis in ("tensor", "shard", "context"):
        count = lax.axis_size(axis)
        if count & (count - 1):
            value = lax.psum(value, axis)
            continue
        span = 1
        while span < count:
            value = value + lax.ppermute(value, axis, [(i, i ^ span) for i in range(count)])
            span *= 2
    return value


def chip_total(grad):
    f32 = jnp.float32
    shard = lax.axis_index("shard")
    mine = half_of(grad, shard)
    other = half_of(grad, 1 - shard)
    got = lax.ppermute(other.astype(jnp.bfloat16), "shard", [(0, 1), (1, 0)])
    return mine.astype(f32) + got.astype(f32)


def line_total(staged):
    return lax.psum_scatter(
        staged.astype(jnp.bfloat16), "context", scatter_dimension=0, tiled=True
    ).astype(jnp.float32)


def rows_total(grad):
    return line_total(chip_total(grad))


def pass_grads(grad_key, grad_value):
    return (
        passed_along(grad_key.astype(jnp.bfloat16), "context", 1).astype(grad_key.dtype),
        passed_along(grad_value.astype(jnp.bfloat16), "context", 1).astype(grad_value.dtype),
    )


def key_scores(query_heads, query_seg, query_pos, piece):
    key_flat, value_flat, key_seg, key_pos = piece
    heads = query_heads.shape[1]
    key_heads = key_flat.reshape(key_flat.shape[0], heads, HD)
    value_heads = value_flat.reshape(value_flat.shape[0], heads, HD)
    scores = jnp.einsum(
        "qhd,khd->hqk", query_heads, key_heads, preferred_element_type=jnp.float32
    ) * (1.0 / math.sqrt(HD))
    allowed = (query_seg[:, None] == key_seg[None, :]) & (key_pos[None, :] <= query_pos[:, None])
    return (jnp.where(allowed[None], scores, NEG), allowed, key_heads, value_heads)


def forward_fold(stats, piece, query_heads, query_seg, query_pos):
    peak, total, accum = stats
    scores, allowed, key_heads, value_heads = key_scores(query_heads, query_seg, query_pos, piece)
    new_peak = jnp.maximum(peak, jnp.max(scores, axis=-1))
    weights = jnp.where(allowed[None], jnp.exp(scores - new_peak[..., None]), 0.0)
    factor = jnp.exp(peak - new_peak)
    total = total * factor + jnp.sum(weights, axis=-1)
    accum = accum * factor[..., None] + jnp.einsum(
        "hqk,khd->hqd",
        weights.astype(jnp.bfloat16),
        value_heads,
        preferred_element_type=jnp.float32,
    )
    return (new_peak, total, accum)


def backward_piece(piece, query_heads, grad_heads, log_total, inner, query_seg, query_pos):
    scores, allowed, key_heads, value_heads = key_scores(query_heads, query_seg, query_pos, piece)
    probs = jnp.where(allowed[None], jnp.exp(scores - log_total[..., None]), 0.0)
    grad_value = jnp.einsum(
        "hqk,qhd->khd", probs.astype(jnp.bfloat16), grad_heads, preferred_element_type=jnp.float32
    )
    grad_probs = jnp.einsum(
        "qhd,khd->hqk", grad_heads, value_heads, preferred_element_type=jnp.float32
    )
    grad_scores = (probs * (grad_probs - inner[..., None]) * (1.0 / math.sqrt(HD))).astype(
        jnp.bfloat16
    )
    grad_query = jnp.einsum(
        "hqk,khd->qhd", grad_scores, key_heads, preferred_element_type=jnp.float32
    )
    grad_key = jnp.einsum(
        "hqk,qhd->khd", grad_scores, query_heads, preferred_element_type=jnp.float32
    )
    key_rows = grad_key.shape[0]
    return (grad_query, grad_key.reshape(key_rows, -1), grad_value.reshape(key_rows, -1))


class RingAttention:
    def __init__(self, query, key_flat, value_flat, segment, position, cosine, sine):
        self.query = query
        self.piece = (key_flat, value_flat, segment, position)
        self.segment = segment
        self.position = position
        self.cosine = cosine
        self.sine = sine

    def forward(self):
        f32 = jnp.float32
        query, segment, position = self.query, self.segment, self.position
        rows, heads = query.shape[0], query.shape[1]
        start_stats = (
            jnp.full((heads, rows), NEG, f32),
            jnp.zeros((heads, rows), f32),
            jnp.zeros((heads, rows, HD), f32),
        )
        stats = forward_fold(start_stats, self.piece, query, segment, position)

        def cycle_turn(index, carry):
            moving, current = carry
            moving = passed_along(moving, "context", 1)
            current = forward_fold(current, moving, query, segment, position)
            return (moving, current)

        peak, total, accum = lax.fori_loop(
            0, lax.axis_size("context") - 1, cycle_turn, (self.piece, stats)
        )[1]
        self.attended = jnp.transpose(accum / total[..., None], (1, 0, 2)).astype(jnp.bfloat16)
        self.log_total = peak + jnp.log(total)
        return self.attended

    def backward(self, grad_heads, early):
        bf16 = jnp.bfloat16
        query, segment, position = self.query, self.segment, self.position
        rows, heads = query.shape[0], query.shape[1]
        inner = jnp.sum(grad_heads.astype(jnp.float32) * self.attended.astype(jnp.float32), axis=-1).T

        def piece_grads(piece):
            return backward_piece(piece, query, grad_heads, self.log_total, inner, segment, position)

        grad_query, grad_key, grad_value = piece_grads(self.piece)

        def grad_turn(index, carry):
            moving, acc_query, acc_key, acc_value = carry
            moving = passed_along(moving, "context", 1)
            acc_key, acc_value = pass_grads(acc_key, acc_value)
            part_query, part_key, part_value = piece_grads(moving)
            return (moving, acc_query + part_query, acc_key + part_key, acc_value + part_value)

        carried = lax.fori_loop(
            0,
            lax.axis_size("context") - 1,
            grad_turn,
            (self.piece, grad_query, grad_key, grad_value),
        )
        grad_query = carried[1]
        grad_key, grad_value = pass_grads(carried[2], carried[3])
        grad_qin = rotate_back(grad_query, self.cosine, self.sine).astype(bf16)
        grad_kin = rotate_back(grad_key.reshape(rows, heads, HD), self.cosine, self.sine).astype(bf16)
        grad_vin = grad_value.astype(bf16).reshape(rows, heads, HD)
        return grad_qin, grad_kin, grad_vin, early


class HeadAttention:
    BLOCK = 512

    def __init__(self, query, key_heads, value_heads, segment, position, cosine, sine):
        ways = lax.axis_size("context")
        rows, heads = query.shape[0], query.shape[1]
        self.ways = ways
        self.rows = rows
        self.heads = heads
        self.group = heads // ways
        stacked = jnp.stack([query, key_heads, value_heads], axis=1)
        stacked = stacked.reshape(rows, 3, ways, self.group, HD)
        stacked = lax.all_to_all(stacked, "context", 2, 0, tiled=True)
        stacked = stacked.reshape(rows * ways, 3, self.group, HD)
        self.query = stacked[:, 0]
        self.keys = stacked[:, 1]
        self.values = stacked[:, 2]
        tags = jnp.stack([segment, position], axis=0)[None]
        tags = jnp.broadcast_to(tags, (ways, 2, rows))
        tags = lax.all_to_all(tags, "context", 0, 0, tiled=True)
        tags = jnp.transpose(tags, (1, 0, 2)).reshape(2, rows * ways)
        self.seg_all = tags[0]
        self.pos_all = tags[1]
        self.cos_all, self.sin_all = rope_tables(self.pos_all)

    def _blocks(self):
        total = self.rows * self.ways
        block = min(self.BLOCK, total)
        return [(start, block) for start in range(0, total, block)]

    def _scores(self, start, size):
        query = lax.dynamic_slice_in_dim(self.query, start, size, axis=0)
        seg_q = lax.dynamic_slice_in_dim(self.seg_all, start, size, axis=0)
        pos_q = lax.dynamic_slice_in_dim(self.pos_all, start, size, axis=0)
        scores = jnp.einsum(
            "qhd,khd->hqk", query, self.keys, preferred_element_type=jnp.float32
        ) * (1.0 / math.sqrt(HD))
        allowed = (seg_q[:, None] == self.seg_all[None, :]) & (
            self.pos_all[None, :] <= pos_q[:, None]
        )
        return query, jnp.where(allowed[None], scores, NEG), allowed

    def forward(self):
        outs = []
        logs = []
        for start, size in self._blocks():
            _, scores, allowed = self._scores(start, size)
            peak = jnp.max(scores, axis=-1)
            weights = jnp.where(allowed[None], jnp.exp(scores - peak[..., None]), 0.0)
            total = jnp.sum(weights, axis=-1)
            mixed = jnp.einsum(
                "hqk,khd->qhd",
                weights.astype(jnp.bfloat16),
                self.values,
                preferred_element_type=jnp.float32,
            )
            outs.append((mixed / total.T[:, :, None]).astype(jnp.bfloat16))
            logs.append(peak + jnp.log(total))
        self.attended = jnp.concatenate(outs, axis=0)
        self.log_total = jnp.concatenate(logs, axis=1)
        back = self.attended.reshape(self.rows * self.ways, 1, self.group, HD)
        back = lax.all_to_all(back, "context", 0, 1, tiled=True)
        return back.reshape(self.rows, self.heads, HD)

    def backward(self, grad_heads, early):
        f32 = jnp.float32
        bf16 = jnp.bfloat16
        scale = 1.0 / math.sqrt(HD)
        grad = grad_heads.reshape(self.rows, self.ways, self.group, HD)
        grad = lax.all_to_all(grad, "context", 1, 0, tiled=True)
        grad, early = lax.optimization_barrier((grad, early))
        grad = grad.reshape(self.rows * self.ways, self.group, HD)
        inner = jnp.sum(grad.astype(f32) * self.attended.astype(f32), axis=-1).T
        grad_key = jnp.zeros(self.keys.shape, f32)
        grad_value = jnp.zeros(self.values.shape, f32)
        grad_queries = []
        for start, size in self._blocks():
            query, scores, allowed = self._scores(start, size)
            log_block = lax.dynamic_slice_in_dim(self.log_total, start, size, axis=1)
            inner_block = lax.dynamic_slice_in_dim(inner, start, size, axis=1)
            grad_block = lax.dynamic_slice_in_dim(grad, start, size, axis=0)
            probs = jnp.where(allowed[None], jnp.exp(scores - log_block[..., None]), 0.0)
            grad_value = grad_value + jnp.einsum(
                "hqk,qhd->khd", probs.astype(bf16), grad_block, preferred_element_type=f32
            )
            grad_probs = jnp.einsum(
                "qhd,khd->hqk", grad_block, self.values, preferred_element_type=f32
            )
            grad_scores = (probs * (grad_probs - inner_block[..., None]) * scale).astype(bf16)
            grad_queries.append(
                jnp.einsum("hqk,khd->qhd", grad_scores, self.keys, preferred_element_type=f32)
            )
            grad_key = grad_key + jnp.einsum(
                "hqk,qhd->khd", grad_scores, query, preferred_element_type=f32
            )
        grad_query = jnp.concatenate(grad_queries, axis=0)
        grad_qin = rotate_back(grad_query, self.cos_all, self.sin_all).astype(bf16)
        grad_kin = rotate_back(grad_key, self.cos_all, self.sin_all).astype(bf16)
        grad_vin = grad_value.astype(bf16)
        returned = []
        for grad_in in (grad_qin, grad_kin, grad_vin):
            grad_in = grad_in.reshape(self.rows * self.ways, 1, self.group, HD)
            grad_in = lax.all_to_all(grad_in, "context", 0, 1, tiled=True)
            returned.append(grad_in.reshape(self.rows, self.heads, HD))
        return returned[0], returned[1], returned[2], early


def mlp_chunks(hidden_cols):
    for count in (2, 1):
        if hidden_cols % (count * 128) == 0:
            return count
    return 1


def on_device(
    inputs, segments, positions, w_q, w_k, w_v, w_o, w_gate, w_up, w_down, g_attn, g_mlp, d_out
):
    f32 = jnp.float32
    bf16 = jnp.bfloat16
    rows = inputs.shape[1]
    width = inputs.shape[2]
    cols = w_q.shape[1]
    hidden_cols = w_gate.shape[1]
    tokens = inputs.reshape(rows, width)
    segment = segments.reshape(rows)
    position = positions.reshape(rows)
    full_qkvo = lax.all_gather(
        jnp.concatenate([w_q, w_k, w_v, w_o], axis=1), ROWS, axis=0, tiled=True
    )
    full_qkv = full_qkvo[:, : 3 * cols]
    full_o = full_qkvo[:, 3 * cols :]
    gains = lax.all_gather(
        jnp.concatenate([g_attn, g_mlp])[None], ROWS, axis=0, tiled=True
    )
    gain_attn = gains[:, : g_attn.shape[0]].reshape(width)
    gain_mlp = gains[:, g_attn.shape[0] :].reshape(width)
    count = mlp_chunks(hidden_cols)
    step = hidden_cols // count
    fetched = []
    for index in range(count):
        part = slice(index * step, (index + 1) * step)
        pair = lax.all_gather(
            jnp.concatenate([w_gate[:, part], w_up[:, part]], axis=1), ROWS, axis=0, tiled=True
        )
        fetched.append(
            (pair[:, :step], pair[:, step:], lax.all_gather(w_down[:, part], ROWS, axis=0, tiled=True))
        )
    heads = cols // HD
    cosine, sine = rope_tables(position)
    resid1 = tokens.astype(f32)
    norm1, inv1 = normalize(resid1)
    h1 = (norm1 * gain_attn.astype(f32)).astype(bf16)
    projected = jnp.dot(h1, full_qkv, preferred_element_type=f32)
    query = rotate(projected[:, :cols].reshape(rows, heads, HD), cosine, sine).astype(bf16)
    key_heads = rotate(projected[:, cols : 2 * cols].reshape(rows, heads, HD), cosine, sine).astype(
        bf16
    )
    value_heads = projected[:, 2 * cols :].astype(bf16).reshape(rows, heads, HD)
    if heads % lax.axis_size("context") == 0:
        attention = HeadAttention(query, key_heads, value_heads, segment, position, cosine, sine)
    else:
        attention = RingAttention(
            query,
            key_heads.reshape(rows, cols),
            value_heads.reshape(rows, cols),
            segment,
            position,
            cosine,
            sine,
        )
    attended = attention.forward()
    attended_flat = attended.reshape(rows, cols)
    resid2 = resid1 + tensor_total(contract_last(attended_flat, full_o))
    norm2, inv2 = normalize(resid2)
    h2_part = (norm2 * gain_mlp.astype(f32)).astype(bf16)
    grad_y = d_out.reshape(rows, width)
    mlp_partial = None
    h2_grad_partial = None
    staged = []
    for full_gate, full_up, full_down in fetched:
        if staged:
            full_gate, staged[-1] = lax.optimization_barrier((full_gate, staged[-1]))
        gate = jnp.dot(h2_part, full_gate, preferred_element_type=f32)
        up = jnp.dot(h2_part, full_up, preferred_element_type=f32)
        active = jax.nn.silu(gate)
        hidden = (active * up).astype(bf16)
        out_part = contract_last(hidden, full_down)
        mlp_partial = out_part if mlp_partial is None else mlp_partial + out_part
        grad_hidden = jnp.dot(grad_y, full_down, preferred_element_type=f32)
        sigma = jax.nn.sigmoid(gate)
        grad_gate = (grad_hidden * up * sigma * (1.0 + gate * (1.0 - sigma))).astype(bf16)
        grad_up = (grad_hidden * active).astype(bf16)
        back_part = contract_last(grad_gate, full_gate) + contract_last(grad_up, full_up)
        pending = (
            contract_first(h2_part, grad_gate),
            contract_first(h2_part, grad_up),
            contract_first(grad_y, hidden),
        )
        h2_grad_partial = back_part if h2_grad_partial is None else h2_grad_partial + back_part
        staged.append(chip_total(jnp.concatenate(pending, axis=1)))
    grad_h2 = tensor_total(h2_grad_partial)
    grad_h2, staged[-1] = lax.optimization_barrier((grad_h2, staged[-1]))
    reduced = [line_total(chunk) for chunk in staged]
    result = (resid2 + tensor_total(mlp_partial)).astype(bf16)
    grad_gmlp = jnp.sum(grad_h2 * norm2, axis=0)
    grad_resid = grad_y.astype(f32) + norm_back(grad_h2, norm2, inv2, gain_mlp)
    grad_resid_part = grad_resid.astype(bf16)
    grad_heads = (
        jnp.dot(grad_resid_part, full_o, preferred_element_type=f32)
        .astype(bf16)
        .reshape(rows, heads, HD)
    )
    grad_heads, partial_o = lax.optimization_barrier(
        (grad_heads, contract_first(grad_resid_part, attended_flat))
    )
    early = (chip_total(partial_o), reduced[:-1])
    grad_qin, grad_kin, grad_vin, early = attention.backward(grad_heads, early)
    staged_o, reduced[:-1] = early
    reduced_o = line_total(staged_o)
    grad_qkv = jnp.concatenate(
        [grad_qin.reshape(rows, cols), grad_kin.reshape(rows, cols), grad_vin.reshape(rows, cols)],
        axis=1,
    )
    h1_grad_partial = contract_last(grad_qkv, full_qkv)
    first_tensor = (lax.axis_index("tensor") == 0).astype(f32)
    gain_parts = jnp.stack(
        [jnp.sum(h1_grad_partial * norm1, axis=0), grad_gmlp * first_tensor], axis=1
    )
    gains_total = exact_total(gain_parts)
    h1_grad_partial, staged_qkv = lax.optimization_barrier(
        (h1_grad_partial, chip_total(contract_first(h1, grad_qkv)))
    )
    grad_h1 = tensor_total(h1_grad_partial)
    grad_h1, reduced_o, reduced[-1], result = lax.optimization_barrier(
        (grad_h1, reduced_o, reduced[-1], result)
    )
    grad_x_part = (grad_resid + norm_back(grad_h1, norm1, inv1, gain_attn)).astype(bf16)
    reduced_qkv = line_total(staged_qkv)
    blocks = lax.axis_size("shard") * lax.axis_size("context")
    block = lax.axis_index("shard") * lax.axis_size("context") + lax.axis_index("context")
    piece = width // blocks
    reduced_gains = lax.dynamic_slice_in_dim(gains_total, block * piece, piece, axis=0)
    reduced_gate, reduced_up, reduced_down = (
        jnp.concatenate([chunk[:, which * step : (which + 1) * step] for chunk in reduced], axis=1)
        for which in range(3)
    )
    return (
        result.reshape(1, rows, width),
        grad_x_part.reshape(1, rows, width),
        reduced_qkv[:, :cols],
        reduced_qkv[:, cols : 2 * cols],
        reduced_qkv[:, 2 * cols :],
        reduced_o,
        reduced_gate,
        reduced_up,
        reduced_down,
        reduced_gains[:, 0],
        reduced_gains[:, 1],
    )


def solution(mesh):
    placed = (
        P("shard", "context", None),
        P("shard", "context"),
        P("shard", "context"),
        P(ROWS, "tensor"),
        P(ROWS, "tensor"),
        P(ROWS, "tensor"),
        P(ROWS, "tensor"),
        P(ROWS, "tensor"),
        P(ROWS, "tensor"),
        P(ROWS, "tensor"),
        P(ROWS),
        P(ROWS),
        P("shard", "context", None),
    )
    return jax.shard_map(
        on_device,
        mesh=mesh,
        in_specs=placed,
        out_specs=(
            P("shard", "context", None),
            P("shard", "context", None),
            P(ROWS, "tensor"),
            P(ROWS, "tensor"),
            P(ROWS, "tensor"),
            P(ROWS, "tensor"),
            P(ROWS, "tensor"),
            P(ROWS, "tensor"),
            P(ROWS, "tensor"),
            P(ROWS),
            P(ROWS),
        ),
        check_vma=False,
    )
```

```python
import math

import jax
import jax.numpy as jnp
from jax import lax
from jax.sharding import PartitionSpec as P

HD = 64


EPS = 1e-05
THETA = 130000.0
NEG = -1e30
ROWS = ("shard", "context")


def passed_along(value, axis, steps):
    count = lax.axis_size(axis)
    pairs = [(source, (source + steps) % count) for source in range(count)]
    return lax.ppermute(value, axis, pairs)


def rope_tables(position):
    index = jnp.arange(HD // 2, dtype=jnp.float32)
    inverse = jnp.power(jnp.float32(THETA), -2.0 * index / HD)
    angle = position.astype(jnp.float32)[:, None] * inverse[None, :]
    return (jnp.cos(angle), jnp.sin(angle))


def rotate(tensor, cosine, sine):
    half = tensor.shape[-1] // 2
    first = tensor[..., :half]
    second = tensor[..., half:]
    cosine = cosine[:, None, :]
    sine = sine[:, None, :]
    return jnp.concatenate(
        [first * cosine - second * sine, second * cosine + first * sine], axis=-1
    )


def rotate_back(grad, cosine, sine):
    half = grad.shape[-1] // 2
    first = grad[..., :half]
    second = grad[..., half:]
    cosine = cosine[:, None, :]
    sine = sine[:, None, :]
    return jnp.concatenate(
        [first * cosine + second * sine, second * cosine - first * sine], axis=-1
    )


def normalize(value):
    inv_rms = lax.rsqrt(jnp.mean(value * value, axis=-1, keepdims=True) + EPS)
    return (value * inv_rms, inv_rms)


def norm_back(grad, normed, inv_rms, gain):
    scaled = grad * gain.astype(jnp.float32)
    return inv_rms * (scaled - normed * jnp.mean(scaled * normed, axis=-1, keepdims=True))


def contract_last(left, right):
    return lax.dot_general(
        left, right, (((1,), (1,)), ((), ())), preferred_element_type=jnp.float32
    )


def contract_first(left, right):
    return lax.dot_general(
        left, right, (((0,), (0,)), ((), ())), preferred_element_type=jnp.float32
    )


def half_of(value, bit):
    size = value.shape[0] // 2
    return lax.dynamic_slice_in_dim(value, bit * size, size, axis=0)


def joined(mine, other, bit):
    low = jnp.where(bit == 0, mine, other)
    high = jnp.where(bit == 0, other, mine)
    return jnp.concatenate([low, high], axis=0)


def tensor_total(partial_sum):
    count = lax.axis_size("tensor")
    rows = partial_sum.shape[0]
    if count != 4 or rows % 8:
        return lax.psum(partial_sum.astype(jnp.bfloat16), "tensor").astype(jnp.float32)
    f32 = jnp.float32
    bf16 = jnp.bfloat16
    index = lax.axis_index("tensor")
    x_bit = index % 2
    y_bit = index // 2
    x_pairs = [(i, i ^ 1) for i in range(4)]
    y_pairs = [(i, i ^ 2) for i in range(4)]

    def swap(value, pairs):
        return lax.ppermute(value.astype(bf16), "tensor", pairs).astype(f32)

    first = partial_sum[: rows // 2]
    second = partial_sum[rows // 2 :]
    first = half_of(first, x_bit) + swap(half_of(first, 1 - x_bit), x_pairs)
    second = half_of(second, y_bit) + swap(half_of(second, 1 - y_bit), y_pairs)
    first = half_of(first, y_bit) + swap(half_of(first, 1 - y_bit), y_pairs)
    second = half_of(second, x_bit) + swap(half_of(second, 1 - x_bit), x_pairs)
    first = first.astype(bf16)
    second = second.astype(bf16)
    first = joined(first, lax.ppermute(first, "tensor", y_pairs), y_bit)
    second = joined(second, lax.ppermute(second, "tensor", x_pairs), x_bit)
    first = joined(first, lax.ppermute(first, "tensor", x_pairs), x_bit)
    second = joined(second, lax.ppermute(second, "tensor", y_pairs), y_bit)
    return jnp.concatenate([first, second], axis=0).astype(f32)


def tensor_exact_total(value):
    if lax.axis_size("tensor") != 4:
        return lax.psum(value, "tensor")
    value = value + lax.ppermute(value, "tensor", [(i, i ^ 1) for i in range(4)])
    return value + lax.ppermute(value, "tensor", [(i, i ^ 2) for i in range(4)])


def exact_total(value):
    for axis in ("tensor", "shard", "context"):
        count = lax.axis_size(axis)
        if count & (count - 1):
            value = lax.psum(value, axis)
            continue
        span = 1
        while span < count:
            value = value + lax.ppermute(value, axis, [(i, i ^ span) for i in range(count)])
            span *= 2
    return value


def chip_total(grad):
    f32 = jnp.float32
    shard = lax.axis_index("shard")
    mine = half_of(grad, shard)
    other = half_of(grad, 1 - shard)
    got = lax.ppermute(other.astype(jnp.bfloat16), "shard", [(0, 1), (1, 0)])
    return mine.astype(f32) + got.astype(f32)


def line_total(staged):
    return lax.psum_scatter(
        staged.astype(jnp.bfloat16), "context", scatter_dimension=0, tiled=True
    ).astype(jnp.float32)


def rows_total(grad):
    return line_total(chip_total(grad))


def pass_grads(grad_key, grad_value):
    return (
        passed_along(grad_key.astype(jnp.bfloat16), "context", 1).astype(grad_key.dtype),
        passed_along(grad_value.astype(jnp.bfloat16), "context", 1).astype(grad_value.dtype),
    )


def key_scores(query_heads, query_seg, query_pos, piece):
    key_flat, value_flat, key_seg, key_pos = piece
    heads = query_heads.shape[1]
    key_heads = key_flat.reshape(key_flat.shape[0], heads, HD)
    value_heads = value_flat.reshape(value_flat.shape[0], heads, HD)
    scores = jnp.einsum(
        "qhd,khd->hqk", query_heads, key_heads, preferred_element_type=jnp.float32
    ) * (1.0 / math.sqrt(HD))
    allowed = (query_seg[:, None] == key_seg[None, :]) & (key_pos[None, :] <= query_pos[:, None])
    return (jnp.where(allowed[None], scores, NEG), allowed, key_heads, value_heads)


def forward_fold(stats, piece, query_heads, query_seg, query_pos):
    peak, total, accum = stats
    scores, allowed, key_heads, value_heads = key_scores(query_heads, query_seg, query_pos, piece)
    new_peak = jnp.maximum(peak, jnp.max(scores, axis=-1))
    weights = jnp.where(allowed[None], jnp.exp(scores - new_peak[..., None]), 0.0)
    factor = jnp.exp(peak - new_peak)
    total = total * factor + jnp.sum(weights, axis=-1)
    accum = accum * factor[..., None] + jnp.einsum(
        "hqk,khd->hqd",
        weights.astype(jnp.bfloat16),
        value_heads,
        preferred_element_type=jnp.float32,
    )
    return (new_peak, total, accum)


def backward_piece(piece, query_heads, grad_heads, log_total, inner, query_seg, query_pos):
    scores, allowed, key_heads, value_heads = key_scores(query_heads, query_seg, query_pos, piece)
    probs = jnp.where(allowed[None], jnp.exp(scores - log_total[..., None]), 0.0)
    grad_value = jnp.einsum(
        "hqk,qhd->khd", probs.astype(jnp.bfloat16), grad_heads, preferred_element_type=jnp.float32
    )
    grad_probs = jnp.einsum(
        "qhd,khd->hqk", grad_heads, value_heads, preferred_element_type=jnp.float32
    )
    grad_scores = (probs * (grad_probs - inner[..., None]) * (1.0 / math.sqrt(HD))).astype(
        jnp.bfloat16
    )
    grad_query = jnp.einsum(
        "hqk,khd->qhd", grad_scores, key_heads, preferred_element_type=jnp.float32
    )
    grad_key = jnp.einsum(
        "hqk,qhd->khd", grad_scores, query_heads, preferred_element_type=jnp.float32
    )
    key_rows = grad_key.shape[0]
    return (grad_query, grad_key.reshape(key_rows, -1), grad_value.reshape(key_rows, -1))


class RingAttention:
    def __init__(self, query, key_flat, value_flat, segment, position, cosine, sine):
        self.query = query
        self.piece = (key_flat, value_flat, segment, position)
        self.segment = segment
        self.position = position
        self.cosine = cosine
        self.sine = sine

    def forward(self):
        f32 = jnp.float32
        query, segment, position = self.query, self.segment, self.position
        rows, heads = query.shape[0], query.shape[1]
        start_stats = (
            jnp.full((heads, rows), NEG, f32),
            jnp.zeros((heads, rows), f32),
            jnp.zeros((heads, rows, HD), f32),
        )
        stats = forward_fold(start_stats, self.piece, query, segment, position)

        def cycle_turn(index, carry):
            moving, current = carry
            moving = passed_along(moving, "context", 1)
            current = forward_fold(current, moving, query, segment, position)
            return (moving, current)

        peak, total, accum = lax.fori_loop(
            0, lax.axis_size("context") - 1, cycle_turn, (self.piece, stats)
        )[1]
        self.attended = jnp.transpose(accum / total[..., None], (1, 0, 2)).astype(jnp.bfloat16)
        self.log_total = peak + jnp.log(total)
        return self.attended

    def backward(self, grad_heads, early):
        bf16 = jnp.bfloat16
        query, segment, position = self.query, self.segment, self.position
        rows, heads = query.shape[0], query.shape[1]
        inner = jnp.sum(grad_heads.astype(jnp.float32) * self.attended.astype(jnp.float32), axis=-1).T

        def piece_grads(piece):
            return backward_piece(piece, query, grad_heads, self.log_total, inner, segment, position)

        grad_query, grad_key, grad_value = piece_grads(self.piece)

        def grad_turn(index, carry):
            moving, acc_query, acc_key, acc_value = carry
            moving = passed_along(moving, "context", 1)
            acc_key, acc_value = pass_grads(acc_key, acc_value)
            part_query, part_key, part_value = piece_grads(moving)
            return (moving, acc_query + part_query, acc_key + part_key, acc_value + part_value)

        carried = lax.fori_loop(
            0,
            lax.axis_size("context") - 1,
            grad_turn,
            (self.piece, grad_query, grad_key, grad_value),
        )
        grad_query = carried[1]
        grad_key, grad_value = pass_grads(carried[2], carried[3])
        grad_qin = rotate_back(grad_query, self.cosine, self.sine).astype(bf16)
        grad_kin = rotate_back(grad_key.reshape(rows, heads, HD), self.cosine, self.sine).astype(bf16)
        grad_vin = grad_value.astype(bf16).reshape(rows, heads, HD)
        return grad_qin, grad_kin, grad_vin, early


class HeadAttention:
    BLOCK = 512

    def __init__(self, query, key_heads, value_heads, segment, position, cosine, sine):
        ways = lax.axis_size("context")
        rows, heads = query.shape[0], query.shape[1]
        self.ways = ways
        self.rows = rows
        self.heads = heads
        self.group = heads // ways
        stacked = jnp.stack([query, key_heads, value_heads], axis=1)
        stacked = stacked.reshape(rows, 3, ways, self.group, HD)
        stacked = lax.all_to_all(stacked, "context", 2, 0, tiled=True)
        stacked = stacked.reshape(rows * ways, 3, self.group, HD)
        self.query = stacked[:, 0]
        self.keys = stacked[:, 1]
        self.values = stacked[:, 2]
        tags = jnp.stack([segment, position], axis=0)[None]
        tags = jnp.broadcast_to(tags, (ways, 2, rows))
        tags = lax.all_to_all(tags, "context", 0, 0, tiled=True)
        tags = jnp.transpose(tags, (1, 0, 2)).reshape(2, rows * ways)
        self.seg_all = tags[0]
        self.pos_all = tags[1]
        self.cos_all, self.sin_all = rope_tables(self.pos_all)

    def _blocks(self):
        total = self.rows * self.ways
        block = min(self.BLOCK, total)
        return [(start, block) for start in range(0, total, block)]

    def _scores(self, start, size):
        query = lax.dynamic_slice_in_dim(self.query, start, size, axis=0)
        seg_q = lax.dynamic_slice_in_dim(self.seg_all, start, size, axis=0)
        pos_q = lax.dynamic_slice_in_dim(self.pos_all, start, size, axis=0)
        scores = jnp.einsum(
            "qhd,khd->hqk", query, self.keys, preferred_element_type=jnp.float32
        ) * (1.0 / math.sqrt(HD))
        allowed = (seg_q[:, None] == self.seg_all[None, :]) & (
            self.pos_all[None, :] <= pos_q[:, None]
        )
        return query, jnp.where(allowed[None], scores, NEG), allowed

    def forward(self):
        outs = []
        logs = []
        for start, size in self._blocks():
            _, scores, allowed = self._scores(start, size)
            peak = jnp.max(scores, axis=-1)
            weights = jnp.where(allowed[None], jnp.exp(scores - peak[..., None]), 0.0)
            total = jnp.sum(weights, axis=-1)
            mixed = jnp.einsum(
                "hqk,khd->qhd",
                weights.astype(jnp.bfloat16),
                self.values,
                preferred_element_type=jnp.float32,
            )
            outs.append((mixed / total.T[:, :, None]).astype(jnp.bfloat16))
            logs.append(peak + jnp.log(total))
        self.attended = jnp.concatenate(outs, axis=0)
        self.log_total = jnp.concatenate(logs, axis=1)
        back = self.attended.reshape(self.rows * self.ways, 1, self.group, HD)
        back = lax.all_to_all(back, "context", 0, 1, tiled=True)
        return back.reshape(self.rows, self.heads, HD)

    def backward(self, grad_heads, early):
        f32 = jnp.float32
        bf16 = jnp.bfloat16
        scale = 1.0 / math.sqrt(HD)
        grad = grad_heads.reshape(self.rows, self.ways, self.group, HD)
        grad = lax.all_to_all(grad, "context", 1, 0, tiled=True)
        grad, early = lax.optimization_barrier((grad, early))
        grad = grad.reshape(self.rows * self.ways, self.group, HD)
        inner = jnp.sum(grad.astype(f32) * self.attended.astype(f32), axis=-1).T
        grad_key = jnp.zeros(self.keys.shape, f32)
        grad_value = jnp.zeros(self.values.shape, f32)
        grad_queries = []
        for start, size in self._blocks():
            query, scores, allowed = self._scores(start, size)
            log_block = lax.dynamic_slice_in_dim(self.log_total, start, size, axis=1)
            inner_block = lax.dynamic_slice_in_dim(inner, start, size, axis=1)
            grad_block = lax.dynamic_slice_in_dim(grad, start, size, axis=0)
            probs = jnp.where(allowed[None], jnp.exp(scores - log_block[..., None]), 0.0)
            grad_value = grad_value + jnp.einsum(
                "hqk,qhd->khd", probs.astype(bf16), grad_block, preferred_element_type=f32
            )
            grad_probs = jnp.einsum(
                "qhd,khd->hqk", grad_block, self.values, preferred_element_type=f32
            )
            grad_scores = (probs * (grad_probs - inner_block[..., None]) * scale).astype(bf16)
            grad_queries.append(
                jnp.einsum("hqk,khd->qhd", grad_scores, self.keys, preferred_element_type=f32)
            )
            grad_key = grad_key + jnp.einsum(
                "hqk,qhd->khd", grad_scores, query, preferred_element_type=f32
            )
        grad_query = jnp.concatenate(grad_queries, axis=0)
        grad_qin = rotate_back(grad_query, self.cos_all, self.sin_all).astype(bf16)
        grad_kin = rotate_back(grad_key, self.cos_all, self.sin_all).astype(bf16)
        grad_vin = grad_value.astype(bf16)
        returned = []
        for grad_in in (grad_qin, grad_kin, grad_vin):
            grad_in = grad_in.reshape(self.rows * self.ways, 1, self.group, HD)
            grad_in = lax.all_to_all(grad_in, "context", 0, 1, tiled=True)
            returned.append(grad_in.reshape(self.rows, self.heads, HD))
        return returned[0], returned[1], returned[2], early


def mlp_chunks(hidden_cols):
    for count in (2, 1):
        if hidden_cols % (count * 128) == 0:
            return count
    return 1


def on_device(
    inputs, segments, positions, w_q, w_k, w_v, w_o, w_gate, w_up, w_down, g_attn, g_mlp, d_out
):
    f32 = jnp.float32
    bf16 = jnp.bfloat16
    rows = inputs.shape[1]
    width = inputs.shape[2]
    cols = w_q.shape[1]
    hidden_cols = w_gate.shape[1]
    tokens = inputs.reshape(rows, width)
    segment = segments.reshape(rows)
    position = positions.reshape(rows)
    full_qkvo = lax.all_gather(
        jnp.concatenate([w_q, w_k, w_v, w_o], axis=1), ROWS, axis=0, tiled=True
    )
    full_qkv = full_qkvo[:, : 3 * cols]
    full_o = full_qkvo[:, 3 * cols :]
    gains = lax.all_gather(
        jnp.concatenate([g_attn, g_mlp])[None], ROWS, axis=0, tiled=True
    )
    gain_attn = gains[:, : g_attn.shape[0]].reshape(width)
    gain_mlp = gains[:, g_attn.shape[0] :].reshape(width)
    count = mlp_chunks(hidden_cols)
    step = hidden_cols // count
    fetched = []
    for index in range(count):
        part = slice(index * step, (index + 1) * step)
        pair = lax.all_gather(
            jnp.concatenate([w_gate[:, part], w_up[:, part]], axis=1), ROWS, axis=0, tiled=True
        )
        fetched.append(
            (pair[:, :step], pair[:, step:], lax.all_gather(w_down[:, part], ROWS, axis=0, tiled=True))
        )
    heads = cols // HD
    cosine, sine = rope_tables(position)
    resid1 = tokens.astype(f32)
    norm1, inv1 = normalize(resid1)
    h1 = (norm1 * gain_attn.astype(f32)).astype(bf16)
    projected = jnp.dot(h1, full_qkv, preferred_element_type=f32)
    query = rotate(projected[:, :cols].reshape(rows, heads, HD), cosine, sine).astype(bf16)
    key_heads = rotate(projected[:, cols : 2 * cols].reshape(rows, heads, HD), cosine, sine).astype(
        bf16
    )
    value_heads = projected[:, 2 * cols :].astype(bf16).reshape(rows, heads, HD)
    if heads % lax.axis_size("context") == 0:
        attention = HeadAttention(query, key_heads, value_heads, segment, position, cosine, sine)
    else:
        attention = RingAttention(
            query,
            key_heads.reshape(rows, cols),
            value_heads.reshape(rows, cols),
            segment,
            position,
            cosine,
            sine,
        )
    attended = attention.forward()
    attended_flat = attended.reshape(rows, cols)
    resid2 = resid1 + tensor_total(contract_last(attended_flat, full_o))
    norm2, inv2 = normalize(resid2)
    h2_part = (norm2 * gain_mlp.astype(f32)).astype(bf16)
    grad_y = d_out.reshape(rows, width)
    mlp_partial = None
    h2_grad_partial = None
    staged = []
    for full_gate, full_up, full_down in fetched:
        if staged:
            full_gate, staged[-1] = lax.optimization_barrier((full_gate, staged[-1]))
        gate = jnp.dot(h2_part, full_gate, preferred_element_type=f32)
        up = jnp.dot(h2_part, full_up, preferred_element_type=f32)
        active = jax.nn.silu(gate)
        hidden = (active * up).astype(bf16)
        out_part = contract_last(hidden, full_down)
        mlp_partial = out_part if mlp_partial is None else mlp_partial + out_part
        grad_hidden = jnp.dot(grad_y, full_down, preferred_element_type=f32)
        sigma = jax.nn.sigmoid(gate)
        grad_gate = (grad_hidden * up * sigma * (1.0 + gate * (1.0 - sigma))).astype(bf16)
        grad_up = (grad_hidden * active).astype(bf16)
        back_part = contract_last(grad_gate, full_gate) + contract_last(grad_up, full_up)
        pending = (
            contract_first(h2_part, grad_gate),
            contract_first(h2_part, grad_up),
            contract_first(grad_y, hidden),
        )
        h2_grad_partial = back_part if h2_grad_partial is None else h2_grad_partial + back_part
        staged.append(chip_total(jnp.concatenate(pending, axis=1)))
    grad_h2 = tensor_total(h2_grad_partial)
    grad_h2, staged[-1] = lax.optimization_barrier((grad_h2, staged[-1]))
    reduced = [line_total(chunk) for chunk in staged]
    result = (resid2 + tensor_total(mlp_partial)).astype(bf16)
    grad_gmlp = jnp.sum(grad_h2 * norm2, axis=0)
    grad_resid = grad_y.astype(f32) + norm_back(grad_h2, norm2, inv2, gain_mlp)
    grad_resid_part = grad_resid.astype(bf16)
    grad_heads = (
        jnp.dot(grad_resid_part, full_o, preferred_element_type=f32)
        .astype(bf16)
        .reshape(rows, heads, HD)
    )
    grad_heads, partial_o = lax.optimization_barrier(
        (grad_heads, contract_first(grad_resid_part, attended_flat))
    )
    early = (chip_total(partial_o), reduced[:-1])
    grad_qin, grad_kin, grad_vin, early = attention.backward(grad_heads, early)
    staged_o, reduced[:-1] = early
    reduced_o = line_total(staged_o)
    grad_qkv = jnp.concatenate(
        [grad_qin.reshape(rows, cols), grad_kin.reshape(rows, cols), grad_vin.reshape(rows, cols)],
        axis=1,
    )
    h1_grad_partial = contract_last(grad_qkv, full_qkv)
    first_tensor = (lax.axis_index("tensor") == 0).astype(f32)
    gain_parts = jnp.stack(
        [jnp.sum(h1_grad_partial * norm1, axis=0), grad_gmlp * first_tensor], axis=1
    )
    gains_total = exact_total(gain_parts)
    h1_grad_partial, staged_qkv = lax.optimization_barrier(
        (h1_grad_partial, chip_total(contract_first(h1, grad_qkv)))
    )
    grad_h1 = tensor_total(h1_grad_partial)
    grad_h1, reduced_o, reduced[-1], result, gains_total = lax.optimization_barrier(
        (grad_h1, reduced_o, reduced[-1], result, gains_total)
    )
    grad_x_part = (grad_resid + norm_back(grad_h1, norm1, inv1, gain_attn)).astype(bf16)
    reduced_qkv = line_total(staged_qkv)
    blocks = lax.axis_size("shard") * lax.axis_size("context")
    block = lax.axis_index("shard") * lax.axis_size("context") + lax.axis_index("context")
    piece = width // blocks
    reduced_gains = lax.dynamic_slice_in_dim(gains_total, block * piece, piece, axis=0)
    reduced_gate, reduced_up, reduced_down = (
        jnp.concatenate([chunk[:, which * step : (which + 1) * step] for chunk in reduced], axis=1)
        for which in range(3)
    )
    return (
        result.reshape(1, rows, width),
        grad_x_part.reshape(1, rows, width),
        reduced_qkv[:, :cols],
        reduced_qkv[:, cols : 2 * cols],
        reduced_qkv[:, 2 * cols :],
        reduced_o,
        reduced_gate,
        reduced_up,
        reduced_down,
        reduced_gains[:, 0],
        reduced_gains[:, 1],
    )


def solution(mesh):
    placed = (
        P("shard", "context", None),
        P("shard", "context"),
        P("shard", "context"),
        P(ROWS, "tensor"),
        P(ROWS, "tensor"),
        P(ROWS, "tensor"),
        P(ROWS, "tensor"),
        P(ROWS, "tensor"),
        P(ROWS, "tensor"),
        P(ROWS, "tensor"),
        P(ROWS),
        P(ROWS),
        P("shard", "context", None),
    )
    return jax.shard_map(
        on_device,
        mesh=mesh,
        in_specs=placed,
        out_specs=(
            P("shard", "context", None),
            P("shard", "context", None),
            P(ROWS, "tensor"),
            P(ROWS, "tensor"),
            P(ROWS, "tensor"),
            P(ROWS, "tensor"),
            P(ROWS, "tensor"),
            P(ROWS, "tensor"),
            P(ROWS, "tensor"),
            P(ROWS),
            P(ROWS),
        ),
        check_vma=False,
    )
```

```python
import math

import jax
import jax.numpy as jnp
from jax import lax
from jax.sharding import PartitionSpec as P

HD = 64


EPS = 1e-05
THETA = 130000.0
NEG = -1e30
ROWS = ("shard", "context")


def passed_along(value, axis, steps):
    count = lax.axis_size(axis)
    pairs = [(source, (source + steps) % count) for source in range(count)]
    return lax.ppermute(value, axis, pairs)


def rope_tables(position):
    index = jnp.arange(HD // 2, dtype=jnp.float32)
    inverse = jnp.power(jnp.float32(THETA), -2.0 * index / HD)
    angle = position.astype(jnp.float32)[:, None] * inverse[None, :]
    return (jnp.cos(angle), jnp.sin(angle))


def rotate(tensor, cosine, sine):
    half = tensor.shape[-1] // 2
    first = tensor[..., :half]
    second = tensor[..., half:]
    cosine = cosine[:, None, :]
    sine = sine[:, None, :]
    return jnp.concatenate(
        [first * cosine - second * sine, second * cosine + first * sine], axis=-1
    )


def rotate_back(grad, cosine, sine):
    half = grad.shape[-1] // 2
    first = grad[..., :half]
    second = grad[..., half:]
    cosine = cosine[:, None, :]
    sine = sine[:, None, :]
    return jnp.concatenate(
        [first * cosine + second * sine, second * cosine - first * sine], axis=-1
    )


def normalize(value):
    inv_rms = lax.rsqrt(jnp.mean(value * value, axis=-1, keepdims=True) + EPS)
    return (value * inv_rms, inv_rms)


def norm_back(grad, normed, inv_rms, gain):
    scaled = grad * gain.astype(jnp.float32)
    return inv_rms * (scaled - normed * jnp.mean(scaled * normed, axis=-1, keepdims=True))


def contract_last(left, right):
    return lax.dot_general(
        left, right, (((1,), (1,)), ((), ())), preferred_element_type=jnp.float32
    )


def contract_first(left, right):
    return lax.dot_general(
        left, right, (((0,), (0,)), ((), ())), preferred_element_type=jnp.float32
    )


def half_of(value, bit):
    size = value.shape[0] // 2
    return lax.dynamic_slice_in_dim(value, bit * size, size, axis=0)


def joined(mine, other, bit):
    low = jnp.where(bit == 0, mine, other)
    high = jnp.where(bit == 0, other, mine)
    return jnp.concatenate([low, high], axis=0)


def tensor_total(partial_sum):
    count = lax.axis_size("tensor")
    rows = partial_sum.shape[0]
    if count != 4 or rows % 8:
        return lax.psum(partial_sum.astype(jnp.bfloat16), "tensor").astype(jnp.float32)
    f32 = jnp.float32
    bf16 = jnp.bfloat16
    index = lax.axis_index("tensor")
    x_bit = index % 2
    y_bit = index // 2
    x_pairs = [(i, i ^ 1) for i in range(4)]
    y_pairs = [(i, i ^ 2) for i in range(4)]

    def swap(value, pairs):
        return lax.ppermute(value.astype(bf16), "tensor", pairs).astype(f32)

    first = partial_sum[: rows // 2]
    second = partial_sum[rows // 2 :]
    first = half_of(first, x_bit) + swap(half_of(first, 1 - x_bit), x_pairs)
    second = half_of(second, y_bit) + swap(half_of(second, 1 - y_bit), y_pairs)
    first = half_of(first, y_bit) + swap(half_of(first, 1 - y_bit), y_pairs)
    second = half_of(second, x_bit) + swap(half_of(second, 1 - x_bit), x_pairs)
    first = first.astype(bf16)
    second = second.astype(bf16)
    first = joined(first, lax.ppermute(first, "tensor", y_pairs), y_bit)
    second = joined(second, lax.ppermute(second, "tensor", x_pairs), x_bit)
    first = joined(first, lax.ppermute(first, "tensor", x_pairs), x_bit)
    second = joined(second, lax.ppermute(second, "tensor", y_pairs), y_bit)
    return jnp.concatenate([first, second], axis=0).astype(f32)


def tensor_exact_total(value):
    if lax.axis_size("tensor") != 4:
        return lax.psum(value, "tensor")
    value = value + lax.ppermute(value, "tensor", [(i, i ^ 1) for i in range(4)])
    return value + lax.ppermute(value, "tensor", [(i, i ^ 2) for i in range(4)])


def exact_total(value):
    for axis in ("tensor", "shard", "context"):
        count = lax.axis_size(axis)
        if count & (count - 1):
            value = lax.psum(value, axis)
            continue
        span = 1
        while span < count:
            value = value + lax.ppermute(value, axis, [(i, i ^ span) for i in range(count)])
            span *= 2
    return value


def chip_total(grad):
    f32 = jnp.float32
    shard = lax.axis_index("shard")
    mine = half_of(grad, shard)
    other = half_of(grad, 1 - shard)
    got = lax.ppermute(other.astype(jnp.bfloat16), "shard", [(0, 1), (1, 0)])
    return mine.astype(f32) + got.astype(f32)


def line_total(staged):
    return lax.psum_scatter(
        staged.astype(jnp.bfloat16), "context", scatter_dimension=0, tiled=True
    ).astype(jnp.float32)


def rows_total(grad):
    return line_total(chip_total(grad))


def pass_grads(grad_key, grad_value):
    return (
        passed_along(grad_key.astype(jnp.bfloat16), "context", 1).astype(grad_key.dtype),
        passed_along(grad_value.astype(jnp.bfloat16), "context", 1).astype(grad_value.dtype),
    )


def key_scores(query_heads, query_seg, query_pos, piece):
    key_flat, value_flat, key_seg, key_pos = piece
    heads = query_heads.shape[1]
    key_heads = key_flat.reshape(key_flat.shape[0], heads, HD)
    value_heads = value_flat.reshape(value_flat.shape[0], heads, HD)
    scores = jnp.einsum(
        "qhd,khd->hqk", query_heads, key_heads, preferred_element_type=jnp.float32
    ) * (1.0 / math.sqrt(HD))
    allowed = (query_seg[:, None] == key_seg[None, :]) & (key_pos[None, :] <= query_pos[:, None])
    return (jnp.where(allowed[None], scores, NEG), allowed, key_heads, value_heads)


def forward_fold(stats, piece, query_heads, query_seg, query_pos):
    peak, total, accum = stats
    scores, allowed, key_heads, value_heads = key_scores(query_heads, query_seg, query_pos, piece)
    new_peak = jnp.maximum(peak, jnp.max(scores, axis=-1))
    weights = jnp.where(allowed[None], jnp.exp(scores - new_peak[..., None]), 0.0)
    factor = jnp.exp(peak - new_peak)
    total = total * factor + jnp.sum(weights, axis=-1)
    accum = accum * factor[..., None] + jnp.einsum(
        "hqk,khd->hqd",
        weights.astype(jnp.bfloat16),
        value_heads,
        preferred_element_type=jnp.float32,
    )
    return (new_peak, total, accum)


def backward_piece(piece, query_heads, grad_heads, log_total, inner, query_seg, query_pos):
    scores, allowed, key_heads, value_heads = key_scores(query_heads, query_seg, query_pos, piece)
    probs = jnp.where(allowed[None], jnp.exp(scores - log_total[..., None]), 0.0)
    grad_value = jnp.einsum(
        "hqk,qhd->khd", probs.astype(jnp.bfloat16), grad_heads, preferred_element_type=jnp.float32
    )
    grad_probs = jnp.einsum(
        "qhd,khd->hqk", grad_heads, value_heads, preferred_element_type=jnp.float32
    )
    grad_scores = (probs * (grad_probs - inner[..., None]) * (1.0 / math.sqrt(HD))).astype(
        jnp.bfloat16
    )
    grad_query = jnp.einsum(
        "hqk,khd->qhd", grad_scores, key_heads, preferred_element_type=jnp.float32
    )
    grad_key = jnp.einsum(
        "hqk,qhd->khd", grad_scores, query_heads, preferred_element_type=jnp.float32
    )
    key_rows = grad_key.shape[0]
    return (grad_query, grad_key.reshape(key_rows, -1), grad_value.reshape(key_rows, -1))


class RingAttention:
    def __init__(self, query, key_flat, value_flat, segment, position, cosine, sine):
        self.query = query
        self.piece = (key_flat, value_flat, segment, position)
        self.segment = segment
        self.position = position
        self.cosine = cosine
        self.sine = sine

    def forward(self):
        f32 = jnp.float32
        query, segment, position = self.query, self.segment, self.position
        rows, heads = query.shape[0], query.shape[1]
        start_stats = (
            jnp.full((heads, rows), NEG, f32),
            jnp.zeros((heads, rows), f32),
            jnp.zeros((heads, rows, HD), f32),
        )
        stats = forward_fold(start_stats, self.piece, query, segment, position)

        def cycle_turn(index, carry):
            moving, current = carry
            moving = passed_along(moving, "context", 1)
            current = forward_fold(current, moving, query, segment, position)
            return (moving, current)

        peak, total, accum = lax.fori_loop(
            0, lax.axis_size("context") - 1, cycle_turn, (self.piece, stats)
        )[1]
        self.attended = jnp.transpose(accum / total[..., None], (1, 0, 2)).astype(jnp.bfloat16)
        self.log_total = peak + jnp.log(total)
        return self.attended

    def backward(self, grad_heads, early):
        bf16 = jnp.bfloat16
        query, segment, position = self.query, self.segment, self.position
        rows, heads = query.shape[0], query.shape[1]
        inner = jnp.sum(grad_heads.astype(jnp.float32) * self.attended.astype(jnp.float32), axis=-1).T

        def piece_grads(piece):
            return backward_piece(piece, query, grad_heads, self.log_total, inner, segment, position)

        grad_query, grad_key, grad_value = piece_grads(self.piece)

        def grad_turn(index, carry):
            moving, acc_query, acc_key, acc_value = carry
            moving = passed_along(moving, "context", 1)
            acc_key, acc_value = pass_grads(acc_key, acc_value)
            part_query, part_key, part_value = piece_grads(moving)
            return (moving, acc_query + part_query, acc_key + part_key, acc_value + part_value)

        carried = lax.fori_loop(
            0,
            lax.axis_size("context") - 1,
            grad_turn,
            (self.piece, grad_query, grad_key, grad_value),
        )
        grad_query = carried[1]
        grad_key, grad_value = pass_grads(carried[2], carried[3])
        grad_qin = rotate_back(grad_query, self.cosine, self.sine).astype(bf16)
        grad_kin = rotate_back(grad_key.reshape(rows, heads, HD), self.cosine, self.sine).astype(bf16)
        grad_vin = grad_value.astype(bf16).reshape(rows, heads, HD)
        return grad_qin, grad_kin, grad_vin, early


class HeadAttention:
    BLOCK = 512

    def __init__(self, query, key_heads, value_heads, segment, position, cosine, sine):
        ways = lax.axis_size("context")
        rows, heads = query.shape[0], query.shape[1]
        self.ways = ways
        self.rows = rows
        self.heads = heads
        self.group = heads // ways
        self.piece = rows // 2
        stacked = jnp.stack([query, key_heads, value_heads], axis=1)
        stacked = stacked.reshape(rows, 3, ways, self.group, HD)
        stacked = lax.all_to_all(stacked, "context", 2, 0, tiled=True)
        stacked = stacked.reshape(rows * ways, 3, self.group, HD)
        tags = jnp.stack([segment, position], axis=0)[None]
        tags = jnp.broadcast_to(tags, (ways, 2, rows))
        tags = lax.all_to_all(tags, "context", 0, 0, tiled=True)
        tags = jnp.transpose(tags, (1, 0, 2)).reshape(2, rows * ways)
        pieces = 2 * ways
        piece_of_slot = tags[1].reshape(pieces, self.piece)[:, 0] // self.piece
        slots = jnp.arange(pieces, dtype=jnp.int32)
        slot_of_piece = jnp.sum(
            jnp.where(piece_of_slot[None, :] == slots[:, None], slots[None, :], 0), axis=1
        )
        self.piece_of_slot = piece_of_slot
        self.slot_of_piece = slot_of_piece
        stacked = self._reorder(stacked, slot_of_piece)
        tags = self._reorder(tags.T, slot_of_piece).T
        self.query = stacked[:, 0]
        self.keys = stacked[:, 1]
        self.values = stacked[:, 2]
        self.seg_all = tags[0]
        self.pos_all = tags[1]
        self.cos_all, self.sin_all = rope_tables(self.pos_all)

    def _reorder(self, value, source):
        parts = [
            lax.dynamic_slice_in_dim(value, source[index] * self.piece, self.piece, axis=0)
            for index in range(source.shape[0])
        ]
        return jnp.concatenate(parts, axis=0)

    def _blocks(self):
        total = self.rows * self.ways
        block = min(self.BLOCK, total)
        return [(start, block) for start in range(0, total, block)]

    def _scores(self, start, size):
        reach = start + size
        query = self.query[start:reach]
        seg_q = self.seg_all[start:reach]
        pos_q = self.pos_all[start:reach]
        scores = jnp.einsum(
            "qhd,khd->hqk", query, self.keys[:reach], preferred_element_type=jnp.float32
        ) * (1.0 / math.sqrt(HD))
        allowed = (seg_q[:, None] == self.seg_all[None, :reach]) & (
            self.pos_all[None, :reach] <= pos_q[:, None]
        )
        return query, jnp.where(allowed[None], scores, NEG), allowed

    def forward(self):
        outs = []
        logs = []
        for start, size in self._blocks():
            reach = start + size
            _, scores, allowed = self._scores(start, size)
            peak = jnp.max(scores, axis=-1)
            weights = jnp.where(allowed[None], jnp.exp(scores - peak[..., None]), 0.0)
            total = jnp.sum(weights, axis=-1)
            mixed = jnp.einsum(
                "hqk,khd->qhd",
                weights.astype(jnp.bfloat16),
                self.values[:reach],
                preferred_element_type=jnp.float32,
            )
            outs.append((mixed / total.T[:, :, None]).astype(jnp.bfloat16))
            logs.append(peak + jnp.log(total))
        self.attended = jnp.concatenate(outs, axis=0)
        self.log_total = jnp.concatenate(logs, axis=1)
        back = self._reorder(self.attended, self.piece_of_slot)
        back = back.reshape(self.rows * self.ways, 1, self.group, HD)
        back = lax.all_to_all(back, "context", 0, 1, tiled=True)
        return back.reshape(self.rows, self.heads, HD)

    def backward(self, grad_heads, early):
        f32 = jnp.float32
        bf16 = jnp.bfloat16
        scale = 1.0 / math.sqrt(HD)
        grad = grad_heads.reshape(self.rows, self.ways, self.group, HD)
        grad = lax.all_to_all(grad, "context", 1, 0, tiled=True)
        grad, early = lax.optimization_barrier((grad, early))
        grad = grad.reshape(self.rows * self.ways, self.group, HD)
        grad = self._reorder(grad, self.slot_of_piece)
        inner = jnp.sum(grad.astype(f32) * self.attended.astype(f32), axis=-1).T
        total_rows = self.rows * self.ways
        grad_key = jnp.zeros(self.keys.shape, f32)
        grad_value = jnp.zeros(self.values.shape, f32)
        grad_queries = []
        for start, size in self._blocks():
            reach = start + size
            query, scores, allowed = self._scores(start, size)
            log_block = self.log_total[:, start:reach]
            inner_block = inner[:, start:reach]
            grad_block = grad[start:reach]
            probs = jnp.where(allowed[None], jnp.exp(scores - log_block[..., None]), 0.0)
            part_value = jnp.einsum(
                "hqk,qhd->khd", probs.astype(bf16), grad_block, preferred_element_type=f32
            )
            grad_probs = jnp.einsum(
                "qhd,khd->hqk", grad_block, self.values[:reach], preferred_element_type=f32
            )
            grad_scores = (probs * (grad_probs - inner_block[..., None]) * scale).astype(bf16)
            grad_queries.append(
                jnp.einsum(
                    "hqk,khd->qhd", grad_scores, self.keys[:reach], preferred_element_type=f32
                )
            )
            part_key = jnp.einsum("hqk,qhd->khd", grad_scores, query, preferred_element_type=f32)
            pad = ((0, total_rows - reach), (0, 0), (0, 0))
            grad_value = grad_value + jnp.pad(part_value, pad)
            grad_key = grad_key + jnp.pad(part_key, pad)
        grad_query = jnp.concatenate(grad_queries, axis=0)
        grad_qin = rotate_back(grad_query, self.cos_all, self.sin_all).astype(bf16)
        grad_kin = rotate_back(grad_key, self.cos_all, self.sin_all).astype(bf16)
        grad_vin = grad_value.astype(bf16)
        returned = []
        for grad_in in (grad_qin, grad_kin, grad_vin):
            grad_in = self._reorder(grad_in, self.piece_of_slot)
            grad_in = grad_in.reshape(self.rows * self.ways, 1, self.group, HD)
            grad_in = lax.all_to_all(grad_in, "context", 0, 1, tiled=True)
            returned.append(grad_in.reshape(self.rows, self.heads, HD))
        return returned[0], returned[1], returned[2], early


def mlp_chunks(hidden_cols):
    for count in (2, 1):
        if hidden_cols % (count * 128) == 0:
            return count
    return 1


def on_device(
    inputs, segments, positions, w_q, w_k, w_v, w_o, w_gate, w_up, w_down, g_attn, g_mlp, d_out
):
    f32 = jnp.float32
    bf16 = jnp.bfloat16
    rows = inputs.shape[1]
    width = inputs.shape[2]
    cols = w_q.shape[1]
    hidden_cols = w_gate.shape[1]
    tokens = inputs.reshape(rows, width)
    segment = segments.reshape(rows)
    position = positions.reshape(rows)
    full_qkvo = lax.all_gather(
        jnp.concatenate([w_q, w_k, w_v, w_o], axis=1), ROWS, axis=0, tiled=True
    )
    full_qkv = full_qkvo[:, : 3 * cols]
    full_o = full_qkvo[:, 3 * cols :]
    gains = lax.all_gather(
        jnp.concatenate([g_attn, g_mlp])[None], ROWS, axis=0, tiled=True
    )
    gain_attn = gains[:, : g_attn.shape[0]].reshape(width)
    gain_mlp = gains[:, g_attn.shape[0] :].reshape(width)
    count = mlp_chunks(hidden_cols)
    step = hidden_cols // count
    fetched = []
    for index in range(count):
        part = slice(index * step, (index + 1) * step)
        pair = lax.all_gather(
            jnp.concatenate([w_gate[:, part], w_up[:, part]], axis=1), ROWS, axis=0, tiled=True
        )
        fetched.append(
            (pair[:, :step], pair[:, step:], lax.all_gather(w_down[:, part], ROWS, axis=0, tiled=True))
        )
    heads = cols // HD
    cosine, sine = rope_tables(position)
    resid1 = tokens.astype(f32)
    norm1, inv1 = normalize(resid1)
    h1 = (norm1 * gain_attn.astype(f32)).astype(bf16)
    projected = jnp.dot(h1, full_qkv, preferred_element_type=f32)
    query = rotate(projected[:, :cols].reshape(rows, heads, HD), cosine, sine).astype(bf16)
    key_heads = rotate(projected[:, cols : 2 * cols].reshape(rows, heads, HD), cosine, sine).astype(
        bf16
    )
    value_heads = projected[:, 2 * cols :].astype(bf16).reshape(rows, heads, HD)
    if heads % lax.axis_size("context") == 0:
        attention = HeadAttention(query, key_heads, value_heads, segment, position, cosine, sine)
    else:
        attention = RingAttention(
            query,
            key_heads.reshape(rows, cols),
            value_heads.reshape(rows, cols),
            segment,
            position,
            cosine,
            sine,
        )
    attended = attention.forward()
    attended_flat = attended.reshape(rows, cols)
    resid2 = resid1 + tensor_total(contract_last(attended_flat, full_o))
    norm2, inv2 = normalize(resid2)
    h2_part = (norm2 * gain_mlp.astype(f32)).astype(bf16)
    grad_y = d_out.reshape(rows, width)
    mlp_partial = None
    h2_grad_partial = None
    staged = []
    for full_gate, full_up, full_down in fetched:
        if staged:
            full_gate, staged[-1] = lax.optimization_barrier((full_gate, staged[-1]))
        gate = jnp.dot(h2_part, full_gate, preferred_element_type=f32)
        up = jnp.dot(h2_part, full_up, preferred_element_type=f32)
        active = jax.nn.silu(gate)
        hidden = (active * up).astype(bf16)
        out_part = contract_last(hidden, full_down)
        mlp_partial = out_part if mlp_partial is None else mlp_partial + out_part
        grad_hidden = jnp.dot(grad_y, full_down, preferred_element_type=f32)
        sigma = jax.nn.sigmoid(gate)
        grad_gate = (grad_hidden * up * sigma * (1.0 + gate * (1.0 - sigma))).astype(bf16)
        grad_up = (grad_hidden * active).astype(bf16)
        back_part = contract_last(grad_gate, full_gate) + contract_last(grad_up, full_up)
        pending = (
            contract_first(h2_part, grad_gate),
            contract_first(h2_part, grad_up),
            contract_first(grad_y, hidden),
        )
        h2_grad_partial = back_part if h2_grad_partial is None else h2_grad_partial + back_part
        staged.append(chip_total(jnp.concatenate(pending, axis=1)))
    grad_h2 = tensor_total(h2_grad_partial)
    grad_h2, staged[-1] = lax.optimization_barrier((grad_h2, staged[-1]))
    reduced = [line_total(chunk) for chunk in staged]
    result = (resid2 + tensor_total(mlp_partial)).astype(bf16)
    grad_gmlp = jnp.sum(grad_h2 * norm2, axis=0)
    grad_resid = grad_y.astype(f32) + norm_back(grad_h2, norm2, inv2, gain_mlp)
    grad_resid_part = grad_resid.astype(bf16)
    grad_heads = (
        jnp.dot(grad_resid_part, full_o, preferred_element_type=f32)
        .astype(bf16)
        .reshape(rows, heads, HD)
    )
    grad_heads, partial_o = lax.optimization_barrier(
        (grad_heads, contract_first(grad_resid_part, attended_flat))
    )
    early = (chip_total(partial_o), reduced[:-1])
    grad_qin, grad_kin, grad_vin, early = attention.backward(grad_heads, early)
    staged_o, reduced[:-1] = early
    reduced_o = line_total(staged_o)
    grad_qkv = jnp.concatenate(
        [grad_qin.reshape(rows, cols), grad_kin.reshape(rows, cols), grad_vin.reshape(rows, cols)],
        axis=1,
    )
    h1_grad_partial = contract_last(grad_qkv, full_qkv)
    first_tensor = (lax.axis_index("tensor") == 0).astype(f32)
    gain_parts = jnp.stack(
        [jnp.sum(h1_grad_partial * norm1, axis=0), grad_gmlp * first_tensor], axis=1
    )
    gains_total = exact_total(gain_parts)
    h1_grad_partial, staged_qkv = lax.optimization_barrier(
        (h1_grad_partial, chip_total(contract_first(h1, grad_qkv)))
    )
    grad_h1 = tensor_total(h1_grad_partial)
    grad_h1, reduced_o, reduced[-1], result = lax.optimization_barrier(
        (grad_h1, reduced_o, reduced[-1], result)
    )
    grad_x_part = (grad_resid + norm_back(grad_h1, norm1, inv1, gain_attn)).astype(bf16)
    reduced_qkv = line_total(staged_qkv)
    blocks = lax.axis_size("shard") * lax.axis_size("context")
    block = lax.axis_index("shard") * lax.axis_size("context") + lax.axis_index("context")
    piece = width // blocks
    reduced_gains = lax.dynamic_slice_in_dim(gains_total, block * piece, piece, axis=0)
    reduced_gate, reduced_up, reduced_down = (
        jnp.concatenate([chunk[:, which * step : (which + 1) * step] for chunk in reduced], axis=1)
        for which in range(3)
    )
    return (
        result.reshape(1, rows, width),
        grad_x_part.reshape(1, rows, width),
        reduced_qkv[:, :cols],
        reduced_qkv[:, cols : 2 * cols],
        reduced_qkv[:, 2 * cols :],
        reduced_o,
        reduced_gate,
        reduced_up,
        reduced_down,
        reduced_gains[:, 0],
        reduced_gains[:, 1],
    )


def solution(mesh):
    placed = (
        P("shard", "context", None),
        P("shard", "context"),
        P("shard", "context"),
        P(ROWS, "tensor"),
        P(ROWS, "tensor"),
        P(ROWS, "tensor"),
        P(ROWS, "tensor"),
        P(ROWS, "tensor"),
        P(ROWS, "tensor"),
        P(ROWS, "tensor"),
        P(ROWS),
        P(ROWS),
        P("shard", "context", None),
    )
    return jax.shard_map(
        on_device,
        mesh=mesh,
        in_specs=placed,
        out_specs=(
            P("shard", "context", None),
            P("shard", "context", None),
            P(ROWS, "tensor"),
            P(ROWS, "tensor"),
            P(ROWS, "tensor"),
            P(ROWS, "tensor"),
            P(ROWS, "tensor"),
            P(ROWS, "tensor"),
            P(ROWS, "tensor"),
            P(ROWS),
            P(ROWS),
        ),
        check_vma=False,
    )
```

```python
import math

import jax
import jax.numpy as jnp
from jax import lax
from jax.sharding import PartitionSpec as P

HD = 64


EPS = 1e-05
THETA = 130000.0
NEG = -1e30
ROWS = ("shard", "context")


def passed_along(value, axis, steps):
    count = lax.axis_size(axis)
    pairs = [(source, (source + steps) % count) for source in range(count)]
    return lax.ppermute(value, axis, pairs)


def rope_tables(position):
    index = jnp.arange(HD // 2, dtype=jnp.float32)
    inverse = jnp.power(jnp.float32(THETA), -2.0 * index / HD)
    angle = position.astype(jnp.float32)[:, None] * inverse[None, :]
    return (jnp.cos(angle), jnp.sin(angle))


def rotate(tensor, cosine, sine):
    half = tensor.shape[-1] // 2
    first = tensor[..., :half]
    second = tensor[..., half:]
    cosine = cosine[:, None, :]
    sine = sine[:, None, :]
    return jnp.concatenate(
        [first * cosine - second * sine, second * cosine + first * sine], axis=-1
    )


def rotate_back(grad, cosine, sine):
    half = grad.shape[-1] // 2
    first = grad[..., :half]
    second = grad[..., half:]
    cosine = cosine[:, None, :]
    sine = sine[:, None, :]
    return jnp.concatenate(
        [first * cosine + second * sine, second * cosine - first * sine], axis=-1
    )


def normalize(value):
    inv_rms = lax.rsqrt(jnp.mean(value * value, axis=-1, keepdims=True) + EPS)
    return (value * inv_rms, inv_rms)


def norm_back(grad, normed, inv_rms, gain):
    scaled = grad * gain.astype(jnp.float32)
    return inv_rms * (scaled - normed * jnp.mean(scaled * normed, axis=-1, keepdims=True))


def contract_last(left, right):
    return lax.dot_general(
        left, right, (((1,), (1,)), ((), ())), preferred_element_type=jnp.float32
    )


def contract_first(left, right):
    return lax.dot_general(
        left, right, (((0,), (0,)), ((), ())), preferred_element_type=jnp.float32
    )


def half_of(value, bit):
    size = value.shape[0] // 2
    return lax.dynamic_slice_in_dim(value, bit * size, size, axis=0)


def joined(mine, other, bit):
    low = jnp.where(bit == 0, mine, other)
    high = jnp.where(bit == 0, other, mine)
    return jnp.concatenate([low, high], axis=0)


def tensor_total(partial_sum):
    count = lax.axis_size("tensor")
    rows = partial_sum.shape[0]
    if count != 4 or rows % 8:
        return lax.psum(partial_sum.astype(jnp.bfloat16), "tensor").astype(jnp.float32)
    f32 = jnp.float32
    bf16 = jnp.bfloat16
    index = lax.axis_index("tensor")
    x_bit = index % 2
    y_bit = index // 2
    x_pairs = [(i, i ^ 1) for i in range(4)]
    y_pairs = [(i, i ^ 2) for i in range(4)]

    def swap(value, pairs):
        return lax.ppermute(value.astype(bf16), "tensor", pairs).astype(f32)

    first = partial_sum[: rows // 2]
    second = partial_sum[rows // 2 :]
    first = half_of(first, x_bit) + swap(half_of(first, 1 - x_bit), x_pairs)
    second = half_of(second, y_bit) + swap(half_of(second, 1 - y_bit), y_pairs)
    first = half_of(first, y_bit) + swap(half_of(first, 1 - y_bit), y_pairs)
    second = half_of(second, x_bit) + swap(half_of(second, 1 - x_bit), x_pairs)
    first = first.astype(bf16)
    second = second.astype(bf16)
    first = joined(first, lax.ppermute(first, "tensor", y_pairs), y_bit)
    second = joined(second, lax.ppermute(second, "tensor", x_pairs), x_bit)
    first = joined(first, lax.ppermute(first, "tensor", x_pairs), x_bit)
    second = joined(second, lax.ppermute(second, "tensor", y_pairs), y_bit)
    return jnp.concatenate([first, second], axis=0).astype(f32)


def tensor_exact_total(value):
    if lax.axis_size("tensor") != 4:
        return lax.psum(value, "tensor")
    value = value + lax.ppermute(value, "tensor", [(i, i ^ 1) for i in range(4)])
    return value + lax.ppermute(value, "tensor", [(i, i ^ 2) for i in range(4)])


def exact_total(value):
    for axis in ("tensor", "shard", "context"):
        count = lax.axis_size(axis)
        if count & (count - 1):
            value = lax.psum(value, axis)
            continue
        span = 1
        while span < count:
            value = value + lax.ppermute(value, axis, [(i, i ^ span) for i in range(count)])
            span *= 2
    return value


def chip_total(grad):
    f32 = jnp.float32
    shard = lax.axis_index("shard")
    mine = half_of(grad, shard)
    other = half_of(grad, 1 - shard)
    got = lax.ppermute(other.astype(jnp.bfloat16), "shard", [(0, 1), (1, 0)])
    return mine.astype(f32) + got.astype(f32)


def line_total(staged):
    return lax.psum_scatter(
        staged.astype(jnp.bfloat16), "context", scatter_dimension=0, tiled=True
    ).astype(jnp.float32)


def rows_total(grad):
    return line_total(chip_total(grad))


def pass_grads(grad_key, grad_value):
    return (
        passed_along(grad_key.astype(jnp.bfloat16), "context", 1).astype(grad_key.dtype),
        passed_along(grad_value.astype(jnp.bfloat16), "context", 1).astype(grad_value.dtype),
    )


def key_scores(query_heads, query_seg, query_pos, piece):
    key_flat, value_flat, key_seg, key_pos = piece
    heads = query_heads.shape[1]
    key_heads = key_flat.reshape(key_flat.shape[0], heads, HD)
    value_heads = value_flat.reshape(value_flat.shape[0], heads, HD)
    scores = jnp.einsum(
        "qhd,khd->hqk", query_heads, key_heads, preferred_element_type=jnp.float32
    ) * (1.0 / math.sqrt(HD))
    allowed = (query_seg[:, None] == key_seg[None, :]) & (key_pos[None, :] <= query_pos[:, None])
    return (jnp.where(allowed[None], scores, NEG), allowed, key_heads, value_heads)


def forward_fold(stats, piece, query_heads, query_seg, query_pos):
    peak, total, accum = stats
    scores, allowed, key_heads, value_heads = key_scores(query_heads, query_seg, query_pos, piece)
    new_peak = jnp.maximum(peak, jnp.max(scores, axis=-1))
    weights = jnp.where(allowed[None], jnp.exp(scores - new_peak[..., None]), 0.0)
    factor = jnp.exp(peak - new_peak)
    total = total * factor + jnp.sum(weights, axis=-1)
    accum = accum * factor[..., None] + jnp.einsum(
        "hqk,khd->hqd",
        weights.astype(jnp.bfloat16),
        value_heads,
        preferred_element_type=jnp.float32,
    )
    return (new_peak, total, accum)


def backward_piece(piece, query_heads, grad_heads, log_total, inner, query_seg, query_pos):
    scores, allowed, key_heads, value_heads = key_scores(query_heads, query_seg, query_pos, piece)
    probs = jnp.where(allowed[None], jnp.exp(scores - log_total[..., None]), 0.0)
    grad_value = jnp.einsum(
        "hqk,qhd->khd", probs.astype(jnp.bfloat16), grad_heads, preferred_element_type=jnp.float32
    )
    grad_probs = jnp.einsum(
        "qhd,khd->hqk", grad_heads, value_heads, preferred_element_type=jnp.float32
    )
    grad_scores = (probs * (grad_probs - inner[..., None]) * (1.0 / math.sqrt(HD))).astype(
        jnp.bfloat16
    )
    grad_query = jnp.einsum(
        "hqk,khd->qhd", grad_scores, key_heads, preferred_element_type=jnp.float32
    )
    grad_key = jnp.einsum(
        "hqk,qhd->khd", grad_scores, query_heads, preferred_element_type=jnp.float32
    )
    key_rows = grad_key.shape[0]
    return (grad_query, grad_key.reshape(key_rows, -1), grad_value.reshape(key_rows, -1))


class RingAttention:
    def __init__(self, query, key_flat, value_flat, segment, position, cosine, sine):
        self.query = query
        self.piece = (key_flat, value_flat, segment, position)
        self.segment = segment
        self.position = position
        self.cosine = cosine
        self.sine = sine

    def forward(self):
        f32 = jnp.float32
        query, segment, position = self.query, self.segment, self.position
        rows, heads = query.shape[0], query.shape[1]
        start_stats = (
            jnp.full((heads, rows), NEG, f32),
            jnp.zeros((heads, rows), f32),
            jnp.zeros((heads, rows, HD), f32),
        )
        stats = forward_fold(start_stats, self.piece, query, segment, position)

        def cycle_turn(index, carry):
            moving, current = carry
            moving = passed_along(moving, "context", 1)
            current = forward_fold(current, moving, query, segment, position)
            return (moving, current)

        peak, total, accum = lax.fori_loop(
            0, lax.axis_size("context") - 1, cycle_turn, (self.piece, stats)
        )[1]
        self.attended = jnp.transpose(accum / total[..., None], (1, 0, 2)).astype(jnp.bfloat16)
        self.log_total = peak + jnp.log(total)
        return self.attended

    def backward(self, grad_heads, early):
        bf16 = jnp.bfloat16
        query, segment, position = self.query, self.segment, self.position
        rows, heads = query.shape[0], query.shape[1]
        inner = jnp.sum(grad_heads.astype(jnp.float32) * self.attended.astype(jnp.float32), axis=-1).T

        def piece_grads(piece):
            return backward_piece(piece, query, grad_heads, self.log_total, inner, segment, position)

        grad_query, grad_key, grad_value = piece_grads(self.piece)

        def grad_turn(index, carry):
            moving, acc_query, acc_key, acc_value = carry
            moving = passed_along(moving, "context", 1)
            acc_key, acc_value = pass_grads(acc_key, acc_value)
            part_query, part_key, part_value = piece_grads(moving)
            return (moving, acc_query + part_query, acc_key + part_key, acc_value + part_value)

        carried = lax.fori_loop(
            0,
            lax.axis_size("context") - 1,
            grad_turn,
            (self.piece, grad_query, grad_key, grad_value),
        )
        grad_query = carried[1]
        grad_key, grad_value = pass_grads(carried[2], carried[3])
        grad_qin = rotate_back(grad_query, self.cosine, self.sine).astype(bf16)
        grad_kin = rotate_back(grad_key.reshape(rows, heads, HD), self.cosine, self.sine).astype(bf16)
        grad_vin = grad_value.astype(bf16).reshape(rows, heads, HD)
        return grad_qin, grad_kin, grad_vin, early


class HeadAttention:
    BLOCK = 512

    def __init__(self, query, key_heads, value_heads, segment, position, cosine, sine):
        ways = lax.axis_size("context")
        rows, heads = query.shape[0], query.shape[1]
        self.ways = ways
        self.rows = rows
        self.heads = heads
        self.group = heads // ways
        self.piece = rows // 2
        stacked = jnp.stack([query, key_heads, value_heads], axis=1)
        stacked = stacked.reshape(rows, 3, ways, self.group, HD)
        stacked = lax.all_to_all(stacked, "context", 2, 0, tiled=True)
        stacked = stacked.reshape(rows * ways, 3, self.group, HD)
        tags = jnp.stack([segment, position], axis=0)[None]
        tags = jnp.broadcast_to(tags, (ways, 2, rows))
        tags = lax.all_to_all(tags, "context", 0, 0, tiled=True)
        tags = jnp.transpose(tags, (1, 0, 2)).reshape(2, rows * ways)
        pieces = 2 * ways
        piece_of_slot = tags[1].reshape(pieces, self.piece)[:, 0] // self.piece
        slots = jnp.arange(pieces, dtype=jnp.int32)
        slot_of_piece = jnp.sum(
            jnp.where(piece_of_slot[None, :] == slots[:, None], slots[None, :], 0), axis=1
        )
        self.piece_of_slot = piece_of_slot
        self.slot_of_piece = slot_of_piece
        stacked = self._reorder(stacked, slot_of_piece)
        tags = self._reorder(tags.T, slot_of_piece).T
        self.query = stacked[:, 0]
        self.keys = stacked[:, 1]
        self.values = stacked[:, 2]
        self.seg_all = tags[0]
        self.pos_all = tags[1]
        self.cos_all, self.sin_all = rope_tables(self.pos_all)

    def _reorder(self, value, source):
        parts = [
            lax.dynamic_slice_in_dim(value, source[index] * self.piece, self.piece, axis=0)
            for index in range(source.shape[0])
        ]
        return jnp.concatenate(parts, axis=0)

    def _blocks(self):
        total = self.rows * self.ways
        block = min(self.BLOCK, total)
        return [(start, block) for start in range(0, total, block)]

    def _scores(self, start, size):
        reach = start + size
        query = self.query[start:reach]
        seg_q = self.seg_all[start:reach]
        pos_q = self.pos_all[start:reach]
        scores = jnp.einsum(
            "qhd,khd->hqk", query, self.keys[:reach], preferred_element_type=jnp.float32
        ) * (1.0 / math.sqrt(HD))
        allowed = (seg_q[:, None] == self.seg_all[None, :reach]) & (
            self.pos_all[None, :reach] <= pos_q[:, None]
        )
        return query, jnp.where(allowed[None], scores, NEG), allowed

    def forward(self):
        outs = []
        logs = []
        for start, size in self._blocks():
            reach = start + size
            _, scores, allowed = self._scores(start, size)
            peak = jnp.max(scores, axis=-1)
            weights = jnp.where(allowed[None], jnp.exp(scores - peak[..., None]), 0.0)
            total = jnp.sum(weights, axis=-1)
            mixed = jnp.einsum(
                "hqk,khd->qhd",
                weights.astype(jnp.bfloat16),
                self.values[:reach],
                preferred_element_type=jnp.float32,
            )
            outs.append((mixed / total.T[:, :, None]).astype(jnp.bfloat16))
            logs.append(peak + jnp.log(total))
        self.attended = jnp.concatenate(outs, axis=0)
        self.log_total = jnp.concatenate(logs, axis=1)
        back = self._reorder(self.attended, self.piece_of_slot)
        back = back.reshape(self.rows * self.ways, 1, self.group, HD)
        back = lax.all_to_all(back, "context", 0, 1, tiled=True)
        return back.reshape(self.rows, self.heads, HD)

    def backward(self, grad_heads, early):
        f32 = jnp.float32
        bf16 = jnp.bfloat16
        scale = 1.0 / math.sqrt(HD)
        grad = grad_heads.reshape(self.rows, self.ways, self.group, HD)
        grad = lax.all_to_all(grad, "context", 1, 0, tiled=True)
        grad, early = lax.optimization_barrier((grad, early))
        grad = grad.reshape(self.rows * self.ways, self.group, HD)
        grad = self._reorder(grad, self.slot_of_piece)
        inner = jnp.sum(grad.astype(f32) * self.attended.astype(f32), axis=-1).T
        total_rows = self.rows * self.ways
        grad_key = jnp.zeros(self.keys.shape, f32)
        grad_value = jnp.zeros(self.values.shape, f32)
        grad_queries = []
        for start, size in self._blocks():
            reach = start + size
            query, scores, allowed = self._scores(start, size)
            log_block = self.log_total[:, start:reach]
            inner_block = inner[:, start:reach]
            grad_block = grad[start:reach]
            probs = jnp.where(allowed[None], jnp.exp(scores - log_block[..., None]), 0.0)
            part_value = jnp.einsum(
                "hqk,qhd->khd", probs.astype(bf16), grad_block, preferred_element_type=f32
            )
            grad_probs = jnp.einsum(
                "qhd,khd->hqk", grad_block, self.values[:reach], preferred_element_type=f32
            )
            grad_scores = (probs * (grad_probs - inner_block[..., None]) * scale).astype(bf16)
            grad_queries.append(
                jnp.einsum(
                    "hqk,khd->qhd", grad_scores, self.keys[:reach], preferred_element_type=f32
                )
            )
            part_key = jnp.einsum("hqk,qhd->khd", grad_scores, query, preferred_element_type=f32)
            pad = ((0, total_rows - reach), (0, 0), (0, 0))
            grad_value = grad_value + jnp.pad(part_value, pad)
            grad_key = grad_key + jnp.pad(part_key, pad)
        grad_query = jnp.concatenate(grad_queries, axis=0)
        grad_qin = rotate_back(grad_query, self.cos_all, self.sin_all).astype(bf16)
        grad_kin = rotate_back(grad_key, self.cos_all, self.sin_all).astype(bf16)
        grad_vin = grad_value.astype(bf16)
        returned = []
        for grad_in in (grad_qin, grad_kin, grad_vin):
            grad_in = self._reorder(grad_in, self.piece_of_slot)
            grad_in = grad_in.reshape(self.rows * self.ways, 1, self.group, HD)
            grad_in = lax.all_to_all(grad_in, "context", 0, 1, tiled=True)
            returned.append(grad_in.reshape(self.rows, self.heads, HD))
        return returned[0], returned[1], returned[2], early


def mlp_chunks(hidden_cols):
    for count in (2, 1):
        if hidden_cols % (count * 128) == 0:
            return count
    return 1


def on_device(
    inputs, segments, positions, w_q, w_k, w_v, w_o, w_gate, w_up, w_down, g_attn, g_mlp, d_out
):
    f32 = jnp.float32
    bf16 = jnp.bfloat16
    rows = inputs.shape[1]
    width = inputs.shape[2]
    cols = w_q.shape[1]
    hidden_cols = w_gate.shape[1]
    tokens = inputs.reshape(rows, width)
    segment = segments.reshape(rows)
    position = positions.reshape(rows)
    full_qkvo = lax.all_gather(
        jnp.concatenate([w_q, w_k, w_v, w_o], axis=1), ROWS, axis=0, tiled=True
    )
    full_qkv = full_qkvo[:, : 3 * cols]
    full_o = full_qkvo[:, 3 * cols :]
    gains = lax.all_gather(
        jnp.concatenate([g_attn, g_mlp])[None], ROWS, axis=0, tiled=True
    )
    gain_attn = gains[:, : g_attn.shape[0]].reshape(width)
    gain_mlp = gains[:, g_attn.shape[0] :].reshape(width)
    count = mlp_chunks(hidden_cols)
    step = hidden_cols // count
    fetched = []
    for index in range(count):
        part = slice(index * step, (index + 1) * step)
        pair = lax.all_gather(
            jnp.concatenate([w_gate[:, part], w_up[:, part]], axis=1), ROWS, axis=0, tiled=True
        )
        fetched.append(
            (pair[:, :step], pair[:, step:], lax.all_gather(w_down[:, part], ROWS, axis=0, tiled=True))
        )
    heads = cols // HD
    cosine, sine = rope_tables(position)
    resid1 = tokens.astype(f32)
    norm1, inv1 = normalize(resid1)
    h1 = (norm1 * gain_attn.astype(f32)).astype(bf16)
    projected = jnp.dot(h1, full_qkv, preferred_element_type=f32)
    query = rotate(projected[:, :cols].reshape(rows, heads, HD), cosine, sine).astype(bf16)
    key_heads = rotate(projected[:, cols : 2 * cols].reshape(rows, heads, HD), cosine, sine).astype(
        bf16
    )
    value_heads = projected[:, 2 * cols :].astype(bf16).reshape(rows, heads, HD)
    if heads % lax.axis_size("context") == 0:
        attention = HeadAttention(query, key_heads, value_heads, segment, position, cosine, sine)
    else:
        attention = RingAttention(
            query,
            key_heads.reshape(rows, cols),
            value_heads.reshape(rows, cols),
            segment,
            position,
            cosine,
            sine,
        )
    attended = attention.forward()
    attended_flat = attended.reshape(rows, cols)
    resid2 = resid1 + tensor_total(contract_last(attended_flat, full_o))
    norm2, inv2 = normalize(resid2)
    h2_part = (norm2 * gain_mlp.astype(f32)).astype(bf16)
    grad_y = d_out.reshape(rows, width)
    mlp_partial = None
    h2_grad_partial = None
    staged = []
    for full_gate, full_up, full_down in fetched:
        if staged:
            full_gate, staged[-1] = lax.optimization_barrier((full_gate, staged[-1]))
        gate = jnp.dot(h2_part, full_gate, preferred_element_type=f32)
        up = jnp.dot(h2_part, full_up, preferred_element_type=f32)
        active = jax.nn.silu(gate)
        hidden = (active * up).astype(bf16)
        out_part = contract_last(hidden, full_down)
        mlp_partial = out_part if mlp_partial is None else mlp_partial + out_part
        grad_hidden = jnp.dot(grad_y, full_down, preferred_element_type=f32)
        sigma = jax.nn.sigmoid(gate)
        grad_gate = (grad_hidden * up * sigma * (1.0 + gate * (1.0 - sigma))).astype(bf16)
        grad_up = (grad_hidden * active).astype(bf16)
        back_part = contract_last(grad_gate, full_gate) + contract_last(grad_up, full_up)
        pending = (
            contract_first(h2_part, grad_gate),
            contract_first(h2_part, grad_up),
            contract_first(grad_y, hidden),
        )
        h2_grad_partial = back_part if h2_grad_partial is None else h2_grad_partial + back_part
        staged.append(chip_total(jnp.concatenate(pending, axis=1)))
    grad_h2 = tensor_total(h2_grad_partial)
    grad_h2, staged[-1] = lax.optimization_barrier((grad_h2, staged[-1]))
    reduced = [line_total(chunk) for chunk in staged]
    grad_gmlp = jnp.sum(grad_h2 * norm2, axis=0)
    grad_resid = grad_y.astype(f32) + norm_back(grad_h2, norm2, inv2, gain_mlp)
    grad_resid_part = grad_resid.astype(bf16)
    grad_heads = (
        jnp.dot(grad_resid_part, full_o, preferred_element_type=f32)
        .astype(bf16)
        .reshape(rows, heads, HD)
    )
    grad_heads, partial_o = lax.optimization_barrier(
        (grad_heads, contract_first(grad_resid_part, attended_flat))
    )
    early = (chip_total(partial_o), reduced[:-1], mlp_partial)
    grad_qin, grad_kin, grad_vin, early = attention.backward(grad_heads, early)
    staged_o, reduced[:-1], mlp_partial = early
    result = (resid2 + tensor_total(mlp_partial)).astype(bf16)
    reduced_o = line_total(staged_o)
    grad_qkv = jnp.concatenate(
        [grad_qin.reshape(rows, cols), grad_kin.reshape(rows, cols), grad_vin.reshape(rows, cols)],
        axis=1,
    )
    h1_grad_partial = contract_last(grad_qkv, full_qkv)
    first_tensor = (lax.axis_index("tensor") == 0).astype(f32)
    gain_parts = jnp.stack(
        [jnp.sum(h1_grad_partial * norm1, axis=0), grad_gmlp * first_tensor], axis=1
    )
    gains_total = exact_total(gain_parts)
    h1_grad_partial, staged_qkv = lax.optimization_barrier(
        (h1_grad_partial, chip_total(contract_first(h1, grad_qkv)))
    )
    grad_h1 = tensor_total(h1_grad_partial)
    grad_h1, reduced_o, reduced[-1], result = lax.optimization_barrier(
        (grad_h1, reduced_o, reduced[-1], result)
    )
    grad_x_part = (grad_resid + norm_back(grad_h1, norm1, inv1, gain_attn)).astype(bf16)
    reduced_qkv = line_total(staged_qkv)
    blocks = lax.axis_size("shard") * lax.axis_size("context")
    block = lax.axis_index("shard") * lax.axis_size("context") + lax.axis_index("context")
    piece = width // blocks
    reduced_gains = lax.dynamic_slice_in_dim(gains_total, block * piece, piece, axis=0)
    reduced_gate, reduced_up, reduced_down = (
        jnp.concatenate([chunk[:, which * step : (which + 1) * step] for chunk in reduced], axis=1)
        for which in range(3)
    )
    return (
        result.reshape(1, rows, width),
        grad_x_part.reshape(1, rows, width),
        reduced_qkv[:, :cols],
        reduced_qkv[:, cols : 2 * cols],
        reduced_qkv[:, 2 * cols :],
        reduced_o,
        reduced_gate,
        reduced_up,
        reduced_down,
        reduced_gains[:, 0],
        reduced_gains[:, 1],
    )


def solution(mesh):
    placed = (
        P("shard", "context", None),
        P("shard", "context"),
        P("shard", "context"),
        P(ROWS, "tensor"),
        P(ROWS, "tensor"),
        P(ROWS, "tensor"),
        P(ROWS, "tensor"),
        P(ROWS, "tensor"),
        P(ROWS, "tensor"),
        P(ROWS, "tensor"),
        P(ROWS),
        P(ROWS),
        P("shard", "context", None),
    )
    return jax.shard_map(
        on_device,
        mesh=mesh,
        in_specs=placed,
        out_specs=(
            P("shard", "context", None),
            P("shard", "context", None),
            P(ROWS, "tensor"),
            P(ROWS, "tensor"),
            P(ROWS, "tensor"),
            P(ROWS, "tensor"),
            P(ROWS, "tensor"),
            P(ROWS, "tensor"),
            P(ROWS, "tensor"),
            P(ROWS),
            P(ROWS),
        ),
        check_vma=False,
    )
```

```python
import math

import jax
import jax.numpy as jnp
from jax import lax
from jax.sharding import PartitionSpec as P

HD = 64


EPS = 1e-05
THETA = 130000.0
NEG = -1e30
ROWS = ("shard", "context")


def passed_along(value, axis, steps):
    count = lax.axis_size(axis)
    pairs = [(source, (source + steps) % count) for source in range(count)]
    return lax.ppermute(value, axis, pairs)


def rope_tables(position):
    index = jnp.arange(HD // 2, dtype=jnp.float32)
    inverse = jnp.power(jnp.float32(THETA), -2.0 * index / HD)
    angle = position.astype(jnp.float32)[:, None] * inverse[None, :]
    return (jnp.cos(angle), jnp.sin(angle))


def rotate(tensor, cosine, sine):
    half = tensor.shape[-1] // 2
    first = tensor[..., :half]
    second = tensor[..., half:]
    cosine = cosine[:, None, :]
    sine = sine[:, None, :]
    return jnp.concatenate(
        [first * cosine - second * sine, second * cosine + first * sine], axis=-1
    )


def rotate_back(grad, cosine, sine):
    half = grad.shape[-1] // 2
    first = grad[..., :half]
    second = grad[..., half:]
    cosine = cosine[:, None, :]
    sine = sine[:, None, :]
    return jnp.concatenate(
        [first * cosine + second * sine, second * cosine - first * sine], axis=-1
    )


def normalize(value):
    inv_rms = lax.rsqrt(jnp.mean(value * value, axis=-1, keepdims=True) + EPS)
    return (value * inv_rms, inv_rms)


def norm_back(grad, normed, inv_rms, gain):
    scaled = grad * gain.astype(jnp.float32)
    return inv_rms * (scaled - normed * jnp.mean(scaled * normed, axis=-1, keepdims=True))


def contract_last(left, right):
    return lax.dot_general(
        left, right, (((1,), (1,)), ((), ())), preferred_element_type=jnp.float32
    )


def contract_first(left, right):
    return lax.dot_general(
        left, right, (((0,), (0,)), ((), ())), preferred_element_type=jnp.float32
    )


def half_of(value, bit):
    size = value.shape[0] // 2
    return lax.dynamic_slice_in_dim(value, bit * size, size, axis=0)


def joined(mine, other, bit):
    low = jnp.where(bit == 0, mine, other)
    high = jnp.where(bit == 0, other, mine)
    return jnp.concatenate([low, high], axis=0)


def tensor_total(partial_sum):
    count = lax.axis_size("tensor")
    rows = partial_sum.shape[0]
    if count != 4 or rows % 8:
        return lax.psum(partial_sum.astype(jnp.bfloat16), "tensor").astype(jnp.float32)
    f32 = jnp.float32
    bf16 = jnp.bfloat16
    index = lax.axis_index("tensor")
    x_bit = index % 2
    y_bit = index // 2
    x_pairs = [(i, i ^ 1) for i in range(4)]
    y_pairs = [(i, i ^ 2) for i in range(4)]

    def swap(value, pairs):
        return lax.ppermute(value.astype(bf16), "tensor", pairs).astype(f32)

    first = partial_sum[: rows // 2]
    second = partial_sum[rows // 2 :]
    first = half_of(first, x_bit) + swap(half_of(first, 1 - x_bit), x_pairs)
    second = half_of(second, y_bit) + swap(half_of(second, 1 - y_bit), y_pairs)
    first = half_of(first, y_bit) + swap(half_of(first, 1 - y_bit), y_pairs)
    second = half_of(second, x_bit) + swap(half_of(second, 1 - x_bit), x_pairs)
    first = first.astype(bf16)
    second = second.astype(bf16)
    first = joined(first, lax.ppermute(first, "tensor", y_pairs), y_bit)
    second = joined(second, lax.ppermute(second, "tensor", x_pairs), x_bit)
    first = joined(first, lax.ppermute(first, "tensor", x_pairs), x_bit)
    second = joined(second, lax.ppermute(second, "tensor", y_pairs), y_bit)
    return jnp.concatenate([first, second], axis=0).astype(f32)


def tensor_exact_total(value):
    if lax.axis_size("tensor") != 4:
        return lax.psum(value, "tensor")
    value = value + lax.ppermute(value, "tensor", [(i, i ^ 1) for i in range(4)])
    return value + lax.ppermute(value, "tensor", [(i, i ^ 2) for i in range(4)])


def exact_total(value):
    for axis in ("tensor", "shard", "context"):
        count = lax.axis_size(axis)
        if count & (count - 1):
            value = lax.psum(value, axis)
            continue
        span = 1
        while span < count:
            value = value + lax.ppermute(value, axis, [(i, i ^ span) for i in range(count)])
            span *= 2
    return value


def chip_total(grad):
    f32 = jnp.float32
    shard = lax.axis_index("shard")
    mine = half_of(grad, shard)
    other = half_of(grad, 1 - shard)
    got = lax.ppermute(other.astype(jnp.bfloat16), "shard", [(0, 1), (1, 0)])
    return mine.astype(f32) + got.astype(f32)


def line_total(staged):
    return lax.psum_scatter(
        staged.astype(jnp.bfloat16), "context", scatter_dimension=0, tiled=True
    ).astype(jnp.float32)


def rows_total(grad):
    return line_total(chip_total(grad))


def pass_grads(grad_key, grad_value):
    return (
        passed_along(grad_key.astype(jnp.bfloat16), "context", 1).astype(grad_key.dtype),
        passed_along(grad_value.astype(jnp.bfloat16), "context", 1).astype(grad_value.dtype),
    )


def key_scores(query_heads, query_seg, query_pos, piece):
    key_flat, value_flat, key_seg, key_pos = piece
    heads = query_heads.shape[1]
    key_heads = key_flat.reshape(key_flat.shape[0], heads, HD)
    value_heads = value_flat.reshape(value_flat.shape[0], heads, HD)
    scores = jnp.einsum(
        "qhd,khd->hqk", query_heads, key_heads, preferred_element_type=jnp.float32
    ) * (1.0 / math.sqrt(HD))
    allowed = (query_seg[:, None] == key_seg[None, :]) & (key_pos[None, :] <= query_pos[:, None])
    return (jnp.where(allowed[None], scores, NEG), allowed, key_heads, value_heads)


def forward_fold(stats, piece, query_heads, query_seg, query_pos):
    peak, total, accum = stats
    scores, allowed, key_heads, value_heads = key_scores(query_heads, query_seg, query_pos, piece)
    new_peak = jnp.maximum(peak, jnp.max(scores, axis=-1))
    weights = jnp.where(allowed[None], jnp.exp(scores - new_peak[..., None]), 0.0)
    factor = jnp.exp(peak - new_peak)
    total = total * factor + jnp.sum(weights, axis=-1)
    accum = accum * factor[..., None] + jnp.einsum(
        "hqk,khd->hqd",
        weights.astype(jnp.bfloat16),
        value_heads,
        preferred_element_type=jnp.float32,
    )
    return (new_peak, total, accum)


def backward_piece(piece, query_heads, grad_heads, log_total, inner, query_seg, query_pos):
    scores, allowed, key_heads, value_heads = key_scores(query_heads, query_seg, query_pos, piece)
    probs = jnp.where(allowed[None], jnp.exp(scores - log_total[..., None]), 0.0)
    grad_value = jnp.einsum(
        "hqk,qhd->khd", probs.astype(jnp.bfloat16), grad_heads, preferred_element_type=jnp.float32
    )
    grad_probs = jnp.einsum(
        "qhd,khd->hqk", grad_heads, value_heads, preferred_element_type=jnp.float32
    )
    grad_scores = (probs * (grad_probs - inner[..., None]) * (1.0 / math.sqrt(HD))).astype(
        jnp.bfloat16
    )
    grad_query = jnp.einsum(
        "hqk,khd->qhd", grad_scores, key_heads, preferred_element_type=jnp.float32
    )
    grad_key = jnp.einsum(
        "hqk,qhd->khd", grad_scores, query_heads, preferred_element_type=jnp.float32
    )
    key_rows = grad_key.shape[0]
    return (grad_query, grad_key.reshape(key_rows, -1), grad_value.reshape(key_rows, -1))


class RingAttention:
    def __init__(self, query, key_flat, value_flat, segment, position, cosine, sine):
        self.query = query
        self.piece = (key_flat, value_flat, segment, position)
        self.segment = segment
        self.position = position
        self.cosine = cosine
        self.sine = sine

    def forward(self):
        f32 = jnp.float32
        query, segment, position = self.query, self.segment, self.position
        rows, heads = query.shape[0], query.shape[1]
        start_stats = (
            jnp.full((heads, rows), NEG, f32),
            jnp.zeros((heads, rows), f32),
            jnp.zeros((heads, rows, HD), f32),
        )
        stats = forward_fold(start_stats, self.piece, query, segment, position)

        def cycle_turn(index, carry):
            moving, current = carry
            moving = passed_along(moving, "context", 1)
            current = forward_fold(current, moving, query, segment, position)
            return (moving, current)

        peak, total, accum = lax.fori_loop(
            0, lax.axis_size("context") - 1, cycle_turn, (self.piece, stats)
        )[1]
        self.attended = jnp.transpose(accum / total[..., None], (1, 0, 2)).astype(jnp.bfloat16)
        self.log_total = peak + jnp.log(total)
        return self.attended

    def backward(self, grad_heads, early):
        bf16 = jnp.bfloat16
        query, segment, position = self.query, self.segment, self.position
        rows, heads = query.shape[0], query.shape[1]
        inner = jnp.sum(grad_heads.astype(jnp.float32) * self.attended.astype(jnp.float32), axis=-1).T

        def piece_grads(piece):
            return backward_piece(piece, query, grad_heads, self.log_total, inner, segment, position)

        grad_query, grad_key, grad_value = piece_grads(self.piece)

        def grad_turn(index, carry):
            moving, acc_query, acc_key, acc_value = carry
            moving = passed_along(moving, "context", 1)
            acc_key, acc_value = pass_grads(acc_key, acc_value)
            part_query, part_key, part_value = piece_grads(moving)
            return (moving, acc_query + part_query, acc_key + part_key, acc_value + part_value)

        carried = lax.fori_loop(
            0,
            lax.axis_size("context") - 1,
            grad_turn,
            (self.piece, grad_query, grad_key, grad_value),
        )
        grad_query = carried[1]
        grad_key, grad_value = pass_grads(carried[2], carried[3])
        grad_qin = rotate_back(grad_query, self.cosine, self.sine).astype(bf16)
        grad_kin = rotate_back(grad_key.reshape(rows, heads, HD), self.cosine, self.sine).astype(bf16)
        grad_vin = grad_value.astype(bf16).reshape(rows, heads, HD)
        return grad_qin, grad_kin, grad_vin, early


class HeadAttention:
    BLOCK = 512

    def __init__(self, query, key_heads, value_heads, segment, position, cosine, sine):
        ways = lax.axis_size("context")
        rows, heads = query.shape[0], query.shape[1]
        self.ways = ways
        self.rows = rows
        self.heads = heads
        self.group = heads // ways
        self.piece = rows // 2
        stacked = jnp.stack([query, key_heads, value_heads], axis=1)
        stacked = stacked.reshape(rows, 3, ways, self.group, HD)
        stacked = lax.all_to_all(stacked, "context", 2, 0, tiled=True)
        stacked = stacked.reshape(rows * ways, 3, self.group, HD)
        tags = jnp.stack([segment, position], axis=0)[None]
        tags = jnp.broadcast_to(tags, (ways, 2, rows))
        tags = lax.all_to_all(tags, "context", 0, 0, tiled=True)
        tags = jnp.transpose(tags, (1, 0, 2)).reshape(2, rows * ways)
        pieces = 2 * ways
        piece_of_slot = tags[1].reshape(pieces, self.piece)[:, 0] // self.piece
        slots = jnp.arange(pieces, dtype=jnp.int32)
        slot_of_piece = jnp.sum(
            jnp.where(piece_of_slot[None, :] == slots[:, None], slots[None, :], 0), axis=1
        )
        self.piece_of_slot = piece_of_slot
        self.slot_of_piece = slot_of_piece
        stacked = self._reorder(stacked, slot_of_piece)
        tags = self._reorder(tags.T, slot_of_piece).T
        self.query = stacked[:, 0]
        self.keys = stacked[:, 1]
        self.values = stacked[:, 2]
        self.seg_all = tags[0]
        self.pos_all = tags[1]
        self.cos_all, self.sin_all = rope_tables(self.pos_all)

    def _reorder(self, value, source):
        parts = [
            lax.dynamic_slice_in_dim(value, source[index] * self.piece, self.piece, axis=0)
            for index in range(source.shape[0])
        ]
        return jnp.concatenate(parts, axis=0)

    def _blocks(self):
        total = self.rows * self.ways
        block = min(self.BLOCK, total)
        return [(start, block) for start in range(0, total, block)]

    def _scores(self, start, size):
        reach = start + size
        query = self.query[start:reach]
        seg_q = self.seg_all[start:reach]
        pos_q = self.pos_all[start:reach]
        scores = jnp.einsum(
            "qhd,khd->hqk", query, self.keys[:reach], preferred_element_type=jnp.float32
        ) * (1.0 / math.sqrt(HD))
        allowed = (seg_q[:, None] == self.seg_all[None, :reach]) & (
            self.pos_all[None, :reach] <= pos_q[:, None]
        )
        return query, jnp.where(allowed[None], scores, NEG), allowed

    def forward(self):
        outs = []
        logs = []
        for start, size in self._blocks():
            reach = start + size
            _, scores, allowed = self._scores(start, size)
            peak = jnp.max(scores, axis=-1)
            weights = jnp.where(allowed[None], jnp.exp(scores - peak[..., None]), 0.0)
            total = jnp.sum(weights, axis=-1)
            mixed = jnp.einsum(
                "hqk,khd->qhd",
                weights.astype(jnp.bfloat16),
                self.values[:reach],
                preferred_element_type=jnp.float32,
            )
            outs.append((mixed / total.T[:, :, None]).astype(jnp.bfloat16))
            logs.append(peak + jnp.log(total))
        self.attended = jnp.concatenate(outs, axis=0)
        self.log_total = jnp.concatenate(logs, axis=1)
        back = self._reorder(self.attended, self.piece_of_slot)
        back = back.reshape(self.rows * self.ways, 1, self.group, HD)
        back = lax.all_to_all(back, "context", 0, 1, tiled=True)
        return back.reshape(self.rows, self.heads, HD)

    def backward(self, grad_heads, early):
        f32 = jnp.float32
        bf16 = jnp.bfloat16
        scale = 1.0 / math.sqrt(HD)
        grad = grad_heads.reshape(self.rows, self.ways, self.group, HD)
        grad = lax.all_to_all(grad, "context", 1, 0, tiled=True)
        grad, early = lax.optimization_barrier((grad, early))
        grad = grad.reshape(self.rows * self.ways, self.group, HD)
        grad = self._reorder(grad, self.slot_of_piece)
        inner = jnp.sum(grad.astype(f32) * self.attended.astype(f32), axis=-1).T
        total_rows = self.rows * self.ways
        grad_key = jnp.zeros(self.keys.shape, f32)
        grad_value = jnp.zeros(self.values.shape, f32)
        grad_queries = []
        for start, size in self._blocks():
            reach = start + size
            query, scores, allowed = self._scores(start, size)
            log_block = self.log_total[:, start:reach]
            inner_block = inner[:, start:reach]
            grad_block = grad[start:reach]
            probs = jnp.where(allowed[None], jnp.exp(scores - log_block[..., None]), 0.0)
            part_value = jnp.einsum(
                "hqk,qhd->khd", probs.astype(bf16), grad_block, preferred_element_type=f32
            )
            grad_probs = jnp.einsum(
                "qhd,khd->hqk", grad_block, self.values[:reach], preferred_element_type=f32
            )
            grad_scores = (probs * (grad_probs - inner_block[..., None]) * scale).astype(bf16)
            grad_queries.append(
                jnp.einsum(
                    "hqk,khd->qhd", grad_scores, self.keys[:reach], preferred_element_type=f32
                )
            )
            part_key = jnp.einsum("hqk,qhd->khd", grad_scores, query, preferred_element_type=f32)
            pad = ((0, total_rows - reach), (0, 0), (0, 0))
            grad_value = grad_value + jnp.pad(part_value, pad)
            grad_key = grad_key + jnp.pad(part_key, pad)
        grad_query = jnp.concatenate(grad_queries, axis=0)
        grad_qin = rotate_back(grad_query, self.cos_all, self.sin_all).astype(bf16)
        grad_kin = rotate_back(grad_key, self.cos_all, self.sin_all).astype(bf16)
        grad_vin = grad_value.astype(bf16)
        returned = []
        for grad_in in (grad_qin, grad_kin, grad_vin):
            grad_in = self._reorder(grad_in, self.piece_of_slot)
            grad_in = grad_in.reshape(self.rows * self.ways, 1, self.group, HD)
            grad_in = lax.all_to_all(grad_in, "context", 0, 1, tiled=True)
            returned.append(grad_in.reshape(self.rows, self.heads, HD))
        return returned[0], returned[1], returned[2], early


def mlp_chunks(hidden_cols):
    for count in (2, 1):
        if hidden_cols % (count * 128) == 0:
            return count
    return 1


def on_device(
    inputs, segments, positions, w_q, w_k, w_v, w_o, w_gate, w_up, w_down, g_attn, g_mlp, d_out
):
    f32 = jnp.float32
    bf16 = jnp.bfloat16
    rows = inputs.shape[1]
    width = inputs.shape[2]
    cols = w_q.shape[1]
    hidden_cols = w_gate.shape[1]
    tokens = inputs.reshape(rows, width)
    segment = segments.reshape(rows)
    position = positions.reshape(rows)
    full_qkvo = lax.all_gather(
        jnp.concatenate([w_q, w_k, w_v, w_o], axis=1), ROWS, axis=0, tiled=True
    )
    full_qkv = full_qkvo[:, : 3 * cols]
    full_o = full_qkvo[:, 3 * cols :]
    gains = lax.all_gather(
        jnp.concatenate([g_attn, g_mlp])[None], ROWS, axis=0, tiled=True
    )
    gain_attn = gains[:, : g_attn.shape[0]].reshape(width)
    gain_mlp = gains[:, g_attn.shape[0] :].reshape(width)
    count = mlp_chunks(hidden_cols)
    step = hidden_cols // count
    fetched = []
    for index in range(count):
        part = slice(index * step, (index + 1) * step)
        pair = lax.all_gather(
            jnp.concatenate([w_gate[:, part], w_up[:, part]], axis=1), ROWS, axis=0, tiled=True
        )
        fetched.append(
            (pair[:, :step], pair[:, step:], lax.all_gather(w_down[:, part], ROWS, axis=0, tiled=True))
        )
    heads = cols // HD
    cosine, sine = rope_tables(position)
    resid1 = tokens.astype(f32)
    norm1, inv1 = normalize(resid1)
    h1 = (norm1 * gain_attn.astype(f32)).astype(bf16)
    projected = jnp.dot(h1, full_qkv, preferred_element_type=f32)
    query = rotate(projected[:, :cols].reshape(rows, heads, HD), cosine, sine).astype(bf16)
    key_heads = rotate(projected[:, cols : 2 * cols].reshape(rows, heads, HD), cosine, sine).astype(
        bf16
    )
    value_heads = projected[:, 2 * cols :].astype(bf16).reshape(rows, heads, HD)
    if heads % lax.axis_size("context") == 0:
        attention = HeadAttention(query, key_heads, value_heads, segment, position, cosine, sine)
    else:
        attention = RingAttention(
            query,
            key_heads.reshape(rows, cols),
            value_heads.reshape(rows, cols),
            segment,
            position,
            cosine,
            sine,
        )
    attended = attention.forward()
    attended_flat = attended.reshape(rows, cols)
    resid2 = resid1 + tensor_total(contract_last(attended_flat, full_o))
    norm2, inv2 = normalize(resid2)
    h2_part = (norm2 * gain_mlp.astype(f32)).astype(bf16)
    grad_y = d_out.reshape(rows, width)
    mlp_partial = None
    h2_grad_partial = None
    staged = []
    for full_gate, full_up, full_down in fetched:
        if staged:
            full_gate, staged[-1] = lax.optimization_barrier((full_gate, staged[-1]))
        gate = jnp.dot(h2_part, full_gate, preferred_element_type=f32)
        up = jnp.dot(h2_part, full_up, preferred_element_type=f32)
        active = jax.nn.silu(gate)
        hidden = (active * up).astype(bf16)
        out_part = contract_last(hidden, full_down)
        mlp_partial = out_part if mlp_partial is None else mlp_partial + out_part
        grad_hidden = jnp.dot(grad_y, full_down, preferred_element_type=f32)
        sigma = jax.nn.sigmoid(gate)
        grad_gate = (grad_hidden * up * sigma * (1.0 + gate * (1.0 - sigma))).astype(bf16)
        grad_up = (grad_hidden * active).astype(bf16)
        back_part = contract_last(grad_gate, full_gate) + contract_last(grad_up, full_up)
        pending = (
            contract_first(h2_part, grad_gate),
            contract_first(h2_part, grad_up),
            contract_first(grad_y, hidden),
        )
        h2_grad_partial = back_part if h2_grad_partial is None else h2_grad_partial + back_part
        staged.append(chip_total(jnp.concatenate(pending, axis=1)))
    grad_h2 = tensor_total(h2_grad_partial)
    grad_h2, staged[-1] = lax.optimization_barrier((grad_h2, staged[-1]))
    reduced = [line_total(chunk) for chunk in staged]
    result = (resid2 + tensor_total(mlp_partial)).astype(bf16)
    grad_gmlp = jnp.sum(grad_h2 * norm2, axis=0)
    grad_resid = grad_y.astype(f32) + norm_back(grad_h2, norm2, inv2, gain_mlp)
    grad_resid_part = grad_resid.astype(bf16)
    grad_heads = (
        jnp.dot(grad_resid_part, full_o, preferred_element_type=f32)
        .astype(bf16)
        .reshape(rows, heads, HD)
    )
    grad_heads, partial_o = lax.optimization_barrier(
        (grad_heads, contract_first(grad_resid_part, attended_flat))
    )
    early = (chip_total(partial_o), reduced[:-1])
    grad_qin, grad_kin, grad_vin, early = attention.backward(grad_heads, early)
    staged_o, reduced[:-1] = early
    reduced_o = line_total(staged_o)
    grad_qkv = jnp.concatenate(
        [grad_qin.reshape(rows, cols), grad_kin.reshape(rows, cols), grad_vin.reshape(rows, cols)],
        axis=1,
    )
    h1_grad_partial = contract_last(grad_qkv, full_qkv)
    first_tensor = (lax.axis_index("tensor") == 0).astype(f32)
    gain_parts = jnp.stack(
        [jnp.sum(h1_grad_partial * norm1, axis=0), grad_gmlp * first_tensor], axis=1
    )
    gains_total = exact_total(gain_parts)
    h1_grad_partial, staged_qkv = lax.optimization_barrier(
        (h1_grad_partial, chip_total(contract_first(h1, grad_qkv)))
    )
    grad_h1 = tensor_total(h1_grad_partial)
    reduced_gate, reduced_up, reduced_down = (
        jnp.concatenate([chunk[:, which * step : (which + 1) * step] for chunk in reduced], axis=1)
        for which in range(3)
    )
    grad_h1, reduced_o, result, reduced_gate, reduced_up, reduced_down = lax.optimization_barrier(
        (grad_h1, reduced_o, result, reduced_gate, reduced_up, reduced_down)
    )
    grad_x_part = (grad_resid + norm_back(grad_h1, norm1, inv1, gain_attn)).astype(bf16)
    reduced_qkv = line_total(staged_qkv)
    blocks = lax.axis_size("shard") * lax.axis_size("context")
    block = lax.axis_index("shard") * lax.axis_size("context") + lax.axis_index("context")
    piece = width // blocks
    reduced_gains = lax.dynamic_slice_in_dim(gains_total, block * piece, piece, axis=0)
    return (
        result.reshape(1, rows, width),
        grad_x_part.reshape(1, rows, width),
        reduced_qkv[:, :cols],
        reduced_qkv[:, cols : 2 * cols],
        reduced_qkv[:, 2 * cols :],
        reduced_o,
        reduced_gate,
        reduced_up,
        reduced_down,
        reduced_gains[:, 0],
        reduced_gains[:, 1],
    )


def solution(mesh):
    placed = (
        P("shard", "context", None),
        P("shard", "context"),
        P("shard", "context"),
        P(ROWS, "tensor"),
        P(ROWS, "tensor"),
        P(ROWS, "tensor"),
        P(ROWS, "tensor"),
        P(ROWS, "tensor"),
        P(ROWS, "tensor"),
        P(ROWS, "tensor"),
        P(ROWS),
        P(ROWS),
        P("shard", "context", None),
    )
    return jax.shard_map(
        on_device,
        mesh=mesh,
        in_specs=placed,
        out_specs=(
            P("shard", "context", None),
            P("shard", "context", None),
            P(ROWS, "tensor"),
            P(ROWS, "tensor"),
            P(ROWS, "tensor"),
            P(ROWS, "tensor"),
            P(ROWS, "tensor"),
            P(ROWS, "tensor"),
            P(ROWS, "tensor"),
            P(ROWS),
            P(ROWS),
        ),
        check_vma=False,
    )
```

```python
import math

import jax
import jax.numpy as jnp
from jax import lax
from jax.sharding import PartitionSpec as P

HD = 64


EPS = 1e-05
THETA = 130000.0
NEG = -1e30
ROWS = ("shard", "context")


def passed_along(value, axis, steps):
    count = lax.axis_size(axis)
    pairs = [(source, (source + steps) % count) for source in range(count)]
    return lax.ppermute(value, axis, pairs)


def rope_tables(position):
    index = jnp.arange(HD // 2, dtype=jnp.float32)
    inverse = jnp.power(jnp.float32(THETA), -2.0 * index / HD)
    angle = position.astype(jnp.float32)[:, None] * inverse[None, :]
    return (jnp.cos(angle), jnp.sin(angle))


def rotate(tensor, cosine, sine):
    half = tensor.shape[-1] // 2
    first = tensor[..., :half]
    second = tensor[..., half:]
    cosine = cosine[:, None, :]
    sine = sine[:, None, :]
    return jnp.concatenate(
        [first * cosine - second * sine, second * cosine + first * sine], axis=-1
    )


def rotate_back(grad, cosine, sine):
    half = grad.shape[-1] // 2
    first = grad[..., :half]
    second = grad[..., half:]
    cosine = cosine[:, None, :]
    sine = sine[:, None, :]
    return jnp.concatenate(
        [first * cosine + second * sine, second * cosine - first * sine], axis=-1
    )


def normalize(value):
    inv_rms = lax.rsqrt(jnp.mean(value * value, axis=-1, keepdims=True) + EPS)
    return (value * inv_rms, inv_rms)


def norm_back(grad, normed, inv_rms, gain):
    scaled = grad * gain.astype(jnp.float32)
    return inv_rms * (scaled - normed * jnp.mean(scaled * normed, axis=-1, keepdims=True))


def contract_last(left, right):
    return lax.dot_general(
        left, right, (((1,), (1,)), ((), ())), preferred_element_type=jnp.float32
    )


def contract_first(left, right):
    return lax.dot_general(
        left, right, (((0,), (0,)), ((), ())), preferred_element_type=jnp.float32
    )


def half_of(value, bit):
    size = value.shape[0] // 2
    return lax.dynamic_slice_in_dim(value, bit * size, size, axis=0)


def joined(mine, other, bit):
    low = jnp.where(bit == 0, mine, other)
    high = jnp.where(bit == 0, other, mine)
    return jnp.concatenate([low, high], axis=0)


def tensor_total(partial_sum):
    count = lax.axis_size("tensor")
    rows = partial_sum.shape[0]
    if count != 4 or rows % 8:
        return lax.psum(partial_sum.astype(jnp.bfloat16), "tensor").astype(jnp.float32)
    f32 = jnp.float32
    bf16 = jnp.bfloat16
    index = lax.axis_index("tensor")
    x_bit = index % 2
    y_bit = index // 2
    x_pairs = [(i, i ^ 1) for i in range(4)]
    y_pairs = [(i, i ^ 2) for i in range(4)]

    def swap(value, pairs):
        return lax.ppermute(value.astype(bf16), "tensor", pairs).astype(f32)

    first = partial_sum[: rows // 2]
    second = partial_sum[rows // 2 :]
    first = half_of(first, x_bit) + swap(half_of(first, 1 - x_bit), x_pairs)
    second = half_of(second, y_bit) + swap(half_of(second, 1 - y_bit), y_pairs)
    first = half_of(first, y_bit) + swap(half_of(first, 1 - y_bit), y_pairs)
    second = half_of(second, x_bit) + swap(half_of(second, 1 - x_bit), x_pairs)
    first = first.astype(bf16)
    second = second.astype(bf16)
    first = joined(first, lax.ppermute(first, "tensor", y_pairs), y_bit)
    second = joined(second, lax.ppermute(second, "tensor", x_pairs), x_bit)
    first = joined(first, lax.ppermute(first, "tensor", x_pairs), x_bit)
    second = joined(second, lax.ppermute(second, "tensor", y_pairs), y_bit)
    return jnp.concatenate([first, second], axis=0).astype(f32)


def tensor_exact_total(value):
    if lax.axis_size("tensor") != 4:
        return lax.psum(value, "tensor")
    value = value + lax.ppermute(value, "tensor", [(i, i ^ 1) for i in range(4)])
    return value + lax.ppermute(value, "tensor", [(i, i ^ 2) for i in range(4)])


def exact_total(value):
    for axis in ("tensor", "shard", "context"):
        count = lax.axis_size(axis)
        if count & (count - 1):
            value = lax.psum(value, axis)
            continue
        span = 1
        while span < count:
            value = value + lax.ppermute(value, axis, [(i, i ^ span) for i in range(count)])
            span *= 2
    return value


def chip_total(grad):
    f32 = jnp.float32
    shard = lax.axis_index("shard")
    mine = half_of(grad, shard)
    other = half_of(grad, 1 - shard)
    got = lax.ppermute(other.astype(jnp.bfloat16), "shard", [(0, 1), (1, 0)])
    return mine.astype(f32) + got.astype(f32)


def line_total(staged):
    return lax.psum_scatter(
        staged.astype(jnp.bfloat16), "context", scatter_dimension=0, tiled=True
    ).astype(jnp.float32)


def rows_total(grad):
    return line_total(chip_total(grad))


def pass_grads(grad_key, grad_value):
    return (
        passed_along(grad_key.astype(jnp.bfloat16), "context", 1).astype(grad_key.dtype),
        passed_along(grad_value.astype(jnp.bfloat16), "context", 1).astype(grad_value.dtype),
    )


def key_scores(query_heads, query_seg, query_pos, piece):
    key_flat, value_flat, key_seg, key_pos = piece
    heads = query_heads.shape[1]
    key_heads = key_flat.reshape(key_flat.shape[0], heads, HD)
    value_heads = value_flat.reshape(value_flat.shape[0], heads, HD)
    scores = jnp.einsum(
        "qhd,khd->hqk", query_heads, key_heads, preferred_element_type=jnp.float32
    ) * (1.0 / math.sqrt(HD))
    allowed = (query_seg[:, None] == key_seg[None, :]) & (key_pos[None, :] <= query_pos[:, None])
    return (jnp.where(allowed[None], scores, NEG), allowed, key_heads, value_heads)


def forward_fold(stats, piece, query_heads, query_seg, query_pos):
    peak, total, accum = stats
    scores, allowed, key_heads, value_heads = key_scores(query_heads, query_seg, query_pos, piece)
    new_peak = jnp.maximum(peak, jnp.max(scores, axis=-1))
    weights = jnp.where(allowed[None], jnp.exp(scores - new_peak[..., None]), 0.0)
    factor = jnp.exp(peak - new_peak)
    total = total * factor + jnp.sum(weights, axis=-1)
    accum = accum * factor[..., None] + jnp.einsum(
        "hqk,khd->hqd",
        weights.astype(jnp.bfloat16),
        value_heads,
        preferred_element_type=jnp.float32,
    )
    return (new_peak, total, accum)


def backward_piece(piece, query_heads, grad_heads, log_total, inner, query_seg, query_pos):
    scores, allowed, key_heads, value_heads = key_scores(query_heads, query_seg, query_pos, piece)
    probs = jnp.where(allowed[None], jnp.exp(scores - log_total[..., None]), 0.0)
    grad_value = jnp.einsum(
        "hqk,qhd->khd", probs.astype(jnp.bfloat16), grad_heads, preferred_element_type=jnp.float32
    )
    grad_probs = jnp.einsum(
        "qhd,khd->hqk", grad_heads, value_heads, preferred_element_type=jnp.float32
    )
    grad_scores = (probs * (grad_probs - inner[..., None]) * (1.0 / math.sqrt(HD))).astype(
        jnp.bfloat16
    )
    grad_query = jnp.einsum(
        "hqk,khd->qhd", grad_scores, key_heads, preferred_element_type=jnp.float32
    )
    grad_key = jnp.einsum(
        "hqk,qhd->khd", grad_scores, query_heads, preferred_element_type=jnp.float32
    )
    key_rows = grad_key.shape[0]
    return (grad_query, grad_key.reshape(key_rows, -1), grad_value.reshape(key_rows, -1))


class RingAttention:
    def __init__(self, query, key_flat, value_flat, segment, position, cosine, sine):
        self.query = query
        self.piece = (key_flat, value_flat, segment, position)
        self.segment = segment
        self.position = position
        self.cosine = cosine
        self.sine = sine

    def forward(self):
        f32 = jnp.float32
        query, segment, position = self.query, self.segment, self.position
        rows, heads = query.shape[0], query.shape[1]
        start_stats = (
            jnp.full((heads, rows), NEG, f32),
            jnp.zeros((heads, rows), f32),
            jnp.zeros((heads, rows, HD), f32),
        )
        stats = forward_fold(start_stats, self.piece, query, segment, position)

        def cycle_turn(index, carry):
            moving, current = carry
            moving = passed_along(moving, "context", 1)
            current = forward_fold(current, moving, query, segment, position)
            return (moving, current)

        peak, total, accum = lax.fori_loop(
            0, lax.axis_size("context") - 1, cycle_turn, (self.piece, stats)
        )[1]
        self.attended = jnp.transpose(accum / total[..., None], (1, 0, 2)).astype(jnp.bfloat16)
        self.log_total = peak + jnp.log(total)
        return self.attended

    def backward(self, grad_heads, early):
        bf16 = jnp.bfloat16
        query, segment, position = self.query, self.segment, self.position
        rows, heads = query.shape[0], query.shape[1]
        inner = jnp.sum(grad_heads.astype(jnp.float32) * self.attended.astype(jnp.float32), axis=-1).T

        def piece_grads(piece):
            return backward_piece(piece, query, grad_heads, self.log_total, inner, segment, position)

        grad_query, grad_key, grad_value = piece_grads(self.piece)

        def grad_turn(index, carry):
            moving, acc_query, acc_key, acc_value = carry
            moving = passed_along(moving, "context", 1)
            acc_key, acc_value = pass_grads(acc_key, acc_value)
            part_query, part_key, part_value = piece_grads(moving)
            return (moving, acc_query + part_query, acc_key + part_key, acc_value + part_value)

        carried = lax.fori_loop(
            0,
            lax.axis_size("context") - 1,
            grad_turn,
            (self.piece, grad_query, grad_key, grad_value),
        )
        grad_query = carried[1]
        grad_key, grad_value = pass_grads(carried[2], carried[3])
        grad_qin = rotate_back(grad_query, self.cosine, self.sine).astype(bf16)
        grad_kin = rotate_back(grad_key.reshape(rows, heads, HD), self.cosine, self.sine).astype(bf16)
        grad_vin = grad_value.astype(bf16).reshape(rows, heads, HD)
        return grad_qin, grad_kin, grad_vin, early


class HeadAttention:
    BLOCK = 512

    def __init__(self, query, key_heads, value_heads, segment, position, cosine, sine):
        ways = lax.axis_size("context")
        rows, heads = query.shape[0], query.shape[1]
        self.ways = ways
        self.rows = rows
        self.heads = heads
        self.group = heads // ways
        self.piece = rows // 2
        stacked = jnp.stack([query, key_heads, value_heads], axis=1)
        stacked = stacked.reshape(rows, 3, ways, self.group, HD)
        stacked = lax.all_to_all(stacked, "context", 2, 0, tiled=True)
        stacked = stacked.reshape(rows * ways, 3, self.group, HD)
        tags = jnp.stack([segment, position], axis=0)[None]
        tags = jnp.broadcast_to(tags, (ways, 2, rows))
        tags = lax.all_to_all(tags, "context", 0, 0, tiled=True)
        tags = jnp.transpose(tags, (1, 0, 2)).reshape(2, rows * ways)
        pieces = 2 * ways
        piece_of_slot = tags[1].reshape(pieces, self.piece)[:, 0] // self.piece
        slots = jnp.arange(pieces, dtype=jnp.int32)
        slot_of_piece = jnp.sum(
            jnp.where(piece_of_slot[None, :] == slots[:, None], slots[None, :], 0), axis=1
        )
        self.piece_of_slot = piece_of_slot
        self.slot_of_piece = slot_of_piece
        stacked = self._reorder(stacked, slot_of_piece)
        tags = self._reorder(tags.T, slot_of_piece).T
        self.query = stacked[:, 0]
        self.keys = stacked[:, 1]
        self.values = stacked[:, 2]
        self.seg_all = tags[0]
        self.pos_all = tags[1]
        self.cos_all, self.sin_all = rope_tables(self.pos_all)

    def _reorder(self, value, source):
        parts = [
            lax.dynamic_slice_in_dim(value, source[index] * self.piece, self.piece, axis=0)
            for index in range(source.shape[0])
        ]
        return jnp.concatenate(parts, axis=0)

    def _blocks(self):
        total = self.rows * self.ways
        block = min(self.BLOCK, total)
        return [(start, block) for start in range(0, total, block)]

    def _scores(self, start, size):
        reach = start + size
        query = self.query[start:reach]
        seg_q = self.seg_all[start:reach]
        pos_q = self.pos_all[start:reach]
        scores = jnp.einsum(
            "qhd,khd->hqk", query, self.keys[:reach], preferred_element_type=jnp.float32
        ) * (1.0 / math.sqrt(HD))
        allowed = (seg_q[:, None] == self.seg_all[None, :reach]) & (
            self.pos_all[None, :reach] <= pos_q[:, None]
        )
        return query, jnp.where(allowed[None], scores, NEG), allowed

    def forward(self):
        outs = []
        logs = []
        for start, size in self._blocks():
            reach = start + size
            _, scores, allowed = self._scores(start, size)
            peak = jnp.max(scores, axis=-1)
            weights = jnp.where(allowed[None], jnp.exp(scores - peak[..., None]), 0.0)
            total = jnp.sum(weights, axis=-1)
            mixed = jnp.einsum(
                "hqk,khd->qhd",
                weights.astype(jnp.bfloat16),
                self.values[:reach],
                preferred_element_type=jnp.float32,
            )
            outs.append((mixed / total.T[:, :, None]).astype(jnp.bfloat16))
            logs.append(peak + jnp.log(total))
        self.attended = jnp.concatenate(outs, axis=0)
        self.log_total = jnp.concatenate(logs, axis=1)
        back = self._reorder(self.attended, self.piece_of_slot)
        back = back.reshape(self.rows * self.ways, 1, self.group, HD)
        back = lax.all_to_all(back, "context", 0, 1, tiled=True)
        return back.reshape(self.rows, self.heads, HD)

    def backward(self, grad_heads, early):
        f32 = jnp.float32
        bf16 = jnp.bfloat16
        scale = 1.0 / math.sqrt(HD)
        grad = grad_heads.reshape(self.rows, self.ways, self.group, HD)
        grad = lax.all_to_all(grad, "context", 1, 0, tiled=True)
        grad, early = lax.optimization_barrier((grad, early))
        grad = grad.reshape(self.rows * self.ways, self.group, HD)
        grad = self._reorder(grad, self.slot_of_piece)
        inner = jnp.sum(grad.astype(f32) * self.attended.astype(f32), axis=-1).T
        total_rows = self.rows * self.ways
        grad_key = jnp.zeros(self.keys.shape, f32)
        grad_value = jnp.zeros(self.values.shape, f32)
        grad_queries = []
        for start, size in self._blocks():
            reach = start + size
            query, scores, allowed = self._scores(start, size)
            log_block = self.log_total[:, start:reach]
            inner_block = inner[:, start:reach]
            grad_block = grad[start:reach]
            probs = jnp.where(allowed[None], jnp.exp(scores - log_block[..., None]), 0.0)
            part_value = jnp.einsum(
                "hqk,qhd->khd", probs.astype(bf16), grad_block, preferred_element_type=f32
            )
            grad_probs = jnp.einsum(
                "qhd,khd->hqk", grad_block, self.values[:reach], preferred_element_type=f32
            )
            grad_scores = (probs * (grad_probs - inner_block[..., None]) * scale).astype(bf16)
            grad_queries.append(
                jnp.einsum(
                    "hqk,khd->qhd", grad_scores, self.keys[:reach], preferred_element_type=f32
                )
            )
            part_key = jnp.einsum("hqk,qhd->khd", grad_scores, query, preferred_element_type=f32)
            pad = ((0, total_rows - reach), (0, 0), (0, 0))
            grad_value = grad_value + jnp.pad(part_value, pad)
            grad_key = grad_key + jnp.pad(part_key, pad)
        grad_query = jnp.concatenate(grad_queries, axis=0)
        grad_qin = rotate_back(grad_query, self.cos_all, self.sin_all).astype(bf16)
        grad_kin = rotate_back(grad_key, self.cos_all, self.sin_all).astype(bf16)
        grad_vin = grad_value.astype(bf16)
        returned = []
        for grad_in in (grad_qin, grad_kin, grad_vin):
            grad_in = self._reorder(grad_in, self.piece_of_slot)
            grad_in = grad_in.reshape(self.rows * self.ways, 1, self.group, HD)
            grad_in = lax.all_to_all(grad_in, "context", 0, 1, tiled=True)
            returned.append(grad_in.reshape(self.rows, self.heads, HD))
        return returned[0], returned[1], returned[2], early


def mlp_chunks(hidden_cols):
    for count in (2, 1):
        if hidden_cols % (count * 128) == 0:
            return count
    return 1


def on_device(
    inputs, segments, positions, w_q, w_k, w_v, w_o, w_gate, w_up, w_down, g_attn, g_mlp, d_out
):
    f32 = jnp.float32
    bf16 = jnp.bfloat16
    rows = inputs.shape[1]
    width = inputs.shape[2]
    cols = w_q.shape[1]
    hidden_cols = w_gate.shape[1]
    tokens = inputs.reshape(rows, width)
    segment = segments.reshape(rows)
    position = positions.reshape(rows)
    full_qkvo = lax.all_gather(
        jnp.concatenate([w_q, w_k, w_v, w_o], axis=1), ROWS, axis=0, tiled=True
    )
    full_qkv = full_qkvo[:, : 3 * cols]
    full_o = full_qkvo[:, 3 * cols :]
    gains = lax.all_gather(
        jnp.concatenate([g_attn, g_mlp])[None], ROWS, axis=0, tiled=True
    )
    gain_attn = gains[:, : g_attn.shape[0]].reshape(width)
    gain_mlp = gains[:, g_attn.shape[0] :].reshape(width)
    count = mlp_chunks(hidden_cols)
    step = hidden_cols // count
    fetched = []
    for index in range(count):
        part = slice(index * step, (index + 1) * step)
        triple = lax.all_gather(
            jnp.concatenate([w_gate[:, part], w_up[:, part], w_down[:, part]], axis=1),
            ROWS,
            axis=0,
            tiled=True,
        )
        fetched.append((triple[:, :step], triple[:, step : 2 * step], triple[:, 2 * step :]))
    heads = cols // HD
    cosine, sine = rope_tables(position)
    resid1 = tokens.astype(f32)
    norm1, inv1 = normalize(resid1)
    h1 = (norm1 * gain_attn.astype(f32)).astype(bf16)
    projected = jnp.dot(h1, full_qkv, preferred_element_type=f32)
    query = rotate(projected[:, :cols].reshape(rows, heads, HD), cosine, sine).astype(bf16)
    key_heads = rotate(projected[:, cols : 2 * cols].reshape(rows, heads, HD), cosine, sine).astype(
        bf16
    )
    value_heads = projected[:, 2 * cols :].astype(bf16).reshape(rows, heads, HD)
    if heads % lax.axis_size("context") == 0:
        attention = HeadAttention(query, key_heads, value_heads, segment, position, cosine, sine)
    else:
        attention = RingAttention(
            query,
            key_heads.reshape(rows, cols),
            value_heads.reshape(rows, cols),
            segment,
            position,
            cosine,
            sine,
        )
    attended = attention.forward()
    attended_flat = attended.reshape(rows, cols)
    resid2 = resid1 + tensor_total(contract_last(attended_flat, full_o))
    norm2, inv2 = normalize(resid2)
    h2_part = (norm2 * gain_mlp.astype(f32)).astype(bf16)
    grad_y = d_out.reshape(rows, width)
    mlp_partial = None
    h2_grad_partial = None
    staged = []
    for full_gate, full_up, full_down in fetched:
        if staged:
            full_gate, staged[-1] = lax.optimization_barrier((full_gate, staged[-1]))
        gate = jnp.dot(h2_part, full_gate, preferred_element_type=f32)
        up = jnp.dot(h2_part, full_up, preferred_element_type=f32)
        active = jax.nn.silu(gate)
        hidden = (active * up).astype(bf16)
        out_part = contract_last(hidden, full_down)
        mlp_partial = out_part if mlp_partial is None else mlp_partial + out_part
        grad_hidden = jnp.dot(grad_y, full_down, preferred_element_type=f32)
        sigma = jax.nn.sigmoid(gate)
        grad_gate = (grad_hidden * up * sigma * (1.0 + gate * (1.0 - sigma))).astype(bf16)
        grad_up = (grad_hidden * active).astype(bf16)
        back_part = contract_last(grad_gate, full_gate) + contract_last(grad_up, full_up)
        pending = (
            contract_first(h2_part, grad_gate),
            contract_first(h2_part, grad_up),
            contract_first(grad_y, hidden),
        )
        h2_grad_partial = back_part if h2_grad_partial is None else h2_grad_partial + back_part
        staged.append(chip_total(jnp.concatenate(pending, axis=1)))
    grad_h2 = tensor_total(h2_grad_partial)
    grad_h2, staged[-1] = lax.optimization_barrier((grad_h2, staged[-1]))
    reduced = [line_total(chunk) for chunk in staged]
    result = (resid2 + tensor_total(mlp_partial)).astype(bf16)
    grad_gmlp = jnp.sum(grad_h2 * norm2, axis=0)
    grad_resid = grad_y.astype(f32) + norm_back(grad_h2, norm2, inv2, gain_mlp)
    grad_resid_part = grad_resid.astype(bf16)
    grad_heads = (
        jnp.dot(grad_resid_part, full_o, preferred_element_type=f32)
        .astype(bf16)
        .reshape(rows, heads, HD)
    )
    grad_heads, partial_o = lax.optimization_barrier(
        (grad_heads, contract_first(grad_resid_part, attended_flat))
    )
    early = (chip_total(partial_o), reduced[:-1])
    grad_qin, grad_kin, grad_vin, early = attention.backward(grad_heads, early)
    staged_o, reduced[:-1] = early
    reduced_o = line_total(staged_o)
    grad_qkv = jnp.concatenate(
        [grad_qin.reshape(rows, cols), grad_kin.reshape(rows, cols), grad_vin.reshape(rows, cols)],
        axis=1,
    )
    h1_grad_partial = contract_last(grad_qkv, full_qkv)
    first_tensor = (lax.axis_index("tensor") == 0).astype(f32)
    gain_parts = jnp.stack(
        [jnp.sum(h1_grad_partial * norm1, axis=0), grad_gmlp * first_tensor], axis=1
    )
    gains_total = exact_total(gain_parts)
    h1_grad_partial, staged_qkv = lax.optimization_barrier(
        (h1_grad_partial, chip_total(contract_first(h1, grad_qkv)))
    )
    grad_h1 = tensor_total(h1_grad_partial)
    grad_h1, reduced_o, reduced[-1], result = lax.optimization_barrier(
        (grad_h1, reduced_o, reduced[-1], result)
    )
    grad_x_part = (grad_resid + norm_back(grad_h1, norm1, inv1, gain_attn)).astype(bf16)
    reduced_qkv = line_total(staged_qkv)
    blocks = lax.axis_size("shard") * lax.axis_size("context")
    block = lax.axis_index("shard") * lax.axis_size("context") + lax.axis_index("context")
    piece = width // blocks
    reduced_gains = lax.dynamic_slice_in_dim(gains_total, block * piece, piece, axis=0)
    reduced_gate, reduced_up, reduced_down = (
        jnp.concatenate([chunk[:, which * step : (which + 1) * step] for chunk in reduced], axis=1)
        for which in range(3)
    )
    return (
        result.reshape(1, rows, width),
        grad_x_part.reshape(1, rows, width),
        reduced_qkv[:, :cols],
        reduced_qkv[:, cols : 2 * cols],
        reduced_qkv[:, 2 * cols :],
        reduced_o,
        reduced_gate,
        reduced_up,
        reduced_down,
        reduced_gains[:, 0],
        reduced_gains[:, 1],
    )


def solution(mesh):
    placed = (
        P("shard", "context", None),
        P("shard", "context"),
        P("shard", "context"),
        P(ROWS, "tensor"),
        P(ROWS, "tensor"),
        P(ROWS, "tensor"),
        P(ROWS, "tensor"),
        P(ROWS, "tensor"),
        P(ROWS, "tensor"),
        P(ROWS, "tensor"),
        P(ROWS),
        P(ROWS),
        P("shard", "context", None),
    )
    return jax.shard_map(
        on_device,
        mesh=mesh,
        in_specs=placed,
        out_specs=(
            P("shard", "context", None),
            P("shard", "context", None),
            P(ROWS, "tensor"),
            P(ROWS, "tensor"),
            P(ROWS, "tensor"),
            P(ROWS, "tensor"),
            P(ROWS, "tensor"),
            P(ROWS, "tensor"),
            P(ROWS, "tensor"),
            P(ROWS),
            P(ROWS),
        ),
        check_vma=False,
    )
```

```python
import math

import jax
import jax.numpy as jnp
from jax import lax
from jax.sharding import PartitionSpec as P

HD = 64


EPS = 1e-05
THETA = 130000.0
NEG = -1e30
ROWS = ("shard", "context")


def passed_along(value, axis, steps):
    count = lax.axis_size(axis)
    pairs = [(source, (source + steps) % count) for source in range(count)]
    return lax.ppermute(value, axis, pairs)


def rope_tables(position):
    index = jnp.arange(HD // 2, dtype=jnp.float32)
    inverse = jnp.power(jnp.float32(THETA), -2.0 * index / HD)
    angle = position.astype(jnp.float32)[:, None] * inverse[None, :]
    return (jnp.cos(angle), jnp.sin(angle))


def rotate(tensor, cosine, sine):
    half = tensor.shape[-1] // 2
    first = tensor[..., :half]
    second = tensor[..., half:]
    cosine = cosine[:, None, :]
    sine = sine[:, None, :]
    return jnp.concatenate(
        [first * cosine - second * sine, second * cosine + first * sine], axis=-1
    )


def rotate_back(grad, cosine, sine):
    half = grad.shape[-1] // 2
    first = grad[..., :half]
    second = grad[..., half:]
    cosine = cosine[:, None, :]
    sine = sine[:, None, :]
    return jnp.concatenate(
        [first * cosine + second * sine, second * cosine - first * sine], axis=-1
    )


def normalize(value):
    inv_rms = lax.rsqrt(jnp.mean(value * value, axis=-1, keepdims=True) + EPS)
    return (value * inv_rms, inv_rms)


def norm_back(grad, normed, inv_rms, gain):
    scaled = grad * gain.astype(jnp.float32)
    return inv_rms * (scaled - normed * jnp.mean(scaled * normed, axis=-1, keepdims=True))


def contract_last(left, right):
    return lax.dot_general(
        left, right, (((1,), (1,)), ((), ())), preferred_element_type=jnp.float32
    )


def contract_first(left, right):
    return lax.dot_general(
        left, right, (((0,), (0,)), ((), ())), preferred_element_type=jnp.float32
    )


def half_of(value, bit):
    size = value.shape[0] // 2
    return lax.dynamic_slice_in_dim(value, bit * size, size, axis=0)


def joined(mine, other, bit):
    low = jnp.where(bit == 0, mine, other)
    high = jnp.where(bit == 0, other, mine)
    return jnp.concatenate([low, high], axis=0)


def tensor_total(partial_sum):
    count = lax.axis_size("tensor")
    rows = partial_sum.shape[0]
    if count != 4 or rows % 8:
        return lax.psum(partial_sum.astype(jnp.bfloat16), "tensor").astype(jnp.float32)
    f32 = jnp.float32
    bf16 = jnp.bfloat16
    index = lax.axis_index("tensor")
    x_bit = index % 2
    y_bit = index // 2
    x_pairs = [(i, i ^ 1) for i in range(4)]
    y_pairs = [(i, i ^ 2) for i in range(4)]

    def swap(value, pairs):
        return lax.ppermute(value.astype(bf16), "tensor", pairs).astype(f32)

    first = partial_sum[: rows // 2]
    second = partial_sum[rows // 2 :]
    first = half_of(first, x_bit) + swap(half_of(first, 1 - x_bit), x_pairs)
    second = half_of(second, y_bit) + swap(half_of(second, 1 - y_bit), y_pairs)
    first = half_of(first, y_bit) + swap(half_of(first, 1 - y_bit), y_pairs)
    second = half_of(second, x_bit) + swap(half_of(second, 1 - x_bit), x_pairs)
    first = first.astype(bf16)
    second = second.astype(bf16)
    first = joined(first, lax.ppermute(first, "tensor", y_pairs), y_bit)
    second = joined(second, lax.ppermute(second, "tensor", x_pairs), x_bit)
    first = joined(first, lax.ppermute(first, "tensor", x_pairs), x_bit)
    second = joined(second, lax.ppermute(second, "tensor", y_pairs), y_bit)
    return jnp.concatenate([first, second], axis=0).astype(f32)


def tensor_exact_total(value):
    if lax.axis_size("tensor") != 4:
        return lax.psum(value, "tensor")
    value = value + lax.ppermute(value, "tensor", [(i, i ^ 1) for i in range(4)])
    return value + lax.ppermute(value, "tensor", [(i, i ^ 2) for i in range(4)])


def exact_total(value):
    for axis in ("tensor", "shard", "context"):
        count = lax.axis_size(axis)
        if count & (count - 1):
            value = lax.psum(value, axis)
            continue
        span = 1
        while span < count:
            value = value + lax.ppermute(value, axis, [(i, i ^ span) for i in range(count)])
            span *= 2
    return value


def chip_total(grad):
    f32 = jnp.float32
    shard = lax.axis_index("shard")
    mine = half_of(grad, shard)
    other = half_of(grad, 1 - shard)
    got = lax.ppermute(other.astype(jnp.bfloat16), "shard", [(0, 1), (1, 0)])
    return mine.astype(f32) + got.astype(f32)


def line_total(staged):
    return lax.psum_scatter(
        staged.astype(jnp.bfloat16), "context", scatter_dimension=0, tiled=True
    ).astype(jnp.float32)


def rows_total(grad):
    return line_total(chip_total(grad))


def pass_grads(grad_key, grad_value):
    return (
        passed_along(grad_key.astype(jnp.bfloat16), "context", 1).astype(grad_key.dtype),
        passed_along(grad_value.astype(jnp.bfloat16), "context", 1).astype(grad_value.dtype),
    )


def key_scores(query_heads, query_seg, query_pos, piece):
    key_flat, value_flat, key_seg, key_pos = piece
    heads = query_heads.shape[1]
    key_heads = key_flat.reshape(key_flat.shape[0], heads, HD)
    value_heads = value_flat.reshape(value_flat.shape[0], heads, HD)
    scores = jnp.einsum(
        "qhd,khd->hqk", query_heads, key_heads, preferred_element_type=jnp.float32
    ) * (1.0 / math.sqrt(HD))
    allowed = (query_seg[:, None] == key_seg[None, :]) & (key_pos[None, :] <= query_pos[:, None])
    return (jnp.where(allowed[None], scores, NEG), allowed, key_heads, value_heads)


def forward_fold(stats, piece, query_heads, query_seg, query_pos):
    peak, total, accum = stats
    scores, allowed, key_heads, value_heads = key_scores(query_heads, query_seg, query_pos, piece)
    new_peak = jnp.maximum(peak, jnp.max(scores, axis=-1))
    weights = jnp.where(allowed[None], jnp.exp(scores - new_peak[..., None]), 0.0)
    factor = jnp.exp(peak - new_peak)
    total = total * factor + jnp.sum(weights, axis=-1)
    accum = accum * factor[..., None] + jnp.einsum(
        "hqk,khd->hqd",
        weights.astype(jnp.bfloat16),
        value_heads,
        preferred_element_type=jnp.float32,
    )
    return (new_peak, total, accum)


def backward_piece(piece, query_heads, grad_heads, log_total, inner, query_seg, query_pos):
    scores, allowed, key_heads, value_heads = key_scores(query_heads, query_seg, query_pos, piece)
    probs = jnp.where(allowed[None], jnp.exp(scores - log_total[..., None]), 0.0)
    grad_value = jnp.einsum(
        "hqk,qhd->khd", probs.astype(jnp.bfloat16), grad_heads, preferred_element_type=jnp.float32
    )
    grad_probs = jnp.einsum(
        "qhd,khd->hqk", grad_heads, value_heads, preferred_element_type=jnp.float32
    )
    grad_scores = (probs * (grad_probs - inner[..., None]) * (1.0 / math.sqrt(HD))).astype(
        jnp.bfloat16
    )
    grad_query = jnp.einsum(
        "hqk,khd->qhd", grad_scores, key_heads, preferred_element_type=jnp.float32
    )
    grad_key = jnp.einsum(
        "hqk,qhd->khd", grad_scores, query_heads, preferred_element_type=jnp.float32
    )
    key_rows = grad_key.shape[0]
    return (grad_query, grad_key.reshape(key_rows, -1), grad_value.reshape(key_rows, -1))


class RingAttention:
    def __init__(self, query, key_flat, value_flat, segment, position, cosine, sine):
        self.query = query
        self.piece = (key_flat, value_flat, segment, position)
        self.segment = segment
        self.position = position
        self.cosine = cosine
        self.sine = sine

    def forward(self):
        f32 = jnp.float32
        query, segment, position = self.query, self.segment, self.position
        rows, heads = query.shape[0], query.shape[1]
        start_stats = (
            jnp.full((heads, rows), NEG, f32),
            jnp.zeros((heads, rows), f32),
            jnp.zeros((heads, rows, HD), f32),
        )
        stats = forward_fold(start_stats, self.piece, query, segment, position)

        def cycle_turn(index, carry):
            moving, current = carry
            moving = passed_along(moving, "context", 1)
            current = forward_fold(current, moving, query, segment, position)
            return (moving, current)

        peak, total, accum = lax.fori_loop(
            0, lax.axis_size("context") - 1, cycle_turn, (self.piece, stats)
        )[1]
        self.attended = jnp.transpose(accum / total[..., None], (1, 0, 2)).astype(jnp.bfloat16)
        self.log_total = peak + jnp.log(total)
        return self.attended

    def backward(self, grad_heads, early):
        bf16 = jnp.bfloat16
        query, segment, position = self.query, self.segment, self.position
        rows, heads = query.shape[0], query.shape[1]
        inner = jnp.sum(grad_heads.astype(jnp.float32) * self.attended.astype(jnp.float32), axis=-1).T

        def piece_grads(piece):
            return backward_piece(piece, query, grad_heads, self.log_total, inner, segment, position)

        grad_query, grad_key, grad_value = piece_grads(self.piece)

        def grad_turn(index, carry):
            moving, acc_query, acc_key, acc_value = carry
            moving = passed_along(moving, "context", 1)
            acc_key, acc_value = pass_grads(acc_key, acc_value)
            part_query, part_key, part_value = piece_grads(moving)
            return (moving, acc_query + part_query, acc_key + part_key, acc_value + part_value)

        carried = lax.fori_loop(
            0,
            lax.axis_size("context") - 1,
            grad_turn,
            (self.piece, grad_query, grad_key, grad_value),
        )
        grad_query = carried[1]
        grad_key, grad_value = pass_grads(carried[2], carried[3])
        grad_qin = rotate_back(grad_query, self.cosine, self.sine).astype(bf16)
        grad_kin = rotate_back(grad_key.reshape(rows, heads, HD), self.cosine, self.sine).astype(bf16)
        grad_vin = grad_value.astype(bf16).reshape(rows, heads, HD)
        return grad_qin, grad_kin, grad_vin, early


class HeadAttention:
    BLOCK = 512

    def __init__(self, query, key_heads, value_heads, segment, position, cosine, sine):
        ways = lax.axis_size("context")
        rows, heads = query.shape[0], query.shape[1]
        self.ways = ways
        self.rows = rows
        self.heads = heads
        self.group = heads // ways
        self.piece = rows // 2
        stacked = jnp.stack([query, key_heads, value_heads], axis=1)
        stacked = stacked.reshape(rows, 3, ways, self.group, HD)
        stacked = lax.all_to_all(stacked, "context", 2, 0, tiled=True)
        stacked = stacked.reshape(rows * ways, 3, self.group, HD)
        tags = jnp.stack([segment, position], axis=0)[None]
        tags = jnp.broadcast_to(tags, (ways, 2, rows))
        tags = lax.all_to_all(tags, "context", 0, 0, tiled=True)
        tags = jnp.transpose(tags, (1, 0, 2)).reshape(2, rows * ways)
        pieces = 2 * ways
        piece_of_slot = tags[1].reshape(pieces, self.piece)[:, 0] // self.piece
        slots = jnp.arange(pieces, dtype=jnp.int32)
        slot_of_piece = jnp.sum(
            jnp.where(piece_of_slot[None, :] == slots[:, None], slots[None, :], 0), axis=1
        )
        self.piece_of_slot = piece_of_slot
        self.slot_of_piece = slot_of_piece
        stacked = self._reorder(stacked, slot_of_piece)
        tags = self._reorder(tags.T, slot_of_piece).T
        self.query = stacked[:, 0]
        self.keys = stacked[:, 1]
        self.values = stacked[:, 2]
        self.seg_all = tags[0]
        self.pos_all = tags[1]
        self.cos_all, self.sin_all = rope_tables(self.pos_all)

    def _reorder(self, value, source):
        parts = [
            lax.dynamic_slice_in_dim(value, source[index] * self.piece, self.piece, axis=0)
            for index in range(source.shape[0])
        ]
        return jnp.concatenate(parts, axis=0)

    def _blocks(self):
        total = self.rows * self.ways
        block = min(self.BLOCK, total)
        return [(start, block) for start in range(0, total, block)]

    def _scores(self, start, size):
        reach = start + size
        query = self.query[start:reach]
        seg_q = self.seg_all[start:reach]
        pos_q = self.pos_all[start:reach]
        scores = jnp.einsum(
            "qhd,khd->hqk", query, self.keys[:reach], preferred_element_type=jnp.float32
        ) * (1.0 / math.sqrt(HD))
        allowed = (seg_q[:, None] == self.seg_all[None, :reach]) & (
            self.pos_all[None, :reach] <= pos_q[:, None]
        )
        return query, jnp.where(allowed[None], scores, NEG), allowed

    def forward(self):
        outs = []
        logs = []
        for start, size in self._blocks():
            reach = start + size
            _, scores, allowed = self._scores(start, size)
            peak = jnp.max(scores, axis=-1)
            weights = jnp.where(allowed[None], jnp.exp(scores - peak[..., None]), 0.0)
            total = jnp.sum(weights, axis=-1)
            mixed = jnp.einsum(
                "hqk,khd->qhd",
                weights.astype(jnp.bfloat16),
                self.values[:reach],
                preferred_element_type=jnp.float32,
            )
            outs.append((mixed / total.T[:, :, None]).astype(jnp.bfloat16))
            logs.append(peak + jnp.log(total))
        self.attended = jnp.concatenate(outs, axis=0)
        self.log_total = jnp.concatenate(logs, axis=1)
        back = self._reorder(self.attended, self.piece_of_slot)
        back = back.reshape(self.rows * self.ways, 1, self.group, HD)
        back = lax.all_to_all(back, "context", 0, 1, tiled=True)
        return back.reshape(self.rows, self.heads, HD)

    def backward(self, grad_heads, early):
        f32 = jnp.float32
        bf16 = jnp.bfloat16
        scale = 1.0 / math.sqrt(HD)
        grad = grad_heads.reshape(self.rows, self.ways, self.group, HD)
        grad = lax.all_to_all(grad, "context", 1, 0, tiled=True)
        grad, early = lax.optimization_barrier((grad, early))
        grad = grad.reshape(self.rows * self.ways, self.group, HD)
        grad = self._reorder(grad, self.slot_of_piece)
        inner = jnp.sum(grad.astype(f32) * self.attended.astype(f32), axis=-1).T
        total_rows = self.rows * self.ways
        grad_key = jnp.zeros(self.keys.shape, f32)
        grad_value = jnp.zeros(self.values.shape, f32)
        grad_queries = []
        for start, size in self._blocks():
            reach = start + size
            query, scores, allowed = self._scores(start, size)
            log_block = self.log_total[:, start:reach]
            inner_block = inner[:, start:reach]
            grad_block = grad[start:reach]
            probs = jnp.where(allowed[None], jnp.exp(scores - log_block[..., None]), 0.0)
            part_value = jnp.einsum(
                "hqk,qhd->khd", probs.astype(bf16), grad_block, preferred_element_type=f32
            )
            grad_probs = jnp.einsum(
                "qhd,khd->hqk", grad_block, self.values[:reach], preferred_element_type=f32
            )
            grad_scores = (probs * (grad_probs - inner_block[..., None]) * scale).astype(bf16)
            grad_queries.append(
                jnp.einsum(
                    "hqk,khd->qhd", grad_scores, self.keys[:reach], preferred_element_type=f32
                )
            )
            part_key = jnp.einsum("hqk,qhd->khd", grad_scores, query, preferred_element_type=f32)
            pad = ((0, total_rows - reach), (0, 0), (0, 0))
            grad_value = grad_value + jnp.pad(part_value, pad)
            grad_key = grad_key + jnp.pad(part_key, pad)
        grad_query = jnp.concatenate(grad_queries, axis=0)
        grad_qin = rotate_back(grad_query, self.cos_all, self.sin_all).astype(bf16)
        grad_kin = rotate_back(grad_key, self.cos_all, self.sin_all).astype(bf16)
        grad_vin = grad_value.astype(bf16)
        returned = []
        for grad_in in (grad_qin, grad_kin, grad_vin):
            grad_in = self._reorder(grad_in, self.piece_of_slot)
            grad_in = grad_in.reshape(self.rows * self.ways, 1, self.group, HD)
            grad_in = lax.all_to_all(grad_in, "context", 0, 1, tiled=True)
            returned.append(grad_in.reshape(self.rows, self.heads, HD))
        return returned[0], returned[1], returned[2], early


def mlp_chunks(hidden_cols):
    if hidden_cols % 512 == 0:
        return [hidden_cols * 3 // 4, hidden_cols // 4]
    return [hidden_cols]


def on_device(
    inputs, segments, positions, w_q, w_k, w_v, w_o, w_gate, w_up, w_down, g_attn, g_mlp, d_out
):
    f32 = jnp.float32
    bf16 = jnp.bfloat16
    rows = inputs.shape[1]
    width = inputs.shape[2]
    cols = w_q.shape[1]
    hidden_cols = w_gate.shape[1]
    tokens = inputs.reshape(rows, width)
    segment = segments.reshape(rows)
    position = positions.reshape(rows)
    full_qkvo = lax.all_gather(
        jnp.concatenate([w_q, w_k, w_v, w_o], axis=1), ROWS, axis=0, tiled=True
    )
    full_qkv = full_qkvo[:, : 3 * cols]
    full_o = full_qkvo[:, 3 * cols :]
    gains = lax.all_gather(
        jnp.concatenate([g_attn, g_mlp])[None], ROWS, axis=0, tiled=True
    )
    gain_attn = gains[:, : g_attn.shape[0]].reshape(width)
    gain_mlp = gains[:, g_attn.shape[0] :].reshape(width)
    widths = mlp_chunks(hidden_cols)
    fetched = []
    for index, step in enumerate(widths):
        begin = sum(widths[:index])
        part = slice(begin, begin + step)
        triple = lax.all_gather(
            jnp.concatenate([w_gate[:, part], w_up[:, part], w_down[:, part]], axis=1),
            ROWS,
            axis=0,
            tiled=True,
        )
        fetched.append((triple[:, :step], triple[:, step : 2 * step], triple[:, 2 * step :]))
    heads = cols // HD
    cosine, sine = rope_tables(position)
    resid1 = tokens.astype(f32)
    norm1, inv1 = normalize(resid1)
    h1 = (norm1 * gain_attn.astype(f32)).astype(bf16)
    projected = jnp.dot(h1, full_qkv, preferred_element_type=f32)
    query = rotate(projected[:, :cols].reshape(rows, heads, HD), cosine, sine).astype(bf16)
    key_heads = rotate(projected[:, cols : 2 * cols].reshape(rows, heads, HD), cosine, sine).astype(
        bf16
    )
    value_heads = projected[:, 2 * cols :].astype(bf16).reshape(rows, heads, HD)
    if heads % lax.axis_size("context") == 0:
        attention = HeadAttention(query, key_heads, value_heads, segment, position, cosine, sine)
    else:
        attention = RingAttention(
            query,
            key_heads.reshape(rows, cols),
            value_heads.reshape(rows, cols),
            segment,
            position,
            cosine,
            sine,
        )
    attended = attention.forward()
    attended_flat = attended.reshape(rows, cols)
    resid2 = resid1 + tensor_total(contract_last(attended_flat, full_o))
    norm2, inv2 = normalize(resid2)
    h2_part = (norm2 * gain_mlp.astype(f32)).astype(bf16)
    grad_y = d_out.reshape(rows, width)
    mlp_partial = None
    h2_grad_partial = None
    staged = []
    for full_gate, full_up, full_down in fetched:
        if staged:
            full_gate, staged[-1] = lax.optimization_barrier((full_gate, staged[-1]))
        gate = jnp.dot(h2_part, full_gate, preferred_element_type=f32)
        up = jnp.dot(h2_part, full_up, preferred_element_type=f32)
        active = jax.nn.silu(gate)
        hidden = (active * up).astype(bf16)
        out_part = contract_last(hidden, full_down)
        mlp_partial = out_part if mlp_partial is None else mlp_partial + out_part
        grad_hidden = jnp.dot(grad_y, full_down, preferred_element_type=f32)
        sigma = jax.nn.sigmoid(gate)
        grad_gate = (grad_hidden * up * sigma * (1.0 + gate * (1.0 - sigma))).astype(bf16)
        grad_up = (grad_hidden * active).astype(bf16)
        back_part = contract_last(grad_gate, full_gate) + contract_last(grad_up, full_up)
        pending = (
            contract_first(h2_part, grad_gate),
            contract_first(h2_part, grad_up),
            contract_first(grad_y, hidden),
        )
        h2_grad_partial = back_part if h2_grad_partial is None else h2_grad_partial + back_part
        staged.append(chip_total(jnp.concatenate(pending, axis=1)))
    grad_h2 = tensor_total(h2_grad_partial)
    grad_h2, staged[-1] = lax.optimization_barrier((grad_h2, staged[-1]))
    reduced = [line_total(chunk) for chunk in staged]
    result = (resid2 + tensor_total(mlp_partial)).astype(bf16)
    grad_gmlp = jnp.sum(grad_h2 * norm2, axis=0)
    grad_resid = grad_y.astype(f32) + norm_back(grad_h2, norm2, inv2, gain_mlp)
    grad_resid_part = grad_resid.astype(bf16)
    grad_heads = (
        jnp.dot(grad_resid_part, full_o, preferred_element_type=f32)
        .astype(bf16)
        .reshape(rows, heads, HD)
    )
    grad_heads, partial_o = lax.optimization_barrier(
        (grad_heads, contract_first(grad_resid_part, attended_flat))
    )
    early = (chip_total(partial_o), reduced[:-1])
    grad_qin, grad_kin, grad_vin, early = attention.backward(grad_heads, early)
    staged_o, reduced[:-1] = early
    reduced_o = line_total(staged_o)
    grad_qkv = jnp.concatenate(
        [grad_qin.reshape(rows, cols), grad_kin.reshape(rows, cols), grad_vin.reshape(rows, cols)],
        axis=1,
    )
    h1_grad_partial = contract_last(grad_qkv, full_qkv)
    first_tensor = (lax.axis_index("tensor") == 0).astype(f32)
    gain_parts = jnp.stack(
        [jnp.sum(h1_grad_partial * norm1, axis=0), grad_gmlp * first_tensor], axis=1
    )
    gains_total = exact_total(gain_parts)
    h1_grad_partial, staged_qkv = lax.optimization_barrier(
        (h1_grad_partial, chip_total(contract_first(h1, grad_qkv)))
    )
    grad_h1 = tensor_total(h1_grad_partial)
    grad_h1, reduced_o, reduced[-1], result = lax.optimization_barrier(
        (grad_h1, reduced_o, reduced[-1], result)
    )
    grad_x_part = (grad_resid + norm_back(grad_h1, norm1, inv1, gain_attn)).astype(bf16)
    reduced_qkv = line_total(staged_qkv)
    blocks = lax.axis_size("shard") * lax.axis_size("context")
    block = lax.axis_index("shard") * lax.axis_size("context") + lax.axis_index("context")
    piece = width // blocks
    reduced_gains = lax.dynamic_slice_in_dim(gains_total, block * piece, piece, axis=0)
    reduced_gate, reduced_up, reduced_down = (
        jnp.concatenate(
            [chunk[:, which * step : (which + 1) * step] for chunk, step in zip(reduced, widths)],
            axis=1,
        )
        for which in range(3)
    )
    return (
        result.reshape(1, rows, width),
        grad_x_part.reshape(1, rows, width),
        reduced_qkv[:, :cols],
        reduced_qkv[:, cols : 2 * cols],
        reduced_qkv[:, 2 * cols :],
        reduced_o,
        reduced_gate,
        reduced_up,
        reduced_down,
        reduced_gains[:, 0],
        reduced_gains[:, 1],
    )


def solution(mesh):
    placed = (
        P("shard", "context", None),
        P("shard", "context"),
        P("shard", "context"),
        P(ROWS, "tensor"),
        P(ROWS, "tensor"),
        P(ROWS, "tensor"),
        P(ROWS, "tensor"),
        P(ROWS, "tensor"),
        P(ROWS, "tensor"),
        P(ROWS, "tensor"),
        P(ROWS),
        P(ROWS),
        P("shard", "context", None),
    )
    return jax.shard_map(
        on_device,
        mesh=mesh,
        in_specs=placed,
        out_specs=(
            P("shard", "context", None),
            P("shard", "context", None),
            P(ROWS, "tensor"),
            P(ROWS, "tensor"),
            P(ROWS, "tensor"),
            P(ROWS, "tensor"),
            P(ROWS, "tensor"),
            P(ROWS, "tensor"),
            P(ROWS, "tensor"),
            P(ROWS),
            P(ROWS),
        ),
        check_vma=False,
    )
```

```python
import math

import jax
import jax.numpy as jnp
from jax import lax
from jax.sharding import PartitionSpec as P

HD = 64


EPS = 1e-05
THETA = 130000.0
NEG = -1e30
ROWS = ("shard", "context")


def passed_along(value, axis, steps):
    count = lax.axis_size(axis)
    pairs = [(source, (source + steps) % count) for source in range(count)]
    return lax.ppermute(value, axis, pairs)


def rope_tables(position):
    index = jnp.arange(HD // 2, dtype=jnp.float32)
    inverse = jnp.power(jnp.float32(THETA), -2.0 * index / HD)
    angle = position.astype(jnp.float32)[:, None] * inverse[None, :]
    return (jnp.cos(angle), jnp.sin(angle))


def rotate(tensor, cosine, sine):
    half = tensor.shape[-1] // 2
    first = tensor[..., :half]
    second = tensor[..., half:]
    cosine = cosine[:, None, :]
    sine = sine[:, None, :]
    return jnp.concatenate(
        [first * cosine - second * sine, second * cosine + first * sine], axis=-1
    )


def rotate_back(grad, cosine, sine):
    half = grad.shape[-1] // 2
    first = grad[..., :half]
    second = grad[..., half:]
    cosine = cosine[:, None, :]
    sine = sine[:, None, :]
    return jnp.concatenate(
        [first * cosine + second * sine, second * cosine - first * sine], axis=-1
    )


def normalize(value):
    inv_rms = lax.rsqrt(jnp.mean(value * value, axis=-1, keepdims=True) + EPS)
    return (value * inv_rms, inv_rms)


def norm_back(grad, normed, inv_rms, gain):
    scaled = grad * gain.astype(jnp.float32)
    return inv_rms * (scaled - normed * jnp.mean(scaled * normed, axis=-1, keepdims=True))


def contract_last(left, right):
    return lax.dot_general(
        left, right, (((1,), (1,)), ((), ())), preferred_element_type=jnp.float32
    )


def contract_first(left, right):
    return lax.dot_general(
        left, right, (((0,), (0,)), ((), ())), preferred_element_type=jnp.float32
    )


def half_of(value, bit):
    size = value.shape[0] // 2
    return lax.dynamic_slice_in_dim(value, bit * size, size, axis=0)


def joined(mine, other, bit):
    low = jnp.where(bit == 0, mine, other)
    high = jnp.where(bit == 0, other, mine)
    return jnp.concatenate([low, high], axis=0)


def tensor_total(partial_sum):
    count = lax.axis_size("tensor")
    rows = partial_sum.shape[0]
    if count != 4 or rows % 8:
        return lax.psum(partial_sum.astype(jnp.bfloat16), "tensor").astype(jnp.float32)
    f32 = jnp.float32
    bf16 = jnp.bfloat16
    index = lax.axis_index("tensor")
    x_bit = index % 2
    y_bit = index // 2
    x_pairs = [(i, i ^ 1) for i in range(4)]
    y_pairs = [(i, i ^ 2) for i in range(4)]

    def swap(value, pairs):
        return lax.ppermute(value.astype(bf16), "tensor", pairs).astype(f32)

    first = partial_sum[: rows // 2]
    second = partial_sum[rows // 2 :]
    first = half_of(first, x_bit) + swap(half_of(first, 1 - x_bit), x_pairs)
    second = half_of(second, y_bit) + swap(half_of(second, 1 - y_bit), y_pairs)
    first = half_of(first, y_bit) + swap(half_of(first, 1 - y_bit), y_pairs)
    second = half_of(second, x_bit) + swap(half_of(second, 1 - x_bit), x_pairs)
    first = first.astype(bf16)
    second = second.astype(bf16)
    first = joined(first, lax.ppermute(first, "tensor", y_pairs), y_bit)
    second = joined(second, lax.ppermute(second, "tensor", x_pairs), x_bit)
    first = joined(first, lax.ppermute(first, "tensor", x_pairs), x_bit)
    second = joined(second, lax.ppermute(second, "tensor", y_pairs), y_bit)
    return jnp.concatenate([first, second], axis=0).astype(f32)


def tensor_exact_total(value):
    if lax.axis_size("tensor") != 4:
        return lax.psum(value, "tensor")
    value = value + lax.ppermute(value, "tensor", [(i, i ^ 1) for i in range(4)])
    return value + lax.ppermute(value, "tensor", [(i, i ^ 2) for i in range(4)])


def exact_total(value):
    for axis in ("tensor", "shard", "context"):
        count = lax.axis_size(axis)
        if count & (count - 1):
            value = lax.psum(value, axis)
            continue
        span = 1
        while span < count:
            value = value + lax.ppermute(value, axis, [(i, i ^ span) for i in range(count)])
            span *= 2
    return value


def chip_total(grad):
    f32 = jnp.float32
    shard = lax.axis_index("shard")
    mine = half_of(grad, shard)
    other = half_of(grad, 1 - shard)
    got = lax.ppermute(other.astype(jnp.bfloat16), "shard", [(0, 1), (1, 0)])
    return mine.astype(f32) + got.astype(f32)


def line_total(staged):
    return lax.psum_scatter(
        staged.astype(jnp.bfloat16), "context", scatter_dimension=0, tiled=True
    ).astype(jnp.float32)


def rows_total(grad):
    return line_total(chip_total(grad))


def pass_grads(grad_key, grad_value):
    return (
        passed_along(grad_key.astype(jnp.bfloat16), "context", 1).astype(grad_key.dtype),
        passed_along(grad_value.astype(jnp.bfloat16), "context", 1).astype(grad_value.dtype),
    )


def key_scores(query_heads, query_seg, query_pos, piece):
    key_flat, value_flat, key_seg, key_pos = piece
    heads = query_heads.shape[1]
    key_heads = key_flat.reshape(key_flat.shape[0], heads, HD)
    value_heads = value_flat.reshape(value_flat.shape[0], heads, HD)
    scores = jnp.einsum(
        "qhd,khd->hqk", query_heads, key_heads, preferred_element_type=jnp.float32
    ) * (1.0 / math.sqrt(HD))
    allowed = (query_seg[:, None] == key_seg[None, :]) & (key_pos[None, :] <= query_pos[:, None])
    return (jnp.where(allowed[None], scores, NEG), allowed, key_heads, value_heads)


def forward_fold(stats, piece, query_heads, query_seg, query_pos):
    peak, total, accum = stats
    scores, allowed, key_heads, value_heads = key_scores(query_heads, query_seg, query_pos, piece)
    new_peak = jnp.maximum(peak, jnp.max(scores, axis=-1))
    weights = jnp.where(allowed[None], jnp.exp(scores - new_peak[..., None]), 0.0)
    factor = jnp.exp(peak - new_peak)
    total = total * factor + jnp.sum(weights, axis=-1)
    accum = accum * factor[..., None] + jnp.einsum(
        "hqk,khd->hqd",
        weights.astype(jnp.bfloat16),
        value_heads,
        preferred_element_type=jnp.float32,
    )
    return (new_peak, total, accum)


def backward_piece(piece, query_heads, grad_heads, log_total, inner, query_seg, query_pos):
    scores, allowed, key_heads, value_heads = key_scores(query_heads, query_seg, query_pos, piece)
    probs = jnp.where(allowed[None], jnp.exp(scores - log_total[..., None]), 0.0)
    grad_value = jnp.einsum(
        "hqk,qhd->khd", probs.astype(jnp.bfloat16), grad_heads, preferred_element_type=jnp.float32
    )
    grad_probs = jnp.einsum(
        "qhd,khd->hqk", grad_heads, value_heads, preferred_element_type=jnp.float32
    )
    grad_scores = (probs * (grad_probs - inner[..., None]) * (1.0 / math.sqrt(HD))).astype(
        jnp.bfloat16
    )
    grad_query = jnp.einsum(
        "hqk,khd->qhd", grad_scores, key_heads, preferred_element_type=jnp.float32
    )
    grad_key = jnp.einsum(
        "hqk,qhd->khd", grad_scores, query_heads, preferred_element_type=jnp.float32
    )
    key_rows = grad_key.shape[0]
    return (grad_query, grad_key.reshape(key_rows, -1), grad_value.reshape(key_rows, -1))


class RingAttention:
    def __init__(self, query, key_flat, value_flat, segment, position, cosine, sine):
        self.query = query
        self.piece = (key_flat, value_flat, segment, position)
        self.segment = segment
        self.position = position
        self.cosine = cosine
        self.sine = sine

    def forward(self):
        f32 = jnp.float32
        query, segment, position = self.query, self.segment, self.position
        rows, heads = query.shape[0], query.shape[1]
        start_stats = (
            jnp.full((heads, rows), NEG, f32),
            jnp.zeros((heads, rows), f32),
            jnp.zeros((heads, rows, HD), f32),
        )
        stats = forward_fold(start_stats, self.piece, query, segment, position)

        def cycle_turn(index, carry):
            moving, current = carry
            moving = passed_along(moving, "context", 1)
            current = forward_fold(current, moving, query, segment, position)
            return (moving, current)

        peak, total, accum = lax.fori_loop(
            0, lax.axis_size("context") - 1, cycle_turn, (self.piece, stats)
        )[1]
        self.attended = jnp.transpose(accum / total[..., None], (1, 0, 2)).astype(jnp.bfloat16)
        self.log_total = peak + jnp.log(total)
        return self.attended

    def backward(self, grad_heads, early):
        bf16 = jnp.bfloat16
        query, segment, position = self.query, self.segment, self.position
        rows, heads = query.shape[0], query.shape[1]
        inner = jnp.sum(grad_heads.astype(jnp.float32) * self.attended.astype(jnp.float32), axis=-1).T

        def piece_grads(piece):
            return backward_piece(piece, query, grad_heads, self.log_total, inner, segment, position)

        grad_query, grad_key, grad_value = piece_grads(self.piece)

        def grad_turn(index, carry):
            moving, acc_query, acc_key, acc_value = carry
            moving = passed_along(moving, "context", 1)
            acc_key, acc_value = pass_grads(acc_key, acc_value)
            part_query, part_key, part_value = piece_grads(moving)
            return (moving, acc_query + part_query, acc_key + part_key, acc_value + part_value)

        carried = lax.fori_loop(
            0,
            lax.axis_size("context") - 1,
            grad_turn,
            (self.piece, grad_query, grad_key, grad_value),
        )
        grad_query = carried[1]
        grad_key, grad_value = pass_grads(carried[2], carried[3])
        grad_qin = rotate_back(grad_query, self.cosine, self.sine).astype(bf16)
        grad_kin = rotate_back(grad_key.reshape(rows, heads, HD), self.cosine, self.sine).astype(bf16)
        grad_vin = grad_value.astype(bf16).reshape(rows, heads, HD)
        return grad_qin, grad_kin, grad_vin, early


class HeadAttention:
    BLOCK = 512

    def __init__(self, query, key_heads, value_heads, segment, position, cosine, sine):
        ways = lax.axis_size("context")
        rows, heads = query.shape[0], query.shape[1]
        self.ways = ways
        self.rows = rows
        self.heads = heads
        self.group = heads // ways
        self.piece = rows // 2
        stacked = jnp.stack([query, key_heads, value_heads], axis=1)
        stacked = stacked.reshape(rows, 3, ways, self.group, HD)
        stacked = lax.all_to_all(stacked, "context", 2, 0, tiled=True)
        stacked = stacked.reshape(rows * ways, 3, self.group, HD)
        tags = jnp.stack([segment, position], axis=0)[None]
        tags = jnp.broadcast_to(tags, (ways, 2, rows))
        tags = lax.all_to_all(tags, "context", 0, 0, tiled=True)
        tags = jnp.transpose(tags, (1, 0, 2)).reshape(2, rows * ways)
        pieces = 2 * ways
        piece_of_slot = tags[1].reshape(pieces, self.piece)[:, 0] // self.piece
        slots = jnp.arange(pieces, dtype=jnp.int32)
        slot_of_piece = jnp.sum(
            jnp.where(piece_of_slot[None, :] == slots[:, None], slots[None, :], 0), axis=1
        )
        self.piece_of_slot = piece_of_slot
        self.slot_of_piece = slot_of_piece
        stacked = self._reorder(stacked, slot_of_piece)
        tags = self._reorder(tags.T, slot_of_piece).T
        self.query = stacked[:, 0]
        self.keys = stacked[:, 1]
        self.values = stacked[:, 2]
        self.seg_all = tags[0]
        self.pos_all = tags[1]
        self.cos_all, self.sin_all = rope_tables(self.pos_all)

    def _reorder(self, value, source):
        parts = [
            lax.dynamic_slice_in_dim(value, source[index] * self.piece, self.piece, axis=0)
            for index in range(source.shape[0])
        ]
        return jnp.concatenate(parts, axis=0)

    def _blocks(self):
        total = self.rows * self.ways
        block = min(self.BLOCK, total)
        return [(start, block) for start in range(0, total, block)]

    def _scores(self, start, size):
        reach = start + size
        query = self.query[start:reach]
        seg_q = self.seg_all[start:reach]
        pos_q = self.pos_all[start:reach]
        scores = jnp.einsum(
            "qhd,khd->hqk", query, self.keys[:reach], preferred_element_type=jnp.float32
        ) * (1.0 / math.sqrt(HD))
        allowed = (seg_q[:, None] == self.seg_all[None, :reach]) & (
            self.pos_all[None, :reach] <= pos_q[:, None]
        )
        return query, jnp.where(allowed[None], scores, NEG), allowed

    def forward(self):
        outs = []
        logs = []
        for start, size in self._blocks():
            reach = start + size
            _, scores, allowed = self._scores(start, size)
            peak = jnp.max(scores, axis=-1)
            weights = jnp.where(allowed[None], jnp.exp(scores - peak[..., None]), 0.0)
            total = jnp.sum(weights, axis=-1)
            mixed = jnp.einsum(
                "hqk,khd->qhd",
                weights.astype(jnp.bfloat16),
                self.values[:reach],
                preferred_element_type=jnp.float32,
            )
            outs.append((mixed / total.T[:, :, None]).astype(jnp.bfloat16))
            logs.append(peak + jnp.log(total))
        self.attended = jnp.concatenate(outs, axis=0)
        self.log_total = jnp.concatenate(logs, axis=1)
        back = self._reorder(self.attended, self.piece_of_slot)
        back = back.reshape(self.rows * self.ways, 1, self.group, HD)
        back = lax.all_to_all(back, "context", 0, 1, tiled=True)
        return back.reshape(self.rows, self.heads, HD)

    def backward(self, grad_heads, early):
        f32 = jnp.float32
        bf16 = jnp.bfloat16
        scale = 1.0 / math.sqrt(HD)
        grad = grad_heads.reshape(self.rows, self.ways, self.group, HD)
        grad = lax.all_to_all(grad, "context", 1, 0, tiled=True)
        grad, early = lax.optimization_barrier((grad, early))
        grad = grad.reshape(self.rows * self.ways, self.group, HD)
        grad = self._reorder(grad, self.slot_of_piece)
        inner = jnp.sum(grad.astype(f32) * self.attended.astype(f32), axis=-1).T
        total_rows = self.rows * self.ways
        grad_key = jnp.zeros(self.keys.shape, f32)
        grad_value = jnp.zeros(self.values.shape, f32)
        grad_queries = []
        for start, size in self._blocks():
            reach = start + size
            query, scores, allowed = self._scores(start, size)
            log_block = self.log_total[:, start:reach]
            inner_block = inner[:, start:reach]
            grad_block = grad[start:reach]
            probs = jnp.where(allowed[None], jnp.exp(scores - log_block[..., None]), 0.0)
            part_value = jnp.einsum(
                "hqk,qhd->khd", probs.astype(bf16), grad_block, preferred_element_type=f32
            )
            grad_probs = jnp.einsum(
                "qhd,khd->hqk", grad_block, self.values[:reach], preferred_element_type=f32
            )
            grad_scores = (probs * (grad_probs - inner_block[..., None]) * scale).astype(bf16)
            grad_queries.append(
                jnp.einsum(
                    "hqk,khd->qhd", grad_scores, self.keys[:reach], preferred_element_type=f32
                )
            )
            part_key = jnp.einsum("hqk,qhd->khd", grad_scores, query, preferred_element_type=f32)
            pad = ((0, total_rows - reach), (0, 0), (0, 0))
            grad_value = grad_value + jnp.pad(part_value, pad)
            grad_key = grad_key + jnp.pad(part_key, pad)
        grad_query = jnp.concatenate(grad_queries, axis=0)
        grad_qin = rotate_back(grad_query, self.cos_all, self.sin_all).astype(bf16)
        grad_kin = rotate_back(grad_key, self.cos_all, self.sin_all).astype(bf16)
        grad_vin = grad_value.astype(bf16)
        returned = []
        for grad_in in (grad_qin, grad_kin, grad_vin):
            grad_in = self._reorder(grad_in, self.piece_of_slot)
            grad_in = grad_in.reshape(self.rows * self.ways, 1, self.group, HD)
            grad_in = lax.all_to_all(grad_in, "context", 0, 1, tiled=True)
            returned.append(grad_in.reshape(self.rows, self.heads, HD))
        return returned[0], returned[1], returned[2], early


def mlp_chunks(hidden_cols):
    for count in (2, 1):
        if hidden_cols % (count * 128) == 0:
            return count
    return 1


def on_device(
    inputs, segments, positions, w_q, w_k, w_v, w_o, w_gate, w_up, w_down, g_attn, g_mlp, d_out
):
    f32 = jnp.float32
    bf16 = jnp.bfloat16
    rows = inputs.shape[1]
    width = inputs.shape[2]
    cols = w_q.shape[1]
    hidden_cols = w_gate.shape[1]
    tokens = inputs.reshape(rows, width)
    segment = segments.reshape(rows)
    position = positions.reshape(rows)
    full_qkvo = lax.all_gather(
        jnp.concatenate([w_q, w_k, w_v, w_o], axis=1), ROWS, axis=0, tiled=True
    )
    full_qkv = full_qkvo[:, : 3 * cols]
    full_o = full_qkvo[:, 3 * cols :]
    gains = lax.all_gather(
        jnp.concatenate([g_attn, g_mlp])[None], ROWS, axis=0, tiled=True
    )
    gain_attn = gains[:, : g_attn.shape[0]].reshape(width)
    gain_mlp = gains[:, g_attn.shape[0] :].reshape(width)
    count = mlp_chunks(hidden_cols)
    step = hidden_cols // count
    fetched = []
    for index in range(count):
        part = slice(index * step, (index + 1) * step)
        pair = lax.all_gather(
            jnp.concatenate([w_gate[:, part], w_up[:, part]], axis=1), ROWS, axis=0, tiled=True
        )
        fetched.append(
            (pair[:, :step], pair[:, step:], lax.all_gather(w_down[:, part], ROWS, axis=0, tiled=True))
        )
    heads = cols // HD
    cosine, sine = rope_tables(position)
    resid1 = tokens.astype(f32)
    norm1, inv1 = normalize(resid1)
    h1 = (norm1 * gain_attn.astype(f32)).astype(bf16)
    projected = jnp.dot(h1, full_qkv, preferred_element_type=f32)
    query = rotate(projected[:, :cols].reshape(rows, heads, HD), cosine, sine).astype(bf16)
    key_heads = rotate(projected[:, cols : 2 * cols].reshape(rows, heads, HD), cosine, sine).astype(
        bf16
    )
    value_heads = projected[:, 2 * cols :].astype(bf16).reshape(rows, heads, HD)
    if heads % lax.axis_size("context") == 0:
        attention = HeadAttention(query, key_heads, value_heads, segment, position, cosine, sine)
    else:
        attention = RingAttention(
            query,
            key_heads.reshape(rows, cols),
            value_heads.reshape(rows, cols),
            segment,
            position,
            cosine,
            sine,
        )
    attended = attention.forward()
    attended_flat = attended.reshape(rows, cols)
    resid2 = resid1 + tensor_total(contract_last(attended_flat, full_o))
    norm2, inv2 = normalize(resid2)
    h2_part = (norm2 * gain_mlp.astype(f32)).astype(bf16)
    grad_y = d_out.reshape(rows, width)
    mlp_partial = None
    h2_grad_partial = None
    staged = []
    for full_gate, full_up, full_down in fetched:
        if staged:
            full_gate, staged[-1] = lax.optimization_barrier((full_gate, staged[-1]))
        gate = jnp.dot(h2_part, full_gate, preferred_element_type=f32)
        up = jnp.dot(h2_part, full_up, preferred_element_type=f32)
        active = jax.nn.silu(gate)
        hidden = (active * up).astype(bf16)
        out_part = contract_last(hidden, full_down)
        mlp_partial = out_part if mlp_partial is None else mlp_partial + out_part
        grad_hidden = jnp.dot(grad_y, full_down, preferred_element_type=f32)
        sigma = jax.nn.sigmoid(gate)
        grad_gate = (grad_hidden * up * sigma * (1.0 + gate * (1.0 - sigma))).astype(bf16)
        grad_up = (grad_hidden * active).astype(bf16)
        back_part = contract_last(grad_gate, full_gate) + contract_last(grad_up, full_up)
        pending = (
            contract_first(h2_part, grad_gate),
            contract_first(h2_part, grad_up),
            contract_first(grad_y, hidden),
        )
        h2_grad_partial = back_part if h2_grad_partial is None else h2_grad_partial + back_part
        staged.append(chip_total(jnp.concatenate(pending, axis=1)))
    both = tensor_total(jnp.concatenate([h2_grad_partial, mlp_partial], axis=1))
    grad_h2 = both[:, :width]
    mlp_total = both[:, width:]
    grad_h2, staged[-1] = lax.optimization_barrier((grad_h2, staged[-1]))
    reduced = [line_total(chunk) for chunk in staged]
    result = (resid2 + mlp_total).astype(bf16)
    grad_gmlp = jnp.sum(grad_h2 * norm2, axis=0)
    grad_resid = grad_y.astype(f32) + norm_back(grad_h2, norm2, inv2, gain_mlp)
    grad_resid_part = grad_resid.astype(bf16)
    grad_heads = (
        jnp.dot(grad_resid_part, full_o, preferred_element_type=f32)
        .astype(bf16)
        .reshape(rows, heads, HD)
    )
    grad_heads, partial_o = lax.optimization_barrier(
        (grad_heads, contract_first(grad_resid_part, attended_flat))
    )
    early = (chip_total(partial_o), reduced[:-1])
    grad_qin, grad_kin, grad_vin, early = attention.backward(grad_heads, early)
    staged_o, reduced[:-1] = early
    reduced_o = line_total(staged_o)
    grad_qkv = jnp.concatenate(
        [grad_qin.reshape(rows, cols), grad_kin.reshape(rows, cols), grad_vin.reshape(rows, cols)],
        axis=1,
    )
    h1_grad_partial = contract_last(grad_qkv, full_qkv)
    first_tensor = (lax.axis_index("tensor") == 0).astype(f32)
    gain_parts = jnp.stack(
        [jnp.sum(h1_grad_partial * norm1, axis=0), grad_gmlp * first_tensor], axis=1
    )
    gains_total = exact_total(gain_parts)
    h1_grad_partial, staged_qkv = lax.optimization_barrier(
        (h1_grad_partial, chip_total(contract_first(h1, grad_qkv)))
    )
    grad_h1 = tensor_total(h1_grad_partial)
    grad_h1, reduced_o, reduced[-1], result = lax.optimization_barrier(
        (grad_h1, reduced_o, reduced[-1], result)
    )
    grad_x_part = (grad_resid + norm_back(grad_h1, norm1, inv1, gain_attn)).astype(bf16)
    reduced_qkv = line_total(staged_qkv)
    blocks = lax.axis_size("shard") * lax.axis_size("context")
    block = lax.axis_index("shard") * lax.axis_size("context") + lax.axis_index("context")
    piece = width // blocks
    reduced_gains = lax.dynamic_slice_in_dim(gains_total, block * piece, piece, axis=0)
    reduced_gate, reduced_up, reduced_down = (
        jnp.concatenate([chunk[:, which * step : (which + 1) * step] for chunk in reduced], axis=1)
        for which in range(3)
    )
    return (
        result.reshape(1, rows, width),
        grad_x_part.reshape(1, rows, width),
        reduced_qkv[:, :cols],
        reduced_qkv[:, cols : 2 * cols],
        reduced_qkv[:, 2 * cols :],
        reduced_o,
        reduced_gate,
        reduced_up,
        reduced_down,
        reduced_gains[:, 0],
        reduced_gains[:, 1],
    )


def solution(mesh):
    placed = (
        P("shard", "context", None),
        P("shard", "context"),
        P("shard", "context"),
        P(ROWS, "tensor"),
        P(ROWS, "tensor"),
        P(ROWS, "tensor"),
        P(ROWS, "tensor"),
        P(ROWS, "tensor"),
        P(ROWS, "tensor"),
        P(ROWS, "tensor"),
        P(ROWS),
        P(ROWS),
        P("shard", "context", None),
    )
    return jax.shard_map(
        on_device,
        mesh=mesh,
        in_specs=placed,
        out_specs=(
            P("shard", "context", None),
            P("shard", "context", None),
            P(ROWS, "tensor"),
            P(ROWS, "tensor"),
            P(ROWS, "tensor"),
            P(ROWS, "tensor"),
            P(ROWS, "tensor"),
            P(ROWS, "tensor"),
            P(ROWS, "tensor"),
            P(ROWS),
            P(ROWS),
        ),
        check_vma=False,
    )
```

```python
import math

import jax
import jax.numpy as jnp
from jax import lax
from jax.sharding import PartitionSpec as P

HD = 64


EPS = 1e-05
THETA = 130000.0
NEG = -1e30
ROWS = ("shard", "context")


def passed_along(value, axis, steps):
    count = lax.axis_size(axis)
    pairs = [(source, (source + steps) % count) for source in range(count)]
    return lax.ppermute(value, axis, pairs)


def rope_tables(position):
    index = jnp.arange(HD // 2, dtype=jnp.float32)
    inverse = jnp.power(jnp.float32(THETA), -2.0 * index / HD)
    angle = position.astype(jnp.float32)[:, None] * inverse[None, :]
    return (jnp.cos(angle), jnp.sin(angle))


def rotate(tensor, cosine, sine):
    half = tensor.shape[-1] // 2
    first = tensor[..., :half]
    second = tensor[..., half:]
    cosine = cosine[:, None, :]
    sine = sine[:, None, :]
    return jnp.concatenate(
        [first * cosine - second * sine, second * cosine + first * sine], axis=-1
    )


def rotate_back(grad, cosine, sine):
    half = grad.shape[-1] // 2
    first = grad[..., :half]
    second = grad[..., half:]
    cosine = cosine[:, None, :]
    sine = sine[:, None, :]
    return jnp.concatenate(
        [first * cosine + second * sine, second * cosine - first * sine], axis=-1
    )


def normalize(value):
    inv_rms = lax.rsqrt(jnp.mean(value * value, axis=-1, keepdims=True) + EPS)
    return (value * inv_rms, inv_rms)


def norm_back(grad, normed, inv_rms, gain):
    scaled = grad * gain.astype(jnp.float32)
    return inv_rms * (scaled - normed * jnp.mean(scaled * normed, axis=-1, keepdims=True))


def contract_last(left, right):
    return lax.dot_general(
        left, right, (((1,), (1,)), ((), ())), preferred_element_type=jnp.float32
    )


def contract_first(left, right):
    return lax.dot_general(
        left, right, (((0,), (0,)), ((), ())), preferred_element_type=jnp.float32
    )


def half_of(value, bit):
    size = value.shape[0] // 2
    return lax.dynamic_slice_in_dim(value, bit * size, size, axis=0)


def joined(mine, other, bit):
    low = jnp.where(bit == 0, mine, other)
    high = jnp.where(bit == 0, other, mine)
    return jnp.concatenate([low, high], axis=0)


def tensor_total(partial_sum):
    count = lax.axis_size("tensor")
    rows = partial_sum.shape[0]
    if count != 4 or rows % 8:
        return lax.psum(partial_sum.astype(jnp.bfloat16), "tensor").astype(jnp.float32)
    f32 = jnp.float32
    bf16 = jnp.bfloat16
    index = lax.axis_index("tensor")
    x_bit = index % 2
    y_bit = index // 2
    x_pairs = [(i, i ^ 1) for i in range(4)]
    y_pairs = [(i, i ^ 2) for i in range(4)]

    def swap(value, pairs):
        return lax.ppermute(value.astype(bf16), "tensor", pairs).astype(f32)

    first = partial_sum[: rows // 2]
    second = partial_sum[rows // 2 :]
    first = half_of(first, x_bit) + swap(half_of(first, 1 - x_bit), x_pairs)
    second = half_of(second, y_bit) + swap(half_of(second, 1 - y_bit), y_pairs)
    first = half_of(first, y_bit) + swap(half_of(first, 1 - y_bit), y_pairs)
    second = half_of(second, x_bit) + swap(half_of(second, 1 - x_bit), x_pairs)
    first = first.astype(bf16)
    second = second.astype(bf16)
    first = joined(first, lax.ppermute(first, "tensor", y_pairs), y_bit)
    second = joined(second, lax.ppermute(second, "tensor", x_pairs), x_bit)
    first = joined(first, lax.ppermute(first, "tensor", x_pairs), x_bit)
    second = joined(second, lax.ppermute(second, "tensor", y_pairs), y_bit)
    return jnp.concatenate([first, second], axis=0).astype(f32)


def tensor_exact_total(value):
    if lax.axis_size("tensor") != 4:
        return lax.psum(value, "tensor")
    value = value + lax.ppermute(value, "tensor", [(i, i ^ 1) for i in range(4)])
    return value + lax.ppermute(value, "tensor", [(i, i ^ 2) for i in range(4)])


def exact_total(value):
    for axis in ("tensor", "shard", "context"):
        count = lax.axis_size(axis)
        if count & (count - 1):
            value = lax.psum(value, axis)
            continue
        span = 1
        while span < count:
            value = value + lax.ppermute(value, axis, [(i, i ^ span) for i in range(count)])
            span *= 2
    return value


def chip_total(grad):
    f32 = jnp.float32
    shard = lax.axis_index("shard")
    mine = half_of(grad, shard)
    other = half_of(grad, 1 - shard)
    got = lax.ppermute(other.astype(jnp.bfloat16), "shard", [(0, 1), (1, 0)])
    return mine.astype(f32) + got.astype(f32)


def line_total(staged):
    return lax.psum_scatter(
        staged.astype(jnp.bfloat16), "context", scatter_dimension=0, tiled=True
    ).astype(jnp.float32)


def rows_total(grad):
    return line_total(chip_total(grad))


def pass_grads(grad_key, grad_value):
    return (
        passed_along(grad_key.astype(jnp.bfloat16), "context", 1).astype(grad_key.dtype),
        passed_along(grad_value.astype(jnp.bfloat16), "context", 1).astype(grad_value.dtype),
    )


def key_scores(query_heads, query_seg, query_pos, piece):
    key_flat, value_flat, key_seg, key_pos = piece
    heads = query_heads.shape[1]
    key_heads = key_flat.reshape(key_flat.shape[0], heads, HD)
    value_heads = value_flat.reshape(value_flat.shape[0], heads, HD)
    scores = jnp.einsum(
        "qhd,khd->hqk", query_heads, key_heads, preferred_element_type=jnp.float32
    ) * (1.0 / math.sqrt(HD))
    allowed = (query_seg[:, None] == key_seg[None, :]) & (key_pos[None, :] <= query_pos[:, None])
    return (jnp.where(allowed[None], scores, NEG), allowed, key_heads, value_heads)


def forward_fold(stats, piece, query_heads, query_seg, query_pos):
    peak, total, accum = stats
    scores, allowed, key_heads, value_heads = key_scores(query_heads, query_seg, query_pos, piece)
    new_peak = jnp.maximum(peak, jnp.max(scores, axis=-1))
    weights = jnp.where(allowed[None], jnp.exp(scores - new_peak[..., None]), 0.0)
    factor = jnp.exp(peak - new_peak)
    total = total * factor + jnp.sum(weights, axis=-1)
    accum = accum * factor[..., None] + jnp.einsum(
        "hqk,khd->hqd",
        weights.astype(jnp.bfloat16),
        value_heads,
        preferred_element_type=jnp.float32,
    )
    return (new_peak, total, accum)


def backward_piece(piece, query_heads, grad_heads, log_total, inner, query_seg, query_pos):
    scores, allowed, key_heads, value_heads = key_scores(query_heads, query_seg, query_pos, piece)
    probs = jnp.where(allowed[None], jnp.exp(scores - log_total[..., None]), 0.0)
    grad_value = jnp.einsum(
        "hqk,qhd->khd", probs.astype(jnp.bfloat16), grad_heads, preferred_element_type=jnp.float32
    )
    grad_probs = jnp.einsum(
        "qhd,khd->hqk", grad_heads, value_heads, preferred_element_type=jnp.float32
    )
    grad_scores = (probs * (grad_probs - inner[..., None]) * (1.0 / math.sqrt(HD))).astype(
        jnp.bfloat16
    )
    grad_query = jnp.einsum(
        "hqk,khd->qhd", grad_scores, key_heads, preferred_element_type=jnp.float32
    )
    grad_key = jnp.einsum(
        "hqk,qhd->khd", grad_scores, query_heads, preferred_element_type=jnp.float32
    )
    key_rows = grad_key.shape[0]
    return (grad_query, grad_key.reshape(key_rows, -1), grad_value.reshape(key_rows, -1))


class RingAttention:
    def __init__(self, query, key_flat, value_flat, segment, position, cosine, sine):
        self.query = query
        self.piece = (key_flat, value_flat, segment, position)
        self.segment = segment
        self.position = position
        self.cosine = cosine
        self.sine = sine

    def forward(self):
        f32 = jnp.float32
        query, segment, position = self.query, self.segment, self.position
        rows, heads = query.shape[0], query.shape[1]
        start_stats = (
            jnp.full((heads, rows), NEG, f32),
            jnp.zeros((heads, rows), f32),
            jnp.zeros((heads, rows, HD), f32),
        )
        stats = forward_fold(start_stats, self.piece, query, segment, position)

        def cycle_turn(index, carry):
            moving, current = carry
            moving = passed_along(moving, "context", 1)
            current = forward_fold(current, moving, query, segment, position)
            return (moving, current)

        peak, total, accum = lax.fori_loop(
            0, lax.axis_size("context") - 1, cycle_turn, (self.piece, stats)
        )[1]
        self.attended = jnp.transpose(accum / total[..., None], (1, 0, 2)).astype(jnp.bfloat16)
        self.log_total = peak + jnp.log(total)
        return self.attended

    def backward(self, grad_heads, early):
        bf16 = jnp.bfloat16
        query, segment, position = self.query, self.segment, self.position
        rows, heads = query.shape[0], query.shape[1]
        inner = jnp.sum(grad_heads.astype(jnp.float32) * self.attended.astype(jnp.float32), axis=-1).T

        def piece_grads(piece):
            return backward_piece(piece, query, grad_heads, self.log_total, inner, segment, position)

        grad_query, grad_key, grad_value = piece_grads(self.piece)

        def grad_turn(index, carry):
            moving, acc_query, acc_key, acc_value = carry
            moving = passed_along(moving, "context", 1)
            acc_key, acc_value = pass_grads(acc_key, acc_value)
            part_query, part_key, part_value = piece_grads(moving)
            return (moving, acc_query + part_query, acc_key + part_key, acc_value + part_value)

        carried = lax.fori_loop(
            0,
            lax.axis_size("context") - 1,
            grad_turn,
            (self.piece, grad_query, grad_key, grad_value),
        )
        grad_query = carried[1]
        grad_key, grad_value = pass_grads(carried[2], carried[3])
        grad_qin = rotate_back(grad_query, self.cosine, self.sine).astype(bf16)
        grad_kin = rotate_back(grad_key.reshape(rows, heads, HD), self.cosine, self.sine).astype(bf16)
        grad_vin = grad_value.astype(bf16).reshape(rows, heads, HD)
        return grad_qin, grad_kin, grad_vin, early


class HeadAttention:
    BLOCK = 256

    def __init__(self, query, key_heads, value_heads, segment, position, cosine, sine):
        ways = lax.axis_size("context")
        rows, heads = query.shape[0], query.shape[1]
        self.ways = ways
        self.rows = rows
        self.heads = heads
        self.group = heads // ways
        self.piece = rows // 2
        stacked = jnp.stack([query, key_heads, value_heads], axis=1)
        stacked = stacked.reshape(rows, 3, ways, self.group, HD)
        stacked = lax.all_to_all(stacked, "context", 2, 0, tiled=True)
        stacked = stacked.reshape(rows * ways, 3, self.group, HD)
        tags = jnp.stack([segment, position], axis=0)[None]
        tags = jnp.broadcast_to(tags, (ways, 2, rows))
        tags = lax.all_to_all(tags, "context", 0, 0, tiled=True)
        tags = jnp.transpose(tags, (1, 0, 2)).reshape(2, rows * ways)
        pieces = 2 * ways
        piece_of_slot = tags[1].reshape(pieces, self.piece)[:, 0] // self.piece
        slots = jnp.arange(pieces, dtype=jnp.int32)
        slot_of_piece = jnp.sum(
            jnp.where(piece_of_slot[None, :] == slots[:, None], slots[None, :], 0), axis=1
        )
        self.piece_of_slot = piece_of_slot
        self.slot_of_piece = slot_of_piece
        stacked = self._reorder(stacked, slot_of_piece)
        tags = self._reorder(tags.T, slot_of_piece).T
        self.query = stacked[:, 0]
        self.keys = stacked[:, 1]
        self.values = stacked[:, 2]
        self.seg_all = tags[0]
        self.pos_all = tags[1]
        self.cos_all, self.sin_all = rope_tables(self.pos_all)

    def _reorder(self, value, source):
        parts = [
            lax.dynamic_slice_in_dim(value, source[index] * self.piece, self.piece, axis=0)
            for index in range(source.shape[0])
        ]
        return jnp.concatenate(parts, axis=0)

    def _blocks(self):
        total = self.rows * self.ways
        block = min(self.BLOCK, total)
        return [(start, block) for start in range(0, total, block)]

    def _scores(self, start, size):
        reach = start + size
        query = self.query[start:reach]
        seg_q = self.seg_all[start:reach]
        pos_q = self.pos_all[start:reach]
        scores = jnp.einsum(
            "qhd,khd->hqk", query, self.keys[:reach], preferred_element_type=jnp.float32
        ) * (1.0 / math.sqrt(HD))
        allowed = (seg_q[:, None] == self.seg_all[None, :reach]) & (
            self.pos_all[None, :reach] <= pos_q[:, None]
        )
        return query, jnp.where(allowed[None], scores, NEG), allowed

    def forward(self):
        outs = []
        logs = []
        for start, size in self._blocks():
            reach = start + size
            _, scores, allowed = self._scores(start, size)
            peak = jnp.max(scores, axis=-1)
            weights = jnp.where(allowed[None], jnp.exp(scores - peak[..., None]), 0.0)
            total = jnp.sum(weights, axis=-1)
            mixed = jnp.einsum(
                "hqk,khd->qhd",
                weights.astype(jnp.bfloat16),
                self.values[:reach],
                preferred_element_type=jnp.float32,
            )
            outs.append((mixed / total.T[:, :, None]).astype(jnp.bfloat16))
            logs.append(peak + jnp.log(total))
        self.attended = jnp.concatenate(outs, axis=0)
        self.log_total = jnp.concatenate(logs, axis=1)
        back = self._reorder(self.attended, self.piece_of_slot)
        back = back.reshape(self.rows * self.ways, 1, self.group, HD)
        back = lax.all_to_all(back, "context", 0, 1, tiled=True)
        return back.reshape(self.rows, self.heads, HD)

    def backward(self, grad_heads, early):
        f32 = jnp.float32
        bf16 = jnp.bfloat16
        scale = 1.0 / math.sqrt(HD)
        grad = grad_heads.reshape(self.rows, self.ways, self.group, HD)
        grad = lax.all_to_all(grad, "context", 1, 0, tiled=True)
        grad, early = lax.optimization_barrier((grad, early))
        grad = grad.reshape(self.rows * self.ways, self.group, HD)
        grad = self._reorder(grad, self.slot_of_piece)
        inner = jnp.sum(grad.astype(f32) * self.attended.astype(f32), axis=-1).T
        total_rows = self.rows * self.ways
        grad_key = jnp.zeros(self.keys.shape, f32)
        grad_value = jnp.zeros(self.values.shape, f32)
        grad_queries = []
        for start, size in self._blocks():
            reach = start + size
            query, scores, allowed = self._scores(start, size)
            log_block = self.log_total[:, start:reach]
            inner_block = inner[:, start:reach]
            grad_block = grad[start:reach]
            probs = jnp.where(allowed[None], jnp.exp(scores - log_block[..., None]), 0.0)
            part_value = jnp.einsum(
                "hqk,qhd->khd", probs.astype(bf16), grad_block, preferred_element_type=f32
            )
            grad_probs = jnp.einsum(
                "qhd,khd->hqk", grad_block, self.values[:reach], preferred_element_type=f32
            )
            grad_scores = (probs * (grad_probs - inner_block[..., None]) * scale).astype(bf16)
            grad_queries.append(
                jnp.einsum(
                    "hqk,khd->qhd", grad_scores, self.keys[:reach], preferred_element_type=f32
                )
            )
            part_key = jnp.einsum("hqk,qhd->khd", grad_scores, query, preferred_element_type=f32)
            pad = ((0, total_rows - reach), (0, 0), (0, 0))
            grad_value = grad_value + jnp.pad(part_value, pad)
            grad_key = grad_key + jnp.pad(part_key, pad)
        grad_query = jnp.concatenate(grad_queries, axis=0)
        grad_qin = rotate_back(grad_query, self.cos_all, self.sin_all).astype(bf16)
        grad_kin = rotate_back(grad_key, self.cos_all, self.sin_all).astype(bf16)
        grad_vin = grad_value.astype(bf16)
        returned = []
        for grad_in in (grad_qin, grad_kin, grad_vin):
            grad_in = self._reorder(grad_in, self.piece_of_slot)
            grad_in = grad_in.reshape(self.rows * self.ways, 1, self.group, HD)
            grad_in = lax.all_to_all(grad_in, "context", 0, 1, tiled=True)
            returned.append(grad_in.reshape(self.rows, self.heads, HD))
        return returned[0], returned[1], returned[2], early


def mlp_chunks(hidden_cols):
    for count in (2, 1):
        if hidden_cols % (count * 128) == 0:
            return count
    return 1


def on_device(
    inputs, segments, positions, w_q, w_k, w_v, w_o, w_gate, w_up, w_down, g_attn, g_mlp, d_out
):
    f32 = jnp.float32
    bf16 = jnp.bfloat16
    rows = inputs.shape[1]
    width = inputs.shape[2]
    cols = w_q.shape[1]
    hidden_cols = w_gate.shape[1]
    tokens = inputs.reshape(rows, width)
    segment = segments.reshape(rows)
    position = positions.reshape(rows)
    full_qkvo = lax.all_gather(
        jnp.concatenate([w_q, w_k, w_v, w_o], axis=1), ROWS, axis=0, tiled=True
    )
    full_qkv = full_qkvo[:, : 3 * cols]
    full_o = full_qkvo[:, 3 * cols :]
    gains = lax.all_gather(
        jnp.concatenate([g_attn, g_mlp])[None], ROWS, axis=0, tiled=True
    )
    gain_attn = gains[:, : g_attn.shape[0]].reshape(width)
    gain_mlp = gains[:, g_attn.shape[0] :].reshape(width)
    count = mlp_chunks(hidden_cols)
    step = hidden_cols // count
    fetched = []
    for index in range(count):
        part = slice(index * step, (index + 1) * step)
        pair = lax.all_gather(
            jnp.concatenate([w_gate[:, part], w_up[:, part]], axis=1), ROWS, axis=0, tiled=True
        )
        fetched.append(
            (pair[:, :step], pair[:, step:], lax.all_gather(w_down[:, part], ROWS, axis=0, tiled=True))
        )
    heads = cols // HD
    cosine, sine = rope_tables(position)
    resid1 = tokens.astype(f32)
    norm1, inv1 = normalize(resid1)
    h1 = (norm1 * gain_attn.astype(f32)).astype(bf16)
    projected = jnp.dot(h1, full_qkv, preferred_element_type=f32)
    query = rotate(projected[:, :cols].reshape(rows, heads, HD), cosine, sine).astype(bf16)
    key_heads = rotate(projected[:, cols : 2 * cols].reshape(rows, heads, HD), cosine, sine).astype(
        bf16
    )
    value_heads = projected[:, 2 * cols :].astype(bf16).reshape(rows, heads, HD)
    if heads % lax.axis_size("context") == 0:
        attention = HeadAttention(query, key_heads, value_heads, segment, position, cosine, sine)
    else:
        attention = RingAttention(
            query,
            key_heads.reshape(rows, cols),
            value_heads.reshape(rows, cols),
            segment,
            position,
            cosine,
            sine,
        )
    attended = attention.forward()
    attended_flat = attended.reshape(rows, cols)
    resid2 = resid1 + tensor_total(contract_last(attended_flat, full_o))
    norm2, inv2 = normalize(resid2)
    h2_part = (norm2 * gain_mlp.astype(f32)).astype(bf16)
    grad_y = d_out.reshape(rows, width)
    mlp_partial = None
    h2_grad_partial = None
    staged = []
    for full_gate, full_up, full_down in fetched:
        if staged:
            full_gate, staged[-1] = lax.optimization_barrier((full_gate, staged[-1]))
        gate = jnp.dot(h2_part, full_gate, preferred_element_type=f32)
        up = jnp.dot(h2_part, full_up, preferred_element_type=f32)
        active = jax.nn.silu(gate)
        hidden = (active * up).astype(bf16)
        out_part = contract_last(hidden, full_down)
        mlp_partial = out_part if mlp_partial is None else mlp_partial + out_part
        grad_hidden = jnp.dot(grad_y, full_down, preferred_element_type=f32)
        sigma = jax.nn.sigmoid(gate)
        grad_gate = (grad_hidden * up * sigma * (1.0 + gate * (1.0 - sigma))).astype(bf16)
        grad_up = (grad_hidden * active).astype(bf16)
        back_part = contract_last(grad_gate, full_gate) + contract_last(grad_up, full_up)
        pending = (
            contract_first(h2_part, grad_gate),
            contract_first(h2_part, grad_up),
            contract_first(grad_y, hidden),
        )
        h2_grad_partial = back_part if h2_grad_partial is None else h2_grad_partial + back_part
        staged.append(chip_total(jnp.concatenate(pending, axis=1)))
    grad_h2 = tensor_total(h2_grad_partial)
    grad_h2, staged[-1] = lax.optimization_barrier((grad_h2, staged[-1]))
    reduced = [line_total(chunk) for chunk in staged]
    result = (resid2 + tensor_total(mlp_partial)).astype(bf16)
    grad_gmlp = jnp.sum(grad_h2 * norm2, axis=0)
    grad_resid = grad_y.astype(f32) + norm_back(grad_h2, norm2, inv2, gain_mlp)
    grad_resid_part = grad_resid.astype(bf16)
    grad_heads = (
        jnp.dot(grad_resid_part, full_o, preferred_element_type=f32)
        .astype(bf16)
        .reshape(rows, heads, HD)
    )
    grad_heads, partial_o = lax.optimization_barrier(
        (grad_heads, contract_first(grad_resid_part, attended_flat))
    )
    early = (chip_total(partial_o), reduced[:-1])
    grad_qin, grad_kin, grad_vin, early = attention.backward(grad_heads, early)
    staged_o, reduced[:-1] = early
    reduced_o = line_total(staged_o)
    grad_qkv = jnp.concatenate(
        [grad_qin.reshape(rows, cols), grad_kin.reshape(rows, cols), grad_vin.reshape(rows, cols)],
        axis=1,
    )
    h1_grad_partial = contract_last(grad_qkv, full_qkv)
    first_tensor = (lax.axis_index("tensor") == 0).astype(f32)
    gain_parts = jnp.stack(
        [jnp.sum(h1_grad_partial * norm1, axis=0), grad_gmlp * first_tensor], axis=1
    )
    gains_total = exact_total(gain_parts)
    h1_grad_partial, staged_qkv = lax.optimization_barrier(
        (h1_grad_partial, chip_total(contract_first(h1, grad_qkv)))
    )
    grad_h1 = tensor_total(h1_grad_partial)
    grad_h1, reduced_o, reduced[-1], result = lax.optimization_barrier(
        (grad_h1, reduced_o, reduced[-1], result)
    )
    grad_x_part = (grad_resid + norm_back(grad_h1, norm1, inv1, gain_attn)).astype(bf16)
    reduced_qkv = line_total(staged_qkv)
    blocks = lax.axis_size("shard") * lax.axis_size("context")
    block = lax.axis_index("shard") * lax.axis_size("context") + lax.axis_index("context")
    piece = width // blocks
    reduced_gains = lax.dynamic_slice_in_dim(gains_total, block * piece, piece, axis=0)
    reduced_gate, reduced_up, reduced_down = (
        jnp.concatenate([chunk[:, which * step : (which + 1) * step] for chunk in reduced], axis=1)
        for which in range(3)
    )
    return (
        result.reshape(1, rows, width),
        grad_x_part.reshape(1, rows, width),
        reduced_qkv[:, :cols],
        reduced_qkv[:, cols : 2 * cols],
        reduced_qkv[:, 2 * cols :],
        reduced_o,
        reduced_gate,
        reduced_up,
        reduced_down,
        reduced_gains[:, 0],
        reduced_gains[:, 1],
    )


def solution(mesh):
    placed = (
        P("shard", "context", None),
        P("shard", "context"),
        P("shard", "context"),
        P(ROWS, "tensor"),
        P(ROWS, "tensor"),
        P(ROWS, "tensor"),
        P(ROWS, "tensor"),
        P(ROWS, "tensor"),
        P(ROWS, "tensor"),
        P(ROWS, "tensor"),
        P(ROWS),
        P(ROWS),
        P("shard", "context", None),
    )
    return jax.shard_map(
        on_device,
        mesh=mesh,
        in_specs=placed,
        out_specs=(
            P("shard", "context", None),
            P("shard", "context", None),
            P(ROWS, "tensor"),
            P(ROWS, "tensor"),
            P(ROWS, "tensor"),
            P(ROWS, "tensor"),
            P(ROWS, "tensor"),
            P(ROWS, "tensor"),
            P(ROWS, "tensor"),
            P(ROWS),
            P(ROWS),
        ),
        check_vma=False,
    )
```

```python
import math

import jax
import jax.numpy as jnp
from jax import lax
from jax.sharding import PartitionSpec as P

HD = 64


EPS = 1e-05
THETA = 130000.0
NEG = -1e30
ROWS = ("shard", "context")


def passed_along(value, axis, steps):
    count = lax.axis_size(axis)
    pairs = [(source, (source + steps) % count) for source in range(count)]
    return lax.ppermute(value, axis, pairs)


def rope_tables(position):
    index = jnp.arange(HD // 2, dtype=jnp.float32)
    inverse = jnp.power(jnp.float32(THETA), -2.0 * index / HD)
    angle = position.astype(jnp.float32)[:, None] * inverse[None, :]
    return (jnp.cos(angle), jnp.sin(angle))


def rotate(tensor, cosine, sine):
    half = tensor.shape[-1] // 2
    first = tensor[..., :half]
    second = tensor[..., half:]
    cosine = cosine[:, None, :]
    sine = sine[:, None, :]
    return jnp.concatenate(
        [first * cosine - second * sine, second * cosine + first * sine], axis=-1
    )


def rotate_back(grad, cosine, sine):
    half = grad.shape[-1] // 2
    first = grad[..., :half]
    second = grad[..., half:]
    cosine = cosine[:, None, :]
    sine = sine[:, None, :]
    return jnp.concatenate(
        [first * cosine + second * sine, second * cosine - first * sine], axis=-1
    )


def normalize(value):
    inv_rms = lax.rsqrt(jnp.mean(value * value, axis=-1, keepdims=True) + EPS)
    return (value * inv_rms, inv_rms)


def norm_back(grad, normed, inv_rms, gain):
    scaled = grad * gain.astype(jnp.float32)
    return inv_rms * (scaled - normed * jnp.mean(scaled * normed, axis=-1, keepdims=True))


def contract_last(left, right):
    return lax.dot_general(
        left, right, (((1,), (1,)), ((), ())), preferred_element_type=jnp.float32
    )


def contract_first(left, right):
    return lax.dot_general(
        left, right, (((0,), (0,)), ((), ())), preferred_element_type=jnp.float32
    )


def half_of(value, bit):
    size = value.shape[0] // 2
    return lax.dynamic_slice_in_dim(value, bit * size, size, axis=0)


def joined(mine, other, bit):
    low = jnp.where(bit == 0, mine, other)
    high = jnp.where(bit == 0, other, mine)
    return jnp.concatenate([low, high], axis=0)


def tensor_total(partial_sum):
    count = lax.axis_size("tensor")
    rows = partial_sum.shape[0]
    if count != 4 or rows % 8:
        return lax.psum(partial_sum.astype(jnp.bfloat16), "tensor").astype(jnp.float32)
    f32 = jnp.float32
    bf16 = jnp.bfloat16
    index = lax.axis_index("tensor")
    x_bit = index % 2
    y_bit = index // 2
    x_pairs = [(i, i ^ 1) for i in range(4)]
    y_pairs = [(i, i ^ 2) for i in range(4)]

    def swap(value, pairs):
        return lax.ppermute(value.astype(bf16), "tensor", pairs).astype(f32)

    first = partial_sum[: rows // 2]
    second = partial_sum[rows // 2 :]
    first = half_of(first, x_bit) + swap(half_of(first, 1 - x_bit), x_pairs)
    second = half_of(second, y_bit) + swap(half_of(second, 1 - y_bit), y_pairs)
    first = half_of(first, y_bit) + swap(half_of(first, 1 - y_bit), y_pairs)
    second = half_of(second, x_bit) + swap(half_of(second, 1 - x_bit), x_pairs)
    first = first.astype(bf16)
    second = second.astype(bf16)
    first = joined(first, lax.ppermute(first, "tensor", y_pairs), y_bit)
    second = joined(second, lax.ppermute(second, "tensor", x_pairs), x_bit)
    first = joined(first, lax.ppermute(first, "tensor", x_pairs), x_bit)
    second = joined(second, lax.ppermute(second, "tensor", y_pairs), y_bit)
    return jnp.concatenate([first, second], axis=0).astype(f32)


def tensor_exact_total(value):
    if lax.axis_size("tensor") != 4:
        return lax.psum(value, "tensor")
    value = value + lax.ppermute(value, "tensor", [(i, i ^ 1) for i in range(4)])
    return value + lax.ppermute(value, "tensor", [(i, i ^ 2) for i in range(4)])


def exact_total(value):
    for axis in ("tensor", "shard", "context"):
        count = lax.axis_size(axis)
        if count & (count - 1):
            value = lax.psum(value, axis)
            continue
        span = 1
        while span < count:
            value = value + lax.ppermute(value, axis, [(i, i ^ span) for i in range(count)])
            span *= 2
    return value


def chip_total(grad):
    f32 = jnp.float32
    shard = lax.axis_index("shard")
    mine = half_of(grad, shard)
    other = half_of(grad, 1 - shard)
    got = lax.ppermute(other.astype(jnp.bfloat16), "shard", [(0, 1), (1, 0)])
    return mine.astype(f32) + got.astype(f32)


def line_total(staged):
    return lax.psum_scatter(
        staged.astype(jnp.bfloat16), "context", scatter_dimension=0, tiled=True
    ).astype(jnp.float32)


def rows_total(grad):
    return line_total(chip_total(grad))


def pass_grads(grad_key, grad_value):
    return (
        passed_along(grad_key.astype(jnp.bfloat16), "context", 1).astype(grad_key.dtype),
        passed_along(grad_value.astype(jnp.bfloat16), "context", 1).astype(grad_value.dtype),
    )


def key_scores(query_heads, query_seg, query_pos, piece):
    key_flat, value_flat, key_seg, key_pos = piece
    heads = query_heads.shape[1]
    key_heads = key_flat.reshape(key_flat.shape[0], heads, HD)
    value_heads = value_flat.reshape(value_flat.shape[0], heads, HD)
    scores = jnp.einsum(
        "qhd,khd->hqk", query_heads, key_heads, preferred_element_type=jnp.float32
    ) * (1.0 / math.sqrt(HD))
    allowed = (query_seg[:, None] == key_seg[None, :]) & (key_pos[None, :] <= query_pos[:, None])
    return (jnp.where(allowed[None], scores, NEG), allowed, key_heads, value_heads)


def forward_fold(stats, piece, query_heads, query_seg, query_pos):
    peak, total, accum = stats
    scores, allowed, key_heads, value_heads = key_scores(query_heads, query_seg, query_pos, piece)
    new_peak = jnp.maximum(peak, jnp.max(scores, axis=-1))
    weights = jnp.where(allowed[None], jnp.exp(scores - new_peak[..., None]), 0.0)
    factor = jnp.exp(peak - new_peak)
    total = total * factor + jnp.sum(weights, axis=-1)
    accum = accum * factor[..., None] + jnp.einsum(
        "hqk,khd->hqd",
        weights.astype(jnp.bfloat16),
        value_heads,
        preferred_element_type=jnp.float32,
    )
    return (new_peak, total, accum)


def backward_piece(piece, query_heads, grad_heads, log_total, inner, query_seg, query_pos):
    scores, allowed, key_heads, value_heads = key_scores(query_heads, query_seg, query_pos, piece)
    probs = jnp.where(allowed[None], jnp.exp(scores - log_total[..., None]), 0.0)
    grad_value = jnp.einsum(
        "hqk,qhd->khd", probs.astype(jnp.bfloat16), grad_heads, preferred_element_type=jnp.float32
    )
    grad_probs = jnp.einsum(
        "qhd,khd->hqk", grad_heads, value_heads, preferred_element_type=jnp.float32
    )
    grad_scores = (probs * (grad_probs - inner[..., None]) * (1.0 / math.sqrt(HD))).astype(
        jnp.bfloat16
    )
    grad_query = jnp.einsum(
        "hqk,khd->qhd", grad_scores, key_heads, preferred_element_type=jnp.float32
    )
    grad_key = jnp.einsum(
        "hqk,qhd->khd", grad_scores, query_heads, preferred_element_type=jnp.float32
    )
    key_rows = grad_key.shape[0]
    return (grad_query, grad_key.reshape(key_rows, -1), grad_value.reshape(key_rows, -1))


class RingAttention:
    def __init__(self, query, key_flat, value_flat, segment, position, cosine, sine):
        self.query = query
        self.piece = (key_flat, value_flat, segment, position)
        self.segment = segment
        self.position = position
        self.cosine = cosine
        self.sine = sine

    def forward(self):
        f32 = jnp.float32
        query, segment, position = self.query, self.segment, self.position
        rows, heads = query.shape[0], query.shape[1]
        start_stats = (
            jnp.full((heads, rows), NEG, f32),
            jnp.zeros((heads, rows), f32),
            jnp.zeros((heads, rows, HD), f32),
        )
        stats = forward_fold(start_stats, self.piece, query, segment, position)

        def cycle_turn(index, carry):
            moving, current = carry
            moving = passed_along(moving, "context", 1)
            current = forward_fold(current, moving, query, segment, position)
            return (moving, current)

        peak, total, accum = lax.fori_loop(
            0, lax.axis_size("context") - 1, cycle_turn, (self.piece, stats)
        )[1]
        self.attended = jnp.transpose(accum / total[..., None], (1, 0, 2)).astype(jnp.bfloat16)
        self.log_total = peak + jnp.log(total)
        return self.attended

    def backward(self, grad_heads, early):
        bf16 = jnp.bfloat16
        query, segment, position = self.query, self.segment, self.position
        rows, heads = query.shape[0], query.shape[1]
        inner = jnp.sum(grad_heads.astype(jnp.float32) * self.attended.astype(jnp.float32), axis=-1).T

        def piece_grads(piece):
            return backward_piece(piece, query, grad_heads, self.log_total, inner, segment, position)

        grad_query, grad_key, grad_value = piece_grads(self.piece)

        def grad_turn(index, carry):
            moving, acc_query, acc_key, acc_value = carry
            moving = passed_along(moving, "context", 1)
            acc_key, acc_value = pass_grads(acc_key, acc_value)
            part_query, part_key, part_value = piece_grads(moving)
            return (moving, acc_query + part_query, acc_key + part_key, acc_value + part_value)

        carried = lax.fori_loop(
            0,
            lax.axis_size("context") - 1,
            grad_turn,
            (self.piece, grad_query, grad_key, grad_value),
        )
        grad_query = carried[1]
        grad_key, grad_value = pass_grads(carried[2], carried[3])
        grad_qin = rotate_back(grad_query, self.cosine, self.sine).astype(bf16)
        grad_kin = rotate_back(grad_key.reshape(rows, heads, HD), self.cosine, self.sine).astype(bf16)
        grad_vin = grad_value.astype(bf16).reshape(rows, heads, HD)
        return grad_qin, grad_kin, grad_vin, early


class HeadAttention:
    BLOCK = 1024

    def __init__(self, query, key_heads, value_heads, segment, position, cosine, sine):
        ways = lax.axis_size("context")
        rows, heads = query.shape[0], query.shape[1]
        self.ways = ways
        self.rows = rows
        self.heads = heads
        self.group = heads // ways
        self.piece = rows // 2
        stacked = jnp.stack([query, key_heads, value_heads], axis=1)
        stacked = stacked.reshape(rows, 3, ways, self.group, HD)
        stacked = lax.all_to_all(stacked, "context", 2, 0, tiled=True)
        stacked = stacked.reshape(rows * ways, 3, self.group, HD)
        tags = jnp.stack([segment, position], axis=0)[None]
        tags = jnp.broadcast_to(tags, (ways, 2, rows))
        tags = lax.all_to_all(tags, "context", 0, 0, tiled=True)
        tags = jnp.transpose(tags, (1, 0, 2)).reshape(2, rows * ways)
        pieces = 2 * ways
        piece_of_slot = tags[1].reshape(pieces, self.piece)[:, 0] // self.piece
        slots = jnp.arange(pieces, dtype=jnp.int32)
        slot_of_piece = jnp.sum(
            jnp.where(piece_of_slot[None, :] == slots[:, None], slots[None, :], 0), axis=1
        )
        self.piece_of_slot = piece_of_slot
        self.slot_of_piece = slot_of_piece
        stacked = self._reorder(stacked, slot_of_piece)
        tags = self._reorder(tags.T, slot_of_piece).T
        self.query = stacked[:, 0]
        self.keys = stacked[:, 1]
        self.values = stacked[:, 2]
        self.seg_all = tags[0]
        self.pos_all = tags[1]
        self.cos_all, self.sin_all = rope_tables(self.pos_all)

    def _reorder(self, value, source):
        parts = [
            lax.dynamic_slice_in_dim(value, source[index] * self.piece, self.piece, axis=0)
            for index in range(source.shape[0])
        ]
        return jnp.concatenate(parts, axis=0)

    def _blocks(self):
        total = self.rows * self.ways
        block = min(self.BLOCK, total)
        return [(start, block) for start in range(0, total, block)]

    def _scores(self, start, size):
        reach = start + size
        query = self.query[start:reach]
        seg_q = self.seg_all[start:reach]
        pos_q = self.pos_all[start:reach]
        scores = jnp.einsum(
            "qhd,khd->hqk", query, self.keys[:reach], preferred_element_type=jnp.float32
        ) * (1.0 / math.sqrt(HD))
        allowed = (seg_q[:, None] == self.seg_all[None, :reach]) & (
            self.pos_all[None, :reach] <= pos_q[:, None]
        )
        return query, jnp.where(allowed[None], scores, NEG), allowed

    def forward(self):
        outs = []
        logs = []
        for start, size in self._blocks():
            reach = start + size
            _, scores, allowed = self._scores(start, size)
            peak = jnp.max(scores, axis=-1)
            weights = jnp.where(allowed[None], jnp.exp(scores - peak[..., None]), 0.0)
            total = jnp.sum(weights, axis=-1)
            mixed = jnp.einsum(
                "hqk,khd->qhd",
                weights.astype(jnp.bfloat16),
                self.values[:reach],
                preferred_element_type=jnp.float32,
            )
            outs.append((mixed / total.T[:, :, None]).astype(jnp.bfloat16))
            logs.append(peak + jnp.log(total))
        self.attended = jnp.concatenate(outs, axis=0)
        self.log_total = jnp.concatenate(logs, axis=1)
        back = self._reorder(self.attended, self.piece_of_slot)
        back = back.reshape(self.rows * self.ways, 1, self.group, HD)
        back = lax.all_to_all(back, "context", 0, 1, tiled=True)
        return back.reshape(self.rows, self.heads, HD)

    def backward(self, grad_heads, early):
        f32 = jnp.float32
        bf16 = jnp.bfloat16
        scale = 1.0 / math.sqrt(HD)
        grad = grad_heads.reshape(self.rows, self.ways, self.group, HD)
        grad = lax.all_to_all(grad, "context", 1, 0, tiled=True)
        grad, early = lax.optimization_barrier((grad, early))
        grad = grad.reshape(self.rows * self.ways, self.group, HD)
        grad = self._reorder(grad, self.slot_of_piece)
        inner = jnp.sum(grad.astype(f32) * self.attended.astype(f32), axis=-1).T
        total_rows = self.rows * self.ways
        grad_key = jnp.zeros(self.keys.shape, f32)
        grad_value = jnp.zeros(self.values.shape, f32)
        grad_queries = []
        for start, size in self._blocks():
            reach = start + size
            query, scores, allowed = self._scores(start, size)
            log_block = self.log_total[:, start:reach]
            inner_block = inner[:, start:reach]
            grad_block = grad[start:reach]
            probs = jnp.where(allowed[None], jnp.exp(scores - log_block[..., None]), 0.0)
            part_value = jnp.einsum(
                "hqk,qhd->khd", probs.astype(bf16), grad_block, preferred_element_type=f32
            )
            grad_probs = jnp.einsum(
                "qhd,khd->hqk", grad_block, self.values[:reach], preferred_element_type=f32
            )
            grad_scores = (probs * (grad_probs - inner_block[..., None]) * scale).astype(bf16)
            grad_queries.append(
                jnp.einsum(
                    "hqk,khd->qhd", grad_scores, self.keys[:reach], preferred_element_type=f32
                )
            )
            part_key = jnp.einsum("hqk,qhd->khd", grad_scores, query, preferred_element_type=f32)
            pad = ((0, total_rows - reach), (0, 0), (0, 0))
            grad_value = grad_value + jnp.pad(part_value, pad)
            grad_key = grad_key + jnp.pad(part_key, pad)
        grad_query = jnp.concatenate(grad_queries, axis=0)
        grad_qin = rotate_back(grad_query, self.cos_all, self.sin_all).astype(bf16)
        grad_kin = rotate_back(grad_key, self.cos_all, self.sin_all).astype(bf16)
        grad_vin = grad_value.astype(bf16)
        returned = []
        for grad_in in (grad_qin, grad_kin, grad_vin):
            grad_in = self._reorder(grad_in, self.piece_of_slot)
            grad_in = grad_in.reshape(self.rows * self.ways, 1, self.group, HD)
            grad_in = lax.all_to_all(grad_in, "context", 0, 1, tiled=True)
            returned.append(grad_in.reshape(self.rows, self.heads, HD))
        return returned[0], returned[1], returned[2], early


def mlp_chunks(hidden_cols):
    for count in (2, 1):
        if hidden_cols % (count * 128) == 0:
            return count
    return 1


def on_device(
    inputs, segments, positions, w_q, w_k, w_v, w_o, w_gate, w_up, w_down, g_attn, g_mlp, d_out
):
    f32 = jnp.float32
    bf16 = jnp.bfloat16
    rows = inputs.shape[1]
    width = inputs.shape[2]
    cols = w_q.shape[1]
    hidden_cols = w_gate.shape[1]
    tokens = inputs.reshape(rows, width)
    segment = segments.reshape(rows)
    position = positions.reshape(rows)
    full_qkvo = lax.all_gather(
        jnp.concatenate([w_q, w_k, w_v, w_o], axis=1), ROWS, axis=0, tiled=True
    )
    full_qkv = full_qkvo[:, : 3 * cols]
    full_o = full_qkvo[:, 3 * cols :]
    gains = lax.all_gather(
        jnp.concatenate([g_attn, g_mlp])[None], ROWS, axis=0, tiled=True
    )
    gain_attn = gains[:, : g_attn.shape[0]].reshape(width)
    gain_mlp = gains[:, g_attn.shape[0] :].reshape(width)
    count = mlp_chunks(hidden_cols)
    step = hidden_cols // count
    fetched = []
    for index in range(count):
        part = slice(index * step, (index + 1) * step)
        pair = lax.all_gather(
            jnp.concatenate([w_gate[:, part], w_up[:, part]], axis=1), ROWS, axis=0, tiled=True
        )
        fetched.append(
            (pair[:, :step], pair[:, step:], lax.all_gather(w_down[:, part], ROWS, axis=0, tiled=True))
        )
    heads = cols // HD
    cosine, sine = rope_tables(position)
    resid1 = tokens.astype(f32)
    norm1, inv1 = normalize(resid1)
    h1 = (norm1 * gain_attn.astype(f32)).astype(bf16)
    projected = jnp.dot(h1, full_qkv, preferred_element_type=f32)
    query = rotate(projected[:, :cols].reshape(rows, heads, HD), cosine, sine).astype(bf16)
    key_heads = rotate(projected[:, cols : 2 * cols].reshape(rows, heads, HD), cosine, sine).astype(
        bf16
    )
    value_heads = projected[:, 2 * cols :].astype(bf16).reshape(rows, heads, HD)
    if heads % lax.axis_size("context") == 0:
        attention = HeadAttention(query, key_heads, value_heads, segment, position, cosine, sine)
    else:
        attention = RingAttention(
            query,
            key_heads.reshape(rows, cols),
            value_heads.reshape(rows, cols),
            segment,
            position,
            cosine,
            sine,
        )
    attended = attention.forward()
    attended_flat = attended.reshape(rows, cols)
    resid2 = resid1 + tensor_total(contract_last(attended_flat, full_o))
    norm2, inv2 = normalize(resid2)
    h2_part = (norm2 * gain_mlp.astype(f32)).astype(bf16)
    grad_y = d_out.reshape(rows, width)
    mlp_partial = None
    h2_grad_partial = None
    staged = []
    for full_gate, full_up, full_down in fetched:
        if staged:
            full_gate, staged[-1] = lax.optimization_barrier((full_gate, staged[-1]))
        gate = jnp.dot(h2_part, full_gate, preferred_element_type=f32)
        up = jnp.dot(h2_part, full_up, preferred_element_type=f32)
        active = jax.nn.silu(gate)
        hidden = (active * up).astype(bf16)
        out_part = contract_last(hidden, full_down)
        mlp_partial = out_part if mlp_partial is None else mlp_partial + out_part
        grad_hidden = jnp.dot(grad_y, full_down, preferred_element_type=f32)
        sigma = jax.nn.sigmoid(gate)
        grad_gate = (grad_hidden * up * sigma * (1.0 + gate * (1.0 - sigma))).astype(bf16)
        grad_up = (grad_hidden * active).astype(bf16)
        back_part = contract_last(grad_gate, full_gate) + contract_last(grad_up, full_up)
        pending = (
            contract_first(h2_part, grad_gate),
            contract_first(h2_part, grad_up),
            contract_first(grad_y, hidden),
        )
        h2_grad_partial = back_part if h2_grad_partial is None else h2_grad_partial + back_part
        staged.append(chip_total(jnp.concatenate(pending, axis=1)))
    grad_h2 = tensor_total(h2_grad_partial)
    grad_h2, staged[-1] = lax.optimization_barrier((grad_h2, staged[-1]))
    reduced = [line_total(chunk) for chunk in staged]
    result = (resid2 + tensor_total(mlp_partial)).astype(bf16)
    grad_gmlp = jnp.sum(grad_h2 * norm2, axis=0)
    grad_resid = grad_y.astype(f32) + norm_back(grad_h2, norm2, inv2, gain_mlp)
    grad_resid_part = grad_resid.astype(bf16)
    grad_heads = (
        jnp.dot(grad_resid_part, full_o, preferred_element_type=f32)
        .astype(bf16)
        .reshape(rows, heads, HD)
    )
    grad_heads, partial_o = lax.optimization_barrier(
        (grad_heads, contract_first(grad_resid_part, attended_flat))
    )
    early = (chip_total(partial_o), reduced[:-1])
    grad_qin, grad_kin, grad_vin, early = attention.backward(grad_heads, early)
    staged_o, reduced[:-1] = early
    reduced_o = line_total(staged_o)
    grad_qkv = jnp.concatenate(
        [grad_qin.reshape(rows, cols), grad_kin.reshape(rows, cols), grad_vin.reshape(rows, cols)],
        axis=1,
    )
    h1_grad_partial = contract_last(grad_qkv, full_qkv)
    first_tensor = (lax.axis_index("tensor") == 0).astype(f32)
    gain_parts = jnp.stack(
        [jnp.sum(h1_grad_partial * norm1, axis=0), grad_gmlp * first_tensor], axis=1
    )
    gains_total = exact_total(gain_parts)
    h1_grad_partial, staged_qkv = lax.optimization_barrier(
        (h1_grad_partial, chip_total(contract_first(h1, grad_qkv)))
    )
    grad_h1 = tensor_total(h1_grad_partial)
    grad_h1, reduced_o, reduced[-1], result = lax.optimization_barrier(
        (grad_h1, reduced_o, reduced[-1], result)
    )
    grad_x_part = (grad_resid + norm_back(grad_h1, norm1, inv1, gain_attn)).astype(bf16)
    reduced_qkv = line_total(staged_qkv)
    blocks = lax.axis_size("shard") * lax.axis_size("context")
    block = lax.axis_index("shard") * lax.axis_size("context") + lax.axis_index("context")
    piece = width // blocks
    reduced_gains = lax.dynamic_slice_in_dim(gains_total, block * piece, piece, axis=0)
    reduced_gate, reduced_up, reduced_down = (
        jnp.concatenate([chunk[:, which * step : (which + 1) * step] for chunk in reduced], axis=1)
        for which in range(3)
    )
    return (
        result.reshape(1, rows, width),
        grad_x_part.reshape(1, rows, width),
        reduced_qkv[:, :cols],
        reduced_qkv[:, cols : 2 * cols],
        reduced_qkv[:, 2 * cols :],
        reduced_o,
        reduced_gate,
        reduced_up,
        reduced_down,
        reduced_gains[:, 0],
        reduced_gains[:, 1],
    )


def solution(mesh):
    placed = (
        P("shard", "context", None),
        P("shard", "context"),
        P("shard", "context"),
        P(ROWS, "tensor"),
        P(ROWS, "tensor"),
        P(ROWS, "tensor"),
        P(ROWS, "tensor"),
        P(ROWS, "tensor"),
        P(ROWS, "tensor"),
        P(ROWS, "tensor"),
        P(ROWS),
        P(ROWS),
        P("shard", "context", None),
    )
    return jax.shard_map(
        on_device,
        mesh=mesh,
        in_specs=placed,
        out_specs=(
            P("shard", "context", None),
            P("shard", "context", None),
            P(ROWS, "tensor"),
            P(ROWS, "tensor"),
            P(ROWS, "tensor"),
            P(ROWS, "tensor"),
            P(ROWS, "tensor"),
            P(ROWS, "tensor"),
            P(ROWS, "tensor"),
            P(ROWS),
            P(ROWS),
        ),
        check_vma=False,
    )
```

```python
import math

import jax
import jax.numpy as jnp
from jax import lax
from jax.sharding import PartitionSpec as P

HD = 64


EPS = 1e-05
THETA = 130000.0
NEG = -1e30
ROWS = ("shard", "context")


def passed_along(value, axis, steps):
    count = lax.axis_size(axis)
    pairs = [(source, (source + steps) % count) for source in range(count)]
    return lax.ppermute(value, axis, pairs)


def rope_tables(position):
    index = jnp.arange(HD // 2, dtype=jnp.float32)
    inverse = jnp.power(jnp.float32(THETA), -2.0 * index / HD)
    angle = position.astype(jnp.float32)[:, None] * inverse[None, :]
    return (jnp.cos(angle), jnp.sin(angle))


def rotate(tensor, cosine, sine):
    half = tensor.shape[-1] // 2
    first = tensor[..., :half]
    second = tensor[..., half:]
    cosine = cosine[:, None, :]
    sine = sine[:, None, :]
    return jnp.concatenate(
        [first * cosine - second * sine, second * cosine + first * sine], axis=-1
    )


def rotate_back(grad, cosine, sine):
    half = grad.shape[-1] // 2
    first = grad[..., :half]
    second = grad[..., half:]
    cosine = cosine[:, None, :]
    sine = sine[:, None, :]
    return jnp.concatenate(
        [first * cosine + second * sine, second * cosine - first * sine], axis=-1
    )


def normalize(value):
    inv_rms = lax.rsqrt(jnp.mean(value * value, axis=-1, keepdims=True) + EPS)
    return (value * inv_rms, inv_rms)


def norm_back(grad, normed, inv_rms, gain):
    scaled = grad * gain.astype(jnp.float32)
    return inv_rms * (scaled - normed * jnp.mean(scaled * normed, axis=-1, keepdims=True))


def contract_last(left, right):
    return lax.dot_general(
        left, right, (((1,), (1,)), ((), ())), preferred_element_type=jnp.float32
    )


def contract_first(left, right):
    return lax.dot_general(
        left, right, (((0,), (0,)), ((), ())), preferred_element_type=jnp.float32
    )


def half_of(value, bit):
    size = value.shape[0] // 2
    return lax.dynamic_slice_in_dim(value, bit * size, size, axis=0)


def joined(mine, other, bit):
    low = jnp.where(bit == 0, mine, other)
    high = jnp.where(bit == 0, other, mine)
    return jnp.concatenate([low, high], axis=0)


def tensor_total(partial_sum):
    count = lax.axis_size("tensor")
    rows = partial_sum.shape[0]
    if count != 4 or rows % 8:
        return lax.psum(partial_sum.astype(jnp.bfloat16), "tensor").astype(jnp.float32)
    f32 = jnp.float32
    bf16 = jnp.bfloat16
    index = lax.axis_index("tensor")
    x_bit = index % 2
    y_bit = index // 2
    x_pairs = [(i, i ^ 1) for i in range(4)]
    y_pairs = [(i, i ^ 2) for i in range(4)]

    def swap(value, pairs):
        return lax.ppermute(value.astype(bf16), "tensor", pairs).astype(f32)

    first = partial_sum[: rows // 2]
    second = partial_sum[rows // 2 :]
    first = half_of(first, x_bit) + swap(half_of(first, 1 - x_bit), x_pairs)
    second = half_of(second, y_bit) + swap(half_of(second, 1 - y_bit), y_pairs)
    first = half_of(first, y_bit) + swap(half_of(first, 1 - y_bit), y_pairs)
    second = half_of(second, x_bit) + swap(half_of(second, 1 - x_bit), x_pairs)
    first = first.astype(bf16)
    second = second.astype(bf16)
    first = joined(first, lax.ppermute(first, "tensor", y_pairs), y_bit)
    second = joined(second, lax.ppermute(second, "tensor", x_pairs), x_bit)
    first = joined(first, lax.ppermute(first, "tensor", x_pairs), x_bit)
    second = joined(second, lax.ppermute(second, "tensor", y_pairs), y_bit)
    return jnp.concatenate([first, second], axis=0).astype(f32)


def tensor_exact_total(value):
    if lax.axis_size("tensor") != 4:
        return lax.psum(value, "tensor")
    value = value + lax.ppermute(value, "tensor", [(i, i ^ 1) for i in range(4)])
    return value + lax.ppermute(value, "tensor", [(i, i ^ 2) for i in range(4)])


def exact_total(value):
    for axis in ("tensor", "shard", "context"):
        count = lax.axis_size(axis)
        if count & (count - 1):
            value = lax.psum(value, axis)
            continue
        span = 1
        while span < count:
            value = value + lax.ppermute(value, axis, [(i, i ^ span) for i in range(count)])
            span *= 2
    return value


def chip_total(grad):
    f32 = jnp.float32
    shard = lax.axis_index("shard")
    mine = half_of(grad, shard)
    other = half_of(grad, 1 - shard)
    got = lax.ppermute(other.astype(jnp.bfloat16), "shard", [(0, 1), (1, 0)])
    return mine.astype(f32) + got.astype(f32)


def line_total(staged):
    return lax.psum_scatter(
        staged.astype(jnp.bfloat16), "context", scatter_dimension=0, tiled=True
    ).astype(jnp.float32)


def rows_total(grad):
    return line_total(chip_total(grad))


def pass_grads(grad_key, grad_value):
    return (
        passed_along(grad_key.astype(jnp.bfloat16), "context", 1).astype(grad_key.dtype),
        passed_along(grad_value.astype(jnp.bfloat16), "context", 1).astype(grad_value.dtype),
    )


def key_scores(query_heads, query_seg, query_pos, piece):
    key_flat, value_flat, key_seg, key_pos = piece
    heads = query_heads.shape[1]
    key_heads = key_flat.reshape(key_flat.shape[0], heads, HD)
    value_heads = value_flat.reshape(value_flat.shape[0], heads, HD)
    scores = jnp.einsum(
        "qhd,khd->hqk", query_heads, key_heads, preferred_element_type=jnp.float32
    ) * (1.0 / math.sqrt(HD))
    allowed = (query_seg[:, None] == key_seg[None, :]) & (key_pos[None, :] <= query_pos[:, None])
    return (jnp.where(allowed[None], scores, NEG), allowed, key_heads, value_heads)


def forward_fold(stats, piece, query_heads, query_seg, query_pos):
    peak, total, accum = stats
    scores, allowed, key_heads, value_heads = key_scores(query_heads, query_seg, query_pos, piece)
    new_peak = jnp.maximum(peak, jnp.max(scores, axis=-1))
    weights = jnp.where(allowed[None], jnp.exp(scores - new_peak[..., None]), 0.0)
    factor = jnp.exp(peak - new_peak)
    total = total * factor + jnp.sum(weights, axis=-1)
    accum = accum * factor[..., None] + jnp.einsum(
        "hqk,khd->hqd",
        weights.astype(jnp.bfloat16),
        value_heads,
        preferred_element_type=jnp.float32,
    )
    return (new_peak, total, accum)


def backward_piece(piece, query_heads, grad_heads, log_total, inner, query_seg, query_pos):
    scores, allowed, key_heads, value_heads = key_scores(query_heads, query_seg, query_pos, piece)
    probs = jnp.where(allowed[None], jnp.exp(scores - log_total[..., None]), 0.0)
    grad_value = jnp.einsum(
        "hqk,qhd->khd", probs.astype(jnp.bfloat16), grad_heads, preferred_element_type=jnp.float32
    )
    grad_probs = jnp.einsum(
        "qhd,khd->hqk", grad_heads, value_heads, preferred_element_type=jnp.float32
    )
    grad_scores = (probs * (grad_probs - inner[..., None]) * (1.0 / math.sqrt(HD))).astype(
        jnp.bfloat16
    )
    grad_query = jnp.einsum(
        "hqk,khd->qhd", grad_scores, key_heads, preferred_element_type=jnp.float32
    )
    grad_key = jnp.einsum(
        "hqk,qhd->khd", grad_scores, query_heads, preferred_element_type=jnp.float32
    )
    key_rows = grad_key.shape[0]
    return (grad_query, grad_key.reshape(key_rows, -1), grad_value.reshape(key_rows, -1))


class RingAttention:
    def __init__(self, query, key_flat, value_flat, segment, position, cosine, sine):
        self.query = query
        self.piece = (key_flat, value_flat, segment, position)
        self.segment = segment
        self.position = position
        self.cosine = cosine
        self.sine = sine

    def forward(self):
        f32 = jnp.float32
        query, segment, position = self.query, self.segment, self.position
        rows, heads = query.shape[0], query.shape[1]
        start_stats = (
            jnp.full((heads, rows), NEG, f32),
            jnp.zeros((heads, rows), f32),
            jnp.zeros((heads, rows, HD), f32),
        )
        stats = forward_fold(start_stats, self.piece, query, segment, position)

        def cycle_turn(index, carry):
            moving, current = carry
            moving = passed_along(moving, "context", 1)
            current = forward_fold(current, moving, query, segment, position)
            return (moving, current)

        peak, total, accum = lax.fori_loop(
            0, lax.axis_size("context") - 1, cycle_turn, (self.piece, stats)
        )[1]
        self.attended = jnp.transpose(accum / total[..., None], (1, 0, 2)).astype(jnp.bfloat16)
        self.log_total = peak + jnp.log(total)
        return self.attended

    def backward(self, grad_heads, early):
        bf16 = jnp.bfloat16
        query, segment, position = self.query, self.segment, self.position
        rows, heads = query.shape[0], query.shape[1]
        inner = jnp.sum(grad_heads.astype(jnp.float32) * self.attended.astype(jnp.float32), axis=-1).T

        def piece_grads(piece):
            return backward_piece(piece, query, grad_heads, self.log_total, inner, segment, position)

        grad_query, grad_key, grad_value = piece_grads(self.piece)

        def grad_turn(index, carry):
            moving, acc_query, acc_key, acc_value = carry
            moving = passed_along(moving, "context", 1)
            acc_key, acc_value = pass_grads(acc_key, acc_value)
            part_query, part_key, part_value = piece_grads(moving)
            return (moving, acc_query + part_query, acc_key + part_key, acc_value + part_value)

        carried = lax.fori_loop(
            0,
            lax.axis_size("context") - 1,
            grad_turn,
            (self.piece, grad_query, grad_key, grad_value),
        )
        grad_query = carried[1]
        grad_key, grad_value = pass_grads(carried[2], carried[3])
        grad_qin = rotate_back(grad_query, self.cosine, self.sine).astype(bf16)
        grad_kin = rotate_back(grad_key.reshape(rows, heads, HD), self.cosine, self.sine).astype(bf16)
        grad_vin = grad_value.astype(bf16).reshape(rows, heads, HD)
        return grad_qin, grad_kin, grad_vin, early


class HeadAttention:
    BLOCK = 512

    def __init__(self, query, key_heads, value_heads, segment, position, cosine, sine):
        ways = lax.axis_size("context")
        rows, heads = query.shape[0], query.shape[1]
        self.ways = ways
        self.rows = rows
        self.heads = heads
        self.group = heads // ways
        self.piece = rows // 2
        stacked = jnp.stack([query, key_heads, value_heads], axis=1)
        stacked = stacked.reshape(rows, 3, ways, self.group, HD)
        stacked = lax.all_to_all(stacked, "context", 2, 0, tiled=True)
        stacked = stacked.reshape(rows * ways, 3, self.group, HD)
        tags = jnp.stack([segment, position], axis=0)[None]
        tags = jnp.broadcast_to(tags, (ways, 2, rows))
        tags = lax.all_to_all(tags, "context", 0, 0, tiled=True)
        tags = jnp.transpose(tags, (1, 0, 2)).reshape(2, rows * ways)
        pieces = 2 * ways
        piece_of_slot = tags[1].reshape(pieces, self.piece)[:, 0] // self.piece
        slots = jnp.arange(pieces, dtype=jnp.int32)
        slot_of_piece = jnp.sum(
            jnp.where(piece_of_slot[None, :] == slots[:, None], slots[None, :], 0), axis=1
        )
        self.piece_of_slot = piece_of_slot
        self.slot_of_piece = slot_of_piece
        stacked = self._reorder(stacked, slot_of_piece)
        tags = self._reorder(tags.T, slot_of_piece).T
        self.query = stacked[:, 0]
        self.keys = stacked[:, 1]
        self.values = stacked[:, 2]
        self.seg_all = tags[0]
        self.pos_all = tags[1]
        self.cos_all, self.sin_all = rope_tables(self.pos_all)

    def _reorder(self, value, source):
        parts = [
            lax.dynamic_slice_in_dim(value, source[index] * self.piece, self.piece, axis=0)
            for index in range(source.shape[0])
        ]
        return jnp.concatenate(parts, axis=0)

    def _blocks(self):
        total = self.rows * self.ways
        block = min(self.BLOCK, total)
        return [(start, block) for start in range(0, total, block)]

    def _scores(self, start, size):
        reach = start + size
        query = self.query[start:reach]
        seg_q = self.seg_all[start:reach]
        pos_q = self.pos_all[start:reach]
        scores = jnp.einsum(
            "qhd,khd->hqk", query, self.keys[:reach], preferred_element_type=jnp.float32
        ) * (1.0 / math.sqrt(HD))
        allowed = (seg_q[:, None] == self.seg_all[None, :reach]) & (
            self.pos_all[None, :reach] <= pos_q[:, None]
        )
        return query, jnp.where(allowed[None], scores, NEG), allowed

    def forward(self):
        outs = []
        logs = []
        for start, size in self._blocks():
            reach = start + size
            _, scores, allowed = self._scores(start, size)
            peak = jnp.max(scores, axis=-1)
            weights = jnp.where(allowed[None], jnp.exp(scores - peak[..., None]), 0.0)
            total = jnp.sum(weights, axis=-1)
            mixed = jnp.einsum(
                "hqk,khd->qhd",
                weights.astype(jnp.bfloat16),
                self.values[:reach],
                preferred_element_type=jnp.float32,
            )
            outs.append((mixed / total.T[:, :, None]).astype(jnp.bfloat16))
            logs.append(peak + jnp.log(total))
        self.attended = jnp.concatenate(outs, axis=0)
        self.log_total = jnp.concatenate(logs, axis=1)
        back = self._reorder(self.attended, self.piece_of_slot)
        back = back.reshape(self.rows * self.ways, 1, self.group, HD)
        back = lax.all_to_all(back, "context", 0, 1, tiled=True)
        return back.reshape(self.rows, self.heads, HD)

    def backward(self, grad_heads, early):
        f32 = jnp.float32
        bf16 = jnp.bfloat16
        scale = 1.0 / math.sqrt(HD)
        grad = grad_heads.reshape(self.rows, self.ways, self.group, HD)
        grad = lax.all_to_all(grad, "context", 1, 0, tiled=True)
        grad, early = lax.optimization_barrier((grad, early))
        grad = grad.reshape(self.rows * self.ways, self.group, HD)
        grad = self._reorder(grad, self.slot_of_piece)
        inner = jnp.sum(grad.astype(f32) * self.attended.astype(f32), axis=-1).T
        total_rows = self.rows * self.ways
        grad_key = jnp.zeros(self.keys.shape, f32)
        grad_value = jnp.zeros(self.values.shape, f32)
        grad_queries = []
        for start, size in self._blocks():
            reach = start + size
            query, scores, allowed = self._scores(start, size)
            log_block = self.log_total[:, start:reach]
            inner_block = inner[:, start:reach]
            grad_block = grad[start:reach]
            probs = jnp.where(allowed[None], jnp.exp(scores - log_block[..., None]), 0.0)
            part_value = jnp.einsum(
                "hqk,qhd->khd", probs.astype(bf16), grad_block, preferred_element_type=f32
            )
            grad_probs = jnp.einsum(
                "qhd,khd->hqk", grad_block, self.values[:reach], preferred_element_type=f32
            )
            grad_scores = (probs * (grad_probs - inner_block[..., None]) * scale).astype(bf16)
            grad_queries.append(
                jnp.einsum(
                    "hqk,khd->qhd", grad_scores, self.keys[:reach], preferred_element_type=f32
                )
            )
            part_key = jnp.einsum("hqk,qhd->khd", grad_scores, query, preferred_element_type=f32)
            pad = ((0, total_rows - reach), (0, 0), (0, 0))
            grad_value = grad_value + jnp.pad(part_value, pad)
            grad_key = grad_key + jnp.pad(part_key, pad)
        grad_query = jnp.concatenate(grad_queries, axis=0)
        grad_qin = rotate_back(grad_query, self.cos_all, self.sin_all).astype(bf16)
        grad_kin = rotate_back(grad_key, self.cos_all, self.sin_all).astype(bf16)
        grad_vin = grad_value.astype(bf16)
        returned = []
        for grad_in in (grad_qin, grad_kin, grad_vin):
            grad_in = self._reorder(grad_in, self.piece_of_slot)
            grad_in = grad_in.reshape(self.rows * self.ways, 1, self.group, HD)
            grad_in = lax.all_to_all(grad_in, "context", 0, 1, tiled=True)
            returned.append(grad_in.reshape(self.rows, self.heads, HD))
        return returned[0], returned[1], returned[2], early


def mlp_chunks(hidden_cols):
    for count in (2, 1):
        if hidden_cols % (count * 128) == 0:
            return count
    return 1


def on_device(
    inputs, segments, positions, w_q, w_k, w_v, w_o, w_gate, w_up, w_down, g_attn, g_mlp, d_out
):
    f32 = jnp.float32
    bf16 = jnp.bfloat16
    rows = inputs.shape[1]
    width = inputs.shape[2]
    cols = w_q.shape[1]
    hidden_cols = w_gate.shape[1]
    tokens = inputs.reshape(rows, width)
    segment = segments.reshape(rows)
    position = positions.reshape(rows)
    full_qkvo = lax.all_gather(
        jnp.concatenate([w_q, w_k, w_v, w_o], axis=1), ROWS, axis=0, tiled=True
    )
    full_qkv = full_qkvo[:, : 3 * cols]
    full_o = full_qkvo[:, 3 * cols :]
    gains = lax.all_gather(
        jnp.concatenate([g_attn, g_mlp])[None], ROWS, axis=0, tiled=True
    )
    gain_attn = gains[:, : g_attn.shape[0]].reshape(width)
    gain_mlp = gains[:, g_attn.shape[0] :].reshape(width)
    count = mlp_chunks(hidden_cols)
    step = hidden_cols // count
    fetched = []
    for index in range(count):
        part = slice(index * step, (index + 1) * step)
        pair = lax.all_gather(
            jnp.concatenate([w_gate[:, part], w_up[:, part]], axis=1), ROWS, axis=0, tiled=True
        )
        fetched.append(
            (pair[:, :step], pair[:, step:], lax.all_gather(w_down[:, part], ROWS, axis=0, tiled=True))
        )
    heads = cols // HD
    cosine, sine = rope_tables(position)
    resid1 = tokens.astype(f32)
    norm1, inv1 = normalize(resid1)
    h1 = (norm1 * gain_attn.astype(f32)).astype(bf16)
    projected = jnp.dot(h1, full_qkv, preferred_element_type=f32)
    query = rotate(projected[:, :cols].reshape(rows, heads, HD), cosine, sine).astype(bf16)
    key_heads = rotate(projected[:, cols : 2 * cols].reshape(rows, heads, HD), cosine, sine).astype(
        bf16
    )
    value_heads = projected[:, 2 * cols :].astype(bf16).reshape(rows, heads, HD)
    if heads % lax.axis_size("context") == 0:
        attention = HeadAttention(query, key_heads, value_heads, segment, position, cosine, sine)
    else:
        attention = RingAttention(
            query,
            key_heads.reshape(rows, cols),
            value_heads.reshape(rows, cols),
            segment,
            position,
            cosine,
            sine,
        )
    attended = attention.forward()
    attended_flat = attended.reshape(rows, cols)
    resid2 = resid1 + tensor_total(contract_last(attended_flat, full_o))
    norm2, inv2 = normalize(resid2)
    h2_part = (norm2 * gain_mlp.astype(f32)).astype(bf16)
    grad_y = d_out.reshape(rows, width)
    mlp_partial = None
    h2_grad_partial = None
    staged = []
    for full_gate, full_up, full_down in fetched:
        if staged:
            full_gate, staged[-1] = lax.optimization_barrier((full_gate, staged[-1]))
        gate = jnp.dot(h2_part, full_gate, preferred_element_type=f32)
        up = jnp.dot(h2_part, full_up, preferred_element_type=f32)
        active = jax.nn.silu(gate)
        hidden = (active * up).astype(bf16)
        out_part = contract_last(hidden, full_down)
        mlp_partial = out_part if mlp_partial is None else mlp_partial + out_part
        grad_hidden = jnp.dot(grad_y, full_down, preferred_element_type=f32)
        sigma = jax.nn.sigmoid(gate)
        grad_gate = (grad_hidden * up * sigma * (1.0 + gate * (1.0 - sigma))).astype(bf16)
        grad_up = (grad_hidden * active).astype(bf16)
        back_part = contract_last(grad_gate, full_gate) + contract_last(grad_up, full_up)
        pending = (
            contract_first(h2_part, grad_gate),
            contract_first(h2_part, grad_up),
            contract_first(grad_y, hidden),
        )
        h2_grad_partial = back_part if h2_grad_partial is None else h2_grad_partial + back_part
        staged.append(chip_total(jnp.concatenate(pending, axis=1)))
    grad_h2 = tensor_total(h2_grad_partial)
    grad_h2, staged[-1] = lax.optimization_barrier((grad_h2, staged[-1]))
    reduced = [line_total(chunk) for chunk in staged]
    result = (resid2 + tensor_total(mlp_partial)).astype(bf16)
    grad_gmlp = jnp.sum(grad_h2 * norm2, axis=0)
    grad_resid = grad_y.astype(f32) + norm_back(grad_h2, norm2, inv2, gain_mlp)
    grad_resid_part = grad_resid.astype(bf16)
    grad_heads = (
        jnp.dot(grad_resid_part, full_o, preferred_element_type=f32)
        .astype(bf16)
        .reshape(rows, heads, HD)
    )
    grad_heads, partial_o = lax.optimization_barrier(
        (grad_heads, contract_first(grad_resid_part, attended_flat))
    )
    early = (chip_total(partial_o), reduced[:-1])
    grad_qin, grad_kin, grad_vin, early = attention.backward(grad_heads, early)
    staged_o, reduced[:-1] = early
    reduced_o = line_total(staged_o)
    grad_qkv = jnp.concatenate(
        [grad_qin.reshape(rows, cols), grad_kin.reshape(rows, cols), grad_vin.reshape(rows, cols)],
        axis=1,
    )
    h1_grad_partial = contract_last(grad_qkv, full_qkv)
    first_tensor = (lax.axis_index("tensor") == 0).astype(f32)
    gain_parts = jnp.stack(
        [jnp.sum(h1_grad_partial * norm1, axis=0), grad_gmlp * first_tensor], axis=1
    )
    gains_total = exact_total(gain_parts)
    h1_grad_partial, staged_qkv = lax.optimization_barrier(
        (h1_grad_partial, chip_total(contract_first(h1, grad_qkv)))
    )
    grad_h1 = tensor_total(h1_grad_partial)
    grad_h1, reduced_o, reduced[-1], result, gains_total = lax.optimization_barrier(
        (grad_h1, reduced_o, reduced[-1], result, gains_total)
    )
    grad_x_part = (grad_resid + norm_back(grad_h1, norm1, inv1, gain_attn)).astype(bf16)
    reduced_qkv = line_total(staged_qkv)
    blocks = lax.axis_size("shard") * lax.axis_size("context")
    block = lax.axis_index("shard") * lax.axis_size("context") + lax.axis_index("context")
    piece = width // blocks
    reduced_gains = lax.dynamic_slice_in_dim(gains_total, block * piece, piece, axis=0)
    reduced_gate, reduced_up, reduced_down = (
        jnp.concatenate([chunk[:, which * step : (which + 1) * step] for chunk in reduced], axis=1)
        for which in range(3)
    )
    return (
        result.reshape(1, rows, width),
        grad_x_part.reshape(1, rows, width),
        reduced_qkv[:, :cols],
        reduced_qkv[:, cols : 2 * cols],
        reduced_qkv[:, 2 * cols :],
        reduced_o,
        reduced_gate,
        reduced_up,
        reduced_down,
        reduced_gains[:, 0],
        reduced_gains[:, 1],
    )


def solution(mesh):
    placed = (
        P("shard", "context", None),
        P("shard", "context"),
        P("shard", "context"),
        P(ROWS, "tensor"),
        P(ROWS, "tensor"),
        P(ROWS, "tensor"),
        P(ROWS, "tensor"),
        P(ROWS, "tensor"),
        P(ROWS, "tensor"),
        P(ROWS, "tensor"),
        P(ROWS),
        P(ROWS),
        P("shard", "context", None),
    )
    return jax.shard_map(
        on_device,
        mesh=mesh,
        in_specs=placed,
        out_specs=(
            P("shard", "context", None),
            P("shard", "context", None),
            P(ROWS, "tensor"),
            P(ROWS, "tensor"),
            P(ROWS, "tensor"),
            P(ROWS, "tensor"),
            P(ROWS, "tensor"),
            P(ROWS, "tensor"),
            P(ROWS, "tensor"),
            P(ROWS),
            P(ROWS),
        ),
        check_vma=False,
    )
```
